32 devices in a mesh: seq: 8 (over z, y), chan: 4 (over x, core).
Axes of the slice: x: 2, y: 2, z: 4, core: 2. Of those that a mesh axis runs over, the one named last changes fastest.
Arguments:
- query_mr: bfloat16 [1024, 8192], P('seq', 'chan'), may hold values from -6 to 6
- key_mr: bfloat16 [1024, 8192], P('seq', 'chan'), may hold values from -6 to 6
- value_mr: bfloat16 [1024, 8192], P('seq', 'chan'), may hold values from -6 to 6
- query_li: bfloat16 [1024, 8192], P('seq', 'chan'), may hold values from -6 to 6
- key_li: bfloat16 [1024, 8192], P('seq', 'chan'), may hold values from -6 to 6
- cotangent: bfloat16 [1024, 8192], P('seq', 'chan'), may hold values from -40 to 40
- mr_filter: float32 [512, 128], P('chan'), may hold values from -3.535534 to 3.535534
- norm_gain: float32 [8192], P('chan'), may hold values from 0.1 to 1.9
- li_decay: float32 [512, 16], P('chan'), may hold values from 0.00048828125 to 0.03
- li_residue: float32 [512, 16], P('chan'), may hold values from -1 to 1
Outputs:
- out_li: bfloat16 [1024, 8192], P('seq', 'chan')
- grad_query_mr: bfloat16 [1024, 8192], P('seq', 'chan')
- grad_key_mr: bfloat16 [1024, 8192], P('seq', 'chan')
- grad_value_mr: bfloat16 [1024, 8192], P('seq', 'chan')
- grad_query_li: bfloat16 [1024, 8192], P('seq', 'chan')
- grad_key_li: bfloat16 [1024, 8192], P('seq', 'chan')
- grad_gain: float32 [8192], P('chan')
- grad_filter: float32 [512, 128], P('chan')
The draws below stay inside these ranges and needn't reach their ends.
All inputs are finite; a program needn't handle non-finite values.
Results may differ from the reference program's by a relative error of at most 0.025.
Values may be sent and summed in bfloat16 or wider, within the bound.
No kernel may reach another device: no remote copies, remote signals or barrier semaphores. Data moves between devices by JAX's collectives and lax.ppermute only.
A program may use at most 192 MiB of HBM per device.

```python
import math
import jax
import jax.numpy as jnp
from jax import lax

D = 8192
G = 512
MR_TAPS = 128
MODES = 16
TOKENS = 1024


def draw_mr_filter(key, part):
    key_base = jax.random.fold_in(key, 11)
    key_spread = jax.random.fold_in(key, 12)
    trend_scale = 3.0 ** (jnp.arange(G, dtype=jnp.float32) / (G - 1))
    spread = jnp.exp(jax.random.uniform(key_spread, (G, 1), jnp.float32, 0.0, math.log(3.3)))
    base_draw = jnp.clip(jax.random.normal(key_base, (G, MR_TAPS), jnp.float32), -4.0, 4.0)
    return base_draw * trend_scale[:, None] * spread / math.sqrt(MR_TAPS)


def draw_cotangent(key, part):
    key_base = jax.random.fold_in(key, 21)
    key_spread = jax.random.fold_in(key, 22)
    trend_scale = 3.0 ** (jnp.arange(TOKENS, dtype=jnp.float32) / (TOKENS - 1))
    spread = jnp.exp(jax.random.uniform(key_spread, (TOKENS, 1), jnp.float32, 0.0, math.log(3.3)))
    base_draw = jnp.clip(jax.random.normal(key_base, (TOKENS, D), jnp.float32), -4.0, 4.0)
    return (base_draw * trend_scale[:, None] * spread).astype(jnp.bfloat16)


def shard_levels(own_key, dims, shards, least, top_value):
    level, own = 1.0, jax.random.fold_in(own_key, 6)
    for position, blocks in shards:
        draws = jnp.exp(jax.random.uniform(jax.random.fold_in(own, position), (blocks,), jnp.float32, least / len(shards), top_value / len(shards)))
        level = level * jnp.repeat(draws, dims[position] // blocks).reshape([-1 if axis == position else 1 for axis in range(len(dims))])
    return level


def normal_values(key, dims, width, most, cuts=(), kind=jnp.bfloat16):
    level = shard_levels(key, dims, cuts, -0.22, 0.18) if cuts else 1.0
    values = jax.random.normal(key, dims, jnp.float32) * width * level
    return jnp.minimum(jnp.maximum(values, -most), most).astype(kind)


def setup_inputs(seed: int = 0) -> dict:
    keys = jax.random.split(jax.random.key(seed), 11)
    return {
        "query_mr": normal_values(keys[0], (TOKENS, D), 1.0, 6.0, ((0, 8), (1, 4))),
        "key_mr": normal_values(keys[1], (TOKENS, D), 1.0, 6.0, ((0, 8), (1, 4))),
        "value_mr": normal_values(keys[2], (TOKENS, D), 1.0, 6.0, ((0, 8), (1, 4))),
        "query_li": normal_values(keys[3], (TOKENS, D), 1.0, 6.0, ((0, 8), (1, 4))),
        "key_li": normal_values(keys[4], (TOKENS, D), 1.0, 6.0, ((0, 8), (1, 4))),
        "cotangent": draw_cotangent(jax.random.fold_in(keys[10], 71), 0),
        "mr_filter": draw_mr_filter(jax.random.fold_in(keys[10], 71), 0),
        "norm_gain": jnp.clip(1.0 + 0.18 * jax.random.normal(keys[7], (D,), jnp.float32), 0.1, 1.9),
        "li_decay": jnp.clip(jnp.exp(math.log(0.03) - 4.118061 * jax.random.uniform(keys[8], (G, MODES), jnp.float32) ** shard_levels(keys[8], (G, MODES), ((0, 4),), -0.2, 0.2)), 0.00048828125, 0.03),
        "li_residue": normal_values(keys[9], (G, MODES), 0.25, 1.0, ((0, 4),), jnp.float32),
    }


def rounded(values):
    return lax.optimization_barrier(values.astype(jnp.bfloat16)).astype(jnp.float32)

def split_blocks(values, block_width):
    return values.reshape(values.shape[0], -1, block_width).transpose(1, 0, 2)

def join_blocks(values):
    return values.transpose(1, 0, 2).reshape(values.shape[1], -1)

def grouped_conv(signal, group_taps, backward):
    seq_len, chan_count = signal.shape
    group_size = chan_count // group_taps.shape[0]
    block_width = math.gcd(chan_count, 512)
    if backward:
        signal = jnp.flip(signal, 0)
    pieces = split_blocks(signal, block_width)
    taps_blocks = group_taps.reshape(chan_count // block_width, block_width // group_size, group_taps.shape[1])
    length = 2 * seq_len

    def convolve(pair):
        piece, piece_taps = pair
        expanded = jnp.repeat(piece_taps, group_size, axis=0)
        spectrum = jnp.fft.rfft(piece, length, axis=0) * jnp.fft.rfft(expanded.T, length, axis=0)
        return jnp.fft.irfft(spectrum, length, axis=0)[:seq_len].astype(jnp.float32)
    result = join_blocks(lax.map(convolve, (pieces, taps_blocks)))
    if backward:
        result = jnp.flip(result, 0)
    return result

def grouped_corr(first, second, group_count, tap_count):
    seq_len, chan_count = first.shape
    group_size = chan_count // group_count
    block_width = math.gcd(chan_count, 512)
    length = 2 * seq_len

    def correlate(pair):
        first_piece, second_piece = pair
        spectrum = jnp.fft.rfft(first_piece, length, axis=0) * jnp.conj(jnp.fft.rfft(second_piece, length, axis=0))
        lagged = jnp.fft.irfft(spectrum, length, axis=0)[:tap_count].astype(jnp.float32)
        return lax.optimization_barrier(jnp.sum(lagged.T.reshape(block_width // group_size, group_size, tap_count), axis=1))
    result = lax.map(correlate, (split_blocks(first, block_width), split_blocks(second, block_width)))
    return result.reshape(group_count, tap_count)

def reference(query_mr, key_mr, value_mr, query_li, key_li, cotangent, mr_filter, norm_gain, li_decay, li_residue):
    seq_len = query_mr.shape[0]
    grad_scale = float(seq_len) ** (-0.5)
    taps_mr = rounded(mr_filter)
    mixed_mr = rounded(key_mr.astype(jnp.float32) * value_mr.astype(jnp.float32))
    conv_mr = grouped_conv(mixed_mr, taps_mr, False)
    out_mr = rounded(query_mr.astype(jnp.float32) * conv_mr)
    squares = lax.optimization_barrier(jnp.sum(out_mr * out_mr, axis=1, keepdims=True))
    inv_rms = lax.rsqrt(squares / D + 1e-06)
    normed = out_mr * inv_rms * norm_gain
    mixed_li = key_li.astype(jnp.float32) * normed
    offsets = jnp.arange(seq_len, dtype=jnp.float32)
    norm_res = li_residue * jnp.sqrt(2.0 * li_decay)
    taps_li = jnp.zeros((li_decay.shape[0], seq_len), jnp.float32)
    for mode_index in range(li_decay.shape[1]):
        taps_li = taps_li + norm_res[:, mode_index:mode_index + 1] * jnp.exp(-li_decay[:, mode_index:mode_index + 1] * offsets)
    conv_li = grouped_conv(mixed_li, taps_li, False)
    out_li = (query_li.astype(jnp.float32) * conv_li).astype(jnp.bfloat16)
    cotan_full = cotangent.astype(jnp.float32)
    grad_query_li = (cotan_full * conv_li).astype(jnp.bfloat16)
    back_li = cotan_full * query_li.astype(jnp.float32)
    grad_mixed_li = grouped_conv(back_li, taps_li, True)
    grad_key_li = (grad_mixed_li * normed).astype(jnp.bfloat16)
    grad_normed = grad_mixed_li * key_li.astype(jnp.float32)
    grad_gain = lax.optimization_barrier(jnp.sum(grad_normed * out_mr * inv_rms, axis=0)) * grad_scale
    weighted = grad_normed * norm_gain
    cross_dots = lax.optimization_barrier(jnp.sum(weighted * out_mr, axis=1, keepdims=True))
    grad_out_mr = inv_rms * weighted - out_mr * inv_rms ** 3 * cross_dots / D
    grad_query_mr = (grad_out_mr * conv_mr).astype(jnp.bfloat16)
    back_mr = rounded(grad_out_mr * query_mr.astype(jnp.float32))
    grad_mixed_mr = grouped_conv(back_mr, taps_mr, True)
    grad_key_mr = (grad_mixed_mr * value_mr.astype(jnp.float32)).astype(jnp.bfloat16)
    grad_value_mr = (grad_mixed_mr * key_mr.astype(jnp.float32)).astype(jnp.bfloat16)
    grad_filter = grouped_corr(back_mr, mixed_mr, mr_filter.shape[0], mr_filter.shape[1]) * grad_scale
    return (out_li, grad_query_mr, grad_key_mr, grad_value_mr, grad_query_li, grad_key_li, grad_gain, grad_filter)
```

```python
import functools

import jax
import jax.numpy as jnp
from jax import lax
from jax.experimental import pallas as pl
from jax.experimental.pallas import tpu as pltpu
from jax.sharding import PartitionSpec as P

D = 8192
G = 512
LANES = 128
HIGHEST = lax.Precision.HIGHEST


def from_behind(value, axis, steps):
    count = lax.axis_size(axis)
    initial, last = (max(0, -steps), min(count, count - steps))
    return lax.ppermute(value, axis, [(source, source + steps) for source in range(initial, last)])


def _band_kernel(*refs, group_size, split, tri, two_inputs, has_states):
    refs = list(refs)
    h_ref = refs.pop(0)
    top_ref = refs.pop(0)
    bot_ref = refs.pop(0) if two_inputs else None
    e_ref = refs.pop(0) if has_states else None
    out_ref = refs.pop(0)
    s_ref = refs.pop(0) if has_states else None
    if two_inputs:
        x = jnp.concatenate([top_ref[...], bot_ref[...]], axis=0)
    else:
        x = top_ref[...]
    width = x.shape[0]
    rows = out_ref.shape[0]
    groups_here = LANES // group_size
    lane_group = lax.broadcasted_iota(jnp.int32, (rows, LANES), 1) // group_size
    row_id = lax.broadcasted_iota(jnp.int32, (rows, width), 0)
    col_id = lax.broadcasted_iota(jnp.int32, (rows, width), 1)
    acc = jnp.zeros((rows, LANES), jnp.float32)
    if has_states:
        modes = s_ref.shape[0]
        state_group = lax.broadcasted_iota(jnp.int32, (modes, LANES), 1) // group_size
        state_acc = jnp.zeros((modes, LANES), jnp.float32)
    for k in range(groups_here):
        band_row = h_ref[pl.ds(k, 1), :]
        band = pltpu.roll(jnp.broadcast_to(band_row, (rows, width)), 0, 1, stride=1, stride_axis=0)
        if tri == "lower":
            band = jnp.where(col_id <= row_id, band, 0.0)
        elif tri == "upper":
            band = jnp.where(col_id >= row_id, band, 0.0)
        high = band.astype(jnp.bfloat16)
        y = jnp.dot(high, x, preferred_element_type=jnp.float32)
        if split:
            low = (band - high.astype(jnp.float32)).astype(jnp.bfloat16)
            y = y + jnp.dot(low, x, preferred_element_type=jnp.float32)
        acc = jnp.where(lane_group == k, y, acc)
        if has_states:
            weights = e_ref[k]
            e_high = weights.astype(jnp.bfloat16)
            e_low = (weights - e_high.astype(jnp.float32)).astype(jnp.bfloat16)
            s = jnp.dot(e_high, x, preferred_element_type=jnp.float32)
            s = s + jnp.dot(e_low, x, preferred_element_type=jnp.float32)
            state_acc = jnp.where(state_group == k, s, state_acc)
    out_ref[...] = acc
    if has_states:
        s_ref[...] = state_acc


def band_conv(band_rows, top, bottom=None, state_rows=None, *, group_size, split, tri):
    rows, chans = top.shape
    groups_here = LANES // group_size
    blocks = chans // LANES
    width = band_rows.shape[1]
    two_inputs = bottom is not None
    has_states = state_rows is not None
    in_specs = [
        pl.BlockSpec((groups_here, width), lambda b: (b, 0)),
        pl.BlockSpec((rows, LANES), lambda b: (0, b)),
    ]
    args = [band_rows, top]
    if two_inputs:
        in_specs.append(pl.BlockSpec((rows, LANES), lambda b: (0, b)))
        args.append(bottom)
    out_shape = [jax.ShapeDtypeStruct((rows, chans), jnp.float32)]
    out_specs = [pl.BlockSpec((rows, LANES), lambda b: (0, b))]
    if has_states:
        modes = state_rows.shape[1]
        in_specs.append(pl.BlockSpec((groups_here, modes, rows), lambda b: (b, 0, 0)))
        args.append(state_rows)
        out_shape.append(jax.ShapeDtypeStruct((modes, chans), jnp.float32))
        out_specs.append(pl.BlockSpec((modes, LANES), lambda b: (0, b)))
    kernel = functools.partial(
        _band_kernel,
        group_size=group_size,
        split=split,
        tri=tri,
        two_inputs=two_inputs,
        has_states=has_states,
    )
    return pl.pallas_call(
        kernel,
        grid=(blocks,),
        in_specs=in_specs,
        out_specs=out_specs,
        out_shape=out_shape,
        compiler_params=pltpu.CompilerParams(dimension_semantics=("parallel",)),
    )(*args)


def _modal_kernel(dec_ref, wt_ref, ent_ref, loc_ref, out_ref, *, group_size, forward):
    rows = out_ref.shape[0]
    modes = dec_ref.shape[1]
    groups_here = LANES // group_size
    lane_group = lax.broadcasted_iota(jnp.int32, (rows, LANES), 1) // group_size
    offsets = lax.broadcasted_iota(jnp.int32, (rows, modes), 0).astype(jnp.float32)
    dist = offsets + 1.0 if forward else float(rows) - offsets
    entering = ent_ref[...]
    acc = loc_ref[...]
    for k in range(groups_here):
        rate = dec_ref[pl.ds(k, 1), :]
        weight = wt_ref[pl.ds(k, 1), :]
        out_w = weight * jnp.exp(-rate * dist)
        y = jnp.dot(out_w, entering, preferred_element_type=jnp.float32, precision=HIGHEST)
        acc = acc + jnp.where(lane_group == k, y, 0.0)
    out_ref[...] = acc


def modal_out(decays, weights, entering, local, *, group_size, forward):
    rows, chans = local.shape
    groups_here = LANES // group_size
    modes = decays.shape[1]
    kernel = functools.partial(_modal_kernel, group_size=group_size, forward=forward)
    return pl.pallas_call(
        kernel,
        grid=(chans // LANES,),
        in_specs=[
            pl.BlockSpec((groups_here, modes), lambda b: (b, 0)),
            pl.BlockSpec((groups_here, modes), lambda b: (b, 0)),
            pl.BlockSpec((modes, LANES), lambda b: (0, b)),
            pl.BlockSpec((rows, LANES), lambda b: (0, b)),
        ],
        out_specs=pl.BlockSpec((rows, LANES), lambda b: (0, b)),
        out_shape=jax.ShapeDtypeStruct((rows, chans), jnp.float32),
        compiler_params=pltpu.CompilerParams(dimension_semantics=("parallel",)),
    )(decays, weights, entering, local)


def _gram_kernel(back_ref, top_ref, bot_ref, f_ref, *, group_size):
    back = back_ref[...]
    x = jnp.concatenate([top_ref[...], bot_ref[...]], axis=0)
    rows = back.shape[0]
    groups_here = LANES // group_size
    r_id = lax.broadcasted_iota(jnp.int32, (rows, rows), 0)
    c_id = lax.broadcasted_iota(jnp.int32, (rows, rows), 1)
    exchange = jnp.where(r_id + c_id == rows - 1, 1.0, 0.0).astype(jnp.bfloat16)
    back_rev = jnp.dot(exchange, back, preferred_element_type=jnp.float32).astype(jnp.bfloat16)
    lane_group = lax.broadcasted_iota(jnp.int32, (rows, LANES), 1) // group_size
    for k in range(groups_here):
        masked = jnp.where(lane_group == k, back_rev, jnp.zeros_like(back_rev))
        gram = lax.dot_general(
            masked, x, (((1,), (1,)), ((), ())), preferred_element_type=jnp.float32
        )
        skew = pltpu.roll(gram, 0, 1, stride=1, stride_axis=0)
        f_ref[pl.ds(k, 1), :] = jnp.sum(skew, axis=0, keepdims=True)


def gram_diag(back, top, bottom, *, group_size):
    rows, chans = back.shape
    groups_here = LANES // group_size
    group_count = chans // group_size
    kernel = functools.partial(_gram_kernel, group_size=group_size)
    return pl.pallas_call(
        kernel,
        grid=(chans // LANES,),
        in_specs=[
            pl.BlockSpec((rows, LANES), lambda b: (0, b)),
            pl.BlockSpec((rows, LANES), lambda b: (0, b)),
            pl.BlockSpec((rows, LANES), lambda b: (0, b)),
        ],
        out_specs=pl.BlockSpec((groups_here, 2 * rows), lambda b: (b, 0)),
        out_shape=jax.ShapeDtypeStruct((group_count, 2 * rows), jnp.float32),
        compiler_params=pltpu.CompilerParams(dimension_semantics=("parallel",)),
    )(back, top, bottom)


def entering_states(states, decays, block_len, group_size, forward):
    gathered = lax.all_gather(states, "seq")
    count = gathered.shape[0]
    here = lax.axis_index("seq")
    rates = jnp.repeat(decays.T, group_size, axis=1)
    source = jnp.arange(count)
    if forward:
        gap = here - 1 - source
    else:
        gap = source - here - 1
    valid = gap >= 0
    steps = jnp.maximum(gap, 0).astype(jnp.float32)
    coef = jnp.exp(-rates[None] * (float(block_len) * steps)[:, None, None])
    coef = jnp.where(valid[:, None, None], coef, 0.0)
    return jnp.sum(coef * gathered, axis=0)


def on_device(
    query_mr,
    key_mr,
    value_mr,
    query_li,
    key_li,
    cotangent,
    mr_filter,
    norm_gain,
    li_decay,
    li_residue,
):
    row_count, chan_count = query_mr.shape
    group_count, tap_count = mr_filter.shape
    group_size = chan_count // group_count
    assert row_count == tap_count
    grad_scale = float(row_count * lax.axis_size("seq")) ** (-0.5)

    taps_mr = mr_filter.astype(jnp.bfloat16).astype(jnp.float32)
    zero_col = jnp.zeros((group_count, 1), jnp.float32)
    fwd_rows = jnp.concatenate(
        [zero_col, jnp.flip(taps_mr, 1), jnp.zeros((group_count, tap_count - 1), jnp.float32)], 1
    )
    bwd_rows = jnp.concatenate([taps_mr, jnp.zeros_like(taps_mr)], 1)

    mixed_mr = (key_mr.astype(jnp.float32) * value_mr.astype(jnp.float32)).astype(jnp.bfloat16)
    rim_rows = from_behind(mixed_mr, "seq", 1)
    (conv_mr,) = band_conv(fwd_rows, rim_rows, mixed_mr, group_size=group_size, split=False, tri=None)
    out_mr = (query_mr.astype(jnp.float32) * conv_mr).astype(jnp.bfloat16)
    out_full = out_mr.astype(jnp.float32)
    squares = lax.psum(jnp.sum(out_full * out_full, axis=1), "chan")
    inv_rms = lax.rsqrt(squares / D + 1e-06)[:, None]
    normed = out_full * inv_rms * norm_gain
    mixed_li = key_li.astype(jnp.float32) * normed
    cotan_full = cotangent.astype(jnp.float32)
    back_li = cotan_full * query_li.astype(jnp.float32)

    offsets = jnp.arange(row_count, dtype=jnp.float32)
    weights_res = li_residue * jnp.sqrt(2.0 * li_decay)
    taps_li = jnp.einsum(
        "gr,grd->gd", weights_res, jnp.exp(-li_decay[:, :, None] * offsets), precision=HIGHEST
    )
    li_fwd_rows = jnp.concatenate([taps_li[:, :1], jnp.flip(taps_li[:, 1:], 1)], 1)
    fwd_states = jnp.exp(-li_decay[:, :, None] * (row_count - 1.0 - offsets))
    bwd_states = jnp.exp(-li_decay[:, :, None] * offsets)

    grad_loc, grad_st = band_conv(
        taps_li, back_li.astype(jnp.bfloat16), None, bwd_states,
        group_size=group_size, split=True, tri="upper",
    )
    conv_loc, conv_st = band_conv(
        li_fwd_rows, mixed_li.astype(jnp.bfloat16), None, fwd_states,
        group_size=group_size, split=True, tri="lower",
    )
    grad_ent = entering_states(grad_st, li_decay, row_count, group_size, False)
    conv_ent = entering_states(conv_st, li_decay, row_count, group_size, True)
    grad_mixed_li = modal_out(
        li_decay, weights_res, grad_ent, grad_loc, group_size=group_size, forward=False
    )
    conv_li = modal_out(li_decay, weights_res, conv_ent, conv_loc, group_size=group_size, forward=True)

    out_li = (query_li.astype(jnp.float32) * conv_li).astype(jnp.bfloat16)
    grad_query_li = (cotan_full * conv_li).astype(jnp.bfloat16)
    grad_key_li = (grad_mixed_li * normed).astype(jnp.bfloat16)
    grad_normed = grad_mixed_li * key_li.astype(jnp.float32)
    gain_part = jnp.sum(grad_normed * out_full * inv_rms, axis=0)
    weighted = grad_normed * norm_gain
    cross_dots = lax.psum(jnp.sum(weighted * out_full, axis=1), "chan")[:, None]
    grad_out_mr = inv_rms * weighted - out_full * inv_rms**3 * cross_dots / D
    grad_query_mr = (grad_out_mr * conv_mr).astype(jnp.bfloat16)
    back_mr = (grad_out_mr * query_mr.astype(jnp.float32)).astype(jnp.bfloat16)
    after_rim = from_behind(back_mr, "seq", -1)
    (grad_mixed_mr,) = band_conv(bwd_rows, back_mr, after_rim, group_size=group_size, split=False, tri=None)
    grad_key_mr = (grad_mixed_mr * value_mr.astype(jnp.float32)).astype(jnp.bfloat16)
    grad_value_mr = (grad_mixed_mr * key_mr.astype(jnp.float32)).astype(jnp.bfloat16)
    diag_sums = gram_diag(back_mr, rim_rows, mixed_mr, group_size=group_size)
    filter_part = jnp.flip(diag_sums[:, tap_count:], 1)
    param_sums = (lax.psum(gain_part, "seq"), lax.psum(filter_part, "seq"))
    grad_gain = param_sums[0] * grad_scale
    grad_filter = param_sums[1] * grad_scale
    return (
        out_li,
        grad_query_mr,
        grad_key_mr,
        grad_value_mr,
        grad_query_li,
        grad_key_li,
        grad_gain,
        grad_filter,
    )


def solution(mesh):
    in_specs = (
        P("seq", "chan"),
        P("seq", "chan"),
        P("seq", "chan"),
        P("seq", "chan"),
        P("seq", "chan"),
        P("seq", "chan"),
        P("chan", None),
        P("chan"),
        P("chan", None),
        P("chan", None),
    )
    out_specs = (
        P("seq", "chan"),
        P("seq", "chan"),
        P("seq", "chan"),
        P("seq", "chan"),
        P("seq", "chan"),
        P("seq", "chan"),
        P("chan"),
        P("chan", None),
    )
    return jax.shard_map(
        on_device, mesh=mesh, in_specs=in_specs, out_specs=out_specs, check_vma=False
    )
```

```python
import functools

import jax
import jax.numpy as jnp
from jax import lax
from jax.experimental import pallas as pl
from jax.experimental.pallas import tpu as pltpu
from jax.sharding import PartitionSpec as P

D = 8192
G = 512
LANES = 128
HIGHEST = lax.Precision.HIGHEST


def from_behind(value, axis, steps):
    count = lax.axis_size(axis)
    initial, last = (max(0, -steps), min(count, count - steps))
    return lax.ppermute(value, axis, [(source, source + steps) for source in range(initial, last)])


def _band_kernel(*refs, group_size, split, tri, two_inputs, has_states):
    refs = list(refs)
    h_ref = refs.pop(0)
    top_ref = refs.pop(0)
    bot_ref = refs.pop(0) if two_inputs else None
    e_ref = refs.pop(0) if has_states else None
    out_ref = refs.pop(0)
    s_ref = refs.pop(0) if has_states else None
    if two_inputs:
        x = jnp.concatenate([top_ref[...], bot_ref[...]], axis=0)
    else:
        x = top_ref[...]
    width = x.shape[0]
    rows = out_ref.shape[0]
    groups_here = LANES // group_size
    lane_group = lax.broadcasted_iota(jnp.int32, (rows, LANES), 1) // group_size
    row_id = lax.broadcasted_iota(jnp.int32, (rows, width), 0)
    col_id = lax.broadcasted_iota(jnp.int32, (rows, width), 1)
    acc = jnp.zeros((rows, LANES), jnp.float32)
    if has_states:
        modes = s_ref.shape[0]
        state_group = lax.broadcasted_iota(jnp.int32, (modes, LANES), 1) // group_size
        state_acc = jnp.zeros((modes, LANES), jnp.float32)
    for k in range(groups_here):
        band_row = h_ref[pl.ds(k, 1), :]
        band = pltpu.roll(jnp.broadcast_to(band_row, (rows, width)), 0, 1, stride=1, stride_axis=0)
        if tri == "lower":
            band = jnp.where(col_id <= row_id, band, 0.0)
        elif tri == "upper":
            band = jnp.where(col_id >= row_id, band, 0.0)
        high = band.astype(jnp.bfloat16)
        y = jnp.dot(high, x, preferred_element_type=jnp.float32)
        if split:
            low = (band - high.astype(jnp.float32)).astype(jnp.bfloat16)
            y = y + jnp.dot(low, x, preferred_element_type=jnp.float32)
        acc = jnp.where(lane_group == k, y, acc)
        if has_states:
            weights = e_ref[k]
            e_high = weights.astype(jnp.bfloat16)
            e_low = (weights - e_high.astype(jnp.float32)).astype(jnp.bfloat16)
            s = jnp.dot(e_high, x, preferred_element_type=jnp.float32)
            s = s + jnp.dot(e_low, x, preferred_element_type=jnp.float32)
            state_acc = jnp.where(state_group == k, s, state_acc)
    out_ref[...] = acc
    if has_states:
        s_ref[...] = state_acc


def band_conv(band_rows, top, bottom=None, state_rows=None, *, group_size, split, tri):
    rows, chans = top.shape
    groups_here = LANES // group_size
    blocks = chans // LANES
    width = band_rows.shape[1]
    two_inputs = bottom is not None
    has_states = state_rows is not None
    in_specs = [
        pl.BlockSpec((groups_here, width), lambda b: (b, 0)),
        pl.BlockSpec((rows, LANES), lambda b: (0, b)),
    ]
    args = [band_rows, top]
    if two_inputs:
        in_specs.append(pl.BlockSpec((rows, LANES), lambda b: (0, b)))
        args.append(bottom)
    out_shape = [jax.ShapeDtypeStruct((rows, chans), jnp.float32)]
    out_specs = [pl.BlockSpec((rows, LANES), lambda b: (0, b))]
    if has_states:
        modes = state_rows.shape[1]
        in_specs.append(pl.BlockSpec((groups_here, modes, rows), lambda b: (b, 0, 0)))
        args.append(state_rows)
        out_shape.append(jax.ShapeDtypeStruct((modes, chans), jnp.float32))
        out_specs.append(pl.BlockSpec((modes, LANES), lambda b: (0, b)))
    kernel = functools.partial(
        _band_kernel,
        group_size=group_size,
        split=split,
        tri=tri,
        two_inputs=two_inputs,
        has_states=has_states,
    )
    return pl.pallas_call(
        kernel,
        grid=(blocks,),
        in_specs=in_specs,
        out_specs=out_specs,
        out_shape=out_shape,
        compiler_params=pltpu.CompilerParams(dimension_semantics=("parallel",)),
    )(*args)


def _modal_kernel(dec_ref, wt_ref, ent_ref, loc_ref, out_ref, *, group_size, forward):
    rows = out_ref.shape[0]
    modes = dec_ref.shape[1]
    groups_here = LANES // group_size
    lane_group = lax.broadcasted_iota(jnp.int32, (rows, LANES), 1) // group_size
    offsets = lax.broadcasted_iota(jnp.int32, (rows, modes), 0).astype(jnp.float32)
    dist = offsets + 1.0 if forward else float(rows) - offsets
    entering = ent_ref[...]
    acc = loc_ref[...]
    for k in range(groups_here):
        rate = dec_ref[pl.ds(k, 1), :]
        weight = wt_ref[pl.ds(k, 1), :]
        out_w = weight * jnp.exp(-rate * dist)
        y = jnp.dot(out_w, entering, preferred_element_type=jnp.float32, precision=HIGHEST)
        acc = acc + jnp.where(lane_group == k, y, 0.0)
    out_ref[...] = acc


def modal_out(decays, weights, entering, local, *, group_size, forward):
    rows, chans = local.shape
    groups_here = LANES // group_size
    modes = decays.shape[1]
    kernel = functools.partial(_modal_kernel, group_size=group_size, forward=forward)
    return pl.pallas_call(
        kernel,
        grid=(chans // LANES,),
        in_specs=[
            pl.BlockSpec((groups_here, modes), lambda b: (b, 0)),
            pl.BlockSpec((groups_here, modes), lambda b: (b, 0)),
            pl.BlockSpec((modes, LANES), lambda b: (0, b)),
            pl.BlockSpec((rows, LANES), lambda b: (0, b)),
        ],
        out_specs=pl.BlockSpec((rows, LANES), lambda b: (0, b)),
        out_shape=jax.ShapeDtypeStruct((rows, chans), jnp.float32),
        compiler_params=pltpu.CompilerParams(dimension_semantics=("parallel",)),
    )(decays, weights, entering, local)


def _gram_kernel(back_ref, top_ref, bot_ref, f_ref, *, group_size):
    back = back_ref[...]
    x = jnp.concatenate([top_ref[...], bot_ref[...]], axis=0)
    rows = back.shape[0]
    groups_here = LANES // group_size
    r_id = lax.broadcasted_iota(jnp.int32, (rows, rows), 0)
    c_id = lax.broadcasted_iota(jnp.int32, (rows, rows), 1)
    exchange = jnp.where(r_id + c_id == rows - 1, 1.0, 0.0).astype(jnp.bfloat16)
    back_rev = jnp.dot(exchange, back, preferred_element_type=jnp.float32).astype(jnp.bfloat16)
    lane_group = lax.broadcasted_iota(jnp.int32, (rows, LANES), 1) // group_size
    for k in range(groups_here):
        masked = jnp.where(lane_group == k, back_rev, jnp.zeros_like(back_rev))
        gram = lax.dot_general(
            masked, x, (((1,), (1,)), ((), ())), preferred_element_type=jnp.float32
        )
        skew = pltpu.roll(gram, 0, 1, stride=1, stride_axis=0)
        f_ref[pl.ds(k, 1), :] = jnp.sum(skew, axis=0, keepdims=True)


def gram_diag(back, top, bottom, *, group_size):
    rows, chans = back.shape
    groups_here = LANES // group_size
    group_count = chans // group_size
    kernel = functools.partial(_gram_kernel, group_size=group_size)
    return pl.pallas_call(
        kernel,
        grid=(chans // LANES,),
        in_specs=[
            pl.BlockSpec((rows, LANES), lambda b: (0, b)),
            pl.BlockSpec((rows, LANES), lambda b: (0, b)),
            pl.BlockSpec((rows, LANES), lambda b: (0, b)),
        ],
        out_specs=pl.BlockSpec((groups_here, 2 * rows), lambda b: (b, 0)),
        out_shape=jax.ShapeDtypeStruct((group_count, 2 * rows), jnp.float32),
        compiler_params=pltpu.CompilerParams(dimension_semantics=("parallel",)),
    )(back, top, bottom)


def gather_seq(value):
    count = lax.axis_size("seq")
    tiled = jnp.broadcast_to(value[None], (count,) + value.shape)
    return lax.all_to_all(tiled, "seq", split_axis=0, concat_axis=0, tiled=True)


def entering_states(states, decays, block_len, group_size, forward):
    gathered = gather_seq(states)
    count = gathered.shape[0]
    here = lax.axis_index("seq")
    rates = jnp.repeat(decays.T, group_size, axis=1)
    source = jnp.arange(count)
    if forward:
        gap = here - 1 - source
    else:
        gap = source - here - 1
    valid = gap >= 0
    steps = jnp.maximum(gap, 0).astype(jnp.float32)
    coef = jnp.exp(-rates[None] * (float(block_len) * steps)[:, None, None])
    coef = jnp.where(valid[:, None, None], coef, 0.0)
    return jnp.sum(coef * gathered, axis=0)


def on_device(
    query_mr,
    key_mr,
    value_mr,
    query_li,
    key_li,
    cotangent,
    mr_filter,
    norm_gain,
    li_decay,
    li_residue,
):
    row_count, chan_count = query_mr.shape
    group_count, tap_count = mr_filter.shape
    group_size = chan_count // group_count
    assert row_count == tap_count
    grad_scale = float(row_count * lax.axis_size("seq")) ** (-0.5)

    taps_mr = mr_filter.astype(jnp.bfloat16).astype(jnp.float32)
    zero_col = jnp.zeros((group_count, 1), jnp.float32)
    fwd_rows = jnp.concatenate(
        [zero_col, jnp.flip(taps_mr, 1), jnp.zeros((group_count, tap_count - 1), jnp.float32)], 1
    )
    bwd_rows = jnp.concatenate([taps_mr, jnp.zeros_like(taps_mr)], 1)

    mixed_mr = (key_mr.astype(jnp.float32) * value_mr.astype(jnp.float32)).astype(jnp.bfloat16)
    rim_rows = from_behind(mixed_mr, "seq", 1)
    (conv_mr,) = band_conv(fwd_rows, rim_rows, mixed_mr, group_size=group_size, split=False, tri=None)
    out_mr = (query_mr.astype(jnp.float32) * conv_mr).astype(jnp.bfloat16)
    out_full = out_mr.astype(jnp.float32)
    squares = lax.psum(jnp.sum(out_full * out_full, axis=1), "chan")
    inv_rms = lax.rsqrt(squares / D + 1e-06)[:, None]
    normed = out_full * inv_rms * norm_gain
    mixed_li = key_li.astype(jnp.float32) * normed
    cotan_full = cotangent.astype(jnp.float32)
    back_li = cotan_full * query_li.astype(jnp.float32)

    offsets = jnp.arange(row_count, dtype=jnp.float32)
    weights_res = li_residue * jnp.sqrt(2.0 * li_decay)
    taps_li = jnp.einsum(
        "gr,grd->gd", weights_res, jnp.exp(-li_decay[:, :, None] * offsets), precision=HIGHEST
    )
    li_fwd_rows = jnp.concatenate([taps_li[:, :1], jnp.flip(taps_li[:, 1:], 1)], 1)
    fwd_states = jnp.exp(-li_decay[:, :, None] * (row_count - 1.0 - offsets))
    bwd_states = jnp.exp(-li_decay[:, :, None] * offsets)

    grad_loc, grad_st = band_conv(
        taps_li, back_li.astype(jnp.bfloat16), None, bwd_states,
        group_size=group_size, split=True, tri="upper",
    )
    conv_loc, conv_st = band_conv(
        li_fwd_rows, mixed_li.astype(jnp.bfloat16), None, fwd_states,
        group_size=group_size, split=True, tri="lower",
    )
    grad_ent = entering_states(grad_st, li_decay, row_count, group_size, False)
    conv_ent = entering_states(conv_st, li_decay, row_count, group_size, True)
    grad_mixed_li = modal_out(
        li_decay, weights_res, grad_ent, grad_loc, group_size=group_size, forward=False
    )
    conv_li = modal_out(li_decay, weights_res, conv_ent, conv_loc, group_size=group_size, forward=True)

    out_li = (query_li.astype(jnp.float32) * conv_li).astype(jnp.bfloat16)
    grad_query_li = (cotan_full * conv_li).astype(jnp.bfloat16)
    grad_key_li = (grad_mixed_li * normed).astype(jnp.bfloat16)
    grad_normed = grad_mixed_li * key_li.astype(jnp.float32)
    gain_part = jnp.sum(grad_normed * out_full * inv_rms, axis=0)
    weighted = grad_normed * norm_gain
    cross_dots = lax.psum(jnp.sum(weighted * out_full, axis=1), "chan")[:, None]
    grad_out_mr = inv_rms * weighted - out_full * inv_rms**3 * cross_dots / D
    grad_query_mr = (grad_out_mr * conv_mr).astype(jnp.bfloat16)
    back_mr = (grad_out_mr * query_mr.astype(jnp.float32)).astype(jnp.bfloat16)
    after_rim = from_behind(back_mr, "seq", -1)
    (grad_mixed_mr,) = band_conv(bwd_rows, back_mr, after_rim, group_size=group_size, split=False, tri=None)
    grad_key_mr = (grad_mixed_mr * value_mr.astype(jnp.float32)).astype(jnp.bfloat16)
    grad_value_mr = (grad_mixed_mr * key_mr.astype(jnp.float32)).astype(jnp.bfloat16)
    diag_sums = gram_diag(back_mr, rim_rows, mixed_mr, group_size=group_size)
    filter_part = jnp.flip(diag_sums[:, tap_count:], 1)
    packed = jnp.concatenate([gain_part, filter_part.reshape(-1)])
    param_sums = jnp.sum(gather_seq(packed), axis=0) * grad_scale
    grad_gain = param_sums[:chan_count]
    grad_filter = param_sums[chan_count:].reshape(group_count, tap_count)
    return (
        out_li,
        grad_query_mr,
        grad_key_mr,
        grad_value_mr,
        grad_query_li,
        grad_key_li,
        grad_gain,
        grad_filter,
    )


def solution(mesh):
    in_specs = (
        P("seq", "chan"),
        P("seq", "chan"),
        P("seq", "chan"),
        P("seq", "chan"),
        P("seq", "chan"),
        P("seq", "chan"),
        P("chan", None),
        P("chan"),
        P("chan", None),
        P("chan", None),
    )
    out_specs = (
        P("seq", "chan"),
        P("seq", "chan"),
        P("seq", "chan"),
        P("seq", "chan"),
        P("seq", "chan"),
        P("seq", "chan"),
        P("chan"),
        P("chan", None),
    )
    return jax.shard_map(
        on_device, mesh=mesh, in_specs=in_specs, out_specs=out_specs, check_vma=False
    )
```

```python
import functools

import jax
import jax.numpy as jnp
from jax import lax
from jax.experimental import pallas as pl
from jax.experimental.pallas import tpu as pltpu
from jax.sharding import PartitionSpec as P

D = 8192
G = 512
LANES = 128
HIGHEST = lax.Precision.HIGHEST


def from_behind(value, axis, steps):
    count = lax.axis_size(axis)
    initial, last = (max(0, -steps), min(count, count - steps))
    return lax.ppermute(value, axis, [(source, source + steps) for source in range(initial, last)])


def _split(value):
    high = value.astype(jnp.bfloat16)
    return high, (value - high.astype(jnp.float32)).astype(jnp.bfloat16)


def _band_kernel(*refs, group_size, split, tri, two_inputs, modal):
    refs = list(refs)
    h_ref = refs.pop(0)
    top_ref = refs.pop(0)
    bot_ref = refs.pop(0) if two_inputs else None
    if modal is not None:
        dec_ref, wt_ref, ent_ref = refs.pop(0), refs.pop(0), refs.pop(0)
    out_ref = refs.pop(0)
    if two_inputs:
        x = jnp.concatenate([top_ref[...], bot_ref[...]], axis=0)
    else:
        x = top_ref[...]
    width = x.shape[0]
    rows = out_ref.shape[0]
    groups_here = LANES // group_size
    lane_group = lax.broadcasted_iota(jnp.int32, (rows, LANES), 1) // group_size
    row_id = lax.broadcasted_iota(jnp.int32, (rows, width), 0)
    col_id = lax.broadcasted_iota(jnp.int32, (rows, width), 1)
    acc = jnp.zeros((rows, LANES), jnp.float32)
    if modal is not None:
        ent_high, ent_low = _split(ent_ref[...])
        modes = dec_ref.shape[1]
        offsets = lax.broadcasted_iota(jnp.int32, (rows, modes), 0).astype(jnp.float32)
        dist = offsets + 1.0 if modal == "forward" else float(rows) - offsets
    for k in range(groups_here):
        band_row = h_ref[pl.ds(k, 1), :]
        band = pltpu.roll(jnp.broadcast_to(band_row, (rows, width)), 0, 1, stride=1, stride_axis=0)
        if tri == "lower":
            band = jnp.where(col_id <= row_id, band, 0.0)
        elif tri == "upper":
            band = jnp.where(col_id >= row_id, band, 0.0)
        if split:
            high, low = _split(band)
            y = jnp.dot(high, x, preferred_element_type=jnp.float32)
            y = y + jnp.dot(low, x, preferred_element_type=jnp.float32)
        else:
            y = jnp.dot(band.astype(jnp.bfloat16), x, preferred_element_type=jnp.float32)
        if modal is not None:
            rate = dec_ref[pl.ds(k, 1), :]
            weight = wt_ref[pl.ds(k, 1), :]
            a_high, a_low = _split(weight * jnp.exp(-rate * dist))
            y = y + jnp.dot(a_high, ent_high, preferred_element_type=jnp.float32)
            y = y + jnp.dot(a_low, ent_high, preferred_element_type=jnp.float32)
            y = y + jnp.dot(a_high, ent_low, preferred_element_type=jnp.float32)
        acc = jnp.where(lane_group == k, y, acc)
    out_ref[...] = acc


def band_conv(band_rows, top, bottom=None, modal_args=None, *, group_size, split, tri, modal=None):
    rows, chans = top.shape
    groups_here = LANES // group_size
    blocks = chans // LANES
    width = band_rows.shape[1]
    two_inputs = bottom is not None
    in_specs = [
        pl.BlockSpec((groups_here, width), lambda b: (b, 0)),
        pl.BlockSpec((rows, LANES), lambda b: (0, b)),
    ]
    args = [band_rows, top]
    if two_inputs:
        in_specs.append(pl.BlockSpec((rows, LANES), lambda b: (0, b)))
        args.append(bottom)
    if modal is not None:
        decays, weights, entering = modal_args
        modes = decays.shape[1]
        in_specs += [
            pl.BlockSpec((groups_here, modes), lambda b: (b, 0)),
            pl.BlockSpec((groups_here, modes), lambda b: (b, 0)),
            pl.BlockSpec((modes, LANES), lambda b: (0, b)),
        ]
        args += [decays, weights, entering]
    kernel = functools.partial(
        _band_kernel,
        group_size=group_size,
        split=split,
        tri=tri,
        two_inputs=two_inputs,
        modal=modal,
    )
    return pl.pallas_call(
        kernel,
        grid=(blocks,),
        in_specs=in_specs,
        out_specs=pl.BlockSpec((rows, LANES), lambda b: (0, b)),
        out_shape=jax.ShapeDtypeStruct((rows, chans), jnp.float32),
        compiler_params=pltpu.CompilerParams(dimension_semantics=("parallel",)),
    )(*args)


def _state_kernel(e_ref, x_ref, s_ref, *, group_size):
    x = x_ref[...]
    modes = s_ref.shape[0]
    groups_here = LANES // group_size
    state_group = lax.broadcasted_iota(jnp.int32, (modes, LANES), 1) // group_size
    acc = jnp.zeros((modes, LANES), jnp.float32)
    for k in range(groups_here):
        high, low = _split(e_ref[k])
        s = jnp.dot(high, x, preferred_element_type=jnp.float32)
        s = s + jnp.dot(low, x, preferred_element_type=jnp.float32)
        acc = jnp.where(state_group == k, s, acc)
    s_ref[...] = acc


def modal_states(state_rows, x, *, group_size):
    rows, chans = x.shape
    groups_here = LANES // group_size
    modes = state_rows.shape[1]
    kernel = functools.partial(_state_kernel, group_size=group_size)
    return pl.pallas_call(
        kernel,
        grid=(chans // LANES,),
        in_specs=[
            pl.BlockSpec((groups_here, modes, rows), lambda b: (b, 0, 0)),
            pl.BlockSpec((rows, LANES), lambda b: (0, b)),
        ],
        out_specs=pl.BlockSpec((modes, LANES), lambda b: (0, b)),
        out_shape=jax.ShapeDtypeStruct((modes, chans), jnp.float32),
        compiler_params=pltpu.CompilerParams(dimension_semantics=("parallel",)),
    )(state_rows, x)


def _gram_kernel(back_ref, top_ref, bot_ref, f_ref, *, group_size):
    back = back_ref[...]
    x = jnp.concatenate([top_ref[...], bot_ref[...]], axis=0)
    rows = back.shape[0]
    groups_here = LANES // group_size
    r_id = lax.broadcasted_iota(jnp.int32, (rows, rows), 0)
    c_id = lax.broadcasted_iota(jnp.int32, (rows, rows), 1)
    exchange = jnp.where(r_id + c_id == rows - 1, 1.0, 0.0).astype(jnp.bfloat16)
    back_rev = jnp.dot(exchange, back, preferred_element_type=jnp.float32).astype(jnp.bfloat16)
    lane_group = lax.broadcasted_iota(jnp.int32, (rows, LANES), 1) // group_size
    for k in range(groups_here):
        masked = jnp.where(lane_group == k, back_rev, jnp.zeros_like(back_rev))
        gram = lax.dot_general(
            masked, x, (((1,), (1,)), ((), ())), preferred_element_type=jnp.float32
        )
        skew = pltpu.roll(gram, 0, 1, stride=1, stride_axis=0)
        f_ref[pl.ds(k, 1), :] = jnp.sum(skew, axis=0, keepdims=True)


def gram_diag(back, top, bottom, *, group_size):
    rows, chans = back.shape
    groups_here = LANES // group_size
    group_count = chans // group_size
    kernel = functools.partial(_gram_kernel, group_size=group_size)
    return pl.pallas_call(
        kernel,
        grid=(chans // LANES,),
        in_specs=[
            pl.BlockSpec((rows, LANES), lambda b: (0, b)),
            pl.BlockSpec((rows, LANES), lambda b: (0, b)),
            pl.BlockSpec((rows, LANES), lambda b: (0, b)),
        ],
        out_specs=pl.BlockSpec((groups_here, 2 * rows), lambda b: (b, 0)),
        out_shape=jax.ShapeDtypeStruct((group_count, 2 * rows), jnp.float32),
        compiler_params=pltpu.CompilerParams(dimension_semantics=("parallel",)),
    )(back, top, bottom)


def gather_seq(value):
    count = lax.axis_size("seq")
    tiled = jnp.broadcast_to(value[None], (count,) + value.shape)
    return lax.all_to_all(tiled, "seq", split_axis=0, concat_axis=0, tiled=True)


def entering_states(states, decays, block_len, group_size, forward):
    gathered = gather_seq(states)
    count = gathered.shape[0]
    here = lax.axis_index("seq")
    rates = jnp.repeat(decays.T, group_size, axis=1)
    source = jnp.arange(count)
    if forward:
        gap = here - 1 - source
    else:
        gap = source - here - 1
    valid = gap >= 0
    steps = jnp.maximum(gap, 0).astype(jnp.float32)
    coef = jnp.exp(-rates[None] * (float(block_len) * steps)[:, None, None])
    coef = jnp.where(valid[:, None, None], coef, 0.0)
    return jnp.sum(coef * gathered, axis=0)


def on_device(
    query_mr,
    key_mr,
    value_mr,
    query_li,
    key_li,
    cotangent,
    mr_filter,
    norm_gain,
    li_decay,
    li_residue,
):
    row_count, chan_count = query_mr.shape
    group_count, tap_count = mr_filter.shape
    group_size = chan_count // group_count
    assert row_count == tap_count
    grad_scale = float(row_count * lax.axis_size("seq")) ** (-0.5)

    taps_mr = mr_filter.astype(jnp.bfloat16).astype(jnp.float32)
    zero_col = jnp.zeros((group_count, 1), jnp.float32)
    fwd_rows = jnp.concatenate(
        [zero_col, jnp.flip(taps_mr, 1), jnp.zeros((group_count, tap_count - 1), jnp.float32)], 1
    )
    bwd_rows = jnp.concatenate([taps_mr, jnp.zeros_like(taps_mr)], 1)

    mixed_mr = (key_mr.astype(jnp.float32) * value_mr.astype(jnp.float32)).astype(jnp.bfloat16)
    rim_rows = from_behind(mixed_mr, "seq", 1)
    conv_mr = band_conv(fwd_rows, rim_rows, mixed_mr, group_size=group_size, split=False, tri=None)
    out_mr = (query_mr.astype(jnp.float32) * conv_mr).astype(jnp.bfloat16)
    out_full = out_mr.astype(jnp.float32)
    squares = lax.psum(jnp.sum(out_full * out_full, axis=1), "chan")
    inv_rms = lax.rsqrt(squares / D + 1e-06)[:, None]
    normed = out_full * inv_rms * norm_gain
    mixed_li = key_li.astype(jnp.float32) * normed
    cotan_full = cotangent.astype(jnp.float32)
    back_li = cotan_full * query_li.astype(jnp.float32)

    offsets = jnp.arange(row_count, dtype=jnp.float32)
    weights_res = li_residue * jnp.sqrt(2.0 * li_decay)
    taps_li = jnp.einsum(
        "gr,grd->gd", weights_res, jnp.exp(-li_decay[:, :, None] * offsets), precision=HIGHEST
    )
    li_fwd_rows = jnp.concatenate([taps_li[:, :1], jnp.flip(taps_li[:, 1:], 1)], 1)
    fwd_states = jnp.exp(-li_decay[:, :, None] * (row_count - 1.0 - offsets))
    bwd_states = jnp.exp(-li_decay[:, :, None] * offsets)

    back_li_bf = back_li.astype(jnp.bfloat16)
    mixed_li_bf = mixed_li.astype(jnp.bfloat16)
    grad_st = modal_states(bwd_states, back_li_bf, group_size=group_size)
    grad_st, conv_mr = lax.optimization_barrier((grad_st, conv_mr))
    grad_ent = entering_states(grad_st, li_decay, row_count, group_size, False)
    grad_mixed_li = band_conv(
        taps_li, back_li_bf, None, (li_decay, weights_res, grad_ent),
        group_size=group_size, split=True, tri="upper", modal="backward",
    )
    conv_st = modal_states(fwd_states, mixed_li_bf, group_size=group_size)
    conv_ent = entering_states(conv_st, li_decay, row_count, group_size, True)
    conv_li = band_conv(
        li_fwd_rows, mixed_li_bf, None, (li_decay, weights_res, conv_ent),
        group_size=group_size, split=True, tri="lower", modal="forward",
    )

    out_li = (query_li.astype(jnp.float32) * conv_li).astype(jnp.bfloat16)
    grad_query_li = (cotan_full * conv_li).astype(jnp.bfloat16)
    grad_key_li = (grad_mixed_li * normed).astype(jnp.bfloat16)
    grad_normed = grad_mixed_li * key_li.astype(jnp.float32)
    gain_part = jnp.sum(grad_normed * out_full * inv_rms, axis=0)
    weighted = grad_normed * norm_gain
    cross_dots = lax.psum(jnp.sum(weighted * out_full, axis=1), "chan")[:, None]
    grad_out_mr = inv_rms * weighted - out_full * inv_rms**3 * cross_dots / D
    grad_query_mr = (grad_out_mr * conv_mr).astype(jnp.bfloat16)
    back_mr = (grad_out_mr * query_mr.astype(jnp.float32)).astype(jnp.bfloat16)
    after_rim = from_behind(back_mr, "seq", -1)
    grad_mixed_mr = band_conv(bwd_rows, back_mr, after_rim, group_size=group_size, split=False, tri=None)
    grad_key_mr = (grad_mixed_mr * value_mr.astype(jnp.float32)).astype(jnp.bfloat16)
    grad_value_mr = (grad_mixed_mr * key_mr.astype(jnp.float32)).astype(jnp.bfloat16)
    diag_sums = gram_diag(back_mr, rim_rows, mixed_mr, group_size=group_size)
    filter_part = jnp.flip(diag_sums[:, tap_count:], 1)
    packed = jnp.concatenate([gain_part, filter_part.reshape(-1)])
    param_sums = jnp.sum(gather_seq(packed), axis=0) * grad_scale
    grad_gain = param_sums[:chan_count]
    grad_filter = param_sums[chan_count:].reshape(group_count, tap_count)
    return (
        out_li,
        grad_query_mr,
        grad_key_mr,
        grad_value_mr,
        grad_query_li,
        grad_key_li,
        grad_gain,
        grad_filter,
    )


def solution(mesh):
    in_specs = (
        P("seq", "chan"),
        P("seq", "chan"),
        P("seq", "chan"),
        P("seq", "chan"),
        P("seq", "chan"),
        P("seq", "chan"),
        P("chan", None),
        P("chan"),
        P("chan", None),
        P("chan", None),
    )
    out_specs = (
        P("seq", "chan"),
        P("seq", "chan"),
        P("seq", "chan"),
        P("seq", "chan"),
        P("seq", "chan"),
        P("seq", "chan"),
        P("chan"),
        P("chan", None),
    )
    return jax.shard_map(
        on_device, mesh=mesh, in_specs=in_specs, out_specs=out_specs, check_vma=False
    )
```

```python
import functools

import jax
import jax.numpy as jnp
from jax import lax
from jax.experimental import pallas as pl
from jax.experimental.pallas import tpu as pltpu
from jax.sharding import PartitionSpec as P

D = 8192
G = 512
LANES = 128
HIGHEST = lax.Precision.HIGHEST


def from_behind(value, axis, steps):
    count = lax.axis_size(axis)
    initial, last = (max(0, -steps), min(count, count - steps))
    return lax.ppermute(value, axis, [(source, source + steps) for source in range(initial, last)])


def _split(value):
    high = value.astype(jnp.bfloat16)
    return high, (value - high.astype(jnp.float32)).astype(jnp.bfloat16)


def _band_kernel(*refs, group_size, split, tri, two_inputs, modal):
    refs = list(refs)
    h_ref = refs.pop(0)
    top_ref = refs.pop(0)
    bot_ref = refs.pop(0) if two_inputs else None
    if modal is not None:
        dec_ref, wt_ref, ent_ref = refs.pop(0), refs.pop(0), refs.pop(0)
    out_ref = refs.pop(0)
    if two_inputs:
        x = jnp.concatenate([top_ref[...], bot_ref[...]], axis=0)
    else:
        x = top_ref[...]
    width = x.shape[0]
    rows = out_ref.shape[0]
    groups_here = LANES // group_size
    lane_group = lax.broadcasted_iota(jnp.int32, (rows, LANES), 1) // group_size
    row_id = lax.broadcasted_iota(jnp.int32, (rows, width), 0)
    col_id = lax.broadcasted_iota(jnp.int32, (rows, width), 1)
    acc = jnp.zeros((rows, LANES), jnp.float32)
    if modal is not None:
        ent_high, ent_low = _split(ent_ref[...])
        modes = dec_ref.shape[1]
        offsets = lax.broadcasted_iota(jnp.int32, (rows, modes), 0).astype(jnp.float32)
        dist = offsets + 1.0 if modal == "forward" else float(rows) - offsets
    bands = []
    for k in range(groups_here):
        band_row = h_ref[pl.ds(k, 1), :]
        band = pltpu.roll(jnp.broadcast_to(band_row, (rows, width)), 0, 1, stride=1, stride_axis=0)
        if tri == "lower":
            band = jnp.where(col_id <= row_id, band, 0.0)
        elif tri == "upper":
            band = jnp.where(col_id >= row_id, band, 0.0)
        bands.append(band)
    stacked = jnp.concatenate(bands, axis=0)
    if split:
        high, low = _split(stacked)
        y = jnp.dot(high, x, preferred_element_type=jnp.float32)
        y = y + jnp.dot(low, x, preferred_element_type=jnp.float32)
    else:
        y = jnp.dot(stacked.astype(jnp.bfloat16), x, preferred_element_type=jnp.float32)
    if modal is not None:
        out_w = []
        for k in range(groups_here):
            rate = dec_ref[pl.ds(k, 1), :]
            weight = wt_ref[pl.ds(k, 1), :]
            out_w.append(weight * jnp.exp(-rate * dist))
        a_high, a_low = _split(jnp.concatenate(out_w, axis=0))
        y = y + jnp.dot(a_high, ent_high, preferred_element_type=jnp.float32)
        y = y + jnp.dot(a_low, ent_high, preferred_element_type=jnp.float32)
        y = y + jnp.dot(a_high, ent_low, preferred_element_type=jnp.float32)
    for k in range(groups_here):
        acc = jnp.where(lane_group == k, y[k * rows:(k + 1) * rows], acc)
    out_ref[...] = acc


def band_conv(band_rows, top, bottom=None, modal_args=None, *, group_size, split, tri, modal=None):
    rows, chans = top.shape
    groups_here = LANES // group_size
    blocks = chans // LANES
    width = band_rows.shape[1]
    two_inputs = bottom is not None
    in_specs = [
        pl.BlockSpec((groups_here, width), lambda b: (b, 0)),
        pl.BlockSpec((rows, LANES), lambda b: (0, b)),
    ]
    args = [band_rows, top]
    if two_inputs:
        in_specs.append(pl.BlockSpec((rows, LANES), lambda b: (0, b)))
        args.append(bottom)
    if modal is not None:
        decays, weights, entering = modal_args
        modes = decays.shape[1]
        in_specs += [
            pl.BlockSpec((groups_here, modes), lambda b: (b, 0)),
            pl.BlockSpec((groups_here, modes), lambda b: (b, 0)),
            pl.BlockSpec((modes, LANES), lambda b: (0, b)),
        ]
        args += [decays, weights, entering]
    kernel = functools.partial(
        _band_kernel,
        group_size=group_size,
        split=split,
        tri=tri,
        two_inputs=two_inputs,
        modal=modal,
    )
    return pl.pallas_call(
        kernel,
        grid=(blocks,),
        in_specs=in_specs,
        out_specs=pl.BlockSpec((rows, LANES), lambda b: (0, b)),
        out_shape=jax.ShapeDtypeStruct((rows, chans), jnp.float32),
        compiler_params=pltpu.CompilerParams(dimension_semantics=("parallel",)),
    )(*args)


def _state_kernel(e_ref, x_ref, s_ref, *, group_size):
    x = x_ref[...]
    modes = s_ref.shape[0]
    groups_here = LANES // group_size
    state_group = lax.broadcasted_iota(jnp.int32, (modes, LANES), 1) // group_size
    acc = jnp.zeros((modes, LANES), jnp.float32)
    weights = e_ref[...]
    high, low = _split(weights.reshape(groups_here * modes, weights.shape[2]))
    y = jnp.dot(high, x, preferred_element_type=jnp.float32)
    y = y + jnp.dot(low, x, preferred_element_type=jnp.float32)
    for k in range(groups_here):
        acc = jnp.where(state_group == k, y[k * modes:(k + 1) * modes], acc)
    s_ref[...] = acc


def modal_states(state_rows, x, *, group_size):
    rows, chans = x.shape
    groups_here = LANES // group_size
    modes = state_rows.shape[1]
    kernel = functools.partial(_state_kernel, group_size=group_size)
    return pl.pallas_call(
        kernel,
        grid=(chans // LANES,),
        in_specs=[
            pl.BlockSpec((groups_here, modes, rows), lambda b: (b, 0, 0)),
            pl.BlockSpec((rows, LANES), lambda b: (0, b)),
        ],
        out_specs=pl.BlockSpec((modes, LANES), lambda b: (0, b)),
        out_shape=jax.ShapeDtypeStruct((modes, chans), jnp.float32),
        compiler_params=pltpu.CompilerParams(dimension_semantics=("parallel",)),
    )(state_rows, x)


def _gram_kernel(back_ref, top_ref, bot_ref, f_ref, *, group_size):
    back = back_ref[...]
    x = jnp.concatenate([top_ref[...], bot_ref[...]], axis=0)
    rows = back.shape[0]
    groups_here = LANES // group_size
    r_id = lax.broadcasted_iota(jnp.int32, (rows, rows), 0)
    c_id = lax.broadcasted_iota(jnp.int32, (rows, rows), 1)
    exchange = jnp.where(r_id + c_id == rows - 1, 1.0, 0.0).astype(jnp.bfloat16)
    back_rev = jnp.dot(exchange, back, preferred_element_type=jnp.float32).astype(jnp.bfloat16)
    lane_group = lax.broadcasted_iota(jnp.int32, (rows, LANES), 1) // group_size
    masked = jnp.concatenate(
        [jnp.where(lane_group == k, back_rev, jnp.zeros_like(back_rev)) for k in range(groups_here)],
        axis=0,
    )
    gram = lax.dot_general(masked, x, (((1,), (1,)), ((), ())), preferred_element_type=jnp.float32)
    for k in range(groups_here):
        skew = pltpu.roll(gram[k * rows:(k + 1) * rows], 0, 1, stride=1, stride_axis=0)
        f_ref[pl.ds(k, 1), :] = jnp.sum(skew, axis=0, keepdims=True)


def gram_diag(back, top, bottom, *, group_size):
    rows, chans = back.shape
    groups_here = LANES // group_size
    group_count = chans // group_size
    kernel = functools.partial(_gram_kernel, group_size=group_size)
    return pl.pallas_call(
        kernel,
        grid=(chans // LANES,),
        in_specs=[
            pl.BlockSpec((rows, LANES), lambda b: (0, b)),
            pl.BlockSpec((rows, LANES), lambda b: (0, b)),
            pl.BlockSpec((rows, LANES), lambda b: (0, b)),
        ],
        out_specs=pl.BlockSpec((groups_here, 2 * rows), lambda b: (b, 0)),
        out_shape=jax.ShapeDtypeStruct((group_count, 2 * rows), jnp.float32),
        compiler_params=pltpu.CompilerParams(dimension_semantics=("parallel",)),
    )(back, top, bottom)


def gather_seq(value):
    count = lax.axis_size("seq")
    tiled = jnp.broadcast_to(value[None], (count,) + value.shape)
    return lax.all_to_all(tiled, "seq", split_axis=0, concat_axis=0, tiled=True)


def entering_states(states, decays, block_len, group_size, forward):
    gathered = gather_seq(states)
    count = gathered.shape[0]
    here = lax.axis_index("seq")
    rates = jnp.repeat(decays.T, group_size, axis=1)
    source = jnp.arange(count)
    if forward:
        gap = here - 1 - source
    else:
        gap = source - here - 1
    valid = gap >= 0
    steps = jnp.maximum(gap, 0).astype(jnp.float32)
    coef = jnp.exp(-rates[None] * (float(block_len) * steps)[:, None, None])
    coef = jnp.where(valid[:, None, None], coef, 0.0)
    return jnp.sum(coef * gathered, axis=0)


def on_device(
    query_mr,
    key_mr,
    value_mr,
    query_li,
    key_li,
    cotangent,
    mr_filter,
    norm_gain,
    li_decay,
    li_residue,
):
    row_count, chan_count = query_mr.shape
    group_count, tap_count = mr_filter.shape
    group_size = chan_count // group_count
    assert row_count == tap_count
    grad_scale = float(row_count * lax.axis_size("seq")) ** (-0.5)

    taps_mr = mr_filter.astype(jnp.bfloat16).astype(jnp.float32)
    zero_col = jnp.zeros((group_count, 1), jnp.float32)
    fwd_rows = jnp.concatenate(
        [zero_col, jnp.flip(taps_mr, 1), jnp.zeros((group_count, tap_count - 1), jnp.float32)], 1
    )
    bwd_rows = jnp.concatenate([taps_mr, jnp.zeros_like(taps_mr)], 1)

    mixed_mr = (key_mr.astype(jnp.float32) * value_mr.astype(jnp.float32)).astype(jnp.bfloat16)
    rim_rows = from_behind(mixed_mr, "seq", 1)
    conv_mr = band_conv(fwd_rows, rim_rows, mixed_mr, group_size=group_size, split=False, tri=None)
    out_mr = (query_mr.astype(jnp.float32) * conv_mr).astype(jnp.bfloat16)
    out_full = out_mr.astype(jnp.float32)
    squares = lax.psum(jnp.sum(out_full * out_full, axis=1), "chan")
    inv_rms = lax.rsqrt(squares / D + 1e-06)[:, None]
    normed = out_full * inv_rms * norm_gain
    mixed_li = key_li.astype(jnp.float32) * normed
    cotan_full = cotangent.astype(jnp.float32)
    back_li = cotan_full * query_li.astype(jnp.float32)

    offsets = jnp.arange(row_count, dtype=jnp.float32)
    weights_res = li_residue * jnp.sqrt(2.0 * li_decay)
    taps_li = jnp.einsum(
        "gr,grd->gd", weights_res, jnp.exp(-li_decay[:, :, None] * offsets), precision=HIGHEST
    )
    li_fwd_rows = jnp.concatenate([taps_li[:, :1], jnp.flip(taps_li[:, 1:], 1)], 1)
    fwd_states = jnp.exp(-li_decay[:, :, None] * (row_count - 1.0 - offsets))
    bwd_states = jnp.exp(-li_decay[:, :, None] * offsets)

    back_li_bf = back_li.astype(jnp.bfloat16)
    mixed_li_bf = mixed_li.astype(jnp.bfloat16)
    grad_st = modal_states(bwd_states, back_li_bf, group_size=group_size)
    grad_st, conv_mr = lax.optimization_barrier((grad_st, conv_mr))
    grad_ent = entering_states(grad_st, li_decay, row_count, group_size, False)
    grad_mixed_li = band_conv(
        taps_li, back_li_bf, None, (li_decay, weights_res, grad_ent),
        group_size=group_size, split=True, tri="upper", modal="backward",
    )
    conv_st = modal_states(fwd_states, mixed_li_bf, group_size=group_size)
    conv_ent = entering_states(conv_st, li_decay, row_count, group_size, True)
    conv_li = band_conv(
        li_fwd_rows, mixed_li_bf, None, (li_decay, weights_res, conv_ent),
        group_size=group_size, split=True, tri="lower", modal="forward",
    )

    out_li = (query_li.astype(jnp.float32) * conv_li).astype(jnp.bfloat16)
    grad_query_li = (cotan_full * conv_li).astype(jnp.bfloat16)
    grad_key_li = (grad_mixed_li * normed).astype(jnp.bfloat16)
    grad_normed = grad_mixed_li * key_li.astype(jnp.float32)
    gain_part = jnp.sum(grad_normed * out_full * inv_rms, axis=0)
    weighted = grad_normed * norm_gain
    cross_dots = lax.psum(jnp.sum(weighted * out_full, axis=1), "chan")[:, None]
    grad_out_mr = inv_rms * weighted - out_full * inv_rms**3 * cross_dots / D
    grad_query_mr = (grad_out_mr * conv_mr).astype(jnp.bfloat16)
    back_mr = (grad_out_mr * query_mr.astype(jnp.float32)).astype(jnp.bfloat16)
    after_rim = from_behind(back_mr, "seq", -1)
    grad_mixed_mr = band_conv(bwd_rows, back_mr, after_rim, group_size=group_size, split=False, tri=None)
    grad_key_mr = (grad_mixed_mr * value_mr.astype(jnp.float32)).astype(jnp.bfloat16)
    grad_value_mr = (grad_mixed_mr * key_mr.astype(jnp.float32)).astype(jnp.bfloat16)
    diag_sums = gram_diag(back_mr, rim_rows, mixed_mr, group_size=group_size)
    filter_part = jnp.flip(diag_sums[:, tap_count:], 1)
    packed = jnp.concatenate([gain_part, filter_part.reshape(-1)])
    param_sums = jnp.sum(gather_seq(packed), axis=0) * grad_scale
    grad_gain = param_sums[:chan_count]
    grad_filter = param_sums[chan_count:].reshape(group_count, tap_count)
    return (
        out_li,
        grad_query_mr,
        grad_key_mr,
        grad_value_mr,
        grad_query_li,
        grad_key_li,
        grad_gain,
        grad_filter,
    )


def solution(mesh):
    in_specs = (
        P("seq", "chan"),
        P("seq", "chan"),
        P("seq", "chan"),
        P("seq", "chan"),
        P("seq", "chan"),
        P("seq", "chan"),
        P("chan", None),
        P("chan"),
        P("chan", None),
        P("chan", None),
    )
    out_specs = (
        P("seq", "chan"),
        P("seq", "chan"),
        P("seq", "chan"),
        P("seq", "chan"),
        P("seq", "chan"),
        P("seq", "chan"),
        P("chan"),
        P("chan", None),
    )
    return jax.shard_map(
        on_device, mesh=mesh, in_specs=in_specs, out_specs=out_specs, check_vma=False
    )
```

```python
import functools

import jax
import jax.numpy as jnp
from jax import lax
from jax.experimental import pallas as pl
from jax.experimental.pallas import tpu as pltpu
from jax.sharding import PartitionSpec as P

D = 8192
G = 512
LANES = 128
BLOCK_LANES = 512
HIGHEST = lax.Precision.HIGHEST


def from_behind(value, axis, steps):
    count = lax.axis_size(axis)
    initial, last = (max(0, -steps), min(count, count - steps))
    return lax.ppermute(value, axis, [(source, source + steps) for source in range(initial, last)])


def _split(value):
    high = value.astype(jnp.bfloat16)
    return high, (value - high.astype(jnp.float32)).astype(jnp.bfloat16)


def _band_kernel(*refs, group_size, split, tri, two_inputs, modal, sub):
    refs = list(refs)
    h_ref = refs.pop(0)
    top_ref = refs.pop(0)
    bot_ref = refs.pop(0) if two_inputs else None
    if modal is not None:
        dec_ref, wt_ref, ent_ref = refs.pop(0), refs.pop(0), refs.pop(0)
    out_ref = refs.pop(0)
    rows = out_ref.shape[0]
    width = h_ref.shape[1]
    groups_here = LANES // group_size
    lane_group = lax.broadcasted_iota(jnp.int32, (rows, LANES), 1) // group_size
    row_id = lax.broadcasted_iota(jnp.int32, (rows, width), 0)
    col_id = lax.broadcasted_iota(jnp.int32, (rows, width), 1)
    if modal is not None:
        modes = dec_ref.shape[1]
        offsets = lax.broadcasted_iota(jnp.int32, (rows, modes), 0).astype(jnp.float32)
        dist = offsets + 1.0 if modal == "forward" else float(rows) - offsets

    def body(j, carry):
        lanes = pl.ds(pl.multiple_of(j * LANES, LANES), LANES)
        if two_inputs:
            x = jnp.concatenate([top_ref[:, lanes], bot_ref[:, lanes]], axis=0)
        else:
            x = top_ref[:, lanes]
        bands = []
        for k in range(groups_here):
            band_row = h_ref[pl.ds(j * groups_here + k, 1), :]
            band = pltpu.roll(jnp.broadcast_to(band_row, (rows, width)), 0, 1, stride=1, stride_axis=0)
            if tri == "lower":
                band = jnp.where(col_id <= row_id, band, 0.0)
            elif tri == "upper":
                band = jnp.where(col_id >= row_id, band, 0.0)
            bands.append(band)
        stacked = jnp.concatenate(bands, axis=0)
        if split:
            high, low = _split(stacked)
            y = jnp.dot(high, x, preferred_element_type=jnp.float32)
            y = y + jnp.dot(low, x, preferred_element_type=jnp.float32)
        else:
            y = jnp.dot(stacked.astype(jnp.bfloat16), x, preferred_element_type=jnp.float32)
        if modal is not None:
            ent_high, ent_low = _split(ent_ref[:, lanes])
            out_w = []
            for k in range(groups_here):
                rate = dec_ref[pl.ds(j * groups_here + k, 1), :]
                weight = wt_ref[pl.ds(j * groups_here + k, 1), :]
                out_w.append(weight * jnp.exp(-rate * dist))
            a_high, a_low = _split(jnp.concatenate(out_w, axis=0))
            y = y + jnp.dot(a_high, ent_high, preferred_element_type=jnp.float32)
            y = y + jnp.dot(a_low, ent_high, preferred_element_type=jnp.float32)
            y = y + jnp.dot(a_high, ent_low, preferred_element_type=jnp.float32)
        acc = y[:rows]
        for k in range(1, groups_here):
            acc = jnp.where(lane_group == k, y[k * rows:(k + 1) * rows], acc)
        out_ref[:, lanes] = acc
        return carry

    lax.fori_loop(0, sub, body, 0)


def band_conv(band_rows, top, bottom=None, modal_args=None, *, group_size, split, tri, modal=None):
    rows, chans = top.shape
    block = min(BLOCK_LANES, chans)
    groups_block = block // group_size
    width = band_rows.shape[1]
    two_inputs = bottom is not None
    in_specs = [
        pl.BlockSpec((groups_block, width), lambda b: (b, 0)),
        pl.BlockSpec((rows, block), lambda b: (0, b)),
    ]
    args = [band_rows, top]
    if two_inputs:
        in_specs.append(pl.BlockSpec((rows, block), lambda b: (0, b)))
        args.append(bottom)
    if modal is not None:
        decays, weights, entering = modal_args
        modes = decays.shape[1]
        in_specs += [
            pl.BlockSpec((groups_block, modes), lambda b: (b, 0)),
            pl.BlockSpec((groups_block, modes), lambda b: (b, 0)),
            pl.BlockSpec((modes, block), lambda b: (0, b)),
        ]
        args += [decays, weights, entering]
    kernel = functools.partial(
        _band_kernel,
        group_size=group_size,
        split=split,
        tri=tri,
        two_inputs=two_inputs,
        modal=modal,
        sub=block // LANES,
    )
    return pl.pallas_call(
        kernel,
        grid=(chans // block,),
        in_specs=in_specs,
        out_specs=pl.BlockSpec((rows, block), lambda b: (0, b)),
        out_shape=jax.ShapeDtypeStruct((rows, chans), jnp.float32),
        compiler_params=pltpu.CompilerParams(dimension_semantics=("parallel",)),
    )(*args)


def _state_kernel(e_ref, x_ref, s_ref, *, group_size, sub):
    modes = s_ref.shape[0]
    groups_here = LANES // group_size
    state_group = lax.broadcasted_iota(jnp.int32, (modes, LANES), 1) // group_size

    def body(j, carry):
        lanes = pl.ds(pl.multiple_of(j * LANES, LANES), LANES)
        x = x_ref[:, lanes]
        weights = e_ref[pl.ds(j * groups_here, groups_here)]
        high, low = _split(weights.reshape(groups_here * modes, weights.shape[2]))
        y = jnp.dot(high, x, preferred_element_type=jnp.float32)
        y = y + jnp.dot(low, x, preferred_element_type=jnp.float32)
        acc = y[:modes]
        for k in range(1, groups_here):
            acc = jnp.where(state_group == k, y[k * modes:(k + 1) * modes], acc)
        s_ref[:, lanes] = acc
        return carry

    lax.fori_loop(0, sub, body, 0)


def modal_states(state_rows, x, *, group_size):
    rows, chans = x.shape
    block = min(BLOCK_LANES, chans)
    groups_block = block // group_size
    modes = state_rows.shape[1]
    kernel = functools.partial(_state_kernel, group_size=group_size, sub=block // LANES)
    return pl.pallas_call(
        kernel,
        grid=(chans // block,),
        in_specs=[
            pl.BlockSpec((groups_block, modes, rows), lambda b: (b, 0, 0)),
            pl.BlockSpec((rows, block), lambda b: (0, b)),
        ],
        out_specs=pl.BlockSpec((modes, block), lambda b: (0, b)),
        out_shape=jax.ShapeDtypeStruct((modes, chans), jnp.float32),
        compiler_params=pltpu.CompilerParams(dimension_semantics=("parallel",)),
    )(state_rows, x)


def _gram_kernel(back_ref, top_ref, bot_ref, f_ref, *, group_size, sub):
    rows = back_ref.shape[0]
    groups_here = LANES // group_size
    r_id = lax.broadcasted_iota(jnp.int32, (rows, rows), 0)
    c_id = lax.broadcasted_iota(jnp.int32, (rows, rows), 1)
    exchange = jnp.where(r_id + c_id == rows - 1, 1.0, 0.0).astype(jnp.bfloat16)
    lane_group = lax.broadcasted_iota(jnp.int32, (rows, LANES), 1) // group_size

    def body(j, carry):
        lanes = pl.ds(pl.multiple_of(j * LANES, LANES), LANES)
        back = back_ref[:, lanes]
        x = jnp.concatenate([top_ref[:, lanes], bot_ref[:, lanes]], axis=0)
        back_rev = jnp.dot(exchange, back, preferred_element_type=jnp.float32).astype(jnp.bfloat16)
        masked = jnp.concatenate(
            [jnp.where(lane_group == k, back_rev, jnp.zeros_like(back_rev)) for k in range(groups_here)],
            axis=0,
        )
        gram = lax.dot_general(
            masked, x, (((1,), (1,)), ((), ())), preferred_element_type=jnp.float32
        )
        sums = []
        for k in range(groups_here):
            skew = pltpu.roll(gram[k * rows:(k + 1) * rows], 0, 1, stride=1, stride_axis=0)
            sums.append(jnp.sum(skew, axis=0, keepdims=True))
        f_ref[pl.ds(pl.multiple_of(j * groups_here, groups_here), groups_here), :] = jnp.concatenate(sums, 0)
        return carry

    lax.fori_loop(0, sub, body, 0)


def gram_diag(back, top, bottom, *, group_size):
    rows, chans = back.shape
    block = min(BLOCK_LANES, chans)
    groups_block = block // group_size
    group_count = chans // group_size
    kernel = functools.partial(_gram_kernel, group_size=group_size, sub=block // LANES)
    return pl.pallas_call(
        kernel,
        grid=(chans // block,),
        in_specs=[
            pl.BlockSpec((rows, block), lambda b: (0, b)),
            pl.BlockSpec((rows, block), lambda b: (0, b)),
            pl.BlockSpec((rows, block), lambda b: (0, b)),
        ],
        out_specs=pl.BlockSpec((groups_block, 2 * rows), lambda b: (b, 0)),
        out_shape=jax.ShapeDtypeStruct((group_count, 2 * rows), jnp.float32),
        compiler_params=pltpu.CompilerParams(dimension_semantics=("parallel",)),
    )(back, top, bottom)


def gather_seq(value):
    count = lax.axis_size("seq")
    tiled = jnp.broadcast_to(value[None], (count,) + value.shape)
    return lax.all_to_all(tiled, "seq", split_axis=0, concat_axis=0, tiled=True)


def entering_states(states, decays, block_len, group_size, forward):
    gathered = gather_seq(states)
    count = gathered.shape[0]
    here = lax.axis_index("seq")
    rates = jnp.repeat(decays.T, group_size, axis=1)
    source = jnp.arange(count)
    if forward:
        gap = here - 1 - source
    else:
        gap = source - here - 1
    valid = gap >= 0
    steps = jnp.maximum(gap, 0).astype(jnp.float32)
    coef = jnp.exp(-rates[None] * (float(block_len) * steps)[:, None, None])
    coef = jnp.where(valid[:, None, None], coef, 0.0)
    return jnp.sum(coef * gathered, axis=0)


def on_device(
    query_mr,
    key_mr,
    value_mr,
    query_li,
    key_li,
    cotangent,
    mr_filter,
    norm_gain,
    li_decay,
    li_residue,
):
    row_count, chan_count = query_mr.shape
    group_count, tap_count = mr_filter.shape
    group_size = chan_count // group_count
    assert row_count == tap_count
    grad_scale = float(row_count * lax.axis_size("seq")) ** (-0.5)

    taps_mr = mr_filter.astype(jnp.bfloat16).astype(jnp.float32)
    zero_col = jnp.zeros((group_count, 1), jnp.float32)
    fwd_rows = jnp.concatenate(
        [zero_col, jnp.flip(taps_mr, 1), jnp.zeros((group_count, tap_count - 1), jnp.float32)], 1
    )
    bwd_rows = jnp.concatenate([taps_mr, jnp.zeros_like(taps_mr)], 1)

    mixed_mr = (key_mr.astype(jnp.float32) * value_mr.astype(jnp.float32)).astype(jnp.bfloat16)
    rim_rows = from_behind(mixed_mr, "seq", 1)
    conv_mr = band_conv(fwd_rows, rim_rows, mixed_mr, group_size=group_size, split=False, tri=None)
    out_mr = (query_mr.astype(jnp.float32) * conv_mr).astype(jnp.bfloat16)
    out_full = out_mr.astype(jnp.float32)
    squares = lax.psum(jnp.sum(out_full * out_full, axis=1), "chan")
    inv_rms = lax.rsqrt(squares / D + 1e-06)[:, None]
    normed = out_full * inv_rms * norm_gain
    mixed_li = key_li.astype(jnp.float32) * normed
    cotan_full = cotangent.astype(jnp.float32)
    back_li = cotan_full * query_li.astype(jnp.float32)

    offsets = jnp.arange(row_count, dtype=jnp.float32)
    weights_res = li_residue * jnp.sqrt(2.0 * li_decay)
    taps_li = jnp.einsum(
        "gr,grd->gd", weights_res, jnp.exp(-li_decay[:, :, None] * offsets), precision=HIGHEST
    )
    li_fwd_rows = jnp.concatenate([taps_li[:, :1], jnp.flip(taps_li[:, 1:], 1)], 1)
    fwd_states = jnp.exp(-li_decay[:, :, None] * (row_count - 1.0 - offsets))
    bwd_states = jnp.exp(-li_decay[:, :, None] * offsets)

    back_li_bf = back_li.astype(jnp.bfloat16)
    mixed_li_bf = mixed_li.astype(jnp.bfloat16)
    grad_st = modal_states(bwd_states, back_li_bf, group_size=group_size)
    grad_st, conv_mr = lax.optimization_barrier((grad_st, conv_mr))
    grad_ent = entering_states(grad_st, li_decay, row_count, group_size, False)
    grad_mixed_li = band_conv(
        taps_li, back_li_bf, None, (li_decay, weights_res, grad_ent),
        group_size=group_size, split=True, tri="upper", modal="backward",
    )
    conv_st = modal_states(fwd_states, mixed_li_bf, group_size=group_size)
    conv_ent = entering_states(conv_st, li_decay, row_count, group_size, True)
    conv_li = band_conv(
        li_fwd_rows, mixed_li_bf, None, (li_decay, weights_res, conv_ent),
        group_size=group_size, split=True, tri="lower", modal="forward",
    )

    out_li = (query_li.astype(jnp.float32) * conv_li).astype(jnp.bfloat16)
    grad_query_li = (cotan_full * conv_li).astype(jnp.bfloat16)
    grad_key_li = (grad_mixed_li * normed).astype(jnp.bfloat16)
    grad_normed = grad_mixed_li * key_li.astype(jnp.float32)
    gain_part = jnp.sum(grad_normed * out_full * inv_rms, axis=0)
    weighted = grad_normed * norm_gain
    cross_dots = lax.psum(jnp.sum(weighted * out_full, axis=1), "chan")[:, None]
    grad_out_mr = inv_rms * weighted - out_full * inv_rms**3 * cross_dots / D
    grad_query_mr = (grad_out_mr * conv_mr).astype(jnp.bfloat16)
    back_mr = (grad_out_mr * query_mr.astype(jnp.float32)).astype(jnp.bfloat16)
    after_rim = from_behind(back_mr, "seq", -1)
    grad_mixed_mr = band_conv(bwd_rows, back_mr, after_rim, group_size=group_size, split=False, tri=None)
    grad_key_mr = (grad_mixed_mr * value_mr.astype(jnp.float32)).astype(jnp.bfloat16)
    grad_value_mr = (grad_mixed_mr * key_mr.astype(jnp.float32)).astype(jnp.bfloat16)
    diag_sums = gram_diag(back_mr, rim_rows, mixed_mr, group_size=group_size)
    filter_part = jnp.flip(diag_sums[:, tap_count:], 1)
    packed = jnp.concatenate([gain_part, filter_part.reshape(-1)])
    param_sums = jnp.sum(gather_seq(packed), axis=0) * grad_scale
    grad_gain = param_sums[:chan_count]
    grad_filter = param_sums[chan_count:].reshape(group_count, tap_count)
    return (
        out_li,
        grad_query_mr,
        grad_key_mr,
        grad_value_mr,
        grad_query_li,
        grad_key_li,
        grad_gain,
        grad_filter,
    )


def solution(mesh):
    in_specs = (
        P("seq", "chan"),
        P("seq", "chan"),
        P("seq", "chan"),
        P("seq", "chan"),
        P("seq", "chan"),
        P("seq", "chan"),
        P("chan", None),
        P("chan"),
        P("chan", None),
        P("chan", None),
    )
    out_specs = (
        P("seq", "chan"),
        P("seq", "chan"),
        P("seq", "chan"),
        P("seq", "chan"),
        P("seq", "chan"),
        P("seq", "chan"),
        P("chan"),
        P("chan", None),
    )
    return jax.shard_map(
        on_device, mesh=mesh, in_specs=in_specs, out_specs=out_specs, check_vma=False
    )
```

```python
import functools

import jax
import jax.numpy as jnp
from jax import lax
from jax.experimental import pallas as pl
from jax.experimental.pallas import tpu as pltpu
from jax.sharding import PartitionSpec as P

D = 8192
G = 512
LANES = 128
BLOCK_LANES = 512
HIGHEST = lax.Precision.HIGHEST


def from_behind(value, axis, steps):
    count = lax.axis_size(axis)
    initial, last = (max(0, -steps), min(count, count - steps))
    return lax.ppermute(value, axis, [(source, source + steps) for source in range(initial, last)])


def _split(value):
    high = value.astype(jnp.bfloat16)
    return high, (value - high.astype(jnp.float32)).astype(jnp.bfloat16)


def _band_kernel(*refs, group_size, split, tri, two_inputs, modal, sub):
    refs = list(refs)
    h_ref = refs.pop(0)
    top_ref = refs.pop(0)
    bot_ref = refs.pop(0) if two_inputs else None
    if modal is not None:
        dec_ref, wt_ref, ent_ref = refs.pop(0), refs.pop(0), refs.pop(0)
    out_ref = refs.pop(0)
    rows = out_ref.shape[0]
    width = h_ref.shape[1]
    groups_here = LANES // group_size
    lane_group = lax.broadcasted_iota(jnp.int32, (rows, LANES), 1) // group_size
    row_id = lax.broadcasted_iota(jnp.int32, (rows, width), 0)
    col_id = lax.broadcasted_iota(jnp.int32, (rows, width), 1)
    if modal is not None:
        modes = dec_ref.shape[1]
        offsets = lax.broadcasted_iota(jnp.int32, (rows, modes), 0).astype(jnp.float32)
        dist = offsets + 1.0 if modal == "forward" else float(rows) - offsets

    def body(j, carry):
        lanes = pl.ds(pl.multiple_of(j * LANES, LANES), LANES)
        if two_inputs:
            x = jnp.concatenate([top_ref[:, lanes], bot_ref[:, lanes]], axis=0)
        else:
            x = top_ref[:, lanes]
        bands = []
        for k in range(groups_here):
            band_row = h_ref[pl.ds(j * groups_here + k, 1), :]
            band = pltpu.roll(jnp.broadcast_to(band_row, (rows, width)), 0, 1, stride=1, stride_axis=0)
            if tri == "lower":
                band = jnp.where(col_id <= row_id, band, 0.0)
            elif tri == "upper":
                band = jnp.where(col_id >= row_id, band, 0.0)
            bands.append(band)
        stacked = jnp.concatenate(bands, axis=0)
        if split:
            high, low = _split(stacked)
            y = jnp.dot(high, x, preferred_element_type=jnp.float32)
            y = y + jnp.dot(low, x, preferred_element_type=jnp.float32)
        else:
            y = jnp.dot(stacked.astype(jnp.bfloat16), x, preferred_element_type=jnp.float32)
        if modal is not None:
            ent_high, ent_low = _split(ent_ref[:, lanes])
            out_w = []
            for k in range(groups_here):
                rate = dec_ref[pl.ds(j * groups_here + k, 1), :]
                weight = wt_ref[pl.ds(j * groups_here + k, 1), :]
                out_w.append(weight * jnp.exp(-rate * dist))
            a_high, a_low = _split(jnp.concatenate(out_w, axis=0))
            y = y + jnp.dot(a_high, ent_high, preferred_element_type=jnp.float32)
            y = y + jnp.dot(a_low, ent_high, preferred_element_type=jnp.float32)
            y = y + jnp.dot(a_high, ent_low, preferred_element_type=jnp.float32)
        acc = y[:rows]
        for k in range(1, groups_here):
            acc = jnp.where(lane_group == k, y[k * rows:(k + 1) * rows], acc)
        out_ref[:, lanes] = acc
        return carry

    lax.fori_loop(0, sub, body, 0)


def band_conv(band_rows, top, bottom=None, modal_args=None, *, group_size, split, tri, modal=None):
    rows, chans = top.shape
    block = min(BLOCK_LANES, chans)
    groups_block = block // group_size
    width = band_rows.shape[1]
    two_inputs = bottom is not None
    in_specs = [
        pl.BlockSpec((groups_block, width), lambda b: (b, 0)),
        pl.BlockSpec((rows, block), lambda b: (0, b)),
    ]
    args = [band_rows, top]
    if two_inputs:
        in_specs.append(pl.BlockSpec((rows, block), lambda b: (0, b)))
        args.append(bottom)
    if modal is not None:
        decays, weights, entering = modal_args
        modes = decays.shape[1]
        in_specs += [
            pl.BlockSpec((groups_block, modes), lambda b: (b, 0)),
            pl.BlockSpec((groups_block, modes), lambda b: (b, 0)),
            pl.BlockSpec((modes, block), lambda b: (0, b)),
        ]
        args += [decays, weights, entering]
    kernel = functools.partial(
        _band_kernel,
        group_size=group_size,
        split=split,
        tri=tri,
        two_inputs=two_inputs,
        modal=modal,
        sub=block // LANES,
    )
    return pl.pallas_call(
        kernel,
        grid=(chans // block,),
        in_specs=in_specs,
        out_specs=pl.BlockSpec((rows, block), lambda b: (0, b)),
        out_shape=jax.ShapeDtypeStruct((rows, chans), jnp.float32),
        compiler_params=pltpu.CompilerParams(dimension_semantics=("parallel",)),
    )(*args)


def _state_kernel(e_ref, x_ref, s_ref, *, group_size, sub):
    modes = s_ref.shape[0]
    groups_here = LANES // group_size
    state_group = lax.broadcasted_iota(jnp.int32, (modes, LANES), 1) // group_size

    def body(j, carry):
        lanes = pl.ds(pl.multiple_of(j * LANES, LANES), LANES)
        x = x_ref[:, lanes]
        weights = e_ref[pl.ds(j * groups_here, groups_here)]
        high, low = _split(weights.reshape(groups_here * modes, weights.shape[2]))
        y = jnp.dot(high, x, preferred_element_type=jnp.float32)
        y = y + jnp.dot(low, x, preferred_element_type=jnp.float32)
        acc = y[:modes]
        for k in range(1, groups_here):
            acc = jnp.where(state_group == k, y[k * modes:(k + 1) * modes], acc)
        s_ref[:, lanes] = acc
        return carry

    lax.fori_loop(0, sub, body, 0)


def modal_states(state_rows, x, *, group_size):
    rows, chans = x.shape
    block = min(BLOCK_LANES, chans)
    groups_block = block // group_size
    modes = state_rows.shape[1]
    kernel = functools.partial(_state_kernel, group_size=group_size, sub=block // LANES)
    return pl.pallas_call(
        kernel,
        grid=(chans // block,),
        in_specs=[
            pl.BlockSpec((groups_block, modes, rows), lambda b: (b, 0, 0)),
            pl.BlockSpec((rows, block), lambda b: (0, b)),
        ],
        out_specs=pl.BlockSpec((modes, block), lambda b: (0, b)),
        out_shape=jax.ShapeDtypeStruct((modes, chans), jnp.float32),
        compiler_params=pltpu.CompilerParams(dimension_semantics=("parallel",)),
    )(state_rows, x)


def _modal_kernel(dec_ref, wt_ref, ent_ref, loc_ref, out_ref, *, group_size, forward, sub):
    rows = out_ref.shape[0]
    modes = dec_ref.shape[1]
    groups_here = LANES // group_size
    lane_group = lax.broadcasted_iota(jnp.int32, (rows, LANES), 1) // group_size
    offsets = lax.broadcasted_iota(jnp.int32, (rows, modes), 0).astype(jnp.float32)
    dist = offsets + 1.0 if forward else float(rows) - offsets

    def body(j, carry):
        lanes = pl.ds(pl.multiple_of(j * LANES, LANES), LANES)
        ent_high, ent_low = _split(ent_ref[:, lanes])
        out_w = []
        for k in range(groups_here):
            rate = dec_ref[pl.ds(j * groups_here + k, 1), :]
            weight = wt_ref[pl.ds(j * groups_here + k, 1), :]
            out_w.append(weight * jnp.exp(-rate * dist))
        a_high, a_low = _split(jnp.concatenate(out_w, axis=0))
        y = jnp.dot(a_high, ent_high, preferred_element_type=jnp.float32)
        y = y + jnp.dot(a_low, ent_high, preferred_element_type=jnp.float32)
        y = y + jnp.dot(a_high, ent_low, preferred_element_type=jnp.float32)
        acc = y[:rows]
        for k in range(1, groups_here):
            acc = jnp.where(lane_group == k, y[k * rows:(k + 1) * rows], acc)
        out_ref[:, lanes] = loc_ref[:, lanes] + acc
        return carry

    lax.fori_loop(0, sub, body, 0)


def modal_out(decays, weights, entering, local, *, group_size, forward):
    rows, chans = local.shape
    block = min(BLOCK_LANES, chans)
    groups_block = block // group_size
    modes = decays.shape[1]
    kernel = functools.partial(
        _modal_kernel, group_size=group_size, forward=forward, sub=block // LANES
    )
    return pl.pallas_call(
        kernel,
        grid=(chans // block,),
        in_specs=[
            pl.BlockSpec((groups_block, modes), lambda b: (b, 0)),
            pl.BlockSpec((groups_block, modes), lambda b: (b, 0)),
            pl.BlockSpec((modes, block), lambda b: (0, b)),
            pl.BlockSpec((rows, block), lambda b: (0, b)),
        ],
        out_specs=pl.BlockSpec((rows, block), lambda b: (0, b)),
        out_shape=jax.ShapeDtypeStruct((rows, chans), jnp.float32),
        compiler_params=pltpu.CompilerParams(dimension_semantics=("parallel",)),
    )(decays, weights, entering, local)


def _gram_kernel(back_ref, top_ref, bot_ref, f_ref, *, group_size, sub):
    rows = back_ref.shape[0]
    groups_here = LANES // group_size
    r_id = lax.broadcasted_iota(jnp.int32, (rows, rows), 0)
    c_id = lax.broadcasted_iota(jnp.int32, (rows, rows), 1)
    exchange = jnp.where(r_id + c_id == rows - 1, 1.0, 0.0).astype(jnp.bfloat16)
    lane_group = lax.broadcasted_iota(jnp.int32, (rows, LANES), 1) // group_size

    def body(j, carry):
        lanes = pl.ds(pl.multiple_of(j * LANES, LANES), LANES)
        back = back_ref[:, lanes]
        x = jnp.concatenate([top_ref[:, lanes], bot_ref[:, lanes]], axis=0)
        back_rev = jnp.dot(exchange, back, preferred_element_type=jnp.float32).astype(jnp.bfloat16)
        masked = jnp.concatenate(
            [jnp.where(lane_group == k, back_rev, jnp.zeros_like(back_rev)) for k in range(groups_here)],
            axis=0,
        )
        gram = lax.dot_general(
            masked, x, (((1,), (1,)), ((), ())), preferred_element_type=jnp.float32
        )
        sums = []
        for k in range(groups_here):
            skew = pltpu.roll(gram[k * rows:(k + 1) * rows], 0, 1, stride=1, stride_axis=0)
            sums.append(jnp.sum(skew, axis=0, keepdims=True))
        f_ref[pl.ds(pl.multiple_of(j * groups_here, groups_here), groups_here), :] = jnp.concatenate(sums, 0)
        return carry

    lax.fori_loop(0, sub, body, 0)


def gram_diag(back, top, bottom, *, group_size):
    rows, chans = back.shape
    block = min(BLOCK_LANES, chans)
    groups_block = block // group_size
    group_count = chans // group_size
    kernel = functools.partial(_gram_kernel, group_size=group_size, sub=block // LANES)
    return pl.pallas_call(
        kernel,
        grid=(chans // block,),
        in_specs=[
            pl.BlockSpec((rows, block), lambda b: (0, b)),
            pl.BlockSpec((rows, block), lambda b: (0, b)),
            pl.BlockSpec((rows, block), lambda b: (0, b)),
        ],
        out_specs=pl.BlockSpec((groups_block, 2 * rows), lambda b: (b, 0)),
        out_shape=jax.ShapeDtypeStruct((group_count, 2 * rows), jnp.float32),
        compiler_params=pltpu.CompilerParams(dimension_semantics=("parallel",)),
    )(back, top, bottom)


def gather_seq(value):
    count = lax.axis_size("seq")
    tiled = jnp.broadcast_to(value[None], (count,) + value.shape)
    return lax.all_to_all(tiled, "seq", split_axis=0, concat_axis=0, tiled=True)


def entering_states(gathered, decays, block_len, group_size, forward):
    count = gathered.shape[0]
    here = lax.axis_index("seq")
    rates = jnp.repeat(decays.T, group_size, axis=1)
    source = jnp.arange(count)
    if forward:
        gap = here - 1 - source
    else:
        gap = source - here - 1
    valid = gap >= 0
    steps = jnp.maximum(gap, 0).astype(jnp.float32)
    coef = jnp.exp(-rates[None] * (float(block_len) * steps)[:, None, None])
    coef = jnp.where(valid[:, None, None], coef, 0.0)
    return jnp.sum(coef * gathered, axis=0)


def on_device(
    query_mr,
    key_mr,
    value_mr,
    query_li,
    key_li,
    cotangent,
    mr_filter,
    norm_gain,
    li_decay,
    li_residue,
):
    row_count, chan_count = query_mr.shape
    group_count, tap_count = mr_filter.shape
    group_size = chan_count // group_count
    assert row_count == tap_count
    grad_scale = float(row_count * lax.axis_size("seq")) ** (-0.5)

    taps_mr = mr_filter.astype(jnp.bfloat16).astype(jnp.float32)
    zero_col = jnp.zeros((group_count, 1), jnp.float32)
    fwd_rows = jnp.concatenate(
        [zero_col, jnp.flip(taps_mr, 1), jnp.zeros((group_count, tap_count - 1), jnp.float32)], 1
    )
    bwd_rows = jnp.concatenate([taps_mr, jnp.zeros_like(taps_mr)], 1)

    mixed_mr = (key_mr.astype(jnp.float32) * value_mr.astype(jnp.float32)).astype(jnp.bfloat16)
    rim_rows = from_behind(mixed_mr, "seq", 1)
    conv_mr = band_conv(fwd_rows, rim_rows, mixed_mr, group_size=group_size, split=False, tri=None)
    out_mr = (query_mr.astype(jnp.float32) * conv_mr).astype(jnp.bfloat16)
    out_full = out_mr.astype(jnp.float32)
    squares = lax.psum(jnp.sum(out_full * out_full, axis=1), "chan")
    inv_rms = lax.rsqrt(squares / D + 1e-06)[:, None]
    normed = out_full * inv_rms * norm_gain
    mixed_li = key_li.astype(jnp.float32) * normed
    cotan_full = cotangent.astype(jnp.float32)
    back_li = cotan_full * query_li.astype(jnp.float32)

    offsets = jnp.arange(row_count, dtype=jnp.float32)
    weights_res = li_residue * jnp.sqrt(2.0 * li_decay)
    taps_li = jnp.einsum(
        "gr,grd->gd", weights_res, jnp.exp(-li_decay[:, :, None] * offsets), precision=HIGHEST
    )
    li_fwd_rows = jnp.concatenate([taps_li[:, :1], jnp.flip(taps_li[:, 1:], 1)], 1)
    fwd_states = jnp.exp(-li_decay[:, :, None] * (row_count - 1.0 - offsets))
    bwd_states = jnp.exp(-li_decay[:, :, None] * offsets)

    back_li_bf = back_li.astype(jnp.bfloat16)
    mixed_li_bf = mixed_li.astype(jnp.bfloat16)
    modes = li_decay.shape[1]
    grad_st = modal_states(bwd_states, back_li_bf, group_size=group_size)
    conv_st = modal_states(fwd_states, mixed_li_bf, group_size=group_size)
    both_st = gather_seq(jnp.concatenate([grad_st, conv_st], 0).astype(jnp.bfloat16))
    both_st = both_st.astype(jnp.float32)
    grad_loc = band_conv(taps_li, back_li_bf, group_size=group_size, split=True, tri="upper")
    conv_loc = band_conv(li_fwd_rows, mixed_li_bf, group_size=group_size, split=True, tri="lower")
    grad_ent = entering_states(both_st[:, :modes], li_decay, row_count, group_size, False)
    conv_ent = entering_states(both_st[:, modes:], li_decay, row_count, group_size, True)
    grad_mixed_li = modal_out(
        li_decay, weights_res, grad_ent, grad_loc, group_size=group_size, forward=False
    )
    conv_li = modal_out(li_decay, weights_res, conv_ent, conv_loc, group_size=group_size, forward=True)

    out_li = (query_li.astype(jnp.float32) * conv_li).astype(jnp.bfloat16)
    grad_query_li = (cotan_full * conv_li).astype(jnp.bfloat16)
    grad_key_li = (grad_mixed_li * normed).astype(jnp.bfloat16)
    grad_normed = grad_mixed_li * key_li.astype(jnp.float32)
    gain_part = jnp.sum(grad_normed * out_full * inv_rms, axis=0)
    weighted = grad_normed * norm_gain
    cross_dots = lax.psum(jnp.sum(weighted * out_full, axis=1), "chan")[:, None]
    grad_out_mr = inv_rms * weighted - out_full * inv_rms**3 * cross_dots / D
    grad_query_mr = (grad_out_mr * conv_mr).astype(jnp.bfloat16)
    back_mr = (grad_out_mr * query_mr.astype(jnp.float32)).astype(jnp.bfloat16)
    after_rim = from_behind(back_mr, "seq", -1)
    grad_mixed_mr = band_conv(bwd_rows, back_mr, after_rim, group_size=group_size, split=False, tri=None)
    grad_key_mr = (grad_mixed_mr * value_mr.astype(jnp.float32)).astype(jnp.bfloat16)
    grad_value_mr = (grad_mixed_mr * key_mr.astype(jnp.float32)).astype(jnp.bfloat16)
    diag_sums = gram_diag(back_mr, rim_rows, mixed_mr, group_size=group_size)
    filter_part = jnp.flip(diag_sums[:, tap_count:], 1)
    packed = jnp.concatenate([gain_part, filter_part.reshape(-1)])
    param_sums = jnp.sum(gather_seq(packed), axis=0) * grad_scale
    grad_gain = param_sums[:chan_count]
    grad_filter = param_sums[chan_count:].reshape(group_count, tap_count)
    return (
        out_li,
        grad_query_mr,
        grad_key_mr,
        grad_value_mr,
        grad_query_li,
        grad_key_li,
        grad_gain,
        grad_filter,
    )


def solution(mesh):
    in_specs = (
        P("seq", "chan"),
        P("seq", "chan"),
        P("seq", "chan"),
        P("seq", "chan"),
        P("seq", "chan"),
        P("seq", "chan"),
        P("chan", None),
        P("chan"),
        P("chan", None),
        P("chan", None),
    )
    out_specs = (
        P("seq", "chan"),
        P("seq", "chan"),
        P("seq", "chan"),
        P("seq", "chan"),
        P("seq", "chan"),
        P("seq", "chan"),
        P("chan"),
        P("chan", None),
    )
    return jax.shard_map(
        on_device, mesh=mesh, in_specs=in_specs, out_specs=out_specs, check_vma=False
    )
```

```python
import functools

import jax
import jax.numpy as jnp
from jax import lax
from jax.experimental import pallas as pl
from jax.experimental.pallas import tpu as pltpu
from jax.sharding import PartitionSpec as P

D = 8192
G = 512
LANES = 128
BLOCK_LANES = 512
HIGHEST = lax.Precision.HIGHEST


def from_behind(value, axis, steps):
    count = lax.axis_size(axis)
    initial, last = (max(0, -steps), min(count, count - steps))
    return lax.ppermute(value, axis, [(source, source + steps) for source in range(initial, last)])


def _split(value):
    high = value.astype(jnp.bfloat16)
    return high, (value - high.astype(jnp.float32)).astype(jnp.bfloat16)


def _band_kernel(*refs, group_size, split, tri, two_inputs, modal, sub):
    refs = list(refs)
    h_ref = refs.pop(0)
    top_ref = refs.pop(0)
    bot_ref = refs.pop(0) if two_inputs else None
    if modal is not None:
        dec_ref, wt_ref, ent_ref = refs.pop(0), refs.pop(0), refs.pop(0)
    out_ref = refs.pop(0)
    rows = out_ref.shape[0]
    width = h_ref.shape[1]
    groups_here = LANES // group_size
    lane_group = lax.broadcasted_iota(jnp.int32, (rows, LANES), 1) // group_size
    row_id = lax.broadcasted_iota(jnp.int32, (rows, width), 0)
    col_id = lax.broadcasted_iota(jnp.int32, (rows, width), 1)
    if modal is not None:
        modes = dec_ref.shape[1]
        offsets = lax.broadcasted_iota(jnp.int32, (rows, modes), 0).astype(jnp.float32)
        dist = offsets + 1.0 if modal == "forward" else float(rows) - offsets

    def body(j, carry):
        lanes = pl.ds(pl.multiple_of(j * LANES, LANES), LANES)
        if two_inputs:
            x = jnp.concatenate([top_ref[:, lanes], bot_ref[:, lanes]], axis=0)
        else:
            x = top_ref[:, lanes]
        bands = []
        for k in range(groups_here):
            band_row = h_ref[pl.ds(j * groups_here + k, 1), :]
            band = pltpu.roll(jnp.broadcast_to(band_row, (rows, width)), 0, 1, stride=1, stride_axis=0)
            if tri == "lower":
                band = jnp.where(col_id <= row_id, band, 0.0)
            elif tri == "upper":
                band = jnp.where(col_id >= row_id, band, 0.0)
            bands.append(band)
        stacked = jnp.concatenate(bands, axis=0)
        if split:
            high, low = _split(stacked)
            y = jnp.dot(high, x, preferred_element_type=jnp.float32)
            y = y + jnp.dot(low, x, preferred_element_type=jnp.float32)
        else:
            y = jnp.dot(stacked.astype(jnp.bfloat16), x, preferred_element_type=jnp.float32)
        if modal is not None:
            ent_high, ent_low = _split(ent_ref[:, lanes])
            out_w = []
            for k in range(groups_here):
                rate = dec_ref[pl.ds(j * groups_here + k, 1), :]
                weight = wt_ref[pl.ds(j * groups_here + k, 1), :]
                out_w.append(weight * jnp.exp(-rate * dist))
            a_high, a_low = _split(jnp.concatenate(out_w, axis=0))
            y = y + jnp.dot(a_high, ent_high, preferred_element_type=jnp.float32)
            y = y + jnp.dot(a_low, ent_high, preferred_element_type=jnp.float32)
            y = y + jnp.dot(a_high, ent_low, preferred_element_type=jnp.float32)
        acc = y[:rows]
        for k in range(1, groups_here):
            acc = jnp.where(lane_group == k, y[k * rows:(k + 1) * rows], acc)
        out_ref[:, lanes] = acc
        return carry

    lax.fori_loop(0, sub, body, 0)


def band_conv(band_rows, top, bottom=None, modal_args=None, *, group_size, split, tri, modal=None):
    rows, chans = top.shape
    block = min(BLOCK_LANES, chans)
    groups_block = block // group_size
    width = band_rows.shape[1]
    two_inputs = bottom is not None
    in_specs = [
        pl.BlockSpec((groups_block, width), lambda b: (b, 0)),
        pl.BlockSpec((rows, block), lambda b: (0, b)),
    ]
    args = [band_rows, top]
    if two_inputs:
        in_specs.append(pl.BlockSpec((rows, block), lambda b: (0, b)))
        args.append(bottom)
    if modal is not None:
        decays, weights, entering = modal_args
        modes = decays.shape[1]
        in_specs += [
            pl.BlockSpec((groups_block, modes), lambda b: (b, 0)),
            pl.BlockSpec((groups_block, modes), lambda b: (b, 0)),
            pl.BlockSpec((modes, block), lambda b: (0, b)),
        ]
        args += [decays, weights, entering]
    kernel = functools.partial(
        _band_kernel,
        group_size=group_size,
        split=split,
        tri=tri,
        two_inputs=two_inputs,
        modal=modal,
        sub=block // LANES,
    )
    return pl.pallas_call(
        kernel,
        grid=(chans // block,),
        in_specs=in_specs,
        out_specs=pl.BlockSpec((rows, block), lambda b: (0, b)),
        out_shape=jax.ShapeDtypeStruct((rows, chans), jnp.float32),
        compiler_params=pltpu.CompilerParams(dimension_semantics=("parallel",)),
    )(*args)


def _state_kernel(e_ref, x_ref, s_ref, *, group_size, sub):
    modes = s_ref.shape[0]
    groups_here = LANES // group_size
    state_group = lax.broadcasted_iota(jnp.int32, (modes, LANES), 1) // group_size

    def body(j, carry):
        lanes = pl.ds(pl.multiple_of(j * LANES, LANES), LANES)
        x = x_ref[:, lanes]
        weights = e_ref[pl.ds(j * groups_here, groups_here)]
        high, low = _split(weights.reshape(groups_here * modes, weights.shape[2]))
        y = jnp.dot(high, x, preferred_element_type=jnp.float32)
        y = y + jnp.dot(low, x, preferred_element_type=jnp.float32)
        acc = y[:modes]
        for k in range(1, groups_here):
            acc = jnp.where(state_group == k, y[k * modes:(k + 1) * modes], acc)
        s_ref[:, lanes] = acc
        return carry

    lax.fori_loop(0, sub, body, 0)


def modal_states(state_rows, x, *, group_size):
    rows, chans = x.shape
    block = min(BLOCK_LANES, chans)
    groups_block = block // group_size
    modes = state_rows.shape[1]
    kernel = functools.partial(_state_kernel, group_size=group_size, sub=block // LANES)
    return pl.pallas_call(
        kernel,
        grid=(chans // block,),
        in_specs=[
            pl.BlockSpec((groups_block, modes, rows), lambda b: (b, 0, 0)),
            pl.BlockSpec((rows, block), lambda b: (0, b)),
        ],
        out_specs=pl.BlockSpec((modes, block), lambda b: (0, b)),
        out_shape=jax.ShapeDtypeStruct((modes, chans), jnp.float32),
        compiler_params=pltpu.CompilerParams(dimension_semantics=("parallel",)),
    )(state_rows, x)


def _modal_kernel(dec_ref, wt_ref, ent_ref, loc_ref, out_ref, *, group_size, forward, sub):
    rows = out_ref.shape[0]
    modes = ent_ref.shape[0]
    groups_here = LANES // group_size
    width = groups_here * modes
    offsets = lax.broadcasted_iota(jnp.int32, (rows, width), 0).astype(jnp.float32)
    dist = offsets + 1.0 if forward else float(rows) - offsets
    row_group = lax.broadcasted_iota(jnp.int32, (width, LANES), 0) // modes
    lane_group = lax.broadcasted_iota(jnp.int32, (width, LANES), 1) // group_size

    def body(j, carry):
        lanes = pl.ds(pl.multiple_of(j * LANES, LANES), LANES)
        row = pl.program_id(0) * sub + j
        rate = dec_ref[pl.ds(row, 1), :]
        weight = wt_ref[pl.ds(row, 1), :]
        a_high, a_low = _split(weight * jnp.exp(-rate * dist))
        entering = ent_ref[:, lanes]
        tiled = jnp.concatenate([entering] * groups_here, axis=0)
        diag = jnp.where(row_group == lane_group, tiled, 0.0)
        ent_high, ent_low = _split(diag)
        y = jnp.dot(a_high, ent_high, preferred_element_type=jnp.float32)
        y = y + jnp.dot(a_low, ent_high, preferred_element_type=jnp.float32)
        y = y + jnp.dot(a_high, ent_low, preferred_element_type=jnp.float32)
        out_ref[:, lanes] = loc_ref[:, lanes] + y
        return carry

    lax.fori_loop(0, sub, body, 0)


def modal_out(decays, weights, entering, local, *, group_size, forward):
    rows, chans = local.shape
    block = min(BLOCK_LANES, chans)
    groups_block = block // group_size
    modes = decays.shape[1]
    per_row = (LANES // group_size) * modes
    flat_decays = decays.reshape(-1, per_row)
    flat_weights = weights.reshape(-1, per_row)
    sub = block // LANES
    kernel = functools.partial(_modal_kernel, group_size=group_size, forward=forward, sub=sub)
    return pl.pallas_call(
        kernel,
        grid=(chans // block,),
        in_specs=[
            pl.BlockSpec(flat_decays.shape, lambda b: (0, 0)),
            pl.BlockSpec(flat_weights.shape, lambda b: (0, 0)),
            pl.BlockSpec((modes, block), lambda b: (0, b)),
            pl.BlockSpec((rows, block), lambda b: (0, b)),
        ],
        out_specs=pl.BlockSpec((rows, block), lambda b: (0, b)),
        out_shape=jax.ShapeDtypeStruct((rows, chans), jnp.float32),
        compiler_params=pltpu.CompilerParams(dimension_semantics=("parallel",)),
    )(flat_decays, flat_weights, entering, local)


def _gram_kernel(back_ref, top_ref, bot_ref, f_ref, *, group_size, sub):
    rows = back_ref.shape[0]
    groups_here = LANES // group_size
    r_id = lax.broadcasted_iota(jnp.int32, (rows, rows), 0)
    c_id = lax.broadcasted_iota(jnp.int32, (rows, rows), 1)
    exchange = jnp.where(r_id + c_id == rows - 1, 1.0, 0.0).astype(jnp.bfloat16)
    lane_group = lax.broadcasted_iota(jnp.int32, (rows, LANES), 1) // group_size

    def body(j, carry):
        lanes = pl.ds(pl.multiple_of(j * LANES, LANES), LANES)
        back = back_ref[:, lanes]
        x = jnp.concatenate([top_ref[:, lanes], bot_ref[:, lanes]], axis=0)
        back_rev = jnp.dot(exchange, back, preferred_element_type=jnp.float32).astype(jnp.bfloat16)
        masked = jnp.concatenate(
            [jnp.where(lane_group == k, back_rev, jnp.zeros_like(back_rev)) for k in range(groups_here)],
            axis=0,
        )
        gram = lax.dot_general(
            masked, x, (((1,), (1,)), ((), ())), preferred_element_type=jnp.float32
        )
        sums = []
        for k in range(groups_here):
            skew = pltpu.roll(gram[k * rows:(k + 1) * rows], 0, 1, stride=1, stride_axis=0)
            sums.append(jnp.sum(skew, axis=0, keepdims=True))
        f_ref[pl.ds(pl.multiple_of(j * groups_here, groups_here), groups_here), :] = jnp.concatenate(sums, 0)
        return carry

    lax.fori_loop(0, sub, body, 0)


def gram_diag(back, top, bottom, *, group_size):
    rows, chans = back.shape
    block = min(BLOCK_LANES, chans)
    groups_block = block // group_size
    group_count = chans // group_size
    kernel = functools.partial(_gram_kernel, group_size=group_size, sub=block // LANES)
    return pl.pallas_call(
        kernel,
        grid=(chans // block,),
        in_specs=[
            pl.BlockSpec((rows, block), lambda b: (0, b)),
            pl.BlockSpec((rows, block), lambda b: (0, b)),
            pl.BlockSpec((rows, block), lambda b: (0, b)),
        ],
        out_specs=pl.BlockSpec((groups_block, 2 * rows), lambda b: (b, 0)),
        out_shape=jax.ShapeDtypeStruct((group_count, 2 * rows), jnp.float32),
        compiler_params=pltpu.CompilerParams(dimension_semantics=("parallel",)),
    )(back, top, bottom)


def gather_seq(value):
    count = lax.axis_size("seq")
    tiled = jnp.broadcast_to(value[None], (count,) + value.shape)
    return lax.all_to_all(tiled, "seq", split_axis=0, concat_axis=0, tiled=True)


def entering_states(gathered, decays, block_len, group_size, forward):
    count = gathered.shape[0]
    here = lax.axis_index("seq")
    rates = jnp.repeat(decays.T, group_size, axis=1)
    source = jnp.arange(count)
    if forward:
        gap = here - 1 - source
    else:
        gap = source - here - 1
    valid = gap >= 0
    steps = jnp.maximum(gap, 0).astype(jnp.float32)
    coef = jnp.exp(-rates[None] * (float(block_len) * steps)[:, None, None])
    coef = jnp.where(valid[:, None, None], coef, 0.0)
    return jnp.sum(coef * gathered, axis=0)


def on_device(
    query_mr,
    key_mr,
    value_mr,
    query_li,
    key_li,
    cotangent,
    mr_filter,
    norm_gain,
    li_decay,
    li_residue,
):
    row_count, chan_count = query_mr.shape
    group_count, tap_count = mr_filter.shape
    group_size = chan_count // group_count
    assert row_count == tap_count
    grad_scale = float(row_count * lax.axis_size("seq")) ** (-0.5)

    taps_mr = mr_filter.astype(jnp.bfloat16).astype(jnp.float32)
    zero_col = jnp.zeros((group_count, 1), jnp.float32)
    fwd_rows = jnp.concatenate(
        [zero_col, jnp.flip(taps_mr, 1), jnp.zeros((group_count, tap_count - 1), jnp.float32)], 1
    )
    bwd_rows = jnp.concatenate([taps_mr, jnp.zeros_like(taps_mr)], 1)

    mixed_mr = (key_mr.astype(jnp.float32) * value_mr.astype(jnp.float32)).astype(jnp.bfloat16)
    rim_rows = from_behind(mixed_mr, "seq", 1)
    conv_mr = band_conv(fwd_rows, rim_rows, mixed_mr, group_size=group_size, split=False, tri=None)
    out_mr = (query_mr.astype(jnp.float32) * conv_mr).astype(jnp.bfloat16)
    out_full = out_mr.astype(jnp.float32)
    squares = lax.psum(jnp.sum(out_full * out_full, axis=1), "chan")
    inv_rms = lax.rsqrt(squares / D + 1e-06)[:, None]
    normed = out_full * inv_rms * norm_gain
    mixed_li = key_li.astype(jnp.float32) * normed
    cotan_full = cotangent.astype(jnp.float32)
    back_li = cotan_full * query_li.astype(jnp.float32)

    offsets = jnp.arange(row_count, dtype=jnp.float32)
    weights_res = li_residue * jnp.sqrt(2.0 * li_decay)
    taps_li = jnp.einsum(
        "gr,grd->gd", weights_res, jnp.exp(-li_decay[:, :, None] * offsets), precision=HIGHEST
    )
    li_fwd_rows = jnp.concatenate([taps_li[:, :1], jnp.flip(taps_li[:, 1:], 1)], 1)
    fwd_states = jnp.exp(-li_decay[:, :, None] * (row_count - 1.0 - offsets))
    bwd_states = jnp.exp(-li_decay[:, :, None] * offsets)

    back_li_bf = back_li.astype(jnp.bfloat16)
    mixed_li_bf = mixed_li.astype(jnp.bfloat16)
    modes = li_decay.shape[1]
    grad_st = modal_states(bwd_states, back_li_bf, group_size=group_size)
    conv_st = modal_states(fwd_states, mixed_li_bf, group_size=group_size)
    both_st = gather_seq(jnp.concatenate([grad_st, conv_st], 0).astype(jnp.bfloat16))
    both_st = both_st.astype(jnp.float32)
    grad_loc = band_conv(taps_li, back_li_bf, group_size=group_size, split=True, tri="upper")
    conv_loc = band_conv(li_fwd_rows, mixed_li_bf, group_size=group_size, split=True, tri="lower")
    grad_ent = entering_states(both_st[:, :modes], li_decay, row_count, group_size, False)
    conv_ent = entering_states(both_st[:, modes:], li_decay, row_count, group_size, True)
    grad_mixed_li = modal_out(
        li_decay, weights_res, grad_ent, grad_loc, group_size=group_size, forward=False
    )
    conv_li = modal_out(li_decay, weights_res, conv_ent, conv_loc, group_size=group_size, forward=True)

    out_li = (query_li.astype(jnp.float32) * conv_li).astype(jnp.bfloat16)
    grad_query_li = (cotan_full * conv_li).astype(jnp.bfloat16)
    grad_key_li = (grad_mixed_li * normed).astype(jnp.bfloat16)
    grad_normed = grad_mixed_li * key_li.astype(jnp.float32)
    gain_part = jnp.sum(grad_normed * out_full * inv_rms, axis=0)
    weighted = grad_normed * norm_gain
    cross_dots = lax.psum(jnp.sum(weighted * out_full, axis=1), "chan")[:, None]
    grad_out_mr = inv_rms * weighted - out_full * inv_rms**3 * cross_dots / D
    grad_query_mr = (grad_out_mr * conv_mr).astype(jnp.bfloat16)
    back_mr = (grad_out_mr * query_mr.astype(jnp.float32)).astype(jnp.bfloat16)
    after_rim = from_behind(back_mr, "seq", -1)
    grad_mixed_mr = band_conv(bwd_rows, back_mr, after_rim, group_size=group_size, split=False, tri=None)
    grad_key_mr = (grad_mixed_mr * value_mr.astype(jnp.float32)).astype(jnp.bfloat16)
    grad_value_mr = (grad_mixed_mr * key_mr.astype(jnp.float32)).astype(jnp.bfloat16)
    diag_sums = gram_diag(back_mr, rim_rows, mixed_mr, group_size=group_size)
    filter_part = jnp.flip(diag_sums[:, tap_count:], 1)
    packed = jnp.concatenate([gain_part, filter_part.reshape(-1)])
    param_sums = jnp.sum(gather_seq(packed), axis=0) * grad_scale
    grad_gain = param_sums[:chan_count]
    grad_filter = param_sums[chan_count:].reshape(group_count, tap_count)
    return (
        out_li,
        grad_query_mr,
        grad_key_mr,
        grad_value_mr,
        grad_query_li,
        grad_key_li,
        grad_gain,
        grad_filter,
    )


def solution(mesh):
    in_specs = (
        P("seq", "chan"),
        P("seq", "chan"),
        P("seq", "chan"),
        P("seq", "chan"),
        P("seq", "chan"),
        P("seq", "chan"),
        P("chan", None),
        P("chan"),
        P("chan", None),
        P("chan", None),
    )
    out_specs = (
        P("seq", "chan"),
        P("seq", "chan"),
        P("seq", "chan"),
        P("seq", "chan"),
        P("seq", "chan"),
        P("seq", "chan"),
        P("chan"),
        P("chan", None),
    )
    return jax.shard_map(
        on_device, mesh=mesh, in_specs=in_specs, out_specs=out_specs, check_vma=False
    )
```

```python
import functools

import jax
import jax.numpy as jnp
from jax import lax
from jax.experimental import pallas as pl
from jax.experimental.pallas import tpu as pltpu
from jax.sharding import PartitionSpec as P

D = 8192
G = 512
LANES = 128
BLOCK_LANES = 512
HIGHEST = lax.Precision.HIGHEST


def from_behind(value, axis, steps):
    count = lax.axis_size(axis)
    initial, last = (max(0, -steps), min(count, count - steps))
    return lax.ppermute(value, axis, [(source, source + steps) for source in range(initial, last)])


def _split(value):
    high = value.astype(jnp.bfloat16)
    return high, (value - high.astype(jnp.float32)).astype(jnp.bfloat16)


def _band_kernel(*refs, group_size, split, tri, two_inputs, modal, sub):
    refs = list(refs)
    h_ref = refs.pop(0)
    top_ref = refs.pop(0)
    bot_ref = refs.pop(0) if two_inputs else None
    if modal is not None:
        dec_ref, wt_ref, ent_ref = refs.pop(0), refs.pop(0), refs.pop(0)
    out_ref = refs.pop(0)
    rows = out_ref.shape[0]
    width = h_ref.shape[1]
    groups_here = LANES // group_size
    lane_group = lax.broadcasted_iota(jnp.int32, (rows, LANES), 1) // group_size
    row_id = lax.broadcasted_iota(jnp.int32, (rows, width), 0)
    col_id = lax.broadcasted_iota(jnp.int32, (rows, width), 1)
    if modal is not None:
        modes = dec_ref.shape[1]
        offsets = lax.broadcasted_iota(jnp.int32, (rows, modes), 0).astype(jnp.float32)
        dist = offsets + 1.0 if modal == "forward" else float(rows) - offsets

    def body(j, carry):
        lanes = pl.ds(pl.multiple_of(j * LANES, LANES), LANES)
        if two_inputs:
            x = jnp.concatenate([top_ref[:, lanes], bot_ref[:, lanes]], axis=0)
        else:
            x = top_ref[:, lanes]
        bands = []
        for k in range(groups_here):
            band_row = h_ref[pl.ds(j * groups_here + k, 1), :]
            band = pltpu.roll(jnp.broadcast_to(band_row, (rows, width)), 0, 1, stride=1, stride_axis=0)
            if tri == "lower":
                band = jnp.where(col_id <= row_id, band, 0.0)
            elif tri == "upper":
                band = jnp.where(col_id >= row_id, band, 0.0)
            bands.append(band)
        stacked = jnp.concatenate(bands, axis=0)
        if split:
            high, low = _split(stacked)
            y = jnp.dot(high, x, preferred_element_type=jnp.float32)
            y = y + jnp.dot(low, x, preferred_element_type=jnp.float32)
        else:
            y = jnp.dot(stacked.astype(jnp.bfloat16), x, preferred_element_type=jnp.float32)
        if modal is not None:
            ent_high, ent_low = _split(ent_ref[:, lanes])
            out_w = []
            for k in range(groups_here):
                rate = dec_ref[pl.ds(j * groups_here + k, 1), :]
                weight = wt_ref[pl.ds(j * groups_here + k, 1), :]
                out_w.append(weight * jnp.exp(-rate * dist))
            a_high, a_low = _split(jnp.concatenate(out_w, axis=0))
            y = y + jnp.dot(a_high, ent_high, preferred_element_type=jnp.float32)
            y = y + jnp.dot(a_low, ent_high, preferred_element_type=jnp.float32)
            y = y + jnp.dot(a_high, ent_low, preferred_element_type=jnp.float32)
        acc = y[:rows]
        for k in range(1, groups_here):
            acc = jnp.where(lane_group == k, y[k * rows:(k + 1) * rows], acc)
        out_ref[:, lanes] = acc
        return carry

    lax.fori_loop(0, sub, body, 0)


def band_conv(band_rows, top, bottom=None, modal_args=None, *, group_size, split, tri, modal=None):
    rows, chans = top.shape
    block = min(BLOCK_LANES, chans)
    groups_block = block // group_size
    width = band_rows.shape[1]
    two_inputs = bottom is not None
    in_specs = [
        pl.BlockSpec((groups_block, width), lambda b: (b, 0)),
        pl.BlockSpec((rows, block), lambda b: (0, b)),
    ]
    args = [band_rows, top]
    if two_inputs:
        in_specs.append(pl.BlockSpec((rows, block), lambda b: (0, b)))
        args.append(bottom)
    if modal is not None:
        decays, weights, entering = modal_args
        modes = decays.shape[1]
        in_specs += [
            pl.BlockSpec((groups_block, modes), lambda b: (b, 0)),
            pl.BlockSpec((groups_block, modes), lambda b: (b, 0)),
            pl.BlockSpec((modes, block), lambda b: (0, b)),
        ]
        args += [decays, weights, entering]
    kernel = functools.partial(
        _band_kernel,
        group_size=group_size,
        split=split,
        tri=tri,
        two_inputs=two_inputs,
        modal=modal,
        sub=block // LANES,
    )
    return pl.pallas_call(
        kernel,
        grid=(chans // block,),
        in_specs=in_specs,
        out_specs=pl.BlockSpec((rows, block), lambda b: (0, b)),
        out_shape=jax.ShapeDtypeStruct((rows, chans), jnp.float32),
        compiler_params=pltpu.CompilerParams(dimension_semantics=("parallel",)),
    )(*args)


def _state_kernel(e_ref, x_ref, s_ref, *, group_size, sub):
    modes = s_ref.shape[0]
    groups_here = LANES // group_size
    state_group = lax.broadcasted_iota(jnp.int32, (modes, LANES), 1) // group_size

    def body(j, carry):
        lanes = pl.ds(pl.multiple_of(j * LANES, LANES), LANES)
        x = x_ref[:, lanes]
        weights = e_ref[pl.ds(j * groups_here, groups_here)]
        high, low = _split(weights.reshape(groups_here * modes, weights.shape[2]))
        y = jnp.dot(high, x, preferred_element_type=jnp.float32)
        y = y + jnp.dot(low, x, preferred_element_type=jnp.float32)
        acc = y[:modes]
        for k in range(1, groups_here):
            acc = jnp.where(state_group == k, y[k * modes:(k + 1) * modes], acc)
        s_ref[:, lanes] = acc
        return carry

    lax.fori_loop(0, sub, body, 0)


def modal_states(state_rows, x, *, group_size):
    rows, chans = x.shape
    block = min(BLOCK_LANES, chans)
    groups_block = block // group_size
    modes = state_rows.shape[1]
    kernel = functools.partial(_state_kernel, group_size=group_size, sub=block // LANES)
    return pl.pallas_call(
        kernel,
        grid=(chans // block,),
        in_specs=[
            pl.BlockSpec((groups_block, modes, rows), lambda b: (b, 0, 0)),
            pl.BlockSpec((rows, block), lambda b: (0, b)),
        ],
        out_specs=pl.BlockSpec((modes, block), lambda b: (0, b)),
        out_shape=jax.ShapeDtypeStruct((modes, chans), jnp.float32),
        compiler_params=pltpu.CompilerParams(dimension_semantics=("parallel",)),
    )(state_rows, x)


def _modal_kernel(dec_ref, wt_ref, ent_ref, loc_ref, out_ref, *, group_size, forward, sub):
    rows = out_ref.shape[0]
    modes = ent_ref.shape[0]
    groups_here = LANES // group_size
    width = groups_here * modes
    offsets = lax.broadcasted_iota(jnp.int32, (rows, width), 0).astype(jnp.float32)
    dist = offsets + 1.0 if forward else float(rows) - offsets
    row_group = lax.broadcasted_iota(jnp.int32, (width, LANES), 0) // modes
    lane_group = lax.broadcasted_iota(jnp.int32, (width, LANES), 1) // group_size

    def body(j, carry):
        lanes = pl.ds(pl.multiple_of(j * LANES, LANES), LANES)
        row = pl.program_id(0) * sub + j
        rate = dec_ref[pl.ds(row, 1), :]
        weight = wt_ref[pl.ds(row, 1), :]
        a_high, a_low = _split(weight * jnp.exp(-rate * dist))
        entering = ent_ref[:, lanes]
        tiled = jnp.concatenate([entering] * groups_here, axis=0)
        diag = jnp.where(row_group == lane_group, tiled, 0.0)
        ent_high, ent_low = _split(diag)
        y = jnp.dot(a_high, ent_high, preferred_element_type=jnp.float32)
        y = y + jnp.dot(a_low, ent_high, preferred_element_type=jnp.float32)
        y = y + jnp.dot(a_high, ent_low, preferred_element_type=jnp.float32)
        out_ref[:, lanes] = loc_ref[:, lanes] + y
        return carry

    lax.fori_loop(0, sub, body, 0)


def modal_out(decays, weights, entering, local, *, group_size, forward):
    rows, chans = local.shape
    block = min(BLOCK_LANES, chans)
    groups_block = block // group_size
    modes = decays.shape[1]
    per_row = (LANES // group_size) * modes
    flat_decays = decays.reshape(-1, per_row)
    flat_weights = weights.reshape(-1, per_row)
    sub = block // LANES
    kernel = functools.partial(_modal_kernel, group_size=group_size, forward=forward, sub=sub)
    return pl.pallas_call(
        kernel,
        grid=(chans // block,),
        in_specs=[
            pl.BlockSpec(flat_decays.shape, lambda b: (0, 0)),
            pl.BlockSpec(flat_weights.shape, lambda b: (0, 0)),
            pl.BlockSpec((modes, block), lambda b: (0, b)),
            pl.BlockSpec((rows, block), lambda b: (0, b)),
        ],
        out_specs=pl.BlockSpec((rows, block), lambda b: (0, b)),
        out_shape=jax.ShapeDtypeStruct((rows, chans), jnp.float32),
        compiler_params=pltpu.CompilerParams(dimension_semantics=("parallel",)),
    )(flat_decays, flat_weights, entering, local)


def _gram_kernel(back_ref, top_ref, bot_ref, f_ref, *, group_size, sub):
    rows = back_ref.shape[0]
    groups_here = LANES // group_size
    r_id = lax.broadcasted_iota(jnp.int32, (rows, rows), 0)
    c_id = lax.broadcasted_iota(jnp.int32, (rows, rows), 1)
    exchange = jnp.where(r_id + c_id == rows - 1, 1.0, 0.0).astype(jnp.bfloat16)
    lane_group = lax.broadcasted_iota(jnp.int32, (rows, LANES), 1) // group_size

    def body(j, carry):
        lanes = pl.ds(pl.multiple_of(j * LANES, LANES), LANES)
        back = back_ref[:, lanes]
        x = jnp.concatenate([top_ref[:, lanes], bot_ref[:, lanes]], axis=0)
        back_rev = jnp.dot(exchange, back, preferred_element_type=jnp.float32).astype(jnp.bfloat16)
        masked = jnp.concatenate(
            [jnp.where(lane_group == k, back_rev, jnp.zeros_like(back_rev)) for k in range(groups_here)],
            axis=0,
        )
        gram = lax.dot_general(
            masked, x, (((1,), (1,)), ((), ())), preferred_element_type=jnp.float32
        )
        sums = []
        for k in range(groups_here):
            skew = pltpu.roll(gram[k * rows:(k + 1) * rows], 0, 1, stride=1, stride_axis=0)
            sums.append(jnp.sum(skew, axis=0, keepdims=True))
        f_ref[pl.ds(pl.multiple_of(j * groups_here, groups_here), groups_here), :] = jnp.concatenate(sums, 0)
        return carry

    lax.fori_loop(0, sub, body, 0)


def gram_diag(back, top, bottom, *, group_size):
    rows, chans = back.shape
    block = min(BLOCK_LANES, chans)
    groups_block = block // group_size
    group_count = chans // group_size
    kernel = functools.partial(_gram_kernel, group_size=group_size, sub=block // LANES)
    return pl.pallas_call(
        kernel,
        grid=(chans // block,),
        in_specs=[
            pl.BlockSpec((rows, block), lambda b: (0, b)),
            pl.BlockSpec((rows, block), lambda b: (0, b)),
            pl.BlockSpec((rows, block), lambda b: (0, b)),
        ],
        out_specs=pl.BlockSpec((groups_block, 2 * rows), lambda b: (b, 0)),
        out_shape=jax.ShapeDtypeStruct((group_count, 2 * rows), jnp.float32),
        compiler_params=pltpu.CompilerParams(dimension_semantics=("parallel",)),
    )(back, top, bottom)


def gather_seq(value):
    count = lax.axis_size("seq")
    tiled = jnp.broadcast_to(value[None], (count,) + value.shape)
    return lax.all_to_all(tiled, "seq", split_axis=0, concat_axis=0, tiled=True)


def entering_states(gathered, decays, block_len, group_size, forward):
    count = gathered.shape[0]
    here = lax.axis_index("seq")
    rates = jnp.repeat(decays.T, group_size, axis=1)
    source = jnp.arange(count)
    if forward:
        gap = here - 1 - source
    else:
        gap = source - here - 1
    valid = gap >= 0
    steps = jnp.maximum(gap, 0).astype(jnp.float32)
    coef = jnp.exp(-rates[None] * (float(block_len) * steps)[:, None, None])
    coef = jnp.where(valid[:, None, None], coef, 0.0)
    return jnp.sum(coef * gathered, axis=0)


def on_device(
    query_mr,
    key_mr,
    value_mr,
    query_li,
    key_li,
    cotangent,
    mr_filter,
    norm_gain,
    li_decay,
    li_residue,
):
    row_count, chan_count = query_mr.shape
    group_count, tap_count = mr_filter.shape
    group_size = chan_count // group_count
    assert row_count == tap_count
    grad_scale = float(row_count * lax.axis_size("seq")) ** (-0.5)

    taps_mr = mr_filter.astype(jnp.bfloat16).astype(jnp.float32)
    zero_col = jnp.zeros((group_count, 1), jnp.float32)
    fwd_rows = jnp.concatenate(
        [zero_col, jnp.flip(taps_mr, 1), jnp.zeros((group_count, tap_count - 1), jnp.float32)], 1
    )
    bwd_rows = jnp.concatenate([taps_mr, jnp.zeros_like(taps_mr)], 1)

    offsets = jnp.arange(row_count, dtype=jnp.float32)
    weights_res = li_residue * jnp.sqrt(2.0 * li_decay)
    taps_li = jnp.einsum(
        "gr,grd->gd", weights_res, jnp.exp(-li_decay[:, :, None] * offsets), precision=HIGHEST
    )
    li_fwd_rows = jnp.concatenate([taps_li[:, :1], jnp.flip(taps_li[:, 1:], 1)], 1)
    fwd_states = jnp.exp(-li_decay[:, :, None] * (row_count - 1.0 - offsets))
    bwd_states = jnp.exp(-li_decay[:, :, None] * offsets)

    cotan_full = cotangent.astype(jnp.float32)
    back_li_bf = (cotan_full * query_li.astype(jnp.float32)).astype(jnp.bfloat16)
    grad_st = modal_states(bwd_states, back_li_bf, group_size=group_size)
    grad_gathered = gather_seq(grad_st.astype(jnp.bfloat16)).astype(jnp.float32)

    mixed_mr = (key_mr.astype(jnp.float32) * value_mr.astype(jnp.float32)).astype(jnp.bfloat16)
    rim_rows = from_behind(mixed_mr, "seq", 1)
    grad_loc = band_conv(taps_li, back_li_bf, group_size=group_size, split=True, tri="upper")
    conv_mr = band_conv(fwd_rows, rim_rows, mixed_mr, group_size=group_size, split=False, tri=None)
    grad_ent = entering_states(grad_gathered, li_decay, row_count, group_size, False)
    grad_mixed_li = modal_out(
        li_decay, weights_res, grad_ent, grad_loc, group_size=group_size, forward=False
    )
    out_mr = (query_mr.astype(jnp.float32) * conv_mr).astype(jnp.bfloat16)
    out_full = out_mr.astype(jnp.float32)
    key_full = key_li.astype(jnp.float32)
    grad_normed = grad_mixed_li * key_full
    weighted = grad_normed * norm_gain
    row_sums = jnp.stack(
        [jnp.sum(out_full * out_full, axis=1), jnp.sum(weighted * out_full, axis=1)]
    )
    row_sums = lax.psum(row_sums, "chan")
    squares = row_sums[0]
    cross_dots = row_sums[1][:, None]
    inv_rms = lax.rsqrt(squares / D + 1e-06)[:, None]
    normed = out_full * inv_rms * norm_gain
    mixed_li_bf = (key_full * normed).astype(jnp.bfloat16)
    conv_st = modal_states(fwd_states, mixed_li_bf, group_size=group_size)
    conv_gathered = gather_seq(conv_st.astype(jnp.bfloat16)).astype(jnp.float32)
    conv_loc = band_conv(li_fwd_rows, mixed_li_bf, group_size=group_size, split=True, tri="lower")
    conv_ent = entering_states(conv_gathered, li_decay, row_count, group_size, True)
    conv_li = modal_out(li_decay, weights_res, conv_ent, conv_loc, group_size=group_size, forward=True)

    out_li = (query_li.astype(jnp.float32) * conv_li).astype(jnp.bfloat16)
    grad_query_li = (cotan_full * conv_li).astype(jnp.bfloat16)
    grad_key_li = (grad_mixed_li * normed).astype(jnp.bfloat16)
    gain_part = jnp.sum(grad_normed * out_full * inv_rms, axis=0)
    grad_out_mr = inv_rms * weighted - out_full * inv_rms**3 * cross_dots / D
    grad_query_mr = (grad_out_mr * conv_mr).astype(jnp.bfloat16)
    back_mr = (grad_out_mr * query_mr.astype(jnp.float32)).astype(jnp.bfloat16)
    after_rim = from_behind(back_mr, "seq", -1)
    grad_mixed_mr = band_conv(bwd_rows, back_mr, after_rim, group_size=group_size, split=False, tri=None)
    grad_key_mr = (grad_mixed_mr * value_mr.astype(jnp.float32)).astype(jnp.bfloat16)
    grad_value_mr = (grad_mixed_mr * key_mr.astype(jnp.float32)).astype(jnp.bfloat16)
    diag_sums = gram_diag(back_mr, rim_rows, mixed_mr, group_size=group_size)
    filter_part = jnp.flip(diag_sums[:, tap_count:], 1)
    packed = jnp.concatenate([gain_part, filter_part.reshape(-1)])
    param_sums = jnp.sum(gather_seq(packed), axis=0) * grad_scale
    grad_gain = param_sums[:chan_count]
    grad_filter = param_sums[chan_count:].reshape(group_count, tap_count)
    return (
        out_li,
        grad_query_mr,
        grad_key_mr,
        grad_value_mr,
        grad_query_li,
        grad_key_li,
        grad_gain,
        grad_filter,
    )


def solution(mesh):
    in_specs = (
        P("seq", "chan"),
        P("seq", "chan"),
        P("seq", "chan"),
        P("seq", "chan"),
        P("seq", "chan"),
        P("seq", "chan"),
        P("chan", None),
        P("chan"),
        P("chan", None),
        P("chan", None),
    )
    out_specs = (
        P("seq", "chan"),
        P("seq", "chan"),
        P("seq", "chan"),
        P("seq", "chan"),
        P("seq", "chan"),
        P("seq", "chan"),
        P("chan"),
        P("chan", None),
    )
    return jax.shard_map(
        on_device, mesh=mesh, in_specs=in_specs, out_specs=out_specs, check_vma=False
    )
```

```python
import functools

import jax
import jax.numpy as jnp
from jax import lax
from jax.experimental import pallas as pl
from jax.experimental.pallas import tpu as pltpu
from jax.sharding import PartitionSpec as P

D = 8192
G = 512
LANES = 128
BLOCK_LANES = 512
HIGHEST = lax.Precision.HIGHEST


def from_behind(value, axis, steps):
    count = lax.axis_size(axis)
    initial, last = (max(0, -steps), min(count, count - steps))
    return lax.ppermute(value, axis, [(source, source + steps) for source in range(initial, last)])


def _split(value):
    high = value.astype(jnp.bfloat16)
    return high, (value - high.astype(jnp.float32)).astype(jnp.bfloat16)


def _band_kernel(*refs, group_size, split, tri, two_inputs, modal, sub):
    refs = list(refs)
    h_ref = refs.pop(0)
    top_ref = refs.pop(0)
    bot_ref = refs.pop(0) if two_inputs else None
    if modal is not None:
        dec_ref, wt_ref, ent_ref = refs.pop(0), refs.pop(0), refs.pop(0)
    out_ref = refs.pop(0)
    rows = out_ref.shape[0]
    width = h_ref.shape[1]
    groups_here = LANES // group_size
    lane_group = lax.broadcasted_iota(jnp.int32, (rows, LANES), 1) // group_size
    row_id = lax.broadcasted_iota(jnp.int32, (rows, width), 0)
    col_id = lax.broadcasted_iota(jnp.int32, (rows, width), 1)
    if modal is not None:
        modes = dec_ref.shape[1]
        offsets = lax.broadcasted_iota(jnp.int32, (rows, modes), 0).astype(jnp.float32)
        dist = offsets + 1.0 if modal == "forward" else float(rows) - offsets

    def body(j, carry):
        lanes = pl.ds(pl.multiple_of(j * LANES, LANES), LANES)
        if two_inputs:
            x = jnp.concatenate([top_ref[:, lanes], bot_ref[:, lanes]], axis=0)
        else:
            x = top_ref[:, lanes]
        bands = []
        for k in range(groups_here):
            band_row = h_ref[pl.ds(j * groups_here + k, 1), :]
            band = pltpu.roll(jnp.broadcast_to(band_row, (rows, width)), 0, 1, stride=1, stride_axis=0)
            if tri == "lower":
                band = jnp.where(col_id <= row_id, band, 0.0)
            elif tri == "upper":
                band = jnp.where(col_id >= row_id, band, 0.0)
            bands.append(band)
        stacked = jnp.concatenate(bands, axis=0)
        if split:
            high, low = _split(stacked)
            y = jnp.dot(high, x, preferred_element_type=jnp.float32)
            y = y + jnp.dot(low, x, preferred_element_type=jnp.float32)
        else:
            y = jnp.dot(stacked.astype(jnp.bfloat16), x, preferred_element_type=jnp.float32)
        if modal is not None:
            ent_high, ent_low = _split(ent_ref[:, lanes])
            out_w = []
            for k in range(groups_here):
                rate = dec_ref[pl.ds(j * groups_here + k, 1), :]
                weight = wt_ref[pl.ds(j * groups_here + k, 1), :]
                out_w.append(weight * jnp.exp(-rate * dist))
            a_high, a_low = _split(jnp.concatenate(out_w, axis=0))
            y = y + jnp.dot(a_high, ent_high, preferred_element_type=jnp.float32)
            y = y + jnp.dot(a_low, ent_high, preferred_element_type=jnp.float32)
            y = y + jnp.dot(a_high, ent_low, preferred_element_type=jnp.float32)
        acc = y[:rows]
        for k in range(1, groups_here):
            acc = jnp.where(lane_group == k, y[k * rows:(k + 1) * rows], acc)
        out_ref[:, lanes] = acc
        return carry

    lax.fori_loop(0, sub, body, 0)


def band_conv(band_rows, top, bottom=None, modal_args=None, *, group_size, split, tri, modal=None):
    rows, chans = top.shape
    block = min(BLOCK_LANES, chans)
    groups_block = block // group_size
    width = band_rows.shape[1]
    two_inputs = bottom is not None
    in_specs = [
        pl.BlockSpec((groups_block, width), lambda b: (b, 0)),
        pl.BlockSpec((rows, block), lambda b: (0, b)),
    ]
    args = [band_rows, top]
    if two_inputs:
        in_specs.append(pl.BlockSpec((rows, block), lambda b: (0, b)))
        args.append(bottom)
    if modal is not None:
        decays, weights, entering = modal_args
        modes = decays.shape[1]
        in_specs += [
            pl.BlockSpec((groups_block, modes), lambda b: (b, 0)),
            pl.BlockSpec((groups_block, modes), lambda b: (b, 0)),
            pl.BlockSpec((modes, block), lambda b: (0, b)),
        ]
        args += [decays, weights, entering]
    kernel = functools.partial(
        _band_kernel,
        group_size=group_size,
        split=split,
        tri=tri,
        two_inputs=two_inputs,
        modal=modal,
        sub=block // LANES,
    )
    return pl.pallas_call(
        kernel,
        grid=(chans // block,),
        in_specs=in_specs,
        out_specs=pl.BlockSpec((rows, block), lambda b: (0, b)),
        out_shape=jax.ShapeDtypeStruct((rows, chans), jnp.float32),
        compiler_params=pltpu.CompilerParams(dimension_semantics=("parallel",)),
    )(*args)


def _state_kernel(e_ref, x_ref, s_ref, *, group_size, sub):
    modes = s_ref.shape[0]
    groups_here = LANES // group_size
    state_group = lax.broadcasted_iota(jnp.int32, (modes, LANES), 1) // group_size

    def body(j, carry):
        lanes = pl.ds(pl.multiple_of(j * LANES, LANES), LANES)
        x = x_ref[:, lanes]
        weights = e_ref[pl.ds(j * groups_here, groups_here)]
        high, low = _split(weights.reshape(groups_here * modes, weights.shape[2]))
        y = jnp.dot(high, x, preferred_element_type=jnp.float32)
        y = y + jnp.dot(low, x, preferred_element_type=jnp.float32)
        acc = y[:modes]
        for k in range(1, groups_here):
            acc = jnp.where(state_group == k, y[k * modes:(k + 1) * modes], acc)
        s_ref[:, lanes] = acc
        return carry

    lax.fori_loop(0, sub, body, 0)


def modal_states(state_rows, x, *, group_size):
    rows, chans = x.shape
    block = min(BLOCK_LANES, chans)
    groups_block = block // group_size
    modes = state_rows.shape[1]
    kernel = functools.partial(_state_kernel, group_size=group_size, sub=block // LANES)
    return pl.pallas_call(
        kernel,
        grid=(chans // block,),
        in_specs=[
            pl.BlockSpec((groups_block, modes, rows), lambda b: (b, 0, 0)),
            pl.BlockSpec((rows, block), lambda b: (0, b)),
        ],
        out_specs=pl.BlockSpec((modes, block), lambda b: (0, b)),
        out_shape=jax.ShapeDtypeStruct((modes, chans), jnp.float32),
        compiler_params=pltpu.CompilerParams(dimension_semantics=("parallel",)),
    )(state_rows, x)


def _modal_kernel(dec_ref, wt_ref, ent_ref, loc_ref, out_ref, *, group_size, forward, sub):
    rows = out_ref.shape[0]
    modes = ent_ref.shape[0]
    groups_here = LANES // group_size
    width = groups_here * modes
    offsets = lax.broadcasted_iota(jnp.int32, (rows, width), 0).astype(jnp.float32)
    dist = offsets + 1.0 if forward else float(rows) - offsets
    row_group = lax.broadcasted_iota(jnp.int32, (width, LANES), 0) // modes
    lane_group = lax.broadcasted_iota(jnp.int32, (width, LANES), 1) // group_size

    def body(j, carry):
        lanes = pl.ds(pl.multiple_of(j * LANES, LANES), LANES)
        row = pl.program_id(0) * sub + j
        rate = dec_ref[pl.ds(row, 1), :]
        weight = wt_ref[pl.ds(row, 1), :]
        a_high, a_low = _split(weight * jnp.exp(-rate * dist))
        entering = ent_ref[:, lanes]
        tiled = jnp.concatenate([entering] * groups_here, axis=0)
        diag = jnp.where(row_group == lane_group, tiled, 0.0)
        ent_high, ent_low = _split(diag)
        y = jnp.dot(a_high, ent_high, preferred_element_type=jnp.float32)
        y = y + jnp.dot(a_low, ent_high, preferred_element_type=jnp.float32)
        y = y + jnp.dot(a_high, ent_low, preferred_element_type=jnp.float32)
        out_ref[:, lanes] = loc_ref[:, lanes] + y
        return carry

    lax.fori_loop(0, sub, body, 0)


def modal_out(decays, weights, entering, local, *, group_size, forward):
    rows, chans = local.shape
    block = min(BLOCK_LANES, chans)
    groups_block = block // group_size
    modes = decays.shape[1]
    per_row = (LANES // group_size) * modes
    flat_decays = decays.reshape(-1, per_row)
    flat_weights = weights.reshape(-1, per_row)
    sub = block // LANES
    kernel = functools.partial(_modal_kernel, group_size=group_size, forward=forward, sub=sub)
    return pl.pallas_call(
        kernel,
        grid=(chans // block,),
        in_specs=[
            pl.BlockSpec(flat_decays.shape, lambda b: (0, 0)),
            pl.BlockSpec(flat_weights.shape, lambda b: (0, 0)),
            pl.BlockSpec((modes, block), lambda b: (0, b)),
            pl.BlockSpec((rows, block), lambda b: (0, b)),
        ],
        out_specs=pl.BlockSpec((rows, block), lambda b: (0, b)),
        out_shape=jax.ShapeDtypeStruct((rows, chans), jnp.float32),
        compiler_params=pltpu.CompilerParams(dimension_semantics=("parallel",)),
    )(flat_decays, flat_weights, entering, local)


def _gram_kernel(back_ref, top_ref, bot_ref, f_ref, *, group_size, sub):
    rows = back_ref.shape[0]
    groups_here = LANES // group_size
    r_id = lax.broadcasted_iota(jnp.int32, (rows, rows), 0)
    c_id = lax.broadcasted_iota(jnp.int32, (rows, rows), 1)
    exchange = jnp.where(r_id + c_id == rows - 1, 1.0, 0.0).astype(jnp.bfloat16)
    lane_group = lax.broadcasted_iota(jnp.int32, (rows, LANES), 1) // group_size

    def body(j, carry):
        lanes = pl.ds(pl.multiple_of(j * LANES, LANES), LANES)
        back = back_ref[:, lanes]
        x = jnp.concatenate([top_ref[:, lanes], bot_ref[:, lanes]], axis=0)
        back_rev = jnp.dot(exchange, back, preferred_element_type=jnp.float32).astype(jnp.bfloat16)
        masked = jnp.concatenate(
            [jnp.where(lane_group == k, back_rev, jnp.zeros_like(back_rev)) for k in range(groups_here)],
            axis=0,
        )
        gram = lax.dot_general(
            masked, x, (((1,), (1,)), ((), ())), preferred_element_type=jnp.float32
        )
        sums = []
        for k in range(groups_here):
            skew = pltpu.roll(gram[k * rows:(k + 1) * rows], 0, 1, stride=1, stride_axis=0)
            sums.append(jnp.sum(skew, axis=0, keepdims=True))
        f_ref[pl.ds(pl.multiple_of(j * groups_here, groups_here), groups_here), :] = jnp.concatenate(sums, 0)
        return carry

    lax.fori_loop(0, sub, body, 0)


def gram_diag(back, top, bottom, *, group_size):
    rows, chans = back.shape
    block = min(BLOCK_LANES, chans)
    groups_block = block // group_size
    group_count = chans // group_size
    kernel = functools.partial(_gram_kernel, group_size=group_size, sub=block // LANES)
    return pl.pallas_call(
        kernel,
        grid=(chans // block,),
        in_specs=[
            pl.BlockSpec((rows, block), lambda b: (0, b)),
            pl.BlockSpec((rows, block), lambda b: (0, b)),
            pl.BlockSpec((rows, block), lambda b: (0, b)),
        ],
        out_specs=pl.BlockSpec((groups_block, 2 * rows), lambda b: (b, 0)),
        out_shape=jax.ShapeDtypeStruct((group_count, 2 * rows), jnp.float32),
        compiler_params=pltpu.CompilerParams(dimension_semantics=("parallel",)),
    )(back, top, bottom)


def gather_seq(value):
    count = lax.axis_size("seq")
    tiled = jnp.broadcast_to(value[None], (count,) + value.shape)
    return lax.all_to_all(tiled, "seq", split_axis=0, concat_axis=0, tiled=True)


def entering_states(gathered, decays, block_len, group_size, forward):
    count = gathered.shape[0]
    here = lax.axis_index("seq")
    rates = jnp.repeat(decays.T, group_size, axis=1)
    source = jnp.arange(count)
    if forward:
        gap = here - 1 - source
    else:
        gap = source - here - 1
    valid = gap >= 0
    steps = jnp.maximum(gap, 0).astype(jnp.float32)
    coef = jnp.exp(-rates[None] * (float(block_len) * steps)[:, None, None])
    coef = jnp.where(valid[:, None, None], coef, 0.0)
    return jnp.sum(coef * gathered, axis=0)


def on_device(
    query_mr,
    key_mr,
    value_mr,
    query_li,
    key_li,
    cotangent,
    mr_filter,
    norm_gain,
    li_decay,
    li_residue,
):
    row_count, chan_count = query_mr.shape
    group_count, tap_count = mr_filter.shape
    group_size = chan_count // group_count
    assert row_count == tap_count
    grad_scale = float(row_count * lax.axis_size("seq")) ** (-0.5)

    taps_mr = mr_filter.astype(jnp.bfloat16).astype(jnp.float32)
    zero_col = jnp.zeros((group_count, 1), jnp.float32)
    fwd_rows = jnp.concatenate(
        [zero_col, jnp.flip(taps_mr, 1), jnp.zeros((group_count, tap_count - 1), jnp.float32)], 1
    )
    bwd_rows = jnp.concatenate([taps_mr, jnp.zeros_like(taps_mr)], 1)

    offsets = jnp.arange(row_count, dtype=jnp.float32)
    weights_res = li_residue * jnp.sqrt(2.0 * li_decay)
    taps_li = jnp.einsum(
        "gr,grd->gd", weights_res, jnp.exp(-li_decay[:, :, None] * offsets), precision=HIGHEST
    )
    li_fwd_rows = jnp.concatenate([taps_li[:, :1], jnp.flip(taps_li[:, 1:], 1)], 1)
    fwd_states = jnp.exp(-li_decay[:, :, None] * (row_count - 1.0 - offsets))
    bwd_states = jnp.exp(-li_decay[:, :, None] * offsets)

    cotan_full = cotangent.astype(jnp.float32)
    back_li_bf = (cotan_full * query_li.astype(jnp.float32)).astype(jnp.bfloat16)
    grad_st = modal_states(bwd_states, back_li_bf, group_size=group_size)
    grad_gathered = gather_seq(grad_st.astype(jnp.bfloat16)).astype(jnp.float32)

    mixed_mr = (key_mr.astype(jnp.float32) * value_mr.astype(jnp.float32)).astype(jnp.bfloat16)
    rim_rows = from_behind(mixed_mr, "seq", 1)
    grad_loc = band_conv(taps_li, back_li_bf, group_size=group_size, split=True, tri="upper")
    conv_mr = band_conv(fwd_rows, rim_rows, mixed_mr, group_size=group_size, split=False, tri=None)
    grad_ent = entering_states(grad_gathered, li_decay, row_count, group_size, False)
    grad_mixed_li = modal_out(
        li_decay, weights_res, grad_ent, grad_loc, group_size=group_size, forward=False
    )
    out_mr = (query_mr.astype(jnp.float32) * conv_mr).astype(jnp.bfloat16)
    out_full = out_mr.astype(jnp.float32)
    key_full = key_li.astype(jnp.float32)
    grad_normed = grad_mixed_li * key_full
    weighted = grad_normed * norm_gain
    row_sums = jnp.stack(
        [jnp.sum(out_full * out_full, axis=1), jnp.sum(weighted * out_full, axis=1)]
    )
    row_sums = lax.psum(row_sums, "chan")
    squares = row_sums[0]
    cross_dots = row_sums[1][:, None]
    inv_rms = lax.rsqrt(squares / D + 1e-06)[:, None]
    normed = out_full * inv_rms * norm_gain
    mixed_li_bf = (key_full * normed).astype(jnp.bfloat16)
    conv_st = modal_states(fwd_states, mixed_li_bf, group_size=group_size)
    conv_loc = band_conv(li_fwd_rows, mixed_li_bf, group_size=group_size, split=True, tri="lower")

    grad_key_li = (grad_mixed_li * normed).astype(jnp.bfloat16)
    gain_part = jnp.sum(grad_normed * out_full * inv_rms, axis=0)
    grad_out_mr = inv_rms * weighted - out_full * inv_rms**3 * cross_dots / D
    grad_query_mr = (grad_out_mr * conv_mr).astype(jnp.bfloat16)
    back_mr = (grad_out_mr * query_mr.astype(jnp.float32)).astype(jnp.bfloat16)
    after_rim = from_behind(back_mr, "seq", -1)
    diag_sums = gram_diag(back_mr, rim_rows, mixed_mr, group_size=group_size)
    filter_part = jnp.flip(diag_sums[:, tap_count:], 1)
    params = jnp.concatenate([gain_part, filter_part.reshape(-1)])
    params_high = params.astype(jnp.bfloat16)
    params_low = (params - params_high.astype(jnp.float32)).astype(jnp.bfloat16)
    state_len = conv_st.size
    packed = jnp.concatenate([conv_st.reshape(-1).astype(jnp.bfloat16), params_high, params_low])
    gathered = gather_seq(packed).astype(jnp.float32)
    conv_gathered = gathered[:, :state_len].reshape((-1,) + conv_st.shape)
    param_count = params.shape[0]
    param_rows = gathered[:, state_len:state_len + param_count] + gathered[:, state_len + param_count:]
    param_sums = jnp.sum(param_rows, axis=0) * grad_scale
    grad_gain = param_sums[:chan_count]
    grad_filter = param_sums[chan_count:].reshape(group_count, tap_count)
    grad_mixed_mr = band_conv(bwd_rows, back_mr, after_rim, group_size=group_size, split=False, tri=None)
    grad_key_mr = (grad_mixed_mr * value_mr.astype(jnp.float32)).astype(jnp.bfloat16)
    grad_value_mr = (grad_mixed_mr * key_mr.astype(jnp.float32)).astype(jnp.bfloat16)
    conv_ent = entering_states(conv_gathered, li_decay, row_count, group_size, True)
    conv_li = modal_out(li_decay, weights_res, conv_ent, conv_loc, group_size=group_size, forward=True)
    out_li = (query_li.astype(jnp.float32) * conv_li).astype(jnp.bfloat16)
    grad_query_li = (cotan_full * conv_li).astype(jnp.bfloat16)
    return (
        out_li,
        grad_query_mr,
        grad_key_mr,
        grad_value_mr,
        grad_query_li,
        grad_key_li,
        grad_gain,
        grad_filter,
    )


def solution(mesh):
    in_specs = (
        P("seq", "chan"),
        P("seq", "chan"),
        P("seq", "chan"),
        P("seq", "chan"),
        P("seq", "chan"),
        P("seq", "chan"),
        P("chan", None),
        P("chan"),
        P("chan", None),
        P("chan", None),
    )
    out_specs = (
        P("seq", "chan"),
        P("seq", "chan"),
        P("seq", "chan"),
        P("seq", "chan"),
        P("seq", "chan"),
        P("seq", "chan"),
        P("chan"),
        P("chan", None),
    )
    return jax.shard_map(
        on_device, mesh=mesh, in_specs=in_specs, out_specs=out_specs, check_vma=False
    )
```

```python
import functools

import jax
import jax.numpy as jnp
from jax import lax
from jax.experimental import pallas as pl
from jax.experimental.pallas import tpu as pltpu
from jax.sharding import PartitionSpec as P

D = 8192
G = 512
LANES = 128
BLOCK_LANES = 512
HIGHEST = lax.Precision.HIGHEST


def from_behind(value, axis, steps):
    count = lax.axis_size(axis)
    initial, last = (max(0, -steps), min(count, count - steps))
    return lax.ppermute(value, axis, [(source, source + steps) for source in range(initial, last)])


def _split(value):
    high = value.astype(jnp.bfloat16)
    return high, (value - high.astype(jnp.float32)).astype(jnp.bfloat16)


def _band_kernel(*refs, group_size, split, tri, two_inputs, modal, sub, scaled):
    refs = list(refs)
    h_ref = refs.pop(0)
    top_ref = refs.pop(0)
    bot_ref = refs.pop(0) if two_inputs else None
    if modal is not None:
        dec_ref, wt_ref, ent_ref = refs.pop(0), refs.pop(0), refs.pop(0)
    if scaled:
        first_ref, second_ref = refs.pop(0), refs.pop(0)
    out_ref = refs.pop(0)
    if scaled:
        other_ref = refs.pop(0)
    rows = out_ref.shape[0]
    width = h_ref.shape[1]
    groups_here = LANES // group_size
    lane_group = lax.broadcasted_iota(jnp.int32, (rows, LANES), 1) // group_size
    row_id = lax.broadcasted_iota(jnp.int32, (rows, width), 0)
    col_id = lax.broadcasted_iota(jnp.int32, (rows, width), 1)
    if modal is not None:
        modes = dec_ref.shape[1]
        offsets = lax.broadcasted_iota(jnp.int32, (rows, modes), 0).astype(jnp.float32)
        dist = offsets + 1.0 if modal == "forward" else float(rows) - offsets

    def body(j, carry):
        lanes = pl.ds(pl.multiple_of(j * LANES, LANES), LANES)
        if two_inputs:
            x = jnp.concatenate([top_ref[:, lanes], bot_ref[:, lanes]], axis=0)
        else:
            x = top_ref[:, lanes]
        bands = []
        for k in range(groups_here):
            band_row = h_ref[pl.ds(j * groups_here + k, 1), :]
            band = pltpu.roll(jnp.broadcast_to(band_row, (rows, width)), 0, 1, stride=1, stride_axis=0)
            if tri == "lower":
                band = jnp.where(col_id <= row_id, band, 0.0)
            elif tri == "upper":
                band = jnp.where(col_id >= row_id, band, 0.0)
            bands.append(band)
        stacked = jnp.concatenate(bands, axis=0)
        if split:
            high, low = _split(stacked)
            y = jnp.dot(high, x, preferred_element_type=jnp.float32)
            y = y + jnp.dot(low, x, preferred_element_type=jnp.float32)
        else:
            y = jnp.dot(stacked.astype(jnp.bfloat16), x, preferred_element_type=jnp.float32)
        if modal is not None:
            ent_high, ent_low = _split(ent_ref[:, lanes])
            out_w = []
            for k in range(groups_here):
                rate = dec_ref[pl.ds(j * groups_here + k, 1), :]
                weight = wt_ref[pl.ds(j * groups_here + k, 1), :]
                out_w.append(weight * jnp.exp(-rate * dist))
            a_high, a_low = _split(jnp.concatenate(out_w, axis=0))
            y = y + jnp.dot(a_high, ent_high, preferred_element_type=jnp.float32)
            y = y + jnp.dot(a_low, ent_high, preferred_element_type=jnp.float32)
            y = y + jnp.dot(a_high, ent_low, preferred_element_type=jnp.float32)
        acc = y[:rows]
        for k in range(1, groups_here):
            acc = jnp.where(lane_group == k, y[k * rows:(k + 1) * rows], acc)
        if scaled:
            out_ref[:, lanes] = (acc * first_ref[:, lanes].astype(jnp.float32)).astype(out_ref.dtype)
            other_ref[:, lanes] = (acc * second_ref[:, lanes].astype(jnp.float32)).astype(other_ref.dtype)
        else:
            out_ref[:, lanes] = acc
        return carry

    lax.fori_loop(0, sub, body, 0)


def band_conv(
    band_rows, top, bottom=None, modal_args=None, scale_pair=None, *, group_size, split, tri, modal=None
):
    rows, chans = top.shape
    block = min(BLOCK_LANES, chans)
    groups_block = block // group_size
    width = band_rows.shape[1]
    two_inputs = bottom is not None
    in_specs = [
        pl.BlockSpec((groups_block, width), lambda b: (b, 0)),
        pl.BlockSpec((rows, block), lambda b: (0, b)),
    ]
    args = [band_rows, top]
    if two_inputs:
        in_specs.append(pl.BlockSpec((rows, block), lambda b: (0, b)))
        args.append(bottom)
    if modal is not None:
        decays, weights, entering = modal_args
        modes = decays.shape[1]
        in_specs += [
            pl.BlockSpec((groups_block, modes), lambda b: (b, 0)),
            pl.BlockSpec((groups_block, modes), lambda b: (b, 0)),
            pl.BlockSpec((modes, block), lambda b: (0, b)),
        ]
        args += [decays, weights, entering]
    scaled = scale_pair is not None
    out_specs = pl.BlockSpec((rows, block), lambda b: (0, b))
    out_shape = jax.ShapeDtypeStruct((rows, chans), jnp.float32)
    if scaled:
        in_specs += [pl.BlockSpec((rows, block), lambda b: (0, b))] * 2
        args += list(scale_pair)
        out_specs = [out_specs, out_specs]
        out_shape = [jax.ShapeDtypeStruct((rows, chans), jnp.bfloat16)] * 2
    kernel = functools.partial(
        _band_kernel,
        group_size=group_size,
        split=split,
        tri=tri,
        two_inputs=two_inputs,
        modal=modal,
        sub=block // LANES,
        scaled=scaled,
    )
    return pl.pallas_call(
        kernel,
        grid=(chans // block,),
        in_specs=in_specs,
        out_specs=out_specs,
        out_shape=out_shape,
        compiler_params=pltpu.CompilerParams(dimension_semantics=("parallel",)),
    )(*args)


def _state_kernel(e_ref, x_ref, s_ref, *, group_size, sub):
    modes = s_ref.shape[0]
    groups_here = LANES // group_size
    state_group = lax.broadcasted_iota(jnp.int32, (modes, LANES), 1) // group_size

    def body(j, carry):
        lanes = pl.ds(pl.multiple_of(j * LANES, LANES), LANES)
        x = x_ref[:, lanes]
        weights = e_ref[pl.ds(j * groups_here, groups_here)]
        stacked = weights.reshape(groups_here * modes, weights.shape[2]).astype(jnp.bfloat16)
        y = jnp.dot(stacked, x, preferred_element_type=jnp.float32)
        acc = y[:modes]
        for k in range(1, groups_here):
            acc = jnp.where(state_group == k, y[k * modes:(k + 1) * modes], acc)
        s_ref[:, lanes] = acc
        return carry

    lax.fori_loop(0, sub, body, 0)


def modal_states(state_rows, x, *, group_size):
    rows, chans = x.shape
    block = min(BLOCK_LANES, chans)
    groups_block = block // group_size
    modes = state_rows.shape[1]
    kernel = functools.partial(_state_kernel, group_size=group_size, sub=block // LANES)
    return pl.pallas_call(
        kernel,
        grid=(chans // block,),
        in_specs=[
            pl.BlockSpec((groups_block, modes, rows), lambda b: (b, 0, 0)),
            pl.BlockSpec((rows, block), lambda b: (0, b)),
        ],
        out_specs=pl.BlockSpec((modes, block), lambda b: (0, b)),
        out_shape=jax.ShapeDtypeStruct((modes, chans), jnp.float32),
        compiler_params=pltpu.CompilerParams(dimension_semantics=("parallel",)),
    )(state_rows, x)


def _modal_kernel(dec_ref, wt_ref, ent_ref, loc_ref, out_ref, *, group_size, forward, sub):
    rows = out_ref.shape[0]
    modes = ent_ref.shape[0]
    groups_here = LANES // group_size
    width = groups_here * modes
    offsets = lax.broadcasted_iota(jnp.int32, (rows, width), 0).astype(jnp.float32)
    dist = offsets + 1.0 if forward else float(rows) - offsets
    row_group = lax.broadcasted_iota(jnp.int32, (width, LANES), 0) // modes
    lane_group = lax.broadcasted_iota(jnp.int32, (width, LANES), 1) // group_size

    def body(j, carry):
        lanes = pl.ds(pl.multiple_of(j * LANES, LANES), LANES)
        row = pl.program_id(0) * sub + j
        rate = dec_ref[pl.ds(row, 1), :]
        weight = wt_ref[pl.ds(row, 1), :]
        a_high, a_low = _split(weight * jnp.exp(-rate * dist))
        entering = ent_ref[:, lanes]
        tiled = jnp.concatenate([entering] * groups_here, axis=0)
        diag = jnp.where(row_group == lane_group, tiled, 0.0)
        ent_high, ent_low = _split(diag)
        y = jnp.dot(a_high, ent_high, preferred_element_type=jnp.float32)
        y = y + jnp.dot(a_low, ent_high, preferred_element_type=jnp.float32)
        y = y + jnp.dot(a_high, ent_low, preferred_element_type=jnp.float32)
        out_ref[:, lanes] = loc_ref[:, lanes] + y
        return carry

    lax.fori_loop(0, sub, body, 0)


def modal_out(decays, weights, entering, local, *, group_size, forward):
    rows, chans = local.shape
    block = min(BLOCK_LANES, chans)
    groups_block = block // group_size
    modes = decays.shape[1]
    per_row = (LANES // group_size) * modes
    flat_decays = decays.reshape(-1, per_row)
    flat_weights = weights.reshape(-1, per_row)
    sub = block // LANES
    kernel = functools.partial(_modal_kernel, group_size=group_size, forward=forward, sub=sub)
    return pl.pallas_call(
        kernel,
        grid=(chans // block,),
        in_specs=[
            pl.BlockSpec(flat_decays.shape, lambda b: (0, 0)),
            pl.BlockSpec(flat_weights.shape, lambda b: (0, 0)),
            pl.BlockSpec((modes, block), lambda b: (0, b)),
            pl.BlockSpec((rows, block), lambda b: (0, b)),
        ],
        out_specs=pl.BlockSpec((rows, block), lambda b: (0, b)),
        out_shape=jax.ShapeDtypeStruct((rows, chans), jnp.float32),
        compiler_params=pltpu.CompilerParams(dimension_semantics=("parallel",)),
    )(flat_decays, flat_weights, entering, local)


def _gram_kernel(back_ref, top_ref, bot_ref, f_ref, *, group_size, sub):
    rows = back_ref.shape[0]
    groups_here = LANES // group_size
    r_id = lax.broadcasted_iota(jnp.int32, (rows, rows), 0)
    c_id = lax.broadcasted_iota(jnp.int32, (rows, rows), 1)
    exchange = jnp.where(r_id + c_id == rows - 1, 1.0, 0.0).astype(jnp.bfloat16)
    lane_group = lax.broadcasted_iota(jnp.int32, (rows, LANES), 1) // group_size

    def body(j, carry):
        lanes = pl.ds(pl.multiple_of(j * LANES, LANES), LANES)
        back = back_ref[:, lanes]
        x = jnp.concatenate([top_ref[:, lanes], bot_ref[:, lanes]], axis=0)
        back_rev = jnp.dot(exchange, back, preferred_element_type=jnp.float32).astype(jnp.bfloat16)
        masked = jnp.concatenate(
            [jnp.where(lane_group == k, back_rev, jnp.zeros_like(back_rev)) for k in range(groups_here)],
            axis=0,
        )
        gram = lax.dot_general(
            masked, x, (((1,), (1,)), ((), ())), preferred_element_type=jnp.float32
        )
        sums = []
        for k in range(groups_here):
            skew = pltpu.roll(gram[k * rows:(k + 1) * rows], 0, 1, stride=1, stride_axis=0)
            sums.append(jnp.sum(skew, axis=0, keepdims=True))
        f_ref[pl.ds(pl.multiple_of(j * groups_here, groups_here), groups_here), :] = jnp.concatenate(sums, 0)
        return carry

    lax.fori_loop(0, sub, body, 0)


def gram_diag(back, top, bottom, *, group_size):
    rows, chans = back.shape
    block = min(BLOCK_LANES, chans)
    groups_block = block // group_size
    group_count = chans // group_size
    kernel = functools.partial(_gram_kernel, group_size=group_size, sub=block // LANES)
    return pl.pallas_call(
        kernel,
        grid=(chans // block,),
        in_specs=[
            pl.BlockSpec((rows, block), lambda b: (0, b)),
            pl.BlockSpec((rows, block), lambda b: (0, b)),
            pl.BlockSpec((rows, block), lambda b: (0, b)),
        ],
        out_specs=pl.BlockSpec((groups_block, 2 * rows), lambda b: (b, 0)),
        out_shape=jax.ShapeDtypeStruct((group_count, 2 * rows), jnp.float32),
        compiler_params=pltpu.CompilerParams(dimension_semantics=("parallel",)),
    )(back, top, bottom)


def gather_seq(value):
    count = lax.axis_size("seq")
    tiled = jnp.broadcast_to(value[None], (count,) + value.shape)
    return lax.all_to_all(tiled, "seq", split_axis=0, concat_axis=0, tiled=True)


def entering_states(gathered, decays, block_len, group_size, forward):
    count = gathered.shape[0]
    here = lax.axis_index("seq")
    rates = jnp.repeat(decays.T, group_size, axis=1)
    source = jnp.arange(count)
    if forward:
        gap = here - 1 - source
    else:
        gap = source - here - 1
    valid = gap >= 0
    steps = jnp.maximum(gap, 0).astype(jnp.float32)
    coef = jnp.exp(-rates[None] * (float(block_len) * steps)[:, None, None])
    coef = jnp.where(valid[:, None, None], coef, 0.0)
    return jnp.sum(coef * gathered, axis=0)


def on_device(
    query_mr,
    key_mr,
    value_mr,
    query_li,
    key_li,
    cotangent,
    mr_filter,
    norm_gain,
    li_decay,
    li_residue,
):
    row_count, chan_count = query_mr.shape
    group_count, tap_count = mr_filter.shape
    group_size = chan_count // group_count
    assert row_count == tap_count
    grad_scale = float(row_count * lax.axis_size("seq")) ** (-0.5)

    taps_mr = mr_filter.astype(jnp.bfloat16).astype(jnp.float32)
    zero_col = jnp.zeros((group_count, 1), jnp.float32)
    fwd_rows = jnp.concatenate(
        [zero_col, jnp.flip(taps_mr, 1), jnp.zeros((group_count, tap_count - 1), jnp.float32)], 1
    )
    bwd_rows = jnp.concatenate([taps_mr, jnp.zeros_like(taps_mr)], 1)

    mixed_mr = (key_mr.astype(jnp.float32) * value_mr.astype(jnp.float32)).astype(jnp.bfloat16)
    rim_rows = from_behind(mixed_mr, "seq", 1)
    conv_mr = band_conv(fwd_rows, rim_rows, mixed_mr, group_size=group_size, split=False, tri=None)
    out_mr = (query_mr.astype(jnp.float32) * conv_mr).astype(jnp.bfloat16)
    out_full = out_mr.astype(jnp.float32)
    squares = lax.psum(jnp.sum(out_full * out_full, axis=1), "chan")
    inv_rms = lax.rsqrt(squares / D + 1e-06)[:, None]
    normed = out_full * inv_rms * norm_gain
    mixed_li = key_li.astype(jnp.float32) * normed
    cotan_full = cotangent.astype(jnp.float32)
    back_li = cotan_full * query_li.astype(jnp.float32)

    offsets = jnp.arange(row_count, dtype=jnp.float32)
    weights_res = li_residue * jnp.sqrt(2.0 * li_decay)
    taps_li = jnp.einsum(
        "gr,grd->gd", weights_res, jnp.exp(-li_decay[:, :, None] * offsets), precision=HIGHEST
    )
    li_fwd_rows = jnp.concatenate([taps_li[:, :1], jnp.flip(taps_li[:, 1:], 1)], 1)
    fwd_states = jnp.exp(-li_decay[:, :, None] * (row_count - 1.0 - offsets))
    bwd_states = jnp.exp(-li_decay[:, :, None] * offsets)

    back_li_bf = back_li.astype(jnp.bfloat16)
    mixed_li_bf = mixed_li.astype(jnp.bfloat16)
    modes = li_decay.shape[1]
    grad_st = modal_states(bwd_states, back_li_bf, group_size=group_size)
    conv_st = modal_states(fwd_states, mixed_li_bf, group_size=group_size)
    both_st = gather_seq(jnp.concatenate([grad_st, conv_st], 0).astype(jnp.bfloat16))
    both_st = both_st.astype(jnp.float32)
    grad_loc = band_conv(taps_li, back_li_bf, group_size=group_size, split=False, tri="upper")
    conv_loc = band_conv(li_fwd_rows, mixed_li_bf, group_size=group_size, split=False, tri="lower")
    grad_ent = entering_states(both_st[:, :modes], li_decay, row_count, group_size, False)
    conv_ent = entering_states(both_st[:, modes:], li_decay, row_count, group_size, True)
    grad_mixed_li = modal_out(
        li_decay, weights_res, grad_ent, grad_loc, group_size=group_size, forward=False
    )
    conv_li = modal_out(li_decay, weights_res, conv_ent, conv_loc, group_size=group_size, forward=True)

    out_li = (query_li.astype(jnp.float32) * conv_li).astype(jnp.bfloat16)
    grad_query_li = (cotan_full * conv_li).astype(jnp.bfloat16)
    grad_key_li = (grad_mixed_li * normed).astype(jnp.bfloat16)
    grad_normed = grad_mixed_li * key_li.astype(jnp.float32)
    gain_part = jnp.sum(grad_normed * out_full * inv_rms, axis=0)
    weighted = grad_normed * norm_gain
    cross_dots = lax.psum(jnp.sum(weighted * out_full, axis=1), "chan")[:, None]
    grad_out_mr = inv_rms * weighted - out_full * inv_rms**3 * cross_dots / D
    grad_query_mr = (grad_out_mr * conv_mr).astype(jnp.bfloat16)
    back_mr = (grad_out_mr * query_mr.astype(jnp.float32)).astype(jnp.bfloat16)
    after_rim = from_behind(back_mr, "seq", -1)
    grad_key_mr, grad_value_mr = band_conv(
        bwd_rows, back_mr, after_rim, scale_pair=(value_mr, key_mr),
        group_size=group_size, split=False, tri=None,
    )
    diag_sums = gram_diag(back_mr, rim_rows, mixed_mr, group_size=group_size)
    filter_part = jnp.flip(diag_sums[:, tap_count:], 1)
    packed = jnp.concatenate([gain_part, filter_part.reshape(-1)])
    param_sums = jnp.sum(gather_seq(packed), axis=0) * grad_scale
    grad_gain = param_sums[:chan_count]
    grad_filter = param_sums[chan_count:].reshape(group_count, tap_count)
    return (
        out_li,
        grad_query_mr,
        grad_key_mr,
        grad_value_mr,
        grad_query_li,
        grad_key_li,
        grad_gain,
        grad_filter,
    )


def solution(mesh):
    in_specs = (
        P("seq", "chan"),
        P("seq", "chan"),
        P("seq", "chan"),
        P("seq", "chan"),
        P("seq", "chan"),
        P("seq", "chan"),
        P("chan", None),
        P("chan"),
        P("chan", None),
        P("chan", None),
    )
    out_specs = (
        P("seq", "chan"),
        P("seq", "chan"),
        P("seq", "chan"),
        P("seq", "chan"),
        P("seq", "chan"),
        P("seq", "chan"),
        P("chan"),
        P("chan", None),
    )
    return jax.shard_map(
        on_device, mesh=mesh, in_specs=in_specs, out_specs=out_specs, check_vma=False
    )
```

```python
import functools

import jax
import jax.numpy as jnp
from jax import lax
from jax.experimental import pallas as pl
from jax.experimental.pallas import tpu as pltpu
from jax.sharding import PartitionSpec as P

D = 8192
G = 512
LANES = 128
BLOCK_LANES = 512
HIGHEST = lax.Precision.HIGHEST


def from_behind(value, axis, steps):
    count = lax.axis_size(axis)
    initial, last = (max(0, -steps), min(count, count - steps))
    return lax.ppermute(value, axis, [(source, source + steps) for source in range(initial, last)])


def _split(value):
    high = value.astype(jnp.bfloat16)
    return high, (value - high.astype(jnp.float32)).astype(jnp.bfloat16)


def _band_kernel(*refs, group_size, split, tri, two_inputs, modal, sub, scaled):
    refs = list(refs)
    h_ref = refs.pop(0)
    top_ref = refs.pop(0)
    bot_ref = refs.pop(0) if two_inputs else None
    if modal is not None:
        dec_ref, wt_ref, ent_ref = refs.pop(0), refs.pop(0), refs.pop(0)
    if scaled:
        first_ref, second_ref = refs.pop(0), refs.pop(0)
    out_ref = refs.pop(0)
    if scaled:
        other_ref = refs.pop(0)
    rows = out_ref.shape[0]
    width = h_ref.shape[1]
    groups_here = LANES // group_size
    lane_group = lax.broadcasted_iota(jnp.int32, (rows, LANES), 1) // group_size
    row_id = lax.broadcasted_iota(jnp.int32, (rows, width), 0)
    col_id = lax.broadcasted_iota(jnp.int32, (rows, width), 1)
    if modal is not None:
        modes = dec_ref.shape[1]
        offsets = lax.broadcasted_iota(jnp.int32, (rows, modes), 0).astype(jnp.float32)
        dist = offsets + 1.0 if modal == "forward" else float(rows) - offsets

    def body(j, carry):
        lanes = pl.ds(pl.multiple_of(j * LANES, LANES), LANES)
        if two_inputs:
            x = jnp.concatenate([top_ref[:, lanes], bot_ref[:, lanes]], axis=0)
        else:
            x = top_ref[:, lanes]
        bands = []
        for k in range(groups_here):
            band_row = h_ref[pl.ds(j * groups_here + k, 1), :]
            band = pltpu.roll(jnp.broadcast_to(band_row, (rows, width)), 0, 1, stride=1, stride_axis=0)
            if tri == "lower":
                band = jnp.where(col_id <= row_id, band, 0.0)
            elif tri == "upper":
                band = jnp.where(col_id >= row_id, band, 0.0)
            bands.append(band)
        stacked = jnp.concatenate(bands, axis=0)
        if split:
            high, low = _split(stacked)
            y = jnp.dot(high, x, preferred_element_type=jnp.float32)
            y = y + jnp.dot(low, x, preferred_element_type=jnp.float32)
        else:
            y = jnp.dot(stacked.astype(jnp.bfloat16), x, preferred_element_type=jnp.float32)
        if modal is not None:
            ent_high, ent_low = _split(ent_ref[:, lanes])
            out_w = []
            for k in range(groups_here):
                rate = dec_ref[pl.ds(j * groups_here + k, 1), :]
                weight = wt_ref[pl.ds(j * groups_here + k, 1), :]
                out_w.append(weight * jnp.exp(-rate * dist))
            a_high, a_low = _split(jnp.concatenate(out_w, axis=0))
            y = y + jnp.dot(a_high, ent_high, preferred_element_type=jnp.float32)
            y = y + jnp.dot(a_low, ent_high, preferred_element_type=jnp.float32)
            y = y + jnp.dot(a_high, ent_low, preferred_element_type=jnp.float32)
        acc = y[:rows]
        for k in range(1, groups_here):
            acc = jnp.where(lane_group == k, y[k * rows:(k + 1) * rows], acc)
        if scaled:
            out_ref[:, lanes] = (acc * first_ref[:, lanes].astype(jnp.float32)).astype(out_ref.dtype)
            other_ref[:, lanes] = (acc * second_ref[:, lanes].astype(jnp.float32)).astype(other_ref.dtype)
        else:
            out_ref[:, lanes] = acc
        return carry

    lax.fori_loop(0, sub, body, 0)


def band_conv(
    band_rows, top, bottom=None, modal_args=None, scale_pair=None, *, group_size, split, tri, modal=None
):
    rows, chans = top.shape
    block = min(BLOCK_LANES, chans)
    groups_block = block // group_size
    width = band_rows.shape[1]
    two_inputs = bottom is not None
    in_specs = [
        pl.BlockSpec((groups_block, width), lambda b: (b, 0)),
        pl.BlockSpec((rows, block), lambda b: (0, b)),
    ]
    args = [band_rows, top]
    if two_inputs:
        in_specs.append(pl.BlockSpec((rows, block), lambda b: (0, b)))
        args.append(bottom)
    if modal is not None:
        decays, weights, entering = modal_args
        modes = decays.shape[1]
        in_specs += [
            pl.BlockSpec((groups_block, modes), lambda b: (b, 0)),
            pl.BlockSpec((groups_block, modes), lambda b: (b, 0)),
            pl.BlockSpec((modes, block), lambda b: (0, b)),
        ]
        args += [decays, weights, entering]
    scaled = scale_pair is not None
    out_specs = pl.BlockSpec((rows, block), lambda b: (0, b))
    out_shape = jax.ShapeDtypeStruct((rows, chans), jnp.float32)
    if scaled:
        in_specs += [pl.BlockSpec((rows, block), lambda b: (0, b))] * 2
        args += list(scale_pair)
        out_specs = [out_specs, out_specs]
        out_shape = [jax.ShapeDtypeStruct((rows, chans), jnp.bfloat16)] * 2
    kernel = functools.partial(
        _band_kernel,
        group_size=group_size,
        split=split,
        tri=tri,
        two_inputs=two_inputs,
        modal=modal,
        sub=block // LANES,
        scaled=scaled,
    )
    return pl.pallas_call(
        kernel,
        grid=(chans // block,),
        in_specs=in_specs,
        out_specs=out_specs,
        out_shape=out_shape,
        compiler_params=pltpu.CompilerParams(dimension_semantics=("parallel",)),
    )(*args)


def _state_kernel(e_ref, x_ref, s_ref, *, group_size, sub):
    modes = s_ref.shape[0]
    groups_here = LANES // group_size
    state_group = lax.broadcasted_iota(jnp.int32, (modes, LANES), 1) // group_size

    def body(j, carry):
        lanes = pl.ds(pl.multiple_of(j * LANES, LANES), LANES)
        x = x_ref[:, lanes]
        weights = e_ref[pl.ds(j * groups_here, groups_here)]
        stacked = weights.reshape(groups_here * modes, weights.shape[2]).astype(jnp.bfloat16)
        y = jnp.dot(stacked, x, preferred_element_type=jnp.float32)
        acc = y[:modes]
        for k in range(1, groups_here):
            acc = jnp.where(state_group == k, y[k * modes:(k + 1) * modes], acc)
        s_ref[:, lanes] = acc
        return carry

    lax.fori_loop(0, sub, body, 0)


def modal_states(state_rows, x, *, group_size):
    rows, chans = x.shape
    block = min(BLOCK_LANES, chans)
    groups_block = block // group_size
    modes = state_rows.shape[1]
    kernel = functools.partial(_state_kernel, group_size=group_size, sub=block // LANES)
    return pl.pallas_call(
        kernel,
        grid=(chans // block,),
        in_specs=[
            pl.BlockSpec((groups_block, modes, rows), lambda b: (b, 0, 0)),
            pl.BlockSpec((rows, block), lambda b: (0, b)),
        ],
        out_specs=pl.BlockSpec((modes, block), lambda b: (0, b)),
        out_shape=jax.ShapeDtypeStruct((modes, chans), jnp.float32),
        compiler_params=pltpu.CompilerParams(dimension_semantics=("parallel",)),
    )(state_rows, x)


def _modal_kernel(dec_ref, wt_ref, ent_ref, loc_ref, out_ref, *, group_size, forward, sub):
    rows = out_ref.shape[0]
    modes = ent_ref.shape[0]
    groups_here = LANES // group_size
    width = groups_here * modes
    offsets = lax.broadcasted_iota(jnp.int32, (rows, width), 0).astype(jnp.float32)
    dist = offsets + 1.0 if forward else float(rows) - offsets
    row_group = lax.broadcasted_iota(jnp.int32, (width, LANES), 0) // modes
    lane_group = lax.broadcasted_iota(jnp.int32, (width, LANES), 1) // group_size

    def body(j, carry):
        lanes = pl.ds(pl.multiple_of(j * LANES, LANES), LANES)
        row = pl.program_id(0) * sub + j
        rate = dec_ref[pl.ds(row, 1), :]
        weight = wt_ref[pl.ds(row, 1), :]
        a_high, a_low = _split(weight * jnp.exp(-rate * dist))
        entering = ent_ref[:, lanes]
        tiled = jnp.concatenate([entering] * groups_here, axis=0)
        diag = jnp.where(row_group == lane_group, tiled, 0.0)
        ent_high, ent_low = _split(diag)
        y = jnp.dot(a_high, ent_high, preferred_element_type=jnp.float32)
        y = y + jnp.dot(a_low, ent_high, preferred_element_type=jnp.float32)
        y = y + jnp.dot(a_high, ent_low, preferred_element_type=jnp.float32)
        out_ref[:, lanes] = loc_ref[:, lanes] + y
        return carry

    lax.fori_loop(0, sub, body, 0)


def modal_out(decays, weights, entering, local, *, group_size, forward):
    rows, chans = local.shape
    block = min(BLOCK_LANES, chans)
    groups_block = block // group_size
    modes = decays.shape[1]
    per_row = (LANES // group_size) * modes
    flat_decays = decays.reshape(-1, per_row)
    flat_weights = weights.reshape(-1, per_row)
    sub = block // LANES
    kernel = functools.partial(_modal_kernel, group_size=group_size, forward=forward, sub=sub)
    return pl.pallas_call(
        kernel,
        grid=(chans // block,),
        in_specs=[
            pl.BlockSpec(flat_decays.shape, lambda b: (0, 0)),
            pl.BlockSpec(flat_weights.shape, lambda b: (0, 0)),
            pl.BlockSpec((modes, block), lambda b: (0, b)),
            pl.BlockSpec((rows, block), lambda b: (0, b)),
        ],
        out_specs=pl.BlockSpec((rows, block), lambda b: (0, b)),
        out_shape=jax.ShapeDtypeStruct((rows, chans), jnp.float32),
        compiler_params=pltpu.CompilerParams(dimension_semantics=("parallel",)),
    )(flat_decays, flat_weights, entering, local)


def _gram_kernel(back_ref, top_ref, bot_ref, f_ref, *, group_size, sub):
    rows = back_ref.shape[0]
    groups_here = LANES // group_size
    r_id = lax.broadcasted_iota(jnp.int32, (rows, rows), 0)
    c_id = lax.broadcasted_iota(jnp.int32, (rows, rows), 1)
    exchange = jnp.where(r_id + c_id == rows - 1, 1.0, 0.0).astype(jnp.bfloat16)
    lane_group = lax.broadcasted_iota(jnp.int32, (rows, LANES), 1) // group_size

    def body(j, carry):
        lanes = pl.ds(pl.multiple_of(j * LANES, LANES), LANES)
        back = back_ref[:, lanes]
        x = jnp.concatenate([top_ref[:, lanes], bot_ref[:, lanes]], axis=0)
        back_rev = jnp.dot(exchange, back, preferred_element_type=jnp.float32).astype(jnp.bfloat16)
        masked = jnp.concatenate(
            [jnp.where(lane_group == k, back_rev, jnp.zeros_like(back_rev)) for k in range(groups_here)],
            axis=0,
        )
        gram = lax.dot_general(
            masked, x, (((1,), (1,)), ((), ())), preferred_element_type=jnp.float32
        )
        sums = []
        for k in range(groups_here):
            skew = pltpu.roll(gram[k * rows:(k + 1) * rows], 0, 1, stride=1, stride_axis=0)
            sums.append(jnp.sum(skew, axis=0, keepdims=True))
        f_ref[pl.ds(pl.multiple_of(j * groups_here, groups_here), groups_here), :] = jnp.concatenate(sums, 0)
        return carry

    lax.fori_loop(0, sub, body, 0)


def gram_diag(back, top, bottom, *, group_size):
    rows, chans = back.shape
    block = min(BLOCK_LANES, chans)
    groups_block = block // group_size
    group_count = chans // group_size
    kernel = functools.partial(_gram_kernel, group_size=group_size, sub=block // LANES)
    return pl.pallas_call(
        kernel,
        grid=(chans // block,),
        in_specs=[
            pl.BlockSpec((rows, block), lambda b: (0, b)),
            pl.BlockSpec((rows, block), lambda b: (0, b)),
            pl.BlockSpec((rows, block), lambda b: (0, b)),
        ],
        out_specs=pl.BlockSpec((groups_block, 2 * rows), lambda b: (b, 0)),
        out_shape=jax.ShapeDtypeStruct((group_count, 2 * rows), jnp.float32),
        compiler_params=pltpu.CompilerParams(dimension_semantics=("parallel",)),
    )(back, top, bottom)


def gather_seq(value):
    count = lax.axis_size("seq")
    tiled = jnp.broadcast_to(value[None], (count,) + value.shape)
    return lax.all_to_all(tiled, "seq", split_axis=0, concat_axis=0, tiled=True)


def entering_states(gathered, decays, block_len, group_size, forward):
    count = gathered.shape[0]
    here = lax.axis_index("seq")
    rates = jnp.repeat(decays.T, group_size, axis=1)
    source = jnp.arange(count)
    if forward:
        gap = here - 1 - source
    else:
        gap = source - here - 1
    valid = gap >= 0
    steps = jnp.maximum(gap, 0).astype(jnp.float32)
    coef = jnp.exp(-rates[None] * (float(block_len) * steps)[:, None, None])
    coef = jnp.where(valid[:, None, None], coef, 0.0)
    return jnp.sum(coef * gathered, axis=0)


def on_device(
    query_mr,
    key_mr,
    value_mr,
    query_li,
    key_li,
    cotangent,
    mr_filter,
    norm_gain,
    li_decay,
    li_residue,
):
    row_count, chan_count = query_mr.shape
    group_count, tap_count = mr_filter.shape
    group_size = chan_count // group_count
    assert row_count == tap_count
    grad_scale = float(row_count * lax.axis_size("seq")) ** (-0.5)

    taps_mr = mr_filter.astype(jnp.bfloat16).astype(jnp.float32)
    zero_col = jnp.zeros((group_count, 1), jnp.float32)
    fwd_rows = jnp.concatenate(
        [zero_col, jnp.flip(taps_mr, 1), jnp.zeros((group_count, tap_count - 1), jnp.float32)], 1
    )
    bwd_rows = jnp.concatenate([taps_mr, jnp.zeros_like(taps_mr)], 1)

    mixed_mr = (key_mr.astype(jnp.float32) * value_mr.astype(jnp.float32)).astype(jnp.bfloat16)
    rim_rows = from_behind(mixed_mr, "seq", 1)
    conv_mr = band_conv(fwd_rows, rim_rows, mixed_mr, group_size=group_size, split=False, tri=None)
    out_mr = (query_mr.astype(jnp.float32) * conv_mr).astype(jnp.bfloat16)
    out_full = out_mr.astype(jnp.float32)
    squares = lax.psum(jnp.sum(out_full * out_full, axis=1), "chan")
    inv_rms = lax.rsqrt(squares / D + 1e-06)[:, None]
    normed = out_full * inv_rms * norm_gain
    mixed_li = key_li.astype(jnp.float32) * normed
    cotan_full = cotangent.astype(jnp.float32)
    back_li = cotan_full * query_li.astype(jnp.float32)

    offsets = jnp.arange(row_count, dtype=jnp.float32)
    weights_res = li_residue * jnp.sqrt(2.0 * li_decay)
    taps_li = jnp.einsum(
        "gr,grd->gd", weights_res, jnp.exp(-li_decay[:, :, None] * offsets), precision=HIGHEST
    )
    li_fwd_rows = jnp.concatenate([taps_li[:, :1], jnp.flip(taps_li[:, 1:], 1)], 1)
    fwd_states = jnp.exp(-li_decay[:, :, None] * (row_count - 1.0 - offsets))
    bwd_states = jnp.exp(-li_decay[:, :, None] * offsets)

    back_li_bf = back_li.astype(jnp.bfloat16)
    mixed_li_bf = mixed_li.astype(jnp.bfloat16)
    modes = li_decay.shape[1]
    grad_st = modal_states(bwd_states, back_li_bf, group_size=group_size)
    conv_st = modal_states(fwd_states, mixed_li_bf, group_size=group_size)
    both_st = gather_seq(jnp.concatenate([grad_st, conv_st], 0).astype(jnp.bfloat16))
    both_st = both_st.astype(jnp.float32)
    grad_loc = band_conv(taps_li, back_li_bf, group_size=group_size, split=False, tri="upper")
    conv_loc = band_conv(li_fwd_rows, mixed_li_bf, group_size=group_size, split=False, tri="lower")
    both_st, grad_loc, conv_loc = lax.optimization_barrier((both_st, grad_loc, conv_loc))
    grad_ent = entering_states(both_st[:, :modes], li_decay, row_count, group_size, False)
    conv_ent = entering_states(both_st[:, modes:], li_decay, row_count, group_size, True)
    grad_mixed_li = modal_out(
        li_decay, weights_res, grad_ent, grad_loc, group_size=group_size, forward=False
    )
    conv_li = modal_out(li_decay, weights_res, conv_ent, conv_loc, group_size=group_size, forward=True)

    out_li = (query_li.astype(jnp.float32) * conv_li).astype(jnp.bfloat16)
    grad_query_li = (cotan_full * conv_li).astype(jnp.bfloat16)
    grad_key_li = (grad_mixed_li * normed).astype(jnp.bfloat16)
    grad_normed = grad_mixed_li * key_li.astype(jnp.float32)
    gain_part = jnp.sum(grad_normed * out_full * inv_rms, axis=0)
    weighted = grad_normed * norm_gain
    cross_dots = lax.psum(jnp.sum(weighted * out_full, axis=1), "chan")[:, None]
    grad_out_mr = inv_rms * weighted - out_full * inv_rms**3 * cross_dots / D
    grad_query_mr = (grad_out_mr * conv_mr).astype(jnp.bfloat16)
    back_mr = (grad_out_mr * query_mr.astype(jnp.float32)).astype(jnp.bfloat16)
    after_rim = from_behind(back_mr, "seq", -1)
    grad_key_mr, grad_value_mr = band_conv(
        bwd_rows, back_mr, after_rim, scale_pair=(value_mr, key_mr),
        group_size=group_size, split=False, tri=None,
    )
    diag_sums = gram_diag(back_mr, rim_rows, mixed_mr, group_size=group_size)
    filter_part = jnp.flip(diag_sums[:, tap_count:], 1)
    packed = jnp.concatenate([gain_part, filter_part.reshape(-1)])
    param_sums = jnp.sum(gather_seq(packed), axis=0) * grad_scale
    grad_gain = param_sums[:chan_count]
    grad_filter = param_sums[chan_count:].reshape(group_count, tap_count)
    return (
        out_li,
        grad_query_mr,
        grad_key_mr,
        grad_value_mr,
        grad_query_li,
        grad_key_li,
        grad_gain,
        grad_filter,
    )


def solution(mesh):
    in_specs = (
        P("seq", "chan"),
        P("seq", "chan"),
        P("seq", "chan"),
        P("seq", "chan"),
        P("seq", "chan"),
        P("seq", "chan"),
        P("chan", None),
        P("chan"),
        P("chan", None),
        P("chan", None),
    )
    out_specs = (
        P("seq", "chan"),
        P("seq", "chan"),
        P("seq", "chan"),
        P("seq", "chan"),
        P("seq", "chan"),
        P("seq", "chan"),
        P("chan"),
        P("chan", None),
    )
    return jax.shard_map(
        on_device, mesh=mesh, in_specs=in_specs, out_specs=out_specs, check_vma=False
    )
```

```python
import functools

import jax
import jax.numpy as jnp
from jax import lax
from jax.experimental import pallas as pl
from jax.experimental.pallas import tpu as pltpu
from jax.sharding import PartitionSpec as P

D = 8192
G = 512
LANES = 128
BLOCK_LANES = 512
HIGHEST = lax.Precision.HIGHEST


def from_behind(value, axis, steps):
    count = lax.axis_size(axis)
    initial, last = (max(0, -steps), min(count, count - steps))
    return lax.ppermute(value, axis, [(source, source + steps) for source in range(initial, last)])


def _split(value):
    high = value.astype(jnp.bfloat16)
    return high, (value - high.astype(jnp.float32)).astype(jnp.bfloat16)


def _band_kernel(*refs, group_size, split, tri, two_inputs, modal, sub, scaled):
    refs = list(refs)
    h_ref = refs.pop(0)
    top_ref = refs.pop(0)
    bot_ref = refs.pop(0) if two_inputs else None
    if modal is not None:
        dec_ref, wt_ref, ent_ref = refs.pop(0), refs.pop(0), refs.pop(0)
    if scaled:
        first_ref, second_ref = refs.pop(0), refs.pop(0)
    out_ref = refs.pop(0)
    if scaled:
        other_ref = refs.pop(0)
    rows = out_ref.shape[0]
    width = h_ref.shape[1]
    groups_here = LANES // group_size
    lane_group = lax.broadcasted_iota(jnp.int32, (rows, LANES), 1) // group_size
    row_id = lax.broadcasted_iota(jnp.int32, (rows, width), 0)
    col_id = lax.broadcasted_iota(jnp.int32, (rows, width), 1)
    if modal is not None:
        modes = dec_ref.shape[1]
        offsets = lax.broadcasted_iota(jnp.int32, (rows, modes), 0).astype(jnp.float32)
        dist = offsets + 1.0 if modal == "forward" else float(rows) - offsets

    def body(j, carry):
        lanes = pl.ds(pl.multiple_of(j * LANES, LANES), LANES)
        if two_inputs:
            x = jnp.concatenate([top_ref[:, lanes], bot_ref[:, lanes]], axis=0)
        else:
            x = top_ref[:, lanes]
        bands = []
        for k in range(groups_here):
            band_row = h_ref[pl.ds(j * groups_here + k, 1), :]
            band = pltpu.roll(jnp.broadcast_to(band_row, (rows, width)), 0, 1, stride=1, stride_axis=0)
            if tri == "lower":
                band = jnp.where(col_id <= row_id, band, 0.0)
            elif tri == "upper":
                band = jnp.where(col_id >= row_id, band, 0.0)
            bands.append(band)
        stacked = jnp.concatenate(bands, axis=0)
        if split:
            high, low = _split(stacked)
            y = jnp.dot(high, x, preferred_element_type=jnp.float32)
            y = y + jnp.dot(low, x, preferred_element_type=jnp.float32)
        else:
            y = jnp.dot(stacked.astype(jnp.bfloat16), x, preferred_element_type=jnp.float32)
        if modal is not None:
            ent_high, ent_low = _split(ent_ref[:, lanes])
            out_w = []
            for k in range(groups_here):
                rate = dec_ref[pl.ds(j * groups_here + k, 1), :]
                weight = wt_ref[pl.ds(j * groups_here + k, 1), :]
                out_w.append(weight * jnp.exp(-rate * dist))
            a_high, a_low = _split(jnp.concatenate(out_w, axis=0))
            y = y + jnp.dot(a_high, ent_high, preferred_element_type=jnp.float32)
            y = y + jnp.dot(a_low, ent_high, preferred_element_type=jnp.float32)
            y = y + jnp.dot(a_high, ent_low, preferred_element_type=jnp.float32)
        acc = y[:rows]
        for k in range(1, groups_here):
            acc = jnp.where(lane_group == k, y[k * rows:(k + 1) * rows], acc)
        if scaled:
            out_ref[:, lanes] = (acc * first_ref[:, lanes].astype(jnp.float32)).astype(out_ref.dtype)
            other_ref[:, lanes] = (acc * second_ref[:, lanes].astype(jnp.float32)).astype(other_ref.dtype)
        else:
            out_ref[:, lanes] = acc
        return carry

    lax.fori_loop(0, sub, body, 0)


def band_conv(
    band_rows, top, bottom=None, modal_args=None, scale_pair=None, *, group_size, split, tri, modal=None
):
    rows, chans = top.shape
    block = min(BLOCK_LANES, chans)
    groups_block = block // group_size
    width = band_rows.shape[1]
    two_inputs = bottom is not None
    in_specs = [
        pl.BlockSpec((groups_block, width), lambda b: (b, 0)),
        pl.BlockSpec((rows, block), lambda b: (0, b)),
    ]
    args = [band_rows, top]
    if two_inputs:
        in_specs.append(pl.BlockSpec((rows, block), lambda b: (0, b)))
        args.append(bottom)
    if modal is not None:
        decays, weights, entering = modal_args
        modes = decays.shape[1]
        in_specs += [
            pl.BlockSpec((groups_block, modes), lambda b: (b, 0)),
            pl.BlockSpec((groups_block, modes), lambda b: (b, 0)),
            pl.BlockSpec((modes, block), lambda b: (0, b)),
        ]
        args += [decays, weights, entering]
    scaled = scale_pair is not None
    out_specs = pl.BlockSpec((rows, block), lambda b: (0, b))
    out_shape = jax.ShapeDtypeStruct((rows, chans), jnp.float32)
    if scaled:
        in_specs += [pl.BlockSpec((rows, block), lambda b: (0, b))] * 2
        args += list(scale_pair)
        out_specs = [out_specs, out_specs]
        out_shape = [jax.ShapeDtypeStruct((rows, chans), jnp.bfloat16)] * 2
    kernel = functools.partial(
        _band_kernel,
        group_size=group_size,
        split=split,
        tri=tri,
        two_inputs=two_inputs,
        modal=modal,
        sub=block // LANES,
        scaled=scaled,
    )
    return pl.pallas_call(
        kernel,
        grid=(chans // block,),
        in_specs=in_specs,
        out_specs=out_specs,
        out_shape=out_shape,
        compiler_params=pltpu.CompilerParams(dimension_semantics=("parallel",)),
    )(*args)


def _state_kernel(e_ref, x_ref, s_ref, *, group_size, sub):
    modes = s_ref.shape[0]
    groups_here = LANES // group_size
    state_group = lax.broadcasted_iota(jnp.int32, (modes, LANES), 1) // group_size

    def body(j, carry):
        lanes = pl.ds(pl.multiple_of(j * LANES, LANES), LANES)
        x = x_ref[:, lanes]
        weights = e_ref[pl.ds(j * groups_here, groups_here)]
        stacked = weights.reshape(groups_here * modes, weights.shape[2]).astype(jnp.bfloat16)
        y = jnp.dot(stacked, x, preferred_element_type=jnp.float32)
        acc = y[:modes]
        for k in range(1, groups_here):
            acc = jnp.where(state_group == k, y[k * modes:(k + 1) * modes], acc)
        s_ref[:, lanes] = acc
        return carry

    lax.fori_loop(0, sub, body, 0)


def modal_states(state_rows, x, *, group_size):
    rows, chans = x.shape
    block = min(BLOCK_LANES, chans)
    groups_block = block // group_size
    modes = state_rows.shape[1]
    kernel = functools.partial(_state_kernel, group_size=group_size, sub=block // LANES)
    return pl.pallas_call(
        kernel,
        grid=(chans // block,),
        in_specs=[
            pl.BlockSpec((groups_block, modes, rows), lambda b: (b, 0, 0)),
            pl.BlockSpec((rows, block), lambda b: (0, b)),
        ],
        out_specs=pl.BlockSpec((modes, block), lambda b: (0, b)),
        out_shape=jax.ShapeDtypeStruct((modes, chans), jnp.float32),
        compiler_params=pltpu.CompilerParams(dimension_semantics=("parallel",)),
    )(state_rows, x)


def _modal_kernel(dec_ref, wt_ref, ent_ref, loc_ref, out_ref, *, group_size, forward, sub):
    rows = out_ref.shape[0]
    modes = ent_ref.shape[0]
    groups_here = LANES // group_size
    width = groups_here * modes
    offsets = lax.broadcasted_iota(jnp.int32, (rows, width), 0).astype(jnp.float32)
    dist = offsets + 1.0 if forward else float(rows) - offsets
    row_group = lax.broadcasted_iota(jnp.int32, (width, LANES), 0) // modes
    lane_group = lax.broadcasted_iota(jnp.int32, (width, LANES), 1) // group_size

    def body(j, carry):
        lanes = pl.ds(pl.multiple_of(j * LANES, LANES), LANES)
        row = pl.program_id(0) * sub + j
        rate = dec_ref[pl.ds(row, 1), :]
        weight = wt_ref[pl.ds(row, 1), :]
        a_high, a_low = _split(weight * jnp.exp(-rate * dist))
        entering = ent_ref[:, lanes]
        tiled = jnp.concatenate([entering] * groups_here, axis=0)
        diag = jnp.where(row_group == lane_group, tiled, 0.0)
        ent_high, ent_low = _split(diag)
        y = jnp.dot(a_high, ent_high, preferred_element_type=jnp.float32)
        y = y + jnp.dot(a_low, ent_high, preferred_element_type=jnp.float32)
        y = y + jnp.dot(a_high, ent_low, preferred_element_type=jnp.float32)
        out_ref[:, lanes] = loc_ref[:, lanes] + y
        return carry

    lax.fori_loop(0, sub, body, 0)


def modal_out(decays, weights, entering, local, *, group_size, forward):
    rows, chans = local.shape
    block = min(BLOCK_LANES, chans)
    groups_block = block // group_size
    modes = decays.shape[1]
    per_row = (LANES // group_size) * modes
    flat_decays = decays.reshape(-1, per_row)
    flat_weights = weights.reshape(-1, per_row)
    sub = block // LANES
    kernel = functools.partial(_modal_kernel, group_size=group_size, forward=forward, sub=sub)
    return pl.pallas_call(
        kernel,
        grid=(chans // block,),
        in_specs=[
            pl.BlockSpec(flat_decays.shape, lambda b: (0, 0)),
            pl.BlockSpec(flat_weights.shape, lambda b: (0, 0)),
            pl.BlockSpec((modes, block), lambda b: (0, b)),
            pl.BlockSpec((rows, block), lambda b: (0, b)),
        ],
        out_specs=pl.BlockSpec((rows, block), lambda b: (0, b)),
        out_shape=jax.ShapeDtypeStruct((rows, chans), jnp.float32),
        compiler_params=pltpu.CompilerParams(dimension_semantics=("parallel",)),
    )(flat_decays, flat_weights, entering, local)


def _gram_kernel(back_ref, top_ref, bot_ref, f_ref, *, group_size, sub):
    rows = back_ref.shape[0]
    groups_here = LANES // group_size
    r_id = lax.broadcasted_iota(jnp.int32, (rows, rows), 0)
    c_id = lax.broadcasted_iota(jnp.int32, (rows, rows), 1)
    exchange = jnp.where(r_id + c_id == rows - 1, 1.0, 0.0).astype(jnp.bfloat16)
    lane_group = lax.broadcasted_iota(jnp.int32, (rows, LANES), 1) // group_size

    def body(j, carry):
        lanes = pl.ds(pl.multiple_of(j * LANES, LANES), LANES)
        back = back_ref[:, lanes]
        x = jnp.concatenate([top_ref[:, lanes], bot_ref[:, lanes]], axis=0)
        back_rev = jnp.dot(exchange, back, preferred_element_type=jnp.float32).astype(jnp.bfloat16)
        masked = jnp.concatenate(
            [jnp.where(lane_group == k, back_rev, jnp.zeros_like(back_rev)) for k in range(groups_here)],
            axis=0,
        )
        gram = lax.dot_general(
            masked, x, (((1,), (1,)), ((), ())), preferred_element_type=jnp.float32
        )
        sums = []
        for k in range(groups_here):
            skew = pltpu.roll(gram[k * rows:(k + 1) * rows], 0, 1, stride=1, stride_axis=0)
            sums.append(jnp.sum(skew, axis=0, keepdims=True))
        f_ref[pl.ds(pl.multiple_of(j * groups_here, groups_here), groups_here), :] = jnp.concatenate(sums, 0)
        return carry

    lax.fori_loop(0, sub, body, 0)


def gram_diag(back, top, bottom, *, group_size):
    rows, chans = back.shape
    block = min(BLOCK_LANES, chans)
    groups_block = block // group_size
    group_count = chans // group_size
    kernel = functools.partial(_gram_kernel, group_size=group_size, sub=block // LANES)
    return pl.pallas_call(
        kernel,
        grid=(chans // block,),
        in_specs=[
            pl.BlockSpec((rows, block), lambda b: (0, b)),
            pl.BlockSpec((rows, block), lambda b: (0, b)),
            pl.BlockSpec((rows, block), lambda b: (0, b)),
        ],
        out_specs=pl.BlockSpec((groups_block, 2 * rows), lambda b: (b, 0)),
        out_shape=jax.ShapeDtypeStruct((group_count, 2 * rows), jnp.float32),
        compiler_params=pltpu.CompilerParams(dimension_semantics=("parallel",)),
    )(back, top, bottom)


def gather_seq(value):
    count = lax.axis_size("seq")
    tiled = jnp.broadcast_to(value[None], (count,) + value.shape)
    return lax.all_to_all(tiled, "seq", split_axis=0, concat_axis=0, tiled=True)


def entering_states(gathered, decays, block_len, group_size, forward):
    count = gathered.shape[0]
    here = lax.axis_index("seq")
    rates = jnp.repeat(decays.T, group_size, axis=1)
    source = jnp.arange(count)
    if forward:
        gap = here - 1 - source
    else:
        gap = source - here - 1
    valid = gap >= 0
    steps = jnp.maximum(gap, 0).astype(jnp.float32)
    coef = jnp.exp(-rates[None] * (float(block_len) * steps)[:, None, None])
    coef = jnp.where(valid[:, None, None], coef, 0.0)
    return jnp.sum(coef * gathered, axis=0)


def on_device(
    query_mr,
    key_mr,
    value_mr,
    query_li,
    key_li,
    cotangent,
    mr_filter,
    norm_gain,
    li_decay,
    li_residue,
):
    row_count, chan_count = query_mr.shape
    group_count, tap_count = mr_filter.shape
    group_size = chan_count // group_count
    assert row_count == tap_count
    grad_scale = float(row_count * lax.axis_size("seq")) ** (-0.5)

    taps_mr = mr_filter.astype(jnp.bfloat16).astype(jnp.float32)
    zero_col = jnp.zeros((group_count, 1), jnp.float32)
    fwd_rows = jnp.concatenate(
        [zero_col, jnp.flip(taps_mr, 1), jnp.zeros((group_count, tap_count - 1), jnp.float32)], 1
    )
    bwd_rows = jnp.concatenate([taps_mr, jnp.zeros_like(taps_mr)], 1)

    mixed_mr = (key_mr.astype(jnp.float32) * value_mr.astype(jnp.float32)).astype(jnp.bfloat16)
    rim_rows = from_behind(mixed_mr, "seq", 1)
    conv_mr = band_conv(fwd_rows, rim_rows, mixed_mr, group_size=group_size, split=False, tri=None)
    out_mr = (query_mr.astype(jnp.float32) * conv_mr).astype(jnp.bfloat16)
    out_full = out_mr.astype(jnp.float32)
    squares = lax.psum(jnp.sum(out_full * out_full, axis=1), "chan")
    inv_rms = lax.rsqrt(squares / D + 1e-06)[:, None]
    normed = out_full * inv_rms * norm_gain
    mixed_li = key_li.astype(jnp.float32) * normed
    cotan_full = cotangent.astype(jnp.float32)
    back_li = cotan_full * query_li.astype(jnp.float32)

    offsets = jnp.arange(row_count, dtype=jnp.float32)
    weights_res = li_residue * jnp.sqrt(2.0 * li_decay)
    taps_li = jnp.einsum(
        "gr,grd->gd", weights_res, jnp.exp(-li_decay[:, :, None] * offsets), precision=HIGHEST
    )
    li_fwd_rows = jnp.concatenate([taps_li[:, :1], jnp.flip(taps_li[:, 1:], 1)], 1)
    fwd_states = jnp.exp(-li_decay[:, :, None] * (row_count - 1.0 - offsets))
    bwd_states = jnp.exp(-li_decay[:, :, None] * offsets)

    back_li_bf = back_li.astype(jnp.bfloat16)
    mixed_li_bf = mixed_li.astype(jnp.bfloat16)
    modes = li_decay.shape[1]
    grad_st = modal_states(bwd_states, back_li_bf, group_size=group_size)
    conv_st = modal_states(fwd_states, mixed_li_bf, group_size=group_size)
    both_st = gather_seq(jnp.concatenate([grad_st, conv_st], 0).astype(jnp.bfloat16))
    both_st = both_st.astype(jnp.float32)
    grad_loc = band_conv(taps_li, back_li_bf, group_size=group_size, split=False, tri="upper")
    conv_loc = band_conv(li_fwd_rows, mixed_li_bf, group_size=group_size, split=False, tri="lower")
    both_st, grad_loc, conv_loc = lax.optimization_barrier((both_st, grad_loc, conv_loc))
    grad_ent = entering_states(both_st[:, :modes], li_decay, row_count, group_size, False)
    conv_ent = entering_states(both_st[:, modes:], li_decay, row_count, group_size, True)
    grad_mixed_li = modal_out(
        li_decay, weights_res, grad_ent, grad_loc, group_size=group_size, forward=False
    )
    conv_li = modal_out(li_decay, weights_res, conv_ent, conv_loc, group_size=group_size, forward=True)

    out_li = (query_li.astype(jnp.float32) * conv_li).astype(jnp.bfloat16)
    grad_query_li = (cotan_full * conv_li).astype(jnp.bfloat16)
    grad_key_li = (grad_mixed_li * normed).astype(jnp.bfloat16)
    grad_normed = grad_mixed_li * key_li.astype(jnp.float32)
    gain_part = jnp.sum(grad_normed * out_full * inv_rms, axis=0)
    weighted = grad_normed * norm_gain
    cross_dots = lax.psum(jnp.sum(weighted * out_full, axis=1), "chan")[:, None]
    grad_out_mr = inv_rms * weighted - out_full * inv_rms**3 * cross_dots / D
    grad_query_mr = (grad_out_mr * conv_mr).astype(jnp.bfloat16)
    back_mr = (grad_out_mr * query_mr.astype(jnp.float32)).astype(jnp.bfloat16)
    after_rim = from_behind(back_mr, "seq", -1)
    grad_key_mr, grad_value_mr = band_conv(
        bwd_rows, back_mr, after_rim, scale_pair=(value_mr, key_mr),
        group_size=group_size, split=False, tri=None,
    )
    diag_sums = gram_diag(back_mr, rim_rows, mixed_mr, group_size=group_size)
    filter_part = jnp.flip(diag_sums[:, tap_count:], 1)
    packed = jnp.concatenate([gain_part, filter_part.reshape(-1)])
    packed, after_rim = lax.optimization_barrier((packed, after_rim))
    param_sums = jnp.sum(gather_seq(packed), axis=0) * grad_scale
    grad_gain = param_sums[:chan_count]
    grad_filter = param_sums[chan_count:].reshape(group_count, tap_count)
    return (
        out_li,
        grad_query_mr,
        grad_key_mr,
        grad_value_mr,
        grad_query_li,
        grad_key_li,
        grad_gain,
        grad_filter,
    )


def solution(mesh):
    in_specs = (
        P("seq", "chan"),
        P("seq", "chan"),
        P("seq", "chan"),
        P("seq", "chan"),
        P("seq", "chan"),
        P("seq", "chan"),
        P("chan", None),
        P("chan"),
        P("chan", None),
        P("chan", None),
    )
    out_specs = (
        P("seq", "chan"),
        P("seq", "chan"),
        P("seq", "chan"),
        P("seq", "chan"),
        P("seq", "chan"),
        P("seq", "chan"),
        P("chan"),
        P("chan", None),
    )
    return jax.shard_map(
        on_device, mesh=mesh, in_specs=in_specs, out_specs=out_specs, check_vma=False
    )
```

```python
import functools

import jax
import jax.numpy as jnp
from jax import lax
from jax.experimental import pallas as pl
from jax.experimental.pallas import tpu as pltpu
from jax.sharding import PartitionSpec as P

D = 8192
G = 512
LANES = 128
BLOCK_LANES = 512
HIGHEST = lax.Precision.HIGHEST


def from_behind(value, axis, steps):
    count = lax.axis_size(axis)
    initial, last = (max(0, -steps), min(count, count - steps))
    return lax.ppermute(value, axis, [(source, source + steps) for source in range(initial, last)])


def _split(value):
    high = value.astype(jnp.bfloat16)
    return high, (value - high.astype(jnp.float32)).astype(jnp.bfloat16)


def _band_kernel(*refs, group_size, split, tri, two_inputs, modal, sub, scaled):
    refs = list(refs)
    h_ref = refs.pop(0)
    top_ref = refs.pop(0)
    bot_ref = refs.pop(0) if two_inputs else None
    if modal is not None:
        dec_ref, wt_ref, ent_ref = refs.pop(0), refs.pop(0), refs.pop(0)
    if scaled:
        first_ref, second_ref = refs.pop(0), refs.pop(0)
    out_ref = refs.pop(0)
    if scaled:
        other_ref = refs.pop(0)
    rows = out_ref.shape[0]
    width = h_ref.shape[1]
    groups_here = LANES // group_size
    lane_group = lax.broadcasted_iota(jnp.int32, (rows, LANES), 1) // group_size
    row_id = lax.broadcasted_iota(jnp.int32, (rows, width), 0)
    col_id = lax.broadcasted_iota(jnp.int32, (rows, width), 1)
    if modal is not None:
        modes = dec_ref.shape[1]
        offsets = lax.broadcasted_iota(jnp.int32, (rows, modes), 0).astype(jnp.float32)
        dist = offsets + 1.0 if modal == "forward" else float(rows) - offsets

    def body(j, carry):
        lanes = pl.ds(pl.multiple_of(j * LANES, LANES), LANES)
        if two_inputs:
            x = jnp.concatenate([top_ref[:, lanes], bot_ref[:, lanes]], axis=0)
        else:
            x = top_ref[:, lanes]
        bands = []
        for k in range(groups_here):
            band_row = h_ref[pl.ds(j * groups_here + k, 1), :]
            band = pltpu.roll(jnp.broadcast_to(band_row, (rows, width)), 0, 1, stride=1, stride_axis=0)
            if tri == "lower":
                band = jnp.where(col_id <= row_id, band, 0.0)
            elif tri == "upper":
                band = jnp.where(col_id >= row_id, band, 0.0)
            bands.append(band)
        stacked = jnp.concatenate(bands, axis=0)
        if split:
            high, low = _split(stacked)
            y = jnp.dot(high, x, preferred_element_type=jnp.float32)
            y = y + jnp.dot(low, x, preferred_element_type=jnp.float32)
        else:
            y = jnp.dot(stacked.astype(jnp.bfloat16), x, preferred_element_type=jnp.float32)
        if modal is not None:
            ent_high, ent_low = _split(ent_ref[:, lanes])
            out_w = []
            for k in range(groups_here):
                rate = dec_ref[pl.ds(j * groups_here + k, 1), :]
                weight = wt_ref[pl.ds(j * groups_here + k, 1), :]
                out_w.append(weight * jnp.exp(-rate * dist))
            a_high, a_low = _split(jnp.concatenate(out_w, axis=0))
            y = y + jnp.dot(a_high, ent_high, preferred_element_type=jnp.float32)
            y = y + jnp.dot(a_low, ent_high, preferred_element_type=jnp.float32)
            y = y + jnp.dot(a_high, ent_low, preferred_element_type=jnp.float32)
        acc = y[:rows]
        for k in range(1, groups_here):
            acc = jnp.where(lane_group == k, y[k * rows:(k + 1) * rows], acc)
        if scaled:
            out_ref[:, lanes] = (acc * first_ref[:, lanes].astype(jnp.float32)).astype(out_ref.dtype)
            other_ref[:, lanes] = (acc * second_ref[:, lanes].astype(jnp.float32)).astype(other_ref.dtype)
        else:
            out_ref[:, lanes] = acc
        return carry

    lax.fori_loop(0, sub, body, 0)


def band_conv(
    band_rows, top, bottom=None, modal_args=None, scale_pair=None, *, group_size, split, tri, modal=None
):
    rows, chans = top.shape
    block = min(BLOCK_LANES, chans)
    groups_block = block // group_size
    width = band_rows.shape[1]
    two_inputs = bottom is not None
    in_specs = [
        pl.BlockSpec((groups_block, width), lambda b: (b, 0)),
        pl.BlockSpec((rows, block), lambda b: (0, b)),
    ]
    args = [band_rows, top]
    if two_inputs:
        in_specs.append(pl.BlockSpec((rows, block), lambda b: (0, b)))
        args.append(bottom)
    if modal is not None:
        decays, weights, entering = modal_args
        modes = decays.shape[1]
        in_specs += [
            pl.BlockSpec((groups_block, modes), lambda b: (b, 0)),
            pl.BlockSpec((groups_block, modes), lambda b: (b, 0)),
            pl.BlockSpec((modes, block), lambda b: (0, b)),
        ]
        args += [decays, weights, entering]
    scaled = scale_pair is not None
    out_specs = pl.BlockSpec((rows, block), lambda b: (0, b))
    out_shape = jax.ShapeDtypeStruct((rows, chans), jnp.float32)
    if scaled:
        in_specs += [pl.BlockSpec((rows, block), lambda b: (0, b))] * 2
        args += list(scale_pair)
        out_specs = [out_specs, out_specs]
        out_shape = [jax.ShapeDtypeStruct((rows, chans), jnp.bfloat16)] * 2
    kernel = functools.partial(
        _band_kernel,
        group_size=group_size,
        split=split,
        tri=tri,
        two_inputs=two_inputs,
        modal=modal,
        sub=block // LANES,
        scaled=scaled,
    )
    return pl.pallas_call(
        kernel,
        grid=(chans // block,),
        in_specs=in_specs,
        out_specs=out_specs,
        out_shape=out_shape,
        compiler_params=pltpu.CompilerParams(dimension_semantics=("parallel",)),
    )(*args)


def _state_kernel(e_ref, x_ref, s_ref, *, group_size, sub):
    modes = s_ref.shape[0]
    groups_here = LANES // group_size
    state_group = lax.broadcasted_iota(jnp.int32, (modes, LANES), 1) // group_size

    def body(j, carry):
        lanes = pl.ds(pl.multiple_of(j * LANES, LANES), LANES)
        x = x_ref[:, lanes]
        weights = e_ref[pl.ds(j * groups_here, groups_here)]
        stacked = weights.reshape(groups_here * modes, weights.shape[2]).astype(jnp.bfloat16)
        y = jnp.dot(stacked, x, preferred_element_type=jnp.float32)
        acc = y[:modes]
        for k in range(1, groups_here):
            acc = jnp.where(state_group == k, y[k * modes:(k + 1) * modes], acc)
        s_ref[:, lanes] = acc
        return carry

    lax.fori_loop(0, sub, body, 0)


def modal_states(state_rows, x, *, group_size):
    rows, chans = x.shape
    block = min(BLOCK_LANES, chans)
    groups_block = block // group_size
    modes = state_rows.shape[1]
    kernel = functools.partial(_state_kernel, group_size=group_size, sub=block // LANES)
    return pl.pallas_call(
        kernel,
        grid=(chans // block,),
        in_specs=[
            pl.BlockSpec((groups_block, modes, rows), lambda b: (b, 0, 0)),
            pl.BlockSpec((rows, block), lambda b: (0, b)),
        ],
        out_specs=pl.BlockSpec((modes, block), lambda b: (0, b)),
        out_shape=jax.ShapeDtypeStruct((modes, chans), jnp.float32),
        compiler_params=pltpu.CompilerParams(dimension_semantics=("parallel",)),
    )(state_rows, x)


def _modal_kernel(*refs, group_size, forward, sub, scaled):
    if scaled:
        dec_ref, wt_ref, ent_ref, loc_ref, first_ref, second_ref, out_ref, other_ref = refs
    else:
        dec_ref, wt_ref, ent_ref, loc_ref, out_ref = refs
    rows = out_ref.shape[0]
    modes = ent_ref.shape[0]
    groups_here = LANES // group_size
    width = groups_here * modes
    offsets = lax.broadcasted_iota(jnp.int32, (rows, width), 0).astype(jnp.float32)
    dist = offsets + 1.0 if forward else float(rows) - offsets
    row_group = lax.broadcasted_iota(jnp.int32, (width, LANES), 0) // modes
    lane_group = lax.broadcasted_iota(jnp.int32, (width, LANES), 1) // group_size

    def body(j, carry):
        lanes = pl.ds(pl.multiple_of(j * LANES, LANES), LANES)
        row = pl.program_id(0) * sub + j
        rate = dec_ref[pl.ds(row, 1), :]
        weight = wt_ref[pl.ds(row, 1), :]
        a_high, a_low = _split(weight * jnp.exp(-rate * dist))
        entering = ent_ref[:, lanes]
        tiled = jnp.concatenate([entering] * groups_here, axis=0)
        diag = jnp.where(row_group == lane_group, tiled, 0.0)
        ent_high, ent_low = _split(diag)
        y = jnp.dot(a_high, ent_high, preferred_element_type=jnp.float32)
        y = y + jnp.dot(a_low, ent_high, preferred_element_type=jnp.float32)
        y = y + jnp.dot(a_high, ent_low, preferred_element_type=jnp.float32)
        total = loc_ref[:, lanes] + y
        if scaled:
            out_ref[:, lanes] = (total * first_ref[:, lanes].astype(jnp.float32)).astype(out_ref.dtype)
            other_ref[:, lanes] = (total * second_ref[:, lanes].astype(jnp.float32)).astype(other_ref.dtype)
        else:
            out_ref[:, lanes] = total
        return carry

    lax.fori_loop(0, sub, body, 0)


def modal_out(decays, weights, entering, local, scale_pair=None, *, group_size, forward):
    rows, chans = local.shape
    block = min(BLOCK_LANES, chans)
    groups_block = block // group_size
    modes = decays.shape[1]
    per_row = (LANES // group_size) * modes
    flat_decays = decays.reshape(-1, per_row)
    flat_weights = weights.reshape(-1, per_row)
    sub = block // LANES
    scaled = scale_pair is not None
    kernel = functools.partial(
        _modal_kernel, group_size=group_size, forward=forward, sub=sub, scaled=scaled
    )
    in_specs = [
        pl.BlockSpec(flat_decays.shape, lambda b: (0, 0)),
        pl.BlockSpec(flat_weights.shape, lambda b: (0, 0)),
        pl.BlockSpec((modes, block), lambda b: (0, b)),
        pl.BlockSpec((rows, block), lambda b: (0, b)),
    ]
    args = [flat_decays, flat_weights, entering, local]
    out_specs = pl.BlockSpec((rows, block), lambda b: (0, b))
    out_shape = jax.ShapeDtypeStruct((rows, chans), jnp.float32)
    if scaled:
        in_specs += [pl.BlockSpec((rows, block), lambda b: (0, b))] * 2
        args += list(scale_pair)
        out_specs = [out_specs, out_specs]
        out_shape = [jax.ShapeDtypeStruct((rows, chans), jnp.bfloat16)] * 2
    return pl.pallas_call(
        kernel,
        grid=(chans // block,),
        in_specs=in_specs,
        out_specs=out_specs,
        out_shape=out_shape,
        compiler_params=pltpu.CompilerParams(dimension_semantics=("parallel",)),
    )(*args)


def _gram_kernel(back_ref, top_ref, bot_ref, f_ref, *, group_size, sub):
    rows = back_ref.shape[0]
    groups_here = LANES // group_size
    r_id = lax.broadcasted_iota(jnp.int32, (rows, rows), 0)
    c_id = lax.broadcasted_iota(jnp.int32, (rows, rows), 1)
    exchange = jnp.where(r_id + c_id == rows - 1, 1.0, 0.0).astype(jnp.bfloat16)
    lane_group = lax.broadcasted_iota(jnp.int32, (rows, LANES), 1) // group_size

    def body(j, carry):
        lanes = pl.ds(pl.multiple_of(j * LANES, LANES), LANES)
        back = back_ref[:, lanes]
        x = jnp.concatenate([top_ref[:, lanes], bot_ref[:, lanes]], axis=0)
        back_rev = jnp.dot(exchange, back, preferred_element_type=jnp.float32).astype(jnp.bfloat16)
        masked = jnp.concatenate(
            [jnp.where(lane_group == k, back_rev, jnp.zeros_like(back_rev)) for k in range(groups_here)],
            axis=0,
        )
        gram = lax.dot_general(
            masked, x, (((1,), (1,)), ((), ())), preferred_element_type=jnp.float32
        )
        sums = []
        for k in range(groups_here):
            skew = pltpu.roll(gram[k * rows:(k + 1) * rows], 0, 1, stride=1, stride_axis=0)
            sums.append(jnp.sum(skew, axis=0, keepdims=True))
        f_ref[pl.ds(pl.multiple_of(j * groups_here, groups_here), groups_here), :] = jnp.concatenate(sums, 0)
        return carry

    lax.fori_loop(0, sub, body, 0)


def gram_diag(back, top, bottom, *, group_size):
    rows, chans = back.shape
    block = min(BLOCK_LANES, chans)
    groups_block = block // group_size
    group_count = chans // group_size
    kernel = functools.partial(_gram_kernel, group_size=group_size, sub=block // LANES)
    return pl.pallas_call(
        kernel,
        grid=(chans // block,),
        in_specs=[
            pl.BlockSpec((rows, block), lambda b: (0, b)),
            pl.BlockSpec((rows, block), lambda b: (0, b)),
            pl.BlockSpec((rows, block), lambda b: (0, b)),
        ],
        out_specs=pl.BlockSpec((groups_block, 2 * rows), lambda b: (b, 0)),
        out_shape=jax.ShapeDtypeStruct((group_count, 2 * rows), jnp.float32),
        compiler_params=pltpu.CompilerParams(dimension_semantics=("parallel",)),
    )(back, top, bottom)


def gather_seq(value):
    count = lax.axis_size("seq")
    tiled = jnp.broadcast_to(value[None], (count,) + value.shape)
    return lax.all_to_all(tiled, "seq", split_axis=0, concat_axis=0, tiled=True)


def entering_states(gathered, decays, block_len, group_size, forward):
    count = gathered.shape[0]
    here = lax.axis_index("seq")
    rates = jnp.repeat(decays.T, group_size, axis=1)
    source = jnp.arange(count)
    if forward:
        gap = here - 1 - source
    else:
        gap = source - here - 1
    valid = gap >= 0
    steps = jnp.maximum(gap, 0).astype(jnp.float32)
    coef = jnp.exp(-rates[None] * (float(block_len) * steps)[:, None, None])
    coef = jnp.where(valid[:, None, None], coef, 0.0)
    return jnp.sum(coef * gathered, axis=0)


def on_device(
    query_mr,
    key_mr,
    value_mr,
    query_li,
    key_li,
    cotangent,
    mr_filter,
    norm_gain,
    li_decay,
    li_residue,
):
    row_count, chan_count = query_mr.shape
    group_count, tap_count = mr_filter.shape
    group_size = chan_count // group_count
    assert row_count == tap_count
    grad_scale = float(row_count * lax.axis_size("seq")) ** (-0.5)

    taps_mr = mr_filter.astype(jnp.bfloat16).astype(jnp.float32)
    zero_col = jnp.zeros((group_count, 1), jnp.float32)
    fwd_rows = jnp.concatenate(
        [zero_col, jnp.flip(taps_mr, 1), jnp.zeros((group_count, tap_count - 1), jnp.float32)], 1
    )
    bwd_rows = jnp.concatenate([taps_mr, jnp.zeros_like(taps_mr)], 1)

    mixed_mr = (key_mr.astype(jnp.float32) * value_mr.astype(jnp.float32)).astype(jnp.bfloat16)
    rim_rows = from_behind(mixed_mr, "seq", 1)
    conv_mr = band_conv(fwd_rows, rim_rows, mixed_mr, group_size=group_size, split=False, tri=None)
    out_mr = (query_mr.astype(jnp.float32) * conv_mr).astype(jnp.bfloat16)
    out_full = out_mr.astype(jnp.float32)
    squares = lax.psum(jnp.sum(out_full * out_full, axis=1), "chan")
    inv_rms = lax.rsqrt(squares / D + 1e-06)[:, None]
    normed = out_full * inv_rms * norm_gain
    mixed_li = key_li.astype(jnp.float32) * normed
    cotan_full = cotangent.astype(jnp.float32)
    back_li = cotan_full * query_li.astype(jnp.float32)

    offsets = jnp.arange(row_count, dtype=jnp.float32)
    weights_res = li_residue * jnp.sqrt(2.0 * li_decay)
    taps_li = jnp.einsum(
        "gr,grd->gd", weights_res, jnp.exp(-li_decay[:, :, None] * offsets), precision=HIGHEST
    )
    li_fwd_rows = jnp.concatenate([taps_li[:, :1], jnp.flip(taps_li[:, 1:], 1)], 1)
    fwd_states = jnp.exp(-li_decay[:, :, None] * (row_count - 1.0 - offsets))
    bwd_states = jnp.exp(-li_decay[:, :, None] * offsets)

    back_li_bf = back_li.astype(jnp.bfloat16)
    mixed_li_bf = mixed_li.astype(jnp.bfloat16)
    modes = li_decay.shape[1]
    grad_st = modal_states(bwd_states, back_li_bf, group_size=group_size)
    conv_st = modal_states(fwd_states, mixed_li_bf, group_size=group_size)
    both_st = gather_seq(jnp.concatenate([grad_st, conv_st], 0).astype(jnp.bfloat16))
    both_st = both_st.astype(jnp.float32)
    grad_loc = band_conv(taps_li, back_li_bf, group_size=group_size, split=False, tri="upper")
    conv_loc = band_conv(li_fwd_rows, mixed_li_bf, group_size=group_size, split=False, tri="lower")
    both_st, grad_loc, conv_loc = lax.optimization_barrier((both_st, grad_loc, conv_loc))
    grad_ent = entering_states(both_st[:, :modes], li_decay, row_count, group_size, False)
    conv_ent = entering_states(both_st[:, modes:], li_decay, row_count, group_size, True)
    grad_mixed_li = modal_out(
        li_decay, weights_res, grad_ent, grad_loc, group_size=group_size, forward=False
    )
    out_li, grad_query_li = modal_out(
        li_decay, weights_res, conv_ent, conv_loc, (query_li, cotangent),
        group_size=group_size, forward=True,
    )

    grad_key_li = (grad_mixed_li * normed).astype(jnp.bfloat16)
    grad_normed = grad_mixed_li * key_li.astype(jnp.float32)
    gain_part = jnp.sum(grad_normed * out_full * inv_rms, axis=0)
    weighted = grad_normed * norm_gain
    cross_dots = lax.psum(jnp.sum(weighted * out_full, axis=1), "chan")[:, None]
    grad_out_mr = inv_rms * weighted - out_full * inv_rms**3 * cross_dots / D
    grad_query_mr = (grad_out_mr * conv_mr).astype(jnp.bfloat16)
    back_mr = (grad_out_mr * query_mr.astype(jnp.float32)).astype(jnp.bfloat16)
    after_rim = from_behind(back_mr, "seq", -1)
    grad_key_mr, grad_value_mr = band_conv(
        bwd_rows, back_mr, after_rim, scale_pair=(value_mr, key_mr),
        group_size=group_size, split=False, tri=None,
    )
    diag_sums = gram_diag(back_mr, rim_rows, mixed_mr, group_size=group_size)
    filter_part = jnp.flip(diag_sums[:, tap_count:], 1)
    packed = jnp.concatenate([gain_part, filter_part.reshape(-1)])
    packed, after_rim = lax.optimization_barrier((packed, after_rim))
    param_sums = jnp.sum(gather_seq(packed), axis=0) * grad_scale
    grad_gain = param_sums[:chan_count]
    grad_filter = param_sums[chan_count:].reshape(group_count, tap_count)
    return (
        out_li,
        grad_query_mr,
        grad_key_mr,
        grad_value_mr,
        grad_query_li,
        grad_key_li,
        grad_gain,
        grad_filter,
    )


def solution(mesh):
    in_specs = (
        P("seq", "chan"),
        P("seq", "chan"),
        P("seq", "chan"),
        P("seq", "chan"),
        P("seq", "chan"),
        P("seq", "chan"),
        P("chan", None),
        P("chan"),
        P("chan", None),
        P("chan", None),
    )
    out_specs = (
        P("seq", "chan"),
        P("seq", "chan"),
        P("seq", "chan"),
        P("seq", "chan"),
        P("seq", "chan"),
        P("seq", "chan"),
        P("chan"),
        P("chan", None),
    )
    return jax.shard_map(
        on_device, mesh=mesh, in_specs=in_specs, out_specs=out_specs, check_vma=False
    )
```

```python
import functools

import jax
import jax.numpy as jnp
from jax import lax
from jax.experimental import pallas as pl
from jax.experimental.pallas import tpu as pltpu
from jax.sharding import PartitionSpec as P

D = 8192
G = 512
LANES = 128
BLOCK_LANES = 512
HIGHEST = lax.Precision.HIGHEST


def from_behind(value, axis, steps):
    count = lax.axis_size(axis)
    initial, last = (max(0, -steps), min(count, count - steps))
    return lax.ppermute(value, axis, [(source, source + steps) for source in range(initial, last)])


def _split(value):
    high = value.astype(jnp.bfloat16)
    return high, (value - high.astype(jnp.float32)).astype(jnp.bfloat16)


def _band_kernel(*refs, group_size, split, tri, two_inputs, modal, sub, scaled):
    refs = list(refs)
    h_ref = refs.pop(0)
    top_ref = refs.pop(0)
    bot_ref = refs.pop(0) if two_inputs else None
    if modal is not None:
        dec_ref, wt_ref, ent_ref = refs.pop(0), refs.pop(0), refs.pop(0)
    if scaled:
        first_ref, second_ref = refs.pop(0), refs.pop(0)
    out_ref = refs.pop(0)
    if scaled:
        other_ref = refs.pop(0)
    rows = out_ref.shape[0]
    width = h_ref.shape[1]
    groups_here = LANES // group_size
    lane_group = lax.broadcasted_iota(jnp.int32, (rows, LANES), 1) // group_size
    row_id = lax.broadcasted_iota(jnp.int32, (rows, width), 0)
    col_id = lax.broadcasted_iota(jnp.int32, (rows, width), 1)
    if modal is not None:
        modes = dec_ref.shape[1]
        offsets = lax.broadcasted_iota(jnp.int32, (rows, modes), 0).astype(jnp.float32)
        dist = offsets + 1.0 if modal == "forward" else float(rows) - offsets

    def body(j, carry):
        lanes = pl.ds(pl.multiple_of(j * LANES, LANES), LANES)
        if two_inputs:
            x = jnp.concatenate([top_ref[:, lanes], bot_ref[:, lanes]], axis=0)
        else:
            x = top_ref[:, lanes]
        bands = []
        for k in range(groups_here):
            band_row = h_ref[pl.ds(j * groups_here + k, 1), :]
            band = pltpu.roll(jnp.broadcast_to(band_row, (rows, width)), 0, 1, stride=1, stride_axis=0)
            if tri == "lower":
                band = jnp.where(col_id <= row_id, band, 0.0)
            elif tri == "upper":
                band = jnp.where(col_id >= row_id, band, 0.0)
            bands.append(band)
        stacked = jnp.concatenate(bands, axis=0)
        if split:
            high, low = _split(stacked)
            y = jnp.dot(high, x, preferred_element_type=jnp.float32)
            y = y + jnp.dot(low, x, preferred_element_type=jnp.float32)
        else:
            y = jnp.dot(stacked.astype(jnp.bfloat16), x, preferred_element_type=jnp.float32)
        if modal is not None:
            ent_high, ent_low = _split(ent_ref[:, lanes])
            out_w = []
            for k in range(groups_here):
                rate = dec_ref[pl.ds(j * groups_here + k, 1), :]
                weight = wt_ref[pl.ds(j * groups_here + k, 1), :]
                out_w.append(weight * jnp.exp(-rate * dist))
            a_high, a_low = _split(jnp.concatenate(out_w, axis=0))
            y = y + jnp.dot(a_high, ent_high, preferred_element_type=jnp.float32)
            y = y + jnp.dot(a_low, ent_high, preferred_element_type=jnp.float32)
            y = y + jnp.dot(a_high, ent_low, preferred_element_type=jnp.float32)
        acc = y[:rows]
        for k in range(1, groups_here):
            acc = jnp.where(lane_group == k, y[k * rows:(k + 1) * rows], acc)
        if scaled:
            out_ref[:, lanes] = (acc * first_ref[:, lanes].astype(jnp.float32)).astype(out_ref.dtype)
            other_ref[:, lanes] = (acc * second_ref[:, lanes].astype(jnp.float32)).astype(other_ref.dtype)
        else:
            out_ref[:, lanes] = acc
        return carry

    lax.fori_loop(0, sub, body, 0)


def band_conv(
    band_rows, top, bottom=None, modal_args=None, scale_pair=None, *, group_size, split, tri, modal=None
):
    rows, chans = top.shape
    block = min(BLOCK_LANES, chans)
    groups_block = block // group_size
    width = band_rows.shape[1]
    two_inputs = bottom is not None
    in_specs = [
        pl.BlockSpec((groups_block, width), lambda b: (b, 0)),
        pl.BlockSpec((rows, block), lambda b: (0, b)),
    ]
    args = [band_rows, top]
    if two_inputs:
        in_specs.append(pl.BlockSpec((rows, block), lambda b: (0, b)))
        args.append(bottom)
    if modal is not None:
        decays, weights, entering = modal_args
        modes = decays.shape[1]
        in_specs += [
            pl.BlockSpec((groups_block, modes), lambda b: (b, 0)),
            pl.BlockSpec((groups_block, modes), lambda b: (b, 0)),
            pl.BlockSpec((modes, block), lambda b: (0, b)),
        ]
        args += [decays, weights, entering]
    scaled = scale_pair is not None
    out_specs = pl.BlockSpec((rows, block), lambda b: (0, b))
    out_shape = jax.ShapeDtypeStruct((rows, chans), jnp.float32)
    if scaled:
        in_specs += [pl.BlockSpec((rows, block), lambda b: (0, b))] * 2
        args += list(scale_pair)
        out_specs = [out_specs, out_specs]
        out_shape = [jax.ShapeDtypeStruct((rows, chans), jnp.bfloat16)] * 2
    kernel = functools.partial(
        _band_kernel,
        group_size=group_size,
        split=split,
        tri=tri,
        two_inputs=two_inputs,
        modal=modal,
        sub=block // LANES,
        scaled=scaled,
    )
    return pl.pallas_call(
        kernel,
        grid=(chans // block,),
        in_specs=in_specs,
        out_specs=out_specs,
        out_shape=out_shape,
        compiler_params=pltpu.CompilerParams(dimension_semantics=("parallel",)),
    )(*args)


def _state_kernel(e_ref, x_ref, s_ref, *, group_size, sub):
    modes = s_ref.shape[0]
    groups_here = LANES // group_size
    state_group = lax.broadcasted_iota(jnp.int32, (modes, LANES), 1) // group_size

    def body(j, carry):
        lanes = pl.ds(pl.multiple_of(j * LANES, LANES), LANES)
        x = x_ref[:, lanes]
        weights = e_ref[pl.ds(j * groups_here, groups_here)]
        stacked = weights.reshape(groups_here * modes, weights.shape[2]).astype(jnp.bfloat16)
        y = jnp.dot(stacked, x, preferred_element_type=jnp.float32)
        acc = y[:modes]
        for k in range(1, groups_here):
            acc = jnp.where(state_group == k, y[k * modes:(k + 1) * modes], acc)
        s_ref[:, lanes] = acc
        return carry

    lax.fori_loop(0, sub, body, 0)


def modal_states(state_rows, x, *, group_size):
    rows, chans = x.shape
    block = min(BLOCK_LANES, chans)
    groups_block = block // group_size
    modes = state_rows.shape[1]
    kernel = functools.partial(_state_kernel, group_size=group_size, sub=block // LANES)
    return pl.pallas_call(
        kernel,
        grid=(chans // block,),
        in_specs=[
            pl.BlockSpec((groups_block, modes, rows), lambda b: (b, 0, 0)),
            pl.BlockSpec((rows, block), lambda b: (0, b)),
        ],
        out_specs=pl.BlockSpec((modes, block), lambda b: (0, b)),
        out_shape=jax.ShapeDtypeStruct((modes, chans), jnp.float32),
        compiler_params=pltpu.CompilerParams(dimension_semantics=("parallel",)),
    )(state_rows, x)


def _modal_kernel(*refs, group_size, forward, sub, scaled):
    if scaled:
        dec_ref, wt_ref, ent_ref, loc_ref, first_ref, second_ref, out_ref, other_ref = refs
    else:
        dec_ref, wt_ref, ent_ref, loc_ref, out_ref = refs
    rows = out_ref.shape[0]
    modes = ent_ref.shape[0]
    groups_here = LANES // group_size
    width = groups_here * modes
    offsets = lax.broadcasted_iota(jnp.int32, (rows, width), 0).astype(jnp.float32)
    dist = offsets + 1.0 if forward else float(rows) - offsets
    row_group = lax.broadcasted_iota(jnp.int32, (width, LANES), 0) // modes
    lane_group = lax.broadcasted_iota(jnp.int32, (width, LANES), 1) // group_size

    def body(j, carry):
        lanes = pl.ds(pl.multiple_of(j * LANES, LANES), LANES)
        row = pl.program_id(0) * sub + j
        rate = dec_ref[pl.ds(row, 1), :]
        weight = wt_ref[pl.ds(row, 1), :]
        out_w = (weight * jnp.exp(-rate * dist)).astype(jnp.bfloat16)
        entering = ent_ref[:, lanes]
        tiled = jnp.concatenate([entering] * groups_here, axis=0)
        diag = jnp.where(row_group == lane_group, tiled, 0.0).astype(jnp.bfloat16)
        y = jnp.dot(out_w, diag, preferred_element_type=jnp.float32)
        total = loc_ref[:, lanes] + y
        if scaled:
            out_ref[:, lanes] = (total * first_ref[:, lanes].astype(jnp.float32)).astype(out_ref.dtype)
            other_ref[:, lanes] = (total * second_ref[:, lanes].astype(jnp.float32)).astype(other_ref.dtype)
        else:
            out_ref[:, lanes] = total
        return carry

    lax.fori_loop(0, sub, body, 0)


def modal_out(decays, weights, entering, local, scale_pair=None, *, group_size, forward):
    rows, chans = local.shape
    block = min(BLOCK_LANES, chans)
    groups_block = block // group_size
    modes = decays.shape[1]
    per_row = (LANES // group_size) * modes
    flat_decays = decays.reshape(-1, per_row)
    flat_weights = weights.reshape(-1, per_row)
    sub = block // LANES
    scaled = scale_pair is not None
    kernel = functools.partial(
        _modal_kernel, group_size=group_size, forward=forward, sub=sub, scaled=scaled
    )
    in_specs = [
        pl.BlockSpec(flat_decays.shape, lambda b: (0, 0)),
        pl.BlockSpec(flat_weights.shape, lambda b: (0, 0)),
        pl.BlockSpec((modes, block), lambda b: (0, b)),
        pl.BlockSpec((rows, block), lambda b: (0, b)),
    ]
    args = [flat_decays, flat_weights, entering, local]
    out_specs = pl.BlockSpec((rows, block), lambda b: (0, b))
    out_shape = jax.ShapeDtypeStruct((rows, chans), jnp.float32)
    if scaled:
        in_specs += [pl.BlockSpec((rows, block), lambda b: (0, b))] * 2
        args += list(scale_pair)
        out_specs = [out_specs, out_specs]
        out_shape = [jax.ShapeDtypeStruct((rows, chans), jnp.bfloat16)] * 2
    return pl.pallas_call(
        kernel,
        grid=(chans // block,),
        in_specs=in_specs,
        out_specs=out_specs,
        out_shape=out_shape,
        compiler_params=pltpu.CompilerParams(dimension_semantics=("parallel",)),
    )(*args)


def _gram_kernel(back_ref, top_ref, bot_ref, f_ref, *, group_size, sub):
    rows = back_ref.shape[0]
    groups_here = LANES // group_size
    r_id = lax.broadcasted_iota(jnp.int32, (rows, rows), 0)
    c_id = lax.broadcasted_iota(jnp.int32, (rows, rows), 1)
    exchange = jnp.where(r_id + c_id == rows - 1, 1.0, 0.0).astype(jnp.bfloat16)
    lane_group = lax.broadcasted_iota(jnp.int32, (rows, LANES), 1) // group_size

    def body(j, carry):
        lanes = pl.ds(pl.multiple_of(j * LANES, LANES), LANES)
        back = back_ref[:, lanes]
        x = jnp.concatenate([top_ref[:, lanes], bot_ref[:, lanes]], axis=0)
        back_rev = jnp.dot(exchange, back, preferred_element_type=jnp.float32).astype(jnp.bfloat16)
        masked = jnp.concatenate(
            [jnp.where(lane_group == k, back_rev, jnp.zeros_like(back_rev)) for k in range(groups_here)],
            axis=0,
        )
        gram = lax.dot_general(
            masked, x, (((1,), (1,)), ((), ())), preferred_element_type=jnp.float32
        )
        sums = []
        for k in range(groups_here):
            skew = pltpu.roll(gram[k * rows:(k + 1) * rows], 0, 1, stride=1, stride_axis=0)
            sums.append(jnp.sum(skew, axis=0, keepdims=True))
        f_ref[pl.ds(pl.multiple_of(j * groups_here, groups_here), groups_here), :] = jnp.concatenate(sums, 0)
        return carry

    lax.fori_loop(0, sub, body, 0)


def gram_diag(back, top, bottom, *, group_size):
    rows, chans = back.shape
    block = min(BLOCK_LANES, chans)
    groups_block = block // group_size
    group_count = chans // group_size
    kernel = functools.partial(_gram_kernel, group_size=group_size, sub=block // LANES)
    return pl.pallas_call(
        kernel,
        grid=(chans // block,),
        in_specs=[
            pl.BlockSpec((rows, block), lambda b: (0, b)),
            pl.BlockSpec((rows, block), lambda b: (0, b)),
            pl.BlockSpec((rows, block), lambda b: (0, b)),
        ],
        out_specs=pl.BlockSpec((groups_block, 2 * rows), lambda b: (b, 0)),
        out_shape=jax.ShapeDtypeStruct((group_count, 2 * rows), jnp.float32),
        compiler_params=pltpu.CompilerParams(dimension_semantics=("parallel",)),
    )(back, top, bottom)


def gather_seq(value):
    count = lax.axis_size("seq")
    tiled = jnp.broadcast_to(value[None], (count,) + value.shape)
    return lax.all_to_all(tiled, "seq", split_axis=0, concat_axis=0, tiled=True)


def entering_states(gathered, decays, block_len, group_size, forward):
    count = gathered.shape[0]
    here = lax.axis_index("seq")
    rates = jnp.repeat(decays.T, group_size, axis=1)
    source = jnp.arange(count)
    if forward:
        gap = here - 1 - source
    else:
        gap = source - here - 1
    valid = gap >= 0
    steps = jnp.maximum(gap, 0).astype(jnp.float32)
    coef = jnp.exp(-rates[None] * (float(block_len) * steps)[:, None, None])
    coef = jnp.where(valid[:, None, None], coef, 0.0)
    return jnp.sum(coef * gathered, axis=0)


def on_device(
    query_mr,
    key_mr,
    value_mr,
    query_li,
    key_li,
    cotangent,
    mr_filter,
    norm_gain,
    li_decay,
    li_residue,
):
    row_count, chan_count = query_mr.shape
    group_count, tap_count = mr_filter.shape
    group_size = chan_count // group_count
    assert row_count == tap_count
    grad_scale = float(row_count * lax.axis_size("seq")) ** (-0.5)

    taps_mr = mr_filter.astype(jnp.bfloat16).astype(jnp.float32)
    zero_col = jnp.zeros((group_count, 1), jnp.float32)
    fwd_rows = jnp.concatenate(
        [zero_col, jnp.flip(taps_mr, 1), jnp.zeros((group_count, tap_count - 1), jnp.float32)], 1
    )
    bwd_rows = jnp.concatenate([taps_mr, jnp.zeros_like(taps_mr)], 1)

    mixed_mr = (key_mr.astype(jnp.float32) * value_mr.astype(jnp.float32)).astype(jnp.bfloat16)
    rim_rows = from_behind(mixed_mr, "seq", 1)
    conv_mr = band_conv(fwd_rows, rim_rows, mixed_mr, group_size=group_size, split=False, tri=None)
    out_mr = (query_mr.astype(jnp.float32) * conv_mr).astype(jnp.bfloat16)
    out_full = out_mr.astype(jnp.float32)
    squares = lax.psum(jnp.sum(out_full * out_full, axis=1), "chan")
    inv_rms = lax.rsqrt(squares / D + 1e-06)[:, None]
    normed = out_full * inv_rms * norm_gain
    mixed_li = key_li.astype(jnp.float32) * normed
    cotan_full = cotangent.astype(jnp.float32)
    back_li = cotan_full * query_li.astype(jnp.float32)

    offsets = jnp.arange(row_count, dtype=jnp.float32)
    weights_res = li_residue * jnp.sqrt(2.0 * li_decay)
    taps_li = jnp.einsum(
        "gr,grd->gd", weights_res, jnp.exp(-li_decay[:, :, None] * offsets), precision=HIGHEST
    )
    li_fwd_rows = jnp.concatenate([taps_li[:, :1], jnp.flip(taps_li[:, 1:], 1)], 1)
    fwd_states = jnp.exp(-li_decay[:, :, None] * (row_count - 1.0 - offsets)).astype(jnp.bfloat16)
    bwd_states = jnp.exp(-li_decay[:, :, None] * offsets).astype(jnp.bfloat16)

    back_li_bf = back_li.astype(jnp.bfloat16)
    mixed_li_bf = mixed_li.astype(jnp.bfloat16)
    modes = li_decay.shape[1]
    grad_st = modal_states(bwd_states, back_li_bf, group_size=group_size)
    conv_st = modal_states(fwd_states, mixed_li_bf, group_size=group_size)
    both_st = gather_seq(jnp.concatenate([grad_st, conv_st], 0).astype(jnp.bfloat16))
    both_st = both_st.astype(jnp.float32)
    grad_loc = band_conv(taps_li, back_li_bf, group_size=group_size, split=False, tri="upper")
    conv_loc = band_conv(li_fwd_rows, mixed_li_bf, group_size=group_size, split=False, tri="lower")
    both_st, grad_loc, conv_loc = lax.optimization_barrier((both_st, grad_loc, conv_loc))
    grad_ent = entering_states(both_st[:, :modes], li_decay, row_count, group_size, False)
    conv_ent = entering_states(both_st[:, modes:], li_decay, row_count, group_size, True)
    grad_mixed_li = modal_out(
        li_decay, weights_res, grad_ent, grad_loc, group_size=group_size, forward=False
    )
    out_li, grad_query_li = modal_out(
        li_decay, weights_res, conv_ent, conv_loc, (query_li, cotangent),
        group_size=group_size, forward=True,
    )

    grad_key_li = (grad_mixed_li * normed).astype(jnp.bfloat16)
    grad_normed = grad_mixed_li * key_li.astype(jnp.float32)
    gain_part = jnp.sum(grad_normed * out_full * inv_rms, axis=0)
    weighted = grad_normed * norm_gain
    cross_dots = lax.psum(jnp.sum(weighted * out_full, axis=1), "chan")[:, None]
    grad_out_mr = inv_rms * weighted - out_full * inv_rms**3 * cross_dots / D
    grad_query_mr = (grad_out_mr * conv_mr).astype(jnp.bfloat16)
    back_mr = (grad_out_mr * query_mr.astype(jnp.float32)).astype(jnp.bfloat16)
    after_rim = from_behind(back_mr, "seq", -1)
    grad_key_mr, grad_value_mr = band_conv(
        bwd_rows, back_mr, after_rim, scale_pair=(value_mr, key_mr),
        group_size=group_size, split=False, tri=None,
    )
    diag_sums = gram_diag(back_mr, rim_rows, mixed_mr, group_size=group_size)
    filter_part = jnp.flip(diag_sums[:, tap_count:], 1)
    packed = jnp.concatenate([gain_part, filter_part.reshape(-1)])
    packed, after_rim = lax.optimization_barrier((packed, after_rim))
    param_sums = jnp.sum(gather_seq(packed), axis=0) * grad_scale
    grad_gain = param_sums[:chan_count]
    grad_filter = param_sums[chan_count:].reshape(group_count, tap_count)
    return (
        out_li,
        grad_query_mr,
        grad_key_mr,
        grad_value_mr,
        grad_query_li,
        grad_key_li,
        grad_gain,
        grad_filter,
    )


def solution(mesh):
    in_specs = (
        P("seq", "chan"),
        P("seq", "chan"),
        P("seq", "chan"),
        P("seq", "chan"),
        P("seq", "chan"),
        P("seq", "chan"),
        P("chan", None),
        P("chan"),
        P("chan", None),
        P("chan", None),
    )
    out_specs = (
        P("seq", "chan"),
        P("seq", "chan"),
        P("seq", "chan"),
        P("seq", "chan"),
        P("seq", "chan"),
        P("seq", "chan"),
        P("chan"),
        P("chan", None),
    )
    return jax.shard_map(
        on_device, mesh=mesh, in_specs=in_specs, out_specs=out_specs, check_vma=False
    )
```

```python
import functools

import jax
import jax.numpy as jnp
from jax import lax
from jax.experimental import pallas as pl
from jax.experimental.pallas import tpu as pltpu
from jax.sharding import PartitionSpec as P

D = 8192
G = 512
LANES = 128
BLOCK_LANES = 512
HIGHEST = lax.Precision.HIGHEST


def from_behind(value, axis, steps):
    count = lax.axis_size(axis)
    initial, last = (max(0, -steps), min(count, count - steps))
    return lax.ppermute(value, axis, [(source, source + steps) for source in range(initial, last)])


def _split(value):
    high = value.astype(jnp.bfloat16)
    return high, (value - high.astype(jnp.float32)).astype(jnp.bfloat16)


def _band_kernel(*refs, group_size, split, tri, two_inputs, modal, sub, scaled):
    refs = list(refs)
    h_ref = refs.pop(0)
    top_ref = refs.pop(0)
    bot_ref = refs.pop(0) if two_inputs else None
    if modal is not None:
        dec_ref, wt_ref, ent_ref = refs.pop(0), refs.pop(0), refs.pop(0)
    if scaled:
        first_ref, second_ref = refs.pop(0), refs.pop(0)
    out_ref = refs.pop(0)
    if scaled:
        other_ref = refs.pop(0)
    rows = out_ref.shape[0]
    width = h_ref.shape[1]
    groups_here = LANES // group_size
    lane_group = lax.broadcasted_iota(jnp.int32, (rows, LANES), 1) // group_size
    row_id = lax.broadcasted_iota(jnp.int32, (rows, width), 0)
    col_id = lax.broadcasted_iota(jnp.int32, (rows, width), 1)
    if modal is not None:
        modes = dec_ref.shape[1]
        offsets = lax.broadcasted_iota(jnp.int32, (rows, modes), 0).astype(jnp.float32)
        dist = offsets + 1.0 if modal == "forward" else float(rows) - offsets

    def body(j, carry):
        lanes = pl.ds(pl.multiple_of(j * LANES, LANES), LANES)
        if two_inputs:
            x = jnp.concatenate([top_ref[:, lanes], bot_ref[:, lanes]], axis=0)
        else:
            x = top_ref[:, lanes]
        bands = []
        for k in range(groups_here):
            band_row = h_ref[pl.ds(j * groups_here + k, 1), :]
            band = pltpu.roll(jnp.broadcast_to(band_row, (rows, width)), 0, 1, stride=1, stride_axis=0)
            if tri == "lower":
                band = jnp.where(col_id <= row_id, band, 0.0)
            elif tri == "upper":
                band = jnp.where(col_id >= row_id, band, 0.0)
            bands.append(band)
        stacked = jnp.concatenate(bands, axis=0)
        if split:
            high, low = _split(stacked)
            y = jnp.dot(high, x, preferred_element_type=jnp.float32)
            y = y + jnp.dot(low, x, preferred_element_type=jnp.float32)
        else:
            y = jnp.dot(stacked.astype(jnp.bfloat16), x, preferred_element_type=jnp.float32)
        if modal is not None:
            ent_high, ent_low = _split(ent_ref[:, lanes])
            out_w = []
            for k in range(groups_here):
                rate = dec_ref[pl.ds(j * groups_here + k, 1), :]
                weight = wt_ref[pl.ds(j * groups_here + k, 1), :]
                out_w.append(weight * jnp.exp(-rate * dist))
            a_high, a_low = _split(jnp.concatenate(out_w, axis=0))
            y = y + jnp.dot(a_high, ent_high, preferred_element_type=jnp.float32)
            y = y + jnp.dot(a_low, ent_high, preferred_element_type=jnp.float32)
            y = y + jnp.dot(a_high, ent_low, preferred_element_type=jnp.float32)
        acc = y[:rows]
        for k in range(1, groups_here):
            acc = jnp.where(lane_group == k, y[k * rows:(k + 1) * rows], acc)
        if scaled:
            out_ref[:, lanes] = (acc * first_ref[:, lanes].astype(jnp.float32)).astype(out_ref.dtype)
            other_ref[:, lanes] = (acc * second_ref[:, lanes].astype(jnp.float32)).astype(other_ref.dtype)
        else:
            out_ref[:, lanes] = acc
        return carry

    lax.fori_loop(0, sub, body, 0)


def band_conv(
    band_rows, top, bottom=None, modal_args=None, scale_pair=None, *, group_size, split, tri, modal=None
):
    rows, chans = top.shape
    block = min(BLOCK_LANES, chans)
    groups_block = block // group_size
    width = band_rows.shape[1]
    two_inputs = bottom is not None
    in_specs = [
        pl.BlockSpec((groups_block, width), lambda b: (b, 0)),
        pl.BlockSpec((rows, block), lambda b: (0, b)),
    ]
    args = [band_rows, top]
    if two_inputs:
        in_specs.append(pl.BlockSpec((rows, block), lambda b: (0, b)))
        args.append(bottom)
    if modal is not None:
        decays, weights, entering = modal_args
        modes = decays.shape[1]
        in_specs += [
            pl.BlockSpec((groups_block, modes), lambda b: (b, 0)),
            pl.BlockSpec((groups_block, modes), lambda b: (b, 0)),
            pl.BlockSpec((modes, block), lambda b: (0, b)),
        ]
        args += [decays, weights, entering]
    scaled = scale_pair is not None
    out_specs = pl.BlockSpec((rows, block), lambda b: (0, b))
    out_shape = jax.ShapeDtypeStruct((rows, chans), jnp.float32)
    if scaled:
        in_specs += [pl.BlockSpec((rows, block), lambda b: (0, b))] * 2
        args += list(scale_pair)
        out_specs = [out_specs, out_specs]
        out_shape = [jax.ShapeDtypeStruct((rows, chans), jnp.bfloat16)] * 2
    kernel = functools.partial(
        _band_kernel,
        group_size=group_size,
        split=split,
        tri=tri,
        two_inputs=two_inputs,
        modal=modal,
        sub=block // LANES,
        scaled=scaled,
    )
    return pl.pallas_call(
        kernel,
        grid=(chans // block,),
        in_specs=in_specs,
        out_specs=out_specs,
        out_shape=out_shape,
        compiler_params=pltpu.CompilerParams(dimension_semantics=("parallel",)),
    )(*args)


def _state_kernel(e_ref, x_ref, s_ref, *, group_size, sub):
    modes = s_ref.shape[0]
    groups_here = LANES // group_size
    state_group = lax.broadcasted_iota(jnp.int32, (modes, LANES), 1) // group_size

    def body(j, carry):
        lanes = pl.ds(pl.multiple_of(j * LANES, LANES), LANES)
        x = x_ref[:, lanes]
        weights = e_ref[pl.ds(j * groups_here, groups_here)]
        stacked = weights.reshape(groups_here * modes, weights.shape[2]).astype(jnp.bfloat16)
        y = jnp.dot(stacked, x, preferred_element_type=jnp.float32)
        acc = y[:modes]
        for k in range(1, groups_here):
            acc = jnp.where(state_group == k, y[k * modes:(k + 1) * modes], acc)
        s_ref[:, lanes] = acc
        return carry

    lax.fori_loop(0, sub, body, 0)


def modal_states(state_rows, x, *, group_size):
    rows, chans = x.shape
    block = min(BLOCK_LANES, chans)
    groups_block = block // group_size
    modes = state_rows.shape[1]
    kernel = functools.partial(_state_kernel, group_size=group_size, sub=block // LANES)
    return pl.pallas_call(
        kernel,
        grid=(chans // block,),
        in_specs=[
            pl.BlockSpec((groups_block, modes, rows), lambda b: (b, 0, 0)),
            pl.BlockSpec((rows, block), lambda b: (0, b)),
        ],
        out_specs=pl.BlockSpec((modes, block), lambda b: (0, b)),
        out_shape=jax.ShapeDtypeStruct((modes, chans), jnp.float32),
        compiler_params=pltpu.CompilerParams(dimension_semantics=("parallel",)),
    )(state_rows, x)


def _modal_kernel(*refs, group_size, forward, sub, scaled):
    if scaled:
        dec_ref, wt_ref, ent_ref, loc_ref, first_ref, second_ref, out_ref, other_ref = refs
    else:
        dec_ref, wt_ref, ent_ref, loc_ref, out_ref = refs
    rows = out_ref.shape[0]
    modes = ent_ref.shape[0]
    groups_here = LANES // group_size
    width = groups_here * modes
    offsets = lax.broadcasted_iota(jnp.int32, (rows, width), 0).astype(jnp.float32)
    dist = offsets + 1.0 if forward else float(rows) - offsets
    row_group = lax.broadcasted_iota(jnp.int32, (width, LANES), 0) // modes
    lane_group = lax.broadcasted_iota(jnp.int32, (width, LANES), 1) // group_size

    def body(j, carry):
        lanes = pl.ds(pl.multiple_of(j * LANES, LANES), LANES)
        row = pl.program_id(0) * sub + j
        rate = dec_ref[pl.ds(row, 1), :]
        weight = wt_ref[pl.ds(row, 1), :]
        out_w = (weight * jnp.exp(-rate * dist)).astype(jnp.bfloat16)
        entering = ent_ref[:, lanes]
        tiled = jnp.concatenate([entering] * groups_here, axis=0)
        diag = jnp.where(row_group == lane_group, tiled, 0.0).astype(jnp.bfloat16)
        y = jnp.dot(out_w, diag, preferred_element_type=jnp.float32)
        total = loc_ref[:, lanes] + y
        if scaled:
            out_ref[:, lanes] = (total * first_ref[:, lanes].astype(jnp.float32)).astype(out_ref.dtype)
            other_ref[:, lanes] = (total * second_ref[:, lanes].astype(jnp.float32)).astype(other_ref.dtype)
        else:
            out_ref[:, lanes] = total
        return carry

    lax.fori_loop(0, sub, body, 0)


def modal_out(decays, weights, entering, local, scale_pair=None, *, group_size, forward):
    rows, chans = local.shape
    block = min(BLOCK_LANES, chans)
    groups_block = block // group_size
    modes = decays.shape[1]
    per_row = (LANES // group_size) * modes
    flat_decays = decays.reshape(-1, per_row)
    flat_weights = weights.reshape(-1, per_row)
    sub = block // LANES
    scaled = scale_pair is not None
    kernel = functools.partial(
        _modal_kernel, group_size=group_size, forward=forward, sub=sub, scaled=scaled
    )
    in_specs = [
        pl.BlockSpec(flat_decays.shape, lambda b: (0, 0)),
        pl.BlockSpec(flat_weights.shape, lambda b: (0, 0)),
        pl.BlockSpec((modes, block), lambda b: (0, b)),
        pl.BlockSpec((rows, block), lambda b: (0, b)),
    ]
    args = [flat_decays, flat_weights, entering, local]
    out_specs = pl.BlockSpec((rows, block), lambda b: (0, b))
    out_shape = jax.ShapeDtypeStruct((rows, chans), jnp.float32)
    if scaled:
        in_specs += [pl.BlockSpec((rows, block), lambda b: (0, b))] * 2
        args += list(scale_pair)
        out_specs = [out_specs, out_specs]
        out_shape = [jax.ShapeDtypeStruct((rows, chans), jnp.bfloat16)] * 2
    return pl.pallas_call(
        kernel,
        grid=(chans // block,),
        in_specs=in_specs,
        out_specs=out_specs,
        out_shape=out_shape,
        compiler_params=pltpu.CompilerParams(dimension_semantics=("parallel",)),
    )(*args)


def _gram_kernel(back_ref, top_ref, bot_ref, f_ref, *, group_size, sub):
    rows = back_ref.shape[0]
    groups_here = LANES // group_size
    r_id = lax.broadcasted_iota(jnp.int32, (rows, rows), 0)
    c_id = lax.broadcasted_iota(jnp.int32, (rows, rows), 1)
    exchange = jnp.where(r_id + c_id == rows - 1, 1.0, 0.0).astype(jnp.bfloat16)
    lane_group = lax.broadcasted_iota(jnp.int32, (rows, LANES), 1) // group_size

    def body(j, carry):
        lanes = pl.ds(pl.multiple_of(j * LANES, LANES), LANES)
        back = back_ref[:, lanes]
        x = jnp.concatenate([top_ref[:, lanes], bot_ref[:, lanes]], axis=0)
        back_rev = jnp.dot(exchange, back, preferred_element_type=jnp.float32).astype(jnp.bfloat16)
        masked = jnp.concatenate(
            [jnp.where(lane_group == k, back_rev, jnp.zeros_like(back_rev)) for k in range(groups_here)],
            axis=0,
        )
        gram = lax.dot_general(
            masked, x, (((1,), (1,)), ((), ())), preferred_element_type=jnp.float32
        )
        sums = []
        for k in range(groups_here):
            skew = pltpu.roll(gram[k * rows:(k + 1) * rows], 0, 1, stride=1, stride_axis=0)
            sums.append(jnp.sum(skew, axis=0, keepdims=True))
        f_ref[pl.ds(pl.multiple_of(j * groups_here, groups_here), groups_here), :] = jnp.concatenate(sums, 0)
        return carry

    lax.fori_loop(0, sub, body, 0)


def gram_diag(back, top, bottom, *, group_size):
    rows, chans = back.shape
    block = min(BLOCK_LANES, chans)
    groups_block = block // group_size
    group_count = chans // group_size
    kernel = functools.partial(_gram_kernel, group_size=group_size, sub=block // LANES)
    return pl.pallas_call(
        kernel,
        grid=(chans // block,),
        in_specs=[
            pl.BlockSpec((rows, block), lambda b: (0, b)),
            pl.BlockSpec((rows, block), lambda b: (0, b)),
            pl.BlockSpec((rows, block), lambda b: (0, b)),
        ],
        out_specs=pl.BlockSpec((groups_block, 2 * rows), lambda b: (b, 0)),
        out_shape=jax.ShapeDtypeStruct((group_count, 2 * rows), jnp.float32),
        compiler_params=pltpu.CompilerParams(dimension_semantics=("parallel",)),
    )(back, top, bottom)


def gather_seq(value):
    count = lax.axis_size("seq")
    tiled = jnp.broadcast_to(value[None], (count,) + value.shape)
    return lax.all_to_all(tiled, "seq", split_axis=0, concat_axis=0, tiled=True)


def entering_states(gathered, decays, block_len, group_size, forward):
    count = gathered.shape[0]
    here = lax.axis_index("seq")
    rates = jnp.repeat(decays.T, group_size, axis=1)
    source = jnp.arange(count)
    if forward:
        gap = here - 1 - source
    else:
        gap = source - here - 1
    valid = gap >= 0
    steps = jnp.maximum(gap, 0).astype(jnp.float32)
    coef = jnp.exp(-rates[None] * (float(block_len) * steps)[:, None, None])
    coef = jnp.where(valid[:, None, None], coef, 0.0)
    return jnp.sum(coef * gathered, axis=0)


def on_device(
    query_mr,
    key_mr,
    value_mr,
    query_li,
    key_li,
    cotangent,
    mr_filter,
    norm_gain,
    li_decay,
    li_residue,
):
    row_count, chan_count = query_mr.shape
    group_count, tap_count = mr_filter.shape
    group_size = chan_count // group_count
    assert row_count == tap_count
    grad_scale = float(row_count * lax.axis_size("seq")) ** (-0.5)

    taps_mr = mr_filter.astype(jnp.bfloat16).astype(jnp.float32)
    zero_col = jnp.zeros((group_count, 1), jnp.float32)
    fwd_rows = jnp.concatenate(
        [zero_col, jnp.flip(taps_mr, 1), jnp.zeros((group_count, tap_count - 1), jnp.float32)], 1
    )
    bwd_rows = jnp.concatenate([taps_mr, jnp.zeros_like(taps_mr)], 1)

    offsets = jnp.arange(row_count, dtype=jnp.float32)
    weights_res = li_residue * jnp.sqrt(2.0 * li_decay)
    taps_li = jnp.einsum(
        "gr,grd->gd", weights_res, jnp.exp(-li_decay[:, :, None] * offsets), precision=HIGHEST
    )
    li_fwd_rows = jnp.concatenate([taps_li[:, :1], jnp.flip(taps_li[:, 1:], 1)], 1)
    fwd_states = jnp.exp(-li_decay[:, :, None] * (row_count - 1.0 - offsets)).astype(jnp.bfloat16)
    bwd_states = jnp.exp(-li_decay[:, :, None] * offsets).astype(jnp.bfloat16)

    cotan_full = cotangent.astype(jnp.float32)
    back_li_bf = (cotan_full * query_li.astype(jnp.float32)).astype(jnp.bfloat16)
    mixed_mr = (key_mr.astype(jnp.float32) * value_mr.astype(jnp.float32)).astype(jnp.bfloat16)
    rim_rows = from_behind(mixed_mr, "seq", 1)
    grad_st = modal_states(bwd_states, back_li_bf, group_size=group_size)
    grad_gathered = gather_seq(grad_st.astype(jnp.bfloat16))
    grad_loc = band_conv(taps_li, back_li_bf, group_size=group_size, split=False, tri="upper")
    conv_mr = band_conv(fwd_rows, rim_rows, mixed_mr, group_size=group_size, split=False, tri=None)
    grad_gathered, grad_loc, conv_mr = lax.optimization_barrier((grad_gathered, grad_loc, conv_mr))
    grad_ent = entering_states(
        grad_gathered.astype(jnp.float32), li_decay, row_count, group_size, False
    )
    grad_mixed_li = modal_out(
        li_decay, weights_res, grad_ent, grad_loc, group_size=group_size, forward=False
    )
    out_mr = (query_mr.astype(jnp.float32) * conv_mr).astype(jnp.bfloat16)
    out_full = out_mr.astype(jnp.float32)
    key_full = key_li.astype(jnp.float32)
    grad_normed = grad_mixed_li * key_full
    weighted = grad_normed * norm_gain
    row_sums = jnp.stack(
        [jnp.sum(out_full * out_full, axis=1), jnp.sum(weighted * out_full, axis=1)]
    )
    row_sums = lax.psum(row_sums, "chan")
    squares = row_sums[0]
    cross_dots = row_sums[1][:, None]
    inv_rms = lax.rsqrt(squares / D + 1e-06)[:, None]
    normed = out_full * inv_rms * norm_gain
    mixed_li_bf = (key_full * normed).astype(jnp.bfloat16)
    conv_st = modal_states(fwd_states, mixed_li_bf, group_size=group_size)
    conv_gathered = gather_seq(conv_st.astype(jnp.bfloat16))
    conv_loc = band_conv(li_fwd_rows, mixed_li_bf, group_size=group_size, split=False, tri="lower")
    conv_gathered, conv_loc = lax.optimization_barrier((conv_gathered, conv_loc))
    conv_ent = entering_states(
        conv_gathered.astype(jnp.float32), li_decay, row_count, group_size, True
    )
    out_li, grad_query_li = modal_out(
        li_decay, weights_res, conv_ent, conv_loc, (query_li, cotangent),
        group_size=group_size, forward=True,
    )

    grad_key_li = (grad_mixed_li * normed).astype(jnp.bfloat16)
    gain_part = jnp.sum(grad_normed * out_full * inv_rms, axis=0)
    grad_out_mr = inv_rms * weighted - out_full * inv_rms**3 * cross_dots / D
    grad_query_mr = (grad_out_mr * conv_mr).astype(jnp.bfloat16)
    back_mr = (grad_out_mr * query_mr.astype(jnp.float32)).astype(jnp.bfloat16)
    after_rim = from_behind(back_mr, "seq", -1)
    grad_key_mr, grad_value_mr = band_conv(
        bwd_rows, back_mr, after_rim, scale_pair=(value_mr, key_mr),
        group_size=group_size, split=False, tri=None,
    )
    diag_sums = gram_diag(back_mr, rim_rows, mixed_mr, group_size=group_size)
    filter_part = jnp.flip(diag_sums[:, tap_count:], 1)
    packed = jnp.concatenate([gain_part, filter_part.reshape(-1)])
    packed, after_rim = lax.optimization_barrier((packed, after_rim))
    param_sums = jnp.sum(gather_seq(packed), axis=0) * grad_scale
    grad_gain = param_sums[:chan_count]
    grad_filter = param_sums[chan_count:].reshape(group_count, tap_count)
    return (
        out_li,
        grad_query_mr,
        grad_key_mr,
        grad_value_mr,
        grad_query_li,
        grad_key_li,
        grad_gain,
        grad_filter,
    )


def solution(mesh):
    in_specs = (
        P("seq", "chan"),
        P("seq", "chan"),
        P("seq", "chan"),
        P("seq", "chan"),
        P("seq", "chan"),
        P("seq", "chan"),
        P("chan", None),
        P("chan"),
        P("chan", None),
        P("chan", None),
    )
    out_specs = (
        P("seq", "chan"),
        P("seq", "chan"),
        P("seq", "chan"),
        P("seq", "chan"),
        P("seq", "chan"),
        P("seq", "chan"),
        P("chan"),
        P("chan", None),
    )
    return jax.shard_map(
        on_device, mesh=mesh, in_specs=in_specs, out_specs=out_specs, check_vma=False
    )
```

```python
import functools

import jax
import jax.numpy as jnp
from jax import lax
from jax.experimental import pallas as pl
from jax.experimental.pallas import tpu as pltpu
from jax.sharding import PartitionSpec as P

D = 8192
G = 512
LANES = 128
BLOCK_LANES = 512
HIGHEST = lax.Precision.HIGHEST


def from_behind(value, axis, steps):
    count = lax.axis_size(axis)
    initial, last = (max(0, -steps), min(count, count - steps))
    return lax.ppermute(value, axis, [(source, source + steps) for source in range(initial, last)])


def _split(value):
    high = value.astype(jnp.bfloat16)
    return high, (value - high.astype(jnp.float32)).astype(jnp.bfloat16)


def _band_kernel(*refs, group_size, split, tri, two_inputs, modal, sub, scaled):
    refs = list(refs)
    h_ref = refs.pop(0)
    top_ref = refs.pop(0)
    bot_ref = refs.pop(0) if two_inputs else None
    if modal is not None:
        dec_ref, wt_ref, ent_ref = refs.pop(0), refs.pop(0), refs.pop(0)
    if scaled:
        first_ref, second_ref = refs.pop(0), refs.pop(0)
    out_ref = refs.pop(0)
    if scaled:
        other_ref = refs.pop(0)
    rows = out_ref.shape[0]
    width = h_ref.shape[1]
    groups_here = LANES // group_size
    lane_group = lax.broadcasted_iota(jnp.int32, (rows, LANES), 1) // group_size
    row_id = lax.broadcasted_iota(jnp.int32, (rows, width), 0)
    col_id = lax.broadcasted_iota(jnp.int32, (rows, width), 1)
    if modal is not None:
        modes = dec_ref.shape[1]
        offsets = lax.broadcasted_iota(jnp.int32, (rows, modes), 0).astype(jnp.float32)
        dist = offsets + 1.0 if modal == "forward" else float(rows) - offsets

    def body(j, carry):
        lanes = pl.ds(pl.multiple_of(j * LANES, LANES), LANES)
        if two_inputs:
            x = jnp.concatenate([top_ref[:, lanes], bot_ref[:, lanes]], axis=0)
        else:
            x = top_ref[:, lanes]
        bands = []
        for k in range(groups_here):
            band_row = h_ref[pl.ds(j * groups_here + k, 1), :]
            band = pltpu.roll(jnp.broadcast_to(band_row, (rows, width)), 0, 1, stride=1, stride_axis=0)
            if tri == "lower":
                band = jnp.where(col_id <= row_id, band, 0.0)
            elif tri == "upper":
                band = jnp.where(col_id >= row_id, band, 0.0)
            bands.append(band)
        stacked = jnp.concatenate(bands, axis=0)
        if split:
            high, low = _split(stacked)
            y = jnp.dot(high, x, preferred_element_type=jnp.float32)
            y = y + jnp.dot(low, x, preferred_element_type=jnp.float32)
        else:
            y = jnp.dot(stacked.astype(jnp.bfloat16), x, preferred_element_type=jnp.float32)
        if modal is not None:
            ent_high, ent_low = _split(ent_ref[:, lanes])
            out_w = []
            for k in range(groups_here):
                rate = dec_ref[pl.ds(j * groups_here + k, 1), :]
                weight = wt_ref[pl.ds(j * groups_here + k, 1), :]
                out_w.append(weight * jnp.exp(-rate * dist))
            a_high, a_low = _split(jnp.concatenate(out_w, axis=0))
            y = y + jnp.dot(a_high, ent_high, preferred_element_type=jnp.float32)
            y = y + jnp.dot(a_low, ent_high, preferred_element_type=jnp.float32)
            y = y + jnp.dot(a_high, ent_low, preferred_element_type=jnp.float32)
        acc = y[:rows]
        for k in range(1, groups_here):
            acc = jnp.where(lane_group == k, y[k * rows:(k + 1) * rows], acc)
        if scaled:
            out_ref[:, lanes] = (acc * first_ref[:, lanes].astype(jnp.float32)).astype(out_ref.dtype)
            other_ref[:, lanes] = (acc * second_ref[:, lanes].astype(jnp.float32)).astype(other_ref.dtype)
        else:
            out_ref[:, lanes] = acc
        return carry

    lax.fori_loop(0, sub, body, 0)


def band_conv(
    band_rows, top, bottom=None, modal_args=None, scale_pair=None, *, group_size, split, tri, modal=None
):
    rows, chans = top.shape
    block = min(BLOCK_LANES, chans)
    groups_block = block // group_size
    width = band_rows.shape[1]
    two_inputs = bottom is not None
    in_specs = [
        pl.BlockSpec((groups_block, width), lambda b: (b, 0)),
        pl.BlockSpec((rows, block), lambda b: (0, b)),
    ]
    args = [band_rows, top]
    if two_inputs:
        in_specs.append(pl.BlockSpec((rows, block), lambda b: (0, b)))
        args.append(bottom)
    if modal is not None:
        decays, weights, entering = modal_args
        modes = decays.shape[1]
        in_specs += [
            pl.BlockSpec((groups_block, modes), lambda b: (b, 0)),
            pl.BlockSpec((groups_block, modes), lambda b: (b, 0)),
            pl.BlockSpec((modes, block), lambda b: (0, b)),
        ]
        args += [decays, weights, entering]
    scaled = scale_pair is not None
    out_specs = pl.BlockSpec((rows, block), lambda b: (0, b))
    out_shape = jax.ShapeDtypeStruct((rows, chans), jnp.float32)
    if scaled:
        in_specs += [pl.BlockSpec((rows, block), lambda b: (0, b))] * 2
        args += list(scale_pair)
        out_specs = [out_specs, out_specs]
        out_shape = [jax.ShapeDtypeStruct((rows, chans), jnp.bfloat16)] * 2
    kernel = functools.partial(
        _band_kernel,
        group_size=group_size,
        split=split,
        tri=tri,
        two_inputs=two_inputs,
        modal=modal,
        sub=block // LANES,
        scaled=scaled,
    )
    return pl.pallas_call(
        kernel,
        grid=(chans // block,),
        in_specs=in_specs,
        out_specs=out_specs,
        out_shape=out_shape,
        compiler_params=pltpu.CompilerParams(dimension_semantics=("parallel",)),
    )(*args)


def _state_kernel(e_ref, x_ref, s_ref, *, group_size, sub):
    modes = s_ref.shape[0]
    groups_here = LANES // group_size
    state_group = lax.broadcasted_iota(jnp.int32, (modes, LANES), 1) // group_size

    def body(j, carry):
        lanes = pl.ds(pl.multiple_of(j * LANES, LANES), LANES)
        x = x_ref[:, lanes]
        weights = e_ref[pl.ds(j * groups_here, groups_here)]
        stacked = weights.reshape(groups_here * modes, weights.shape[2]).astype(jnp.bfloat16)
        y = jnp.dot(stacked, x, preferred_element_type=jnp.float32)
        acc = y[:modes]
        for k in range(1, groups_here):
            acc = jnp.where(state_group == k, y[k * modes:(k + 1) * modes], acc)
        s_ref[:, lanes] = acc.astype(s_ref.dtype)
        return carry

    lax.fori_loop(0, sub, body, 0)


def modal_states(state_rows, x, *, group_size):
    rows, chans = x.shape
    block = min(BLOCK_LANES, chans)
    groups_block = block // group_size
    modes = state_rows.shape[1]
    kernel = functools.partial(_state_kernel, group_size=group_size, sub=block // LANES)
    return pl.pallas_call(
        kernel,
        grid=(chans // block,),
        in_specs=[
            pl.BlockSpec((groups_block, modes, rows), lambda b: (b, 0, 0)),
            pl.BlockSpec((rows, block), lambda b: (0, b)),
        ],
        out_specs=pl.BlockSpec((modes, block), lambda b: (0, b)),
        out_shape=jax.ShapeDtypeStruct((modes, chans), jnp.bfloat16),
        compiler_params=pltpu.CompilerParams(dimension_semantics=("parallel",)),
    )(state_rows, x)


def _modal_kernel(*refs, group_size, forward, sub, scaled):
    if scaled:
        dec_ref, wt_ref, ent_ref, loc_ref, first_ref, second_ref, out_ref, other_ref = refs
    else:
        dec_ref, wt_ref, ent_ref, loc_ref, out_ref = refs
    rows = out_ref.shape[0]
    modes = ent_ref.shape[0]
    groups_here = LANES // group_size
    width = groups_here * modes
    offsets = lax.broadcasted_iota(jnp.int32, (rows, width), 0).astype(jnp.float32)
    dist = offsets + 1.0 if forward else float(rows) - offsets
    row_group = lax.broadcasted_iota(jnp.int32, (width, LANES), 0) // modes
    lane_group = lax.broadcasted_iota(jnp.int32, (width, LANES), 1) // group_size

    def body(j, carry):
        lanes = pl.ds(pl.multiple_of(j * LANES, LANES), LANES)
        row = pl.program_id(0) * sub + j
        rate = dec_ref[pl.ds(row, 1), :]
        weight = wt_ref[pl.ds(row, 1), :]
        out_w = (weight * jnp.exp(-rate * dist)).astype(jnp.bfloat16)
        entering = ent_ref[:, lanes]
        tiled = jnp.concatenate([entering] * groups_here, axis=0)
        diag = jnp.where(row_group == lane_group, tiled, 0.0).astype(jnp.bfloat16)
        y = jnp.dot(out_w, diag, preferred_element_type=jnp.float32)
        total = loc_ref[:, lanes] + y
        if scaled:
            out_ref[:, lanes] = (total * first_ref[:, lanes].astype(jnp.float32)).astype(out_ref.dtype)
            other_ref[:, lanes] = (total * second_ref[:, lanes].astype(jnp.float32)).astype(other_ref.dtype)
        else:
            out_ref[:, lanes] = total
        return carry

    lax.fori_loop(0, sub, body, 0)


def modal_out(decays, weights, entering, local, scale_pair=None, *, group_size, forward):
    rows, chans = local.shape
    block = min(BLOCK_LANES, chans)
    groups_block = block // group_size
    modes = decays.shape[1]
    per_row = (LANES // group_size) * modes
    flat_decays = decays.reshape(-1, per_row)
    flat_weights = weights.reshape(-1, per_row)
    sub = block // LANES
    scaled = scale_pair is not None
    kernel = functools.partial(
        _modal_kernel, group_size=group_size, forward=forward, sub=sub, scaled=scaled
    )
    in_specs = [
        pl.BlockSpec(flat_decays.shape, lambda b: (0, 0)),
        pl.BlockSpec(flat_weights.shape, lambda b: (0, 0)),
        pl.BlockSpec((modes, block), lambda b: (0, b)),
        pl.BlockSpec((rows, block), lambda b: (0, b)),
    ]
    args = [flat_decays, flat_weights, entering, local]
    out_specs = pl.BlockSpec((rows, block), lambda b: (0, b))
    out_shape = jax.ShapeDtypeStruct((rows, chans), jnp.float32)
    if scaled:
        in_specs += [pl.BlockSpec((rows, block), lambda b: (0, b))] * 2
        args += list(scale_pair)
        out_specs = [out_specs, out_specs]
        out_shape = [jax.ShapeDtypeStruct((rows, chans), jnp.bfloat16)] * 2
    return pl.pallas_call(
        kernel,
        grid=(chans // block,),
        in_specs=in_specs,
        out_specs=out_specs,
        out_shape=out_shape,
        compiler_params=pltpu.CompilerParams(dimension_semantics=("parallel",)),
    )(*args)


def _gram_kernel(back_ref, top_ref, bot_ref, f_ref, *, group_size, sub):
    rows = back_ref.shape[0]
    groups_here = LANES // group_size
    r_id = lax.broadcasted_iota(jnp.int32, (rows, rows), 0)
    c_id = lax.broadcasted_iota(jnp.int32, (rows, rows), 1)
    exchange = jnp.where(r_id + c_id == rows - 1, 1.0, 0.0).astype(jnp.bfloat16)
    lane_group = lax.broadcasted_iota(jnp.int32, (rows, LANES), 1) // group_size

    def body(j, carry):
        lanes = pl.ds(pl.multiple_of(j * LANES, LANES), LANES)
        back = back_ref[:, lanes]
        x = jnp.concatenate([top_ref[:, lanes], bot_ref[:, lanes]], axis=0)
        back_rev = jnp.dot(exchange, back, preferred_element_type=jnp.float32).astype(jnp.bfloat16)
        masked = jnp.concatenate(
            [jnp.where(lane_group == k, back_rev, jnp.zeros_like(back_rev)) for k in range(groups_here)],
            axis=0,
        )
        gram = lax.dot_general(
            masked, x, (((1,), (1,)), ((), ())), preferred_element_type=jnp.float32
        )
        sums = []
        for k in range(groups_here):
            skew = pltpu.roll(gram[k * rows:(k + 1) * rows], 0, 1, stride=1, stride_axis=0)
            sums.append(jnp.sum(skew, axis=0, keepdims=True))
        f_ref[pl.ds(pl.multiple_of(j * groups_here, groups_here), groups_here), :] = jnp.concatenate(sums, 0)
        return carry

    lax.fori_loop(0, sub, body, 0)


def gram_diag(back, top, bottom, *, group_size):
    rows, chans = back.shape
    block = min(BLOCK_LANES, chans)
    groups_block = block // group_size
    group_count = chans // group_size
    kernel = functools.partial(_gram_kernel, group_size=group_size, sub=block // LANES)
    return pl.pallas_call(
        kernel,
        grid=(chans // block,),
        in_specs=[
            pl.BlockSpec((rows, block), lambda b: (0, b)),
            pl.BlockSpec((rows, block), lambda b: (0, b)),
            pl.BlockSpec((rows, block), lambda b: (0, b)),
        ],
        out_specs=pl.BlockSpec((groups_block, 2 * rows), lambda b: (b, 0)),
        out_shape=jax.ShapeDtypeStruct((group_count, 2 * rows), jnp.float32),
        compiler_params=pltpu.CompilerParams(dimension_semantics=("parallel",)),
    )(back, top, bottom)


def gather_seq(value):
    count = lax.axis_size("seq")
    tiled = jnp.broadcast_to(value[None], (count,) + value.shape)
    return lax.all_to_all(tiled, "seq", split_axis=0, concat_axis=0, tiled=True)


def entering_states(gathered, decays, block_len, group_size, forward):
    count = gathered.shape[0]
    here = lax.axis_index("seq")
    rates = jnp.repeat(decays.T, group_size, axis=1)
    source = jnp.arange(count)
    if forward:
        gap = here - 1 - source
    else:
        gap = source - here - 1
    valid = gap >= 0
    steps = jnp.maximum(gap, 0).astype(jnp.float32)
    coef = jnp.exp(-rates[None] * (float(block_len) * steps)[:, None, None])
    coef = jnp.where(valid[:, None, None], coef, 0.0)
    return jnp.sum(coef * gathered, axis=0)


def on_device(
    query_mr,
    key_mr,
    value_mr,
    query_li,
    key_li,
    cotangent,
    mr_filter,
    norm_gain,
    li_decay,
    li_residue,
):
    row_count, chan_count = query_mr.shape
    group_count, tap_count = mr_filter.shape
    group_size = chan_count // group_count
    assert row_count == tap_count
    grad_scale = float(row_count * lax.axis_size("seq")) ** (-0.5)

    taps_mr = mr_filter.astype(jnp.bfloat16).astype(jnp.float32)
    zero_col = jnp.zeros((group_count, 1), jnp.float32)
    fwd_rows = jnp.concatenate(
        [zero_col, jnp.flip(taps_mr, 1), jnp.zeros((group_count, tap_count - 1), jnp.float32)], 1
    )
    bwd_rows = jnp.concatenate([taps_mr, jnp.zeros_like(taps_mr)], 1)

    mixed_mr = (key_mr.astype(jnp.float32) * value_mr.astype(jnp.float32)).astype(jnp.bfloat16)
    rim_rows = from_behind(mixed_mr, "seq", 1)
    conv_mr = band_conv(fwd_rows, rim_rows, mixed_mr, group_size=group_size, split=False, tri=None)
    out_mr = (query_mr.astype(jnp.float32) * conv_mr).astype(jnp.bfloat16)
    out_full = out_mr.astype(jnp.float32)
    squares = lax.psum(jnp.sum(out_full * out_full, axis=1), "chan")
    inv_rms = lax.rsqrt(squares / D + 1e-06)[:, None]
    normed = out_full * inv_rms * norm_gain
    mixed_li = key_li.astype(jnp.float32) * normed
    cotan_full = cotangent.astype(jnp.float32)
    back_li = cotan_full * query_li.astype(jnp.float32)

    offsets = jnp.arange(row_count, dtype=jnp.float32)
    weights_res = li_residue * jnp.sqrt(2.0 * li_decay)
    taps_li = jnp.einsum(
        "gr,grd->gd", weights_res, jnp.exp(-li_decay[:, :, None] * offsets), precision=HIGHEST
    )
    li_fwd_rows = jnp.concatenate([taps_li[:, :1], jnp.flip(taps_li[:, 1:], 1)], 1)
    fwd_states = jnp.exp(-li_decay[:, :, None] * (row_count - 1.0 - offsets)).astype(jnp.bfloat16)
    bwd_states = jnp.exp(-li_decay[:, :, None] * offsets).astype(jnp.bfloat16)

    back_li_bf = back_li.astype(jnp.bfloat16)
    mixed_li_bf = mixed_li.astype(jnp.bfloat16)
    modes = li_decay.shape[1]
    grad_st = modal_states(bwd_states, back_li_bf, group_size=group_size)
    conv_st = modal_states(fwd_states, mixed_li_bf, group_size=group_size)
    both_st = gather_seq(jnp.concatenate([grad_st, conv_st], 0))
    both_st = both_st.astype(jnp.float32)
    grad_loc = band_conv(taps_li, back_li_bf, group_size=group_size, split=False, tri="upper")
    conv_loc = band_conv(li_fwd_rows, mixed_li_bf, group_size=group_size, split=False, tri="lower")
    both_st, grad_loc, conv_loc = lax.optimization_barrier((both_st, grad_loc, conv_loc))
    grad_ent = entering_states(both_st[:, :modes], li_decay, row_count, group_size, False)
    conv_ent = entering_states(both_st[:, modes:], li_decay, row_count, group_size, True)
    grad_mixed_li = modal_out(
        li_decay, weights_res, grad_ent, grad_loc, group_size=group_size, forward=False
    )
    out_li, grad_query_li = modal_out(
        li_decay, weights_res, conv_ent, conv_loc, (query_li, cotangent),
        group_size=group_size, forward=True,
    )

    grad_key_li = (grad_mixed_li * normed).astype(jnp.bfloat16)
    grad_normed = grad_mixed_li * key_li.astype(jnp.float32)
    gain_part = jnp.sum(grad_normed * out_full * inv_rms, axis=0)
    weighted = grad_normed * norm_gain
    cross_dots = lax.psum(jnp.sum(weighted * out_full, axis=1), "chan")[:, None]
    grad_out_mr = inv_rms * weighted - out_full * inv_rms**3 * cross_dots / D
    grad_query_mr = (grad_out_mr * conv_mr).astype(jnp.bfloat16)
    back_mr = (grad_out_mr * query_mr.astype(jnp.float32)).astype(jnp.bfloat16)
    after_rim = from_behind(back_mr, "seq", -1)
    grad_key_mr, grad_value_mr = band_conv(
        bwd_rows, back_mr, after_rim, scale_pair=(value_mr, key_mr),
        group_size=group_size, split=False, tri=None,
    )
    diag_sums = gram_diag(back_mr, rim_rows, mixed_mr, group_size=group_size)
    filter_part = jnp.flip(diag_sums[:, tap_count:], 1)
    packed = jnp.concatenate([gain_part, filter_part.reshape(-1)])
    packed, after_rim = lax.optimization_barrier((packed, after_rim))
    param_sums = jnp.sum(gather_seq(packed), axis=0) * grad_scale
    grad_gain = param_sums[:chan_count]
    grad_filter = param_sums[chan_count:].reshape(group_count, tap_count)
    return (
        out_li,
        grad_query_mr,
        grad_key_mr,
        grad_value_mr,
        grad_query_li,
        grad_key_li,
        grad_gain,
        grad_filter,
    )


def solution(mesh):
    in_specs = (
        P("seq", "chan"),
        P("seq", "chan"),
        P("seq", "chan"),
        P("seq", "chan"),
        P("seq", "chan"),
        P("seq", "chan"),
        P("chan", None),
        P("chan"),
        P("chan", None),
        P("chan", None),
    )
    out_specs = (
        P("seq", "chan"),
        P("seq", "chan"),
        P("seq", "chan"),
        P("seq", "chan"),
        P("seq", "chan"),
        P("seq", "chan"),
        P("chan"),
        P("chan", None),
    )
    return jax.shard_map(
        on_device, mesh=mesh, in_specs=in_specs, out_specs=out_specs, check_vma=False
    )
```

```python
import functools

import jax
import jax.numpy as jnp
from jax import lax
from jax.experimental import pallas as pl
from jax.experimental.pallas import tpu as pltpu
from jax.sharding import PartitionSpec as P

D = 8192
G = 512
LANES = 128
BLOCK_LANES = 512
HIGHEST = lax.Precision.HIGHEST


def from_behind(value, axis, steps):
    count = lax.axis_size(axis)
    initial, last = (max(0, -steps), min(count, count - steps))
    return lax.ppermute(value, axis, [(source, source + steps) for source in range(initial, last)])


def _split(value):
    high = value.astype(jnp.bfloat16)
    return high, (value - high.astype(jnp.float32)).astype(jnp.bfloat16)


def _band_kernel(*refs, group_size, split, tri, two_inputs, modal, sub, scaled):
    refs = list(refs)
    h_ref = refs.pop(0)
    top_ref = refs.pop(0)
    bot_ref = refs.pop(0) if two_inputs else None
    if modal is not None:
        dec_ref, wt_ref, ent_ref = refs.pop(0), refs.pop(0), refs.pop(0)
    if scaled:
        first_ref, second_ref = refs.pop(0), refs.pop(0)
    out_ref = refs.pop(0)
    if scaled:
        other_ref = refs.pop(0)
    rows = out_ref.shape[0]
    width = h_ref.shape[1]
    groups_here = LANES // group_size
    lane_group = lax.broadcasted_iota(jnp.int32, (rows, LANES), 1) // group_size
    row_id = lax.broadcasted_iota(jnp.int32, (rows, width), 0)
    col_id = lax.broadcasted_iota(jnp.int32, (rows, width), 1)
    if modal is not None:
        modes = dec_ref.shape[1]
        offsets = lax.broadcasted_iota(jnp.int32, (rows, modes), 0).astype(jnp.float32)
        dist = offsets + 1.0 if modal == "forward" else float(rows) - offsets

    def body(j, carry):
        lanes = pl.ds(pl.multiple_of(j * LANES, LANES), LANES)
        if two_inputs:
            x = jnp.concatenate([top_ref[:, lanes], bot_ref[:, lanes]], axis=0)
        else:
            x = top_ref[:, lanes]
        bands = []
        for k in range(groups_here):
            band_row = h_ref[pl.ds(j * groups_here + k, 1), :]
            band = pltpu.roll(jnp.broadcast_to(band_row, (rows, width)), 0, 1, stride=1, stride_axis=0)
            if tri == "lower":
                band = jnp.where(col_id <= row_id, band, 0.0)
            elif tri == "upper":
                band = jnp.where(col_id >= row_id, band, 0.0)
            bands.append(band)
        stacked = jnp.concatenate(bands, axis=0)
        if split:
            high, low = _split(stacked)
            y = jnp.dot(high, x, preferred_element_type=jnp.float32)
            y = y + jnp.dot(low, x, preferred_element_type=jnp.float32)
        else:
            y = jnp.dot(stacked.astype(jnp.bfloat16), x, preferred_element_type=jnp.float32)
        if modal is not None:
            ent_high, ent_low = _split(ent_ref[:, lanes])
            out_w = []
            for k in range(groups_here):
                rate = dec_ref[pl.ds(j * groups_here + k, 1), :]
                weight = wt_ref[pl.ds(j * groups_here + k, 1), :]
                out_w.append(weight * jnp.exp(-rate * dist))
            a_high, a_low = _split(jnp.concatenate(out_w, axis=0))
            y = y + jnp.dot(a_high, ent_high, preferred_element_type=jnp.float32)
            y = y + jnp.dot(a_low, ent_high, preferred_element_type=jnp.float32)
            y = y + jnp.dot(a_high, ent_low, preferred_element_type=jnp.float32)
        acc = y[:rows]
        for k in range(1, groups_here):
            acc = jnp.where(lane_group == k, y[k * rows:(k + 1) * rows], acc)
        if scaled:
            out_ref[:, lanes] = (acc * first_ref[:, lanes].astype(jnp.float32)).astype(out_ref.dtype)
            other_ref[:, lanes] = (acc * second_ref[:, lanes].astype(jnp.float32)).astype(other_ref.dtype)
        else:
            out_ref[:, lanes] = acc
        return carry

    lax.fori_loop(0, sub, body, 0)


def band_conv(
    band_rows, top, bottom=None, modal_args=None, scale_pair=None, *, group_size, split, tri, modal=None
):
    rows, chans = top.shape
    block = min(BLOCK_LANES, chans)
    groups_block = block // group_size
    width = band_rows.shape[1]
    two_inputs = bottom is not None
    in_specs = [
        pl.BlockSpec((groups_block, width), lambda b: (b, 0)),
        pl.BlockSpec((rows, block), lambda b: (0, b)),
    ]
    args = [band_rows, top]
    if two_inputs:
        in_specs.append(pl.BlockSpec((rows, block), lambda b: (0, b)))
        args.append(bottom)
    if modal is not None:
        decays, weights, entering = modal_args
        modes = decays.shape[1]
        in_specs += [
            pl.BlockSpec((groups_block, modes), lambda b: (b, 0)),
            pl.BlockSpec((groups_block, modes), lambda b: (b, 0)),
            pl.BlockSpec((modes, block), lambda b: (0, b)),
        ]
        args += [decays, weights, entering]
    scaled = scale_pair is not None
    out_specs = pl.BlockSpec((rows, block), lambda b: (0, b))
    out_shape = jax.ShapeDtypeStruct((rows, chans), jnp.float32)
    if scaled:
        in_specs += [pl.BlockSpec((rows, block), lambda b: (0, b))] * 2
        args += list(scale_pair)
        out_specs = [out_specs, out_specs]
        out_shape = [jax.ShapeDtypeStruct((rows, chans), jnp.bfloat16)] * 2
    kernel = functools.partial(
        _band_kernel,
        group_size=group_size,
        split=split,
        tri=tri,
        two_inputs=two_inputs,
        modal=modal,
        sub=block // LANES,
        scaled=scaled,
    )
    return pl.pallas_call(
        kernel,
        grid=(chans // block,),
        in_specs=in_specs,
        out_specs=out_specs,
        out_shape=out_shape,
        compiler_params=pltpu.CompilerParams(dimension_semantics=("parallel",)),
    )(*args)


def _state_kernel(e_ref, x_ref, s_ref, *, group_size, sub):
    modes = s_ref.shape[0]
    groups_here = LANES // group_size
    state_group = lax.broadcasted_iota(jnp.int32, (modes, LANES), 1) // group_size

    def body(j, carry):
        lanes = pl.ds(pl.multiple_of(j * LANES, LANES), LANES)
        x = x_ref[:, lanes]
        weights = e_ref[pl.ds(j * groups_here, groups_here)]
        stacked = weights.reshape(groups_here * modes, weights.shape[2]).astype(jnp.bfloat16)
        y = jnp.dot(stacked, x, preferred_element_type=jnp.float32)
        acc = y[:modes]
        for k in range(1, groups_here):
            acc = jnp.where(state_group == k, y[k * modes:(k + 1) * modes], acc)
        s_ref[:, lanes] = acc.astype(s_ref.dtype)
        return carry

    lax.fori_loop(0, sub, body, 0)


def modal_states(state_rows, x, *, group_size):
    rows, chans = x.shape
    block = min(BLOCK_LANES, chans)
    groups_block = block // group_size
    modes = state_rows.shape[1]
    kernel = functools.partial(_state_kernel, group_size=group_size, sub=block // LANES)
    return pl.pallas_call(
        kernel,
        grid=(chans // block,),
        in_specs=[
            pl.BlockSpec((groups_block, modes, rows), lambda b: (b, 0, 0)),
            pl.BlockSpec((rows, block), lambda b: (0, b)),
        ],
        out_specs=pl.BlockSpec((modes, block), lambda b: (0, b)),
        out_shape=jax.ShapeDtypeStruct((modes, chans), jnp.bfloat16),
        compiler_params=pltpu.CompilerParams(dimension_semantics=("parallel",)),
    )(state_rows, x)


def _modal_kernel(*refs, group_size, forward, sub, scaled):
    if scaled:
        dec_ref, wt_ref, ent_ref, loc_ref, first_ref, second_ref, out_ref, other_ref = refs
    else:
        dec_ref, wt_ref, ent_ref, loc_ref, out_ref = refs
    rows = out_ref.shape[0]
    modes = ent_ref.shape[0]
    groups_here = LANES // group_size
    width = groups_here * modes
    offsets = lax.broadcasted_iota(jnp.int32, (rows, width), 0).astype(jnp.float32)
    dist = offsets + 1.0 if forward else float(rows) - offsets
    row_group = lax.broadcasted_iota(jnp.int32, (width, LANES), 0) // modes
    lane_group = lax.broadcasted_iota(jnp.int32, (width, LANES), 1) // group_size

    def body(j, carry):
        lanes = pl.ds(pl.multiple_of(j * LANES, LANES), LANES)
        row = pl.program_id(0) * sub + j
        rate = dec_ref[pl.ds(row, 1), :]
        weight = wt_ref[pl.ds(row, 1), :]
        out_w = (weight * jnp.exp(-rate * dist)).astype(jnp.bfloat16)
        entering = ent_ref[:, lanes]
        tiled = jnp.concatenate([entering] * groups_here, axis=0)
        diag = jnp.where(row_group == lane_group, tiled, 0.0).astype(jnp.bfloat16)
        y = jnp.dot(out_w, diag, preferred_element_type=jnp.float32)
        total = loc_ref[:, lanes] + y
        if scaled:
            out_ref[:, lanes] = (total * first_ref[:, lanes].astype(jnp.float32)).astype(out_ref.dtype)
            other_ref[:, lanes] = (total * second_ref[:, lanes].astype(jnp.float32)).astype(other_ref.dtype)
        else:
            out_ref[:, lanes] = total
        return carry

    lax.fori_loop(0, sub, body, 0)


def modal_out(decays, weights, entering, local, scale_pair=None, *, group_size, forward):
    rows, chans = local.shape
    block = min(BLOCK_LANES, chans)
    groups_block = block // group_size
    modes = decays.shape[1]
    per_row = (LANES // group_size) * modes
    flat_decays = decays.reshape(-1, per_row)
    flat_weights = weights.reshape(-1, per_row)
    sub = block // LANES
    scaled = scale_pair is not None
    kernel = functools.partial(
        _modal_kernel, group_size=group_size, forward=forward, sub=sub, scaled=scaled
    )
    in_specs = [
        pl.BlockSpec(flat_decays.shape, lambda b: (0, 0)),
        pl.BlockSpec(flat_weights.shape, lambda b: (0, 0)),
        pl.BlockSpec((modes, block), lambda b: (0, b)),
        pl.BlockSpec((rows, block), lambda b: (0, b)),
    ]
    args = [flat_decays, flat_weights, entering, local]
    out_specs = pl.BlockSpec((rows, block), lambda b: (0, b))
    out_shape = jax.ShapeDtypeStruct((rows, chans), jnp.float32)
    if scaled:
        in_specs += [pl.BlockSpec((rows, block), lambda b: (0, b))] * 2
        args += list(scale_pair)
        out_specs = [out_specs, out_specs]
        out_shape = [jax.ShapeDtypeStruct((rows, chans), jnp.bfloat16)] * 2
    return pl.pallas_call(
        kernel,
        grid=(chans // block,),
        in_specs=in_specs,
        out_specs=out_specs,
        out_shape=out_shape,
        compiler_params=pltpu.CompilerParams(dimension_semantics=("parallel",)),
    )(*args)


def _gram_kernel(back_ref, top_ref, bot_ref, f_ref, *, group_size, sub):
    rows = back_ref.shape[0]
    groups_here = LANES // group_size
    r_id = lax.broadcasted_iota(jnp.int32, (rows, rows), 0)
    c_id = lax.broadcasted_iota(jnp.int32, (rows, rows), 1)
    exchange = jnp.where(r_id + c_id == rows - 1, 1.0, 0.0).astype(jnp.bfloat16)
    lane_group = lax.broadcasted_iota(jnp.int32, (rows, LANES), 1) // group_size

    def body(j, carry):
        lanes = pl.ds(pl.multiple_of(j * LANES, LANES), LANES)
        back = back_ref[:, lanes]
        x = jnp.concatenate([top_ref[:, lanes], bot_ref[:, lanes]], axis=0)
        back_rev = jnp.dot(exchange, back, preferred_element_type=jnp.float32).astype(jnp.bfloat16)
        masked = jnp.concatenate(
            [jnp.where(lane_group == k, back_rev, jnp.zeros_like(back_rev)) for k in range(groups_here)],
            axis=0,
        )
        gram = lax.dot_general(
            masked, x, (((1,), (1,)), ((), ())), preferred_element_type=jnp.float32
        )
        sums = []
        for k in range(groups_here):
            skew = pltpu.roll(gram[k * rows:(k + 1) * rows], 0, 1, stride=1, stride_axis=0)
            sums.append(jnp.sum(skew, axis=0, keepdims=True))
        f_ref[pl.ds(pl.multiple_of(j * groups_here, groups_here), groups_here), :] = jnp.concatenate(sums, 0)
        return carry

    lax.fori_loop(0, sub, body, 0)


def gram_diag(back, top, bottom, *, group_size):
    rows, chans = back.shape
    block = min(BLOCK_LANES, chans)
    groups_block = block // group_size
    group_count = chans // group_size
    kernel = functools.partial(_gram_kernel, group_size=group_size, sub=block // LANES)
    return pl.pallas_call(
        kernel,
        grid=(chans // block,),
        in_specs=[
            pl.BlockSpec((rows, block), lambda b: (0, b)),
            pl.BlockSpec((rows, block), lambda b: (0, b)),
            pl.BlockSpec((rows, block), lambda b: (0, b)),
        ],
        out_specs=pl.BlockSpec((groups_block, 2 * rows), lambda b: (b, 0)),
        out_shape=jax.ShapeDtypeStruct((group_count, 2 * rows), jnp.float32),
        compiler_params=pltpu.CompilerParams(dimension_semantics=("parallel",)),
    )(back, top, bottom)


def gather_seq(value):
    count = lax.axis_size("seq")
    tiled = jnp.broadcast_to(value[None], (count,) + value.shape)
    return lax.all_to_all(tiled, "seq", split_axis=0, concat_axis=0, tiled=True)


def entering_states(gathered, decays, block_len, group_size, forward):
    count = gathered.shape[0]
    here = lax.axis_index("seq")
    rates = jnp.repeat(decays.T, group_size, axis=1)
    source = jnp.arange(count)
    if forward:
        gap = here - 1 - source
    else:
        gap = source - here - 1
    valid = gap >= 0
    steps = jnp.maximum(gap, 0).astype(jnp.float32)
    coef = jnp.exp(-rates[None] * (float(block_len) * steps)[:, None, None])
    coef = jnp.where(valid[:, None, None], coef, 0.0)
    return jnp.sum(coef * gathered, axis=0)


def on_device(
    query_mr,
    key_mr,
    value_mr,
    query_li,
    key_li,
    cotangent,
    mr_filter,
    norm_gain,
    li_decay,
    li_residue,
):
    row_count, chan_count = query_mr.shape
    group_count, tap_count = mr_filter.shape
    group_size = chan_count // group_count
    assert row_count == tap_count
    grad_scale = float(row_count * lax.axis_size("seq")) ** (-0.5)

    taps_mr = mr_filter.astype(jnp.bfloat16).astype(jnp.float32)
    zero_col = jnp.zeros((group_count, 1), jnp.float32)
    fwd_rows = jnp.concatenate(
        [zero_col, jnp.flip(taps_mr, 1), jnp.zeros((group_count, tap_count - 1), jnp.float32)], 1
    )
    bwd_rows = jnp.concatenate([taps_mr, jnp.zeros_like(taps_mr)], 1)

    mixed_mr = (key_mr.astype(jnp.float32) * value_mr.astype(jnp.float32)).astype(jnp.bfloat16)
    rim_rows = from_behind(mixed_mr, "seq", 1)
    conv_mr = band_conv(fwd_rows, rim_rows, mixed_mr, group_size=group_size, split=False, tri=None)
    out_mr = (query_mr.astype(jnp.float32) * conv_mr).astype(jnp.bfloat16)
    out_full = out_mr.astype(jnp.float32)
    squares = lax.psum(jnp.sum(out_full * out_full, axis=1), "chan")
    inv_rms = lax.rsqrt(squares / D + 1e-06)[:, None]
    normed = out_full * inv_rms * norm_gain
    mixed_li = key_li.astype(jnp.float32) * normed
    cotan_full = cotangent.astype(jnp.float32)
    back_li = cotan_full * query_li.astype(jnp.float32)

    offsets = jnp.arange(row_count, dtype=jnp.float32)
    weights_res = li_residue * jnp.sqrt(2.0 * li_decay)
    taps_li = jnp.einsum(
        "gr,grd->gd", weights_res, jnp.exp(-li_decay[:, :, None] * offsets), precision=HIGHEST
    )
    li_fwd_rows = jnp.concatenate([taps_li[:, :1], jnp.flip(taps_li[:, 1:], 1)], 1)
    fwd_states = jnp.exp(-li_decay[:, :, None] * (row_count - 1.0 - offsets)).astype(jnp.bfloat16)
    bwd_states = jnp.exp(-li_decay[:, :, None] * offsets).astype(jnp.bfloat16)

    back_li_bf = back_li.astype(jnp.bfloat16)
    mixed_li_bf = mixed_li.astype(jnp.bfloat16)
    modes = li_decay.shape[1]
    grad_st = modal_states(bwd_states, back_li_bf, group_size=group_size)
    conv_st = modal_states(fwd_states, mixed_li_bf, group_size=group_size)
    count = lax.axis_size("seq")
    later = (jnp.arange(count) > lax.axis_index("seq"))[:, None, None]
    outgoing = jnp.where(later, conv_st[None], grad_st[None])
    both_st = lax.all_to_all(outgoing, "seq", split_axis=0, concat_axis=0, tiled=True)
    both_st = both_st.astype(jnp.float32)
    grad_loc = band_conv(taps_li, back_li_bf, group_size=group_size, split=False, tri="upper")
    conv_loc = band_conv(li_fwd_rows, mixed_li_bf, group_size=group_size, split=False, tri="lower")
    both_st, grad_loc, conv_loc = lax.optimization_barrier((both_st, grad_loc, conv_loc))
    grad_ent = entering_states(both_st, li_decay, row_count, group_size, False)
    conv_ent = entering_states(both_st, li_decay, row_count, group_size, True)
    grad_mixed_li = modal_out(
        li_decay, weights_res, grad_ent, grad_loc, group_size=group_size, forward=False
    )
    out_li, grad_query_li = modal_out(
        li_decay, weights_res, conv_ent, conv_loc, (query_li, cotangent),
        group_size=group_size, forward=True,
    )

    grad_key_li = (grad_mixed_li * normed).astype(jnp.bfloat16)
    grad_normed = grad_mixed_li * key_li.astype(jnp.float32)
    gain_part = jnp.sum(grad_normed * out_full * inv_rms, axis=0)
    weighted = grad_normed * norm_gain
    cross_dots = lax.psum(jnp.sum(weighted * out_full, axis=1), "chan")[:, None]
    grad_out_mr = inv_rms * weighted - out_full * inv_rms**3 * cross_dots / D
    grad_query_mr = (grad_out_mr * conv_mr).astype(jnp.bfloat16)
    back_mr = (grad_out_mr * query_mr.astype(jnp.float32)).astype(jnp.bfloat16)
    after_rim = from_behind(back_mr, "seq", -1)
    grad_key_mr, grad_value_mr = band_conv(
        bwd_rows, back_mr, after_rim, scale_pair=(value_mr, key_mr),
        group_size=group_size, split=False, tri=None,
    )
    diag_sums = gram_diag(back_mr, rim_rows, mixed_mr, group_size=group_size)
    filter_part = jnp.flip(diag_sums[:, tap_count:], 1)
    packed = jnp.concatenate([gain_part, filter_part.reshape(-1)])
    packed, after_rim = lax.optimization_barrier((packed, after_rim))
    param_sums = jnp.sum(gather_seq(packed), axis=0) * grad_scale
    grad_gain = param_sums[:chan_count]
    grad_filter = param_sums[chan_count:].reshape(group_count, tap_count)
    return (
        out_li,
        grad_query_mr,
        grad_key_mr,
        grad_value_mr,
        grad_query_li,
        grad_key_li,
        grad_gain,
        grad_filter,
    )


def solution(mesh):
    in_specs = (
        P("seq", "chan"),
        P("seq", "chan"),
        P("seq", "chan"),
        P("seq", "chan"),
        P("seq", "chan"),
        P("seq", "chan"),
        P("chan", None),
        P("chan"),
        P("chan", None),
        P("chan", None),
    )
    out_specs = (
        P("seq", "chan"),
        P("seq", "chan"),
        P("seq", "chan"),
        P("seq", "chan"),
        P("seq", "chan"),
        P("seq", "chan"),
        P("chan"),
        P("chan", None),
    )
    return jax.shard_map(
        on_device, mesh=mesh, in_specs=in_specs, out_specs=out_specs, check_vma=False
    )
```

```python
import functools

import jax
import jax.numpy as jnp
from jax import lax
from jax.experimental import pallas as pl
from jax.experimental.pallas import tpu as pltpu
from jax.sharding import PartitionSpec as P

D = 8192
G = 512
LANES = 128
BLOCK_LANES = 512
HIGHEST = lax.Precision.HIGHEST


def from_behind(value, axis, steps):
    count = lax.axis_size(axis)
    initial, last = (max(0, -steps), min(count, count - steps))
    return lax.ppermute(value, axis, [(source, source + steps) for source in range(initial, last)])


def _split(value):
    high = value.astype(jnp.bfloat16)
    return high, (value - high.astype(jnp.float32)).astype(jnp.bfloat16)


def _band_kernel(*refs, group_size, split, tri, two_inputs, modal, sub, scaled):
    refs = list(refs)
    h_ref = refs.pop(0)
    top_ref = refs.pop(0)
    bot_ref = refs.pop(0) if two_inputs else None
    if modal is not None:
        dec_ref, wt_ref, ent_ref = refs.pop(0), refs.pop(0), refs.pop(0)
    if scaled:
        first_ref, second_ref = refs.pop(0), refs.pop(0)
    out_ref = refs.pop(0)
    if scaled:
        other_ref = refs.pop(0)
    rows = out_ref.shape[0]
    width = h_ref.shape[1]
    groups_here = LANES // group_size
    lane_group = lax.broadcasted_iota(jnp.int32, (rows, LANES), 1) // group_size
    row_id = lax.broadcasted_iota(jnp.int32, (rows, width), 0)
    col_id = lax.broadcasted_iota(jnp.int32, (rows, width), 1)
    if modal is not None:
        modes = dec_ref.shape[1]
        offsets = lax.broadcasted_iota(jnp.int32, (rows, modes), 0).astype(jnp.float32)
        dist = offsets + 1.0 if modal == "forward" else float(rows) - offsets

    def body(j, carry):
        lanes = pl.ds(pl.multiple_of(j * LANES, LANES), LANES)
        if two_inputs:
            x = jnp.concatenate([top_ref[:, lanes], bot_ref[:, lanes]], axis=0)
        else:
            x = top_ref[:, lanes]
        bands = []
        for k in range(groups_here):
            band_row = h_ref[pl.ds(j * groups_here + k, 1), :]
            band = pltpu.roll(jnp.broadcast_to(band_row, (rows, width)), 0, 1, stride=1, stride_axis=0)
            if tri == "lower":
                band = jnp.where(col_id <= row_id, band, 0.0)
            elif tri == "upper":
                band = jnp.where(col_id >= row_id, band, 0.0)
            bands.append(band)
        stacked = jnp.concatenate(bands, axis=0)
        if split:
            high, low = _split(stacked)
            y = jnp.dot(high, x, preferred_element_type=jnp.float32)
            y = y + jnp.dot(low, x, preferred_element_type=jnp.float32)
        else:
            y = jnp.dot(stacked.astype(jnp.bfloat16), x, preferred_element_type=jnp.float32)
        if modal is not None:
            ent_high, ent_low = _split(ent_ref[:, lanes])
            out_w = []
            for k in range(groups_here):
                rate = dec_ref[pl.ds(j * groups_here + k, 1), :]
                weight = wt_ref[pl.ds(j * groups_here + k, 1), :]
                out_w.append(weight * jnp.exp(-rate * dist))
            a_high, a_low = _split(jnp.concatenate(out_w, axis=0))
            y = y + jnp.dot(a_high, ent_high, preferred_element_type=jnp.float32)
            y = y + jnp.dot(a_low, ent_high, preferred_element_type=jnp.float32)
            y = y + jnp.dot(a_high, ent_low, preferred_element_type=jnp.float32)
        acc = y[:rows]
        for k in range(1, groups_here):
            acc = jnp.where(lane_group == k, y[k * rows:(k + 1) * rows], acc)
        if scaled:
            out_ref[:, lanes] = (acc * first_ref[:, lanes].astype(jnp.float32)).astype(out_ref.dtype)
            other_ref[:, lanes] = (acc * second_ref[:, lanes].astype(jnp.float32)).astype(other_ref.dtype)
        else:
            out_ref[:, lanes] = acc
        return carry

    lax.fori_loop(0, sub, body, 0)


def band_conv(
    band_rows, top, bottom=None, modal_args=None, scale_pair=None, *, group_size, split, tri, modal=None
):
    rows, chans = top.shape
    block = min(BLOCK_LANES, chans)
    groups_block = block // group_size
    width = band_rows.shape[1]
    two_inputs = bottom is not None
    in_specs = [
        pl.BlockSpec((groups_block, width), lambda b: (b, 0)),
        pl.BlockSpec((rows, block), lambda b: (0, b)),
    ]
    args = [band_rows, top]
    if two_inputs:
        in_specs.append(pl.BlockSpec((rows, block), lambda b: (0, b)))
        args.append(bottom)
    if modal is not None:
        decays, weights, entering = modal_args
        modes = decays.shape[1]
        in_specs += [
            pl.BlockSpec((groups_block, modes), lambda b: (b, 0)),
            pl.BlockSpec((groups_block, modes), lambda b: (b, 0)),
            pl.BlockSpec((modes, block), lambda b: (0, b)),
        ]
        args += [decays, weights, entering]
    scaled = scale_pair is not None
    out_specs = pl.BlockSpec((rows, block), lambda b: (0, b))
    out_shape = jax.ShapeDtypeStruct((rows, chans), jnp.float32)
    if scaled:
        in_specs += [pl.BlockSpec((rows, block), lambda b: (0, b))] * 2
        args += list(scale_pair)
        out_specs = [out_specs, out_specs]
        out_shape = [jax.ShapeDtypeStruct((rows, chans), jnp.bfloat16)] * 2
    kernel = functools.partial(
        _band_kernel,
        group_size=group_size,
        split=split,
        tri=tri,
        two_inputs=two_inputs,
        modal=modal,
        sub=block // LANES,
        scaled=scaled,
    )
    return pl.pallas_call(
        kernel,
        grid=(chans // block,),
        in_specs=in_specs,
        out_specs=out_specs,
        out_shape=out_shape,
        compiler_params=pltpu.CompilerParams(dimension_semantics=("parallel",)),
    )(*args)


def _state_kernel(e_ref, x_ref, s_ref, *, group_size, sub):
    modes = s_ref.shape[0]
    groups_here = LANES // group_size
    state_group = lax.broadcasted_iota(jnp.int32, (modes, LANES), 1) // group_size

    def body(j, carry):
        lanes = pl.ds(pl.multiple_of(j * LANES, LANES), LANES)
        x = x_ref[:, lanes]
        weights = e_ref[pl.ds(j * groups_here, groups_here)]
        stacked = weights.reshape(groups_here * modes, weights.shape[2]).astype(jnp.bfloat16)
        y = jnp.dot(stacked, x, preferred_element_type=jnp.float32)
        acc = y[:modes]
        for k in range(1, groups_here):
            acc = jnp.where(state_group == k, y[k * modes:(k + 1) * modes], acc)
        s_ref[:, lanes] = acc.astype(s_ref.dtype)
        return carry

    lax.fori_loop(0, sub, body, 0)


def modal_states(state_rows, x, *, group_size):
    rows, chans = x.shape
    block = min(BLOCK_LANES, chans)
    groups_block = block // group_size
    modes = state_rows.shape[1]
    kernel = functools.partial(_state_kernel, group_size=group_size, sub=block // LANES)
    return pl.pallas_call(
        kernel,
        grid=(chans // block,),
        in_specs=[
            pl.BlockSpec((groups_block, modes, rows), lambda b: (b, 0, 0)),
            pl.BlockSpec((rows, block), lambda b: (0, b)),
        ],
        out_specs=pl.BlockSpec((modes, block), lambda b: (0, b)),
        out_shape=jax.ShapeDtypeStruct((modes, chans), jnp.bfloat16),
        compiler_params=pltpu.CompilerParams(dimension_semantics=("parallel",)),
    )(state_rows, x)


def _modal_kernel(*refs, group_size, forward, sub, scaled):
    if scaled:
        dec_ref, wt_ref, ent_ref, loc_ref, first_ref, second_ref, out_ref, other_ref = refs
    else:
        dec_ref, wt_ref, ent_ref, loc_ref, out_ref = refs
    rows = out_ref.shape[0]
    modes = ent_ref.shape[0]
    groups_here = LANES // group_size
    width = groups_here * modes
    offsets = lax.broadcasted_iota(jnp.int32, (rows, width), 0).astype(jnp.float32)
    dist = offsets + 1.0 if forward else float(rows) - offsets
    row_group = lax.broadcasted_iota(jnp.int32, (width, LANES), 0) // modes
    lane_group = lax.broadcasted_iota(jnp.int32, (width, LANES), 1) // group_size

    def body(j, carry):
        lanes = pl.ds(pl.multiple_of(j * LANES, LANES), LANES)
        row = pl.program_id(0) * sub + j
        rate = dec_ref[pl.ds(row, 1), :]
        weight = wt_ref[pl.ds(row, 1), :]
        out_w = (weight * jnp.exp(-rate * dist)).astype(jnp.bfloat16)
        entering = ent_ref[:, lanes]
        tiled = jnp.concatenate([entering] * groups_here, axis=0)
        diag = jnp.where(row_group == lane_group, tiled, 0.0).astype(jnp.bfloat16)
        y = jnp.dot(out_w, diag, preferred_element_type=jnp.float32)
        total = loc_ref[:, lanes] + y
        if scaled:
            out_ref[:, lanes] = (total * first_ref[:, lanes].astype(jnp.float32)).astype(out_ref.dtype)
            other_ref[:, lanes] = (total * second_ref[:, lanes].astype(jnp.float32)).astype(other_ref.dtype)
        else:
            out_ref[:, lanes] = total
        return carry

    lax.fori_loop(0, sub, body, 0)


def modal_out(decays, weights, entering, local, scale_pair=None, *, group_size, forward):
    rows, chans = local.shape
    block = min(BLOCK_LANES, chans)
    groups_block = block // group_size
    modes = decays.shape[1]
    per_row = (LANES // group_size) * modes
    flat_decays = decays.reshape(-1, per_row)
    flat_weights = weights.reshape(-1, per_row)
    sub = block // LANES
    scaled = scale_pair is not None
    kernel = functools.partial(
        _modal_kernel, group_size=group_size, forward=forward, sub=sub, scaled=scaled
    )
    in_specs = [
        pl.BlockSpec(flat_decays.shape, lambda b: (0, 0)),
        pl.BlockSpec(flat_weights.shape, lambda b: (0, 0)),
        pl.BlockSpec((modes, block), lambda b: (0, b)),
        pl.BlockSpec((rows, block), lambda b: (0, b)),
    ]
    args = [flat_decays, flat_weights, entering, local]
    out_specs = pl.BlockSpec((rows, block), lambda b: (0, b))
    out_shape = jax.ShapeDtypeStruct((rows, chans), jnp.float32)
    if scaled:
        in_specs += [pl.BlockSpec((rows, block), lambda b: (0, b))] * 2
        args += list(scale_pair)
        out_specs = [out_specs, out_specs]
        out_shape = [jax.ShapeDtypeStruct((rows, chans), jnp.bfloat16)] * 2
    return pl.pallas_call(
        kernel,
        grid=(chans // block,),
        in_specs=in_specs,
        out_specs=out_specs,
        out_shape=out_shape,
        compiler_params=pltpu.CompilerParams(dimension_semantics=("parallel",)),
    )(*args)


def _gram_kernel(back_ref, top_ref, bot_ref, f_ref, *, group_size, sub):
    rows = back_ref.shape[0]
    groups_here = LANES // group_size
    r_id = lax.broadcasted_iota(jnp.int32, (rows, rows), 0)
    c_id = lax.broadcasted_iota(jnp.int32, (rows, rows), 1)
    exchange = jnp.where(r_id + c_id == rows - 1, 1.0, 0.0).astype(jnp.bfloat16)
    lane_group = lax.broadcasted_iota(jnp.int32, (rows, LANES), 1) // group_size

    def body(j, carry):
        lanes = pl.ds(pl.multiple_of(j * LANES, LANES), LANES)
        back = back_ref[:, lanes]
        x = jnp.concatenate([top_ref[:, lanes], bot_ref[:, lanes]], axis=0)
        back_rev = jnp.dot(exchange, back, preferred_element_type=jnp.float32).astype(jnp.bfloat16)
        masked = jnp.concatenate(
            [jnp.where(lane_group == k, back_rev, jnp.zeros_like(back_rev)) for k in range(groups_here)],
            axis=0,
        )
        gram = lax.dot_general(
            masked, x, (((1,), (1,)), ((), ())), preferred_element_type=jnp.float32
        )
        sums = []
        for k in range(groups_here):
            skew = pltpu.roll(gram[k * rows:(k + 1) * rows], 0, 1, stride=1, stride_axis=0)
            sums.append(jnp.sum(skew, axis=0, keepdims=True))
        f_ref[pl.ds(pl.multiple_of(j * groups_here, groups_here), groups_here), :] = jnp.concatenate(sums, 0)
        return carry

    lax.fori_loop(0, sub, body, 0)


def gram_diag(back, top, bottom, *, group_size):
    rows, chans = back.shape
    block = min(BLOCK_LANES, chans)
    groups_block = block // group_size
    group_count = chans // group_size
    kernel = functools.partial(_gram_kernel, group_size=group_size, sub=block // LANES)
    return pl.pallas_call(
        kernel,
        grid=(chans // block,),
        in_specs=[
            pl.BlockSpec((rows, block), lambda b: (0, b)),
            pl.BlockSpec((rows, block), lambda b: (0, b)),
            pl.BlockSpec((rows, block), lambda b: (0, b)),
        ],
        out_specs=pl.BlockSpec((groups_block, 2 * rows), lambda b: (b, 0)),
        out_shape=jax.ShapeDtypeStruct((group_count, 2 * rows), jnp.float32),
        compiler_params=pltpu.CompilerParams(dimension_semantics=("parallel",)),
    )(back, top, bottom)


def gather_seq(value):
    count = lax.axis_size("seq")
    tiled = jnp.broadcast_to(value[None], (count,) + value.shape)
    return lax.all_to_all(tiled, "seq", split_axis=0, concat_axis=0, tiled=True)


def entering_states(gathered, decays, block_len, group_size, forward):
    count = gathered.shape[0]
    here = lax.axis_index("seq")
    rates = jnp.repeat(decays.T, group_size, axis=1)
    source = jnp.arange(count)
    if forward:
        gap = here - 1 - source
    else:
        gap = source - here - 1
    valid = gap >= 0
    steps = jnp.maximum(gap, 0).astype(jnp.float32)
    coef = jnp.exp(-rates[None] * (float(block_len) * steps)[:, None, None])
    coef = jnp.where(valid[:, None, None], coef, 0.0)
    return jnp.sum(coef * gathered, axis=0)


def on_device(
    query_mr,
    key_mr,
    value_mr,
    query_li,
    key_li,
    cotangent,
    mr_filter,
    norm_gain,
    li_decay,
    li_residue,
):
    row_count, chan_count = query_mr.shape
    group_count, tap_count = mr_filter.shape
    group_size = chan_count // group_count
    assert row_count == tap_count
    grad_scale = float(row_count * lax.axis_size("seq")) ** (-0.5)

    taps_mr = mr_filter.astype(jnp.bfloat16).astype(jnp.float32)
    zero_col = jnp.zeros((group_count, 1), jnp.float32)
    fwd_rows = jnp.concatenate(
        [zero_col, jnp.flip(taps_mr, 1), jnp.zeros((group_count, tap_count - 1), jnp.float32)], 1
    )
    bwd_rows = jnp.concatenate([taps_mr, jnp.zeros_like(taps_mr)], 1)

    mixed_mr = (key_mr.astype(jnp.float32) * value_mr.astype(jnp.float32)).astype(jnp.bfloat16)
    rim_rows = from_behind(mixed_mr, "seq", 1)
    conv_mr = band_conv(fwd_rows, rim_rows, mixed_mr, group_size=group_size, split=False, tri=None)
    out_mr = (query_mr.astype(jnp.float32) * conv_mr).astype(jnp.bfloat16)
    out_full = out_mr.astype(jnp.float32)
    squares = lax.psum(jnp.sum(out_full * out_full, axis=1), "chan")
    inv_rms = lax.rsqrt(squares / D + 1e-06)[:, None]
    normed = out_full * inv_rms * norm_gain
    mixed_li = key_li.astype(jnp.float32) * normed
    cotan_full = cotangent.astype(jnp.float32)
    back_li = cotan_full * query_li.astype(jnp.float32)

    offsets = jnp.arange(row_count, dtype=jnp.float32)
    weights_res = li_residue * jnp.sqrt(2.0 * li_decay)
    taps_li = jnp.einsum(
        "gr,grd->gd", weights_res, jnp.exp(-li_decay[:, :, None] * offsets), precision=HIGHEST
    )
    li_fwd_rows = jnp.concatenate([taps_li[:, :1], jnp.flip(taps_li[:, 1:], 1)], 1)
    fwd_states = jnp.exp(-li_decay[:, :, None] * (row_count - 1.0 - offsets)).astype(jnp.bfloat16)
    bwd_states = jnp.exp(-li_decay[:, :, None] * offsets).astype(jnp.bfloat16)

    back_li_bf = back_li.astype(jnp.bfloat16)
    mixed_li_bf = mixed_li.astype(jnp.bfloat16)
    modes = li_decay.shape[1]
    grad_st = modal_states(bwd_states, back_li_bf, group_size=group_size)
    conv_st = modal_states(fwd_states, mixed_li_bf, group_size=group_size)
    count = lax.axis_size("seq")
    later = (jnp.arange(count) > lax.axis_index("seq"))[:, None, None]
    outgoing = jnp.where(later, conv_st[None], grad_st[None])
    both_st = lax.all_to_all(outgoing, "seq", split_axis=0, concat_axis=0, tiled=True)
    both_st = both_st.astype(jnp.float32)
    grad_loc = band_conv(taps_li, back_li_bf, group_size=group_size, split=False, tri="upper")
    conv_loc = band_conv(li_fwd_rows, mixed_li_bf, group_size=group_size, split=False, tri="lower")
    both_st, grad_loc, conv_loc = lax.optimization_barrier((both_st, grad_loc, conv_loc))
    grad_ent = entering_states(both_st, li_decay, row_count, group_size, False)
    conv_ent = entering_states(both_st, li_decay, row_count, group_size, True)
    grad_mixed_li = modal_out(
        li_decay, weights_res, grad_ent, grad_loc, group_size=group_size, forward=False
    )
    out_li, grad_query_li = modal_out(
        li_decay, weights_res, conv_ent, conv_loc, (query_li, cotangent),
        group_size=group_size, forward=True,
    )

    grad_key_li = (grad_mixed_li * normed).astype(jnp.bfloat16)
    grad_normed = grad_mixed_li * key_li.astype(jnp.float32)
    gain_part = jnp.sum(grad_normed * out_full * inv_rms, axis=0)
    weighted = grad_normed * norm_gain
    cross_dots = lax.psum(jnp.sum(weighted * out_full, axis=1), "chan")[:, None]
    grad_out_mr = inv_rms * weighted - out_full * inv_rms**3 * cross_dots / D
    grad_query_mr = (grad_out_mr * conv_mr).astype(jnp.bfloat16)
    back_mr = (grad_out_mr * query_mr.astype(jnp.float32)).astype(jnp.bfloat16)
    after_rim = from_behind(back_mr, "seq", -1)
    grad_key_mr, grad_value_mr = band_conv(
        bwd_rows, back_mr, after_rim, scale_pair=(value_mr, key_mr),
        group_size=group_size, split=False, tri=None,
    )
    diag_sums = gram_diag(back_mr, rim_rows, mixed_mr, group_size=group_size)
    filter_part = jnp.flip(diag_sums[:, tap_count:], 1)
    packed = jnp.concatenate([gain_part, filter_part.reshape(-1)])
    packed, after_rim = lax.optimization_barrier((packed, after_rim))
    gathered = gather_seq(packed.astype(jnp.bfloat16)).astype(jnp.float32)
    param_sums = jnp.sum(gathered, axis=0) * grad_scale
    grad_gain = param_sums[:chan_count]
    grad_filter = param_sums[chan_count:].reshape(group_count, tap_count)
    return (
        out_li,
        grad_query_mr,
        grad_key_mr,
        grad_value_mr,
        grad_query_li,
        grad_key_li,
        grad_gain,
        grad_filter,
    )


def solution(mesh):
    in_specs = (
        P("seq", "chan"),
        P("seq", "chan"),
        P("seq", "chan"),
        P("seq", "chan"),
        P("seq", "chan"),
        P("seq", "chan"),
        P("chan", None),
        P("chan"),
        P("chan", None),
        P("chan", None),
    )
    out_specs = (
        P("seq", "chan"),
        P("seq", "chan"),
        P("seq", "chan"),
        P("seq", "chan"),
        P("seq", "chan"),
        P("seq", "chan"),
        P("chan"),
        P("chan", None),
    )
    return jax.shard_map(
        on_device, mesh=mesh, in_specs=in_specs, out_specs=out_specs, check_vma=False
    )
```

```python
import functools

import jax
import jax.numpy as jnp
from jax import lax
from jax.experimental import pallas as pl
from jax.experimental.pallas import tpu as pltpu
from jax.sharding import PartitionSpec as P

D = 8192
G = 512
LANES = 128
BLOCK_LANES = 1024
HIGHEST = lax.Precision.HIGHEST


def from_behind(value, axis, steps):
    count = lax.axis_size(axis)
    initial, last = (max(0, -steps), min(count, count - steps))
    return lax.ppermute(value, axis, [(source, source + steps) for source in range(initial, last)])


def _split(value):
    high = value.astype(jnp.bfloat16)
    return high, (value - high.astype(jnp.float32)).astype(jnp.bfloat16)


def _band_kernel(*refs, group_size, split, tri, two_inputs, modal, sub, scaled):
    refs = list(refs)
    h_ref = refs.pop(0)
    top_ref = refs.pop(0)
    bot_ref = refs.pop(0) if two_inputs else None
    if modal is not None:
        dec_ref, wt_ref, ent_ref = refs.pop(0), refs.pop(0), refs.pop(0)
    if scaled:
        first_ref, second_ref = refs.pop(0), refs.pop(0)
    out_ref = refs.pop(0)
    if scaled:
        other_ref = refs.pop(0)
    rows = out_ref.shape[0]
    width = h_ref.shape[1]
    groups_here = LANES // group_size
    lane_group = lax.broadcasted_iota(jnp.int32, (rows, LANES), 1) // group_size
    row_id = lax.broadcasted_iota(jnp.int32, (rows, width), 0)
    col_id = lax.broadcasted_iota(jnp.int32, (rows, width), 1)
    if modal is not None:
        modes = dec_ref.shape[1]
        offsets = lax.broadcasted_iota(jnp.int32, (rows, modes), 0).astype(jnp.float32)
        dist = offsets + 1.0 if modal == "forward" else float(rows) - offsets

    def body(j, carry):
        lanes = pl.ds(pl.multiple_of(j * LANES, LANES), LANES)
        if two_inputs:
            x = jnp.concatenate([top_ref[:, lanes], bot_ref[:, lanes]], axis=0)
        else:
            x = top_ref[:, lanes]
        bands = []
        for k in range(groups_here):
            band_row = h_ref[pl.ds(j * groups_here + k, 1), :]
            band = pltpu.roll(jnp.broadcast_to(band_row, (rows, width)), 0, 1, stride=1, stride_axis=0)
            if tri == "lower":
                band = jnp.where(col_id <= row_id, band, 0.0)
            elif tri == "upper":
                band = jnp.where(col_id >= row_id, band, 0.0)
            bands.append(band)
        stacked = jnp.concatenate(bands, axis=0)
        if split:
            high, low = _split(stacked)
            y = jnp.dot(high, x, preferred_element_type=jnp.float32)
            y = y + jnp.dot(low, x, preferred_element_type=jnp.float32)
        else:
            y = jnp.dot(stacked.astype(jnp.bfloat16), x, preferred_element_type=jnp.float32)
        if modal is not None:
            ent_high, ent_low = _split(ent_ref[:, lanes])
            out_w = []
            for k in range(groups_here):
                rate = dec_ref[pl.ds(j * groups_here + k, 1), :]
                weight = wt_ref[pl.ds(j * groups_here + k, 1), :]
                out_w.append(weight * jnp.exp(-rate * dist))
            a_high, a_low = _split(jnp.concatenate(out_w, axis=0))
            y = y + jnp.dot(a_high, ent_high, preferred_element_type=jnp.float32)
            y = y + jnp.dot(a_low, ent_high, preferred_element_type=jnp.float32)
            y = y + jnp.dot(a_high, ent_low, preferred_element_type=jnp.float32)
        acc = y[:rows]
        for k in range(1, groups_here):
            acc = jnp.where(lane_group == k, y[k * rows:(k + 1) * rows], acc)
        if scaled:
            out_ref[:, lanes] = (acc * first_ref[:, lanes].astype(jnp.float32)).astype(out_ref.dtype)
            other_ref[:, lanes] = (acc * second_ref[:, lanes].astype(jnp.float32)).astype(other_ref.dtype)
        else:
            out_ref[:, lanes] = acc
        return carry

    lax.fori_loop(0, sub, body, 0)


def band_conv(
    band_rows, top, bottom=None, modal_args=None, scale_pair=None, *, group_size, split, tri, modal=None
):
    rows, chans = top.shape
    block = min(BLOCK_LANES, chans)
    groups_block = block // group_size
    width = band_rows.shape[1]
    two_inputs = bottom is not None
    in_specs = [
        pl.BlockSpec((groups_block, width), lambda b: (b, 0)),
        pl.BlockSpec((rows, block), lambda b: (0, b)),
    ]
    args = [band_rows, top]
    if two_inputs:
        in_specs.append(pl.BlockSpec((rows, block), lambda b: (0, b)))
        args.append(bottom)
    if modal is not None:
        decays, weights, entering = modal_args
        modes = decays.shape[1]
        in_specs += [
            pl.BlockSpec((groups_block, modes), lambda b: (b, 0)),
            pl.BlockSpec((groups_block, modes), lambda b: (b, 0)),
            pl.BlockSpec((modes, block), lambda b: (0, b)),
        ]
        args += [decays, weights, entering]
    scaled = scale_pair is not None
    out_specs = pl.BlockSpec((rows, block), lambda b: (0, b))
    out_shape = jax.ShapeDtypeStruct((rows, chans), jnp.float32)
    if scaled:
        in_specs += [pl.BlockSpec((rows, block), lambda b: (0, b))] * 2
        args += list(scale_pair)
        out_specs = [out_specs, out_specs]
        out_shape = [jax.ShapeDtypeStruct((rows, chans), jnp.bfloat16)] * 2
    kernel = functools.partial(
        _band_kernel,
        group_size=group_size,
        split=split,
        tri=tri,
        two_inputs=two_inputs,
        modal=modal,
        sub=block // LANES,
        scaled=scaled,
    )
    return pl.pallas_call(
        kernel,
        grid=(chans // block,),
        in_specs=in_specs,
        out_specs=out_specs,
        out_shape=out_shape,
        compiler_params=pltpu.CompilerParams(dimension_semantics=("parallel",)),
    )(*args)


def _state_kernel(e_ref, x_ref, s_ref, *, group_size, sub):
    modes = s_ref.shape[0]
    groups_here = LANES // group_size
    state_group = lax.broadcasted_iota(jnp.int32, (modes, LANES), 1) // group_size

    def body(j, carry):
        lanes = pl.ds(pl.multiple_of(j * LANES, LANES), LANES)
        x = x_ref[:, lanes]
        weights = e_ref[pl.ds(j * groups_here, groups_here)]
        stacked = weights.reshape(groups_here * modes, weights.shape[2]).astype(jnp.bfloat16)
        y = jnp.dot(stacked, x, preferred_element_type=jnp.float32)
        acc = y[:modes]
        for k in range(1, groups_here):
            acc = jnp.where(state_group == k, y[k * modes:(k + 1) * modes], acc)
        s_ref[:, lanes] = acc.astype(s_ref.dtype)
        return carry

    lax.fori_loop(0, sub, body, 0)


def modal_states(state_rows, x, *, group_size):
    rows, chans = x.shape
    block = min(BLOCK_LANES, chans)
    groups_block = block // group_size
    modes = state_rows.shape[1]
    kernel = functools.partial(_state_kernel, group_size=group_size, sub=block // LANES)
    return pl.pallas_call(
        kernel,
        grid=(chans // block,),
        in_specs=[
            pl.BlockSpec((groups_block, modes, rows), lambda b: (b, 0, 0)),
            pl.BlockSpec((rows, block), lambda b: (0, b)),
        ],
        out_specs=pl.BlockSpec((modes, block), lambda b: (0, b)),
        out_shape=jax.ShapeDtypeStruct((modes, chans), jnp.bfloat16),
        compiler_params=pltpu.CompilerParams(dimension_semantics=("parallel",)),
    )(state_rows, x)


def _modal_kernel(*refs, group_size, forward, sub, scaled):
    if scaled:
        dec_ref, wt_ref, ent_ref, loc_ref, first_ref, second_ref, out_ref, other_ref = refs
    else:
        dec_ref, wt_ref, ent_ref, loc_ref, out_ref = refs
    rows = out_ref.shape[0]
    modes = ent_ref.shape[0]
    groups_here = LANES // group_size
    width = groups_here * modes
    offsets = lax.broadcasted_iota(jnp.int32, (rows, width), 0).astype(jnp.float32)
    dist = offsets + 1.0 if forward else float(rows) - offsets
    row_group = lax.broadcasted_iota(jnp.int32, (width, LANES), 0) // modes
    lane_group = lax.broadcasted_iota(jnp.int32, (width, LANES), 1) // group_size

    def body(j, carry):
        lanes = pl.ds(pl.multiple_of(j * LANES, LANES), LANES)
        row = pl.program_id(0) * sub + j
        rate = dec_ref[pl.ds(row, 1), :]
        weight = wt_ref[pl.ds(row, 1), :]
        out_w = (weight * jnp.exp(-rate * dist)).astype(jnp.bfloat16)
        entering = ent_ref[:, lanes]
        tiled = jnp.concatenate([entering] * groups_here, axis=0)
        diag = jnp.where(row_group == lane_group, tiled, 0.0).astype(jnp.bfloat16)
        y = jnp.dot(out_w, diag, preferred_element_type=jnp.float32)
        total = loc_ref[:, lanes] + y
        if scaled:
            out_ref[:, lanes] = (total * first_ref[:, lanes].astype(jnp.float32)).astype(out_ref.dtype)
            other_ref[:, lanes] = (total * second_ref[:, lanes].astype(jnp.float32)).astype(other_ref.dtype)
        else:
            out_ref[:, lanes] = total
        return carry

    lax.fori_loop(0, sub, body, 0)


def modal_out(decays, weights, entering, local, scale_pair=None, *, group_size, forward):
    rows, chans = local.shape
    block = min(BLOCK_LANES, chans)
    groups_block = block // group_size
    modes = decays.shape[1]
    per_row = (LANES // group_size) * modes
    flat_decays = decays.reshape(-1, per_row)
    flat_weights = weights.reshape(-1, per_row)
    sub = block // LANES
    scaled = scale_pair is not None
    kernel = functools.partial(
        _modal_kernel, group_size=group_size, forward=forward, sub=sub, scaled=scaled
    )
    in_specs = [
        pl.BlockSpec(flat_decays.shape, lambda b: (0, 0)),
        pl.BlockSpec(flat_weights.shape, lambda b: (0, 0)),
        pl.BlockSpec((modes, block), lambda b: (0, b)),
        pl.BlockSpec((rows, block), lambda b: (0, b)),
    ]
    args = [flat_decays, flat_weights, entering, local]
    out_specs = pl.BlockSpec((rows, block), lambda b: (0, b))
    out_shape = jax.ShapeDtypeStruct((rows, chans), jnp.float32)
    if scaled:
        in_specs += [pl.BlockSpec((rows, block), lambda b: (0, b))] * 2
        args += list(scale_pair)
        out_specs = [out_specs, out_specs]
        out_shape = [jax.ShapeDtypeStruct((rows, chans), jnp.bfloat16)] * 2
    return pl.pallas_call(
        kernel,
        grid=(chans // block,),
        in_specs=in_specs,
        out_specs=out_specs,
        out_shape=out_shape,
        compiler_params=pltpu.CompilerParams(dimension_semantics=("parallel",)),
    )(*args)


def _gram_kernel(back_ref, top_ref, bot_ref, f_ref, *, group_size, sub):
    rows = back_ref.shape[0]
    groups_here = LANES // group_size
    r_id = lax.broadcasted_iota(jnp.int32, (rows, rows), 0)
    c_id = lax.broadcasted_iota(jnp.int32, (rows, rows), 1)
    exchange = jnp.where(r_id + c_id == rows - 1, 1.0, 0.0).astype(jnp.bfloat16)
    lane_group = lax.broadcasted_iota(jnp.int32, (rows, LANES), 1) // group_size

    def body(j, carry):
        lanes = pl.ds(pl.multiple_of(j * LANES, LANES), LANES)
        back = back_ref[:, lanes]
        x = jnp.concatenate([top_ref[:, lanes], bot_ref[:, lanes]], axis=0)
        back_rev = jnp.dot(exchange, back, preferred_element_type=jnp.float32).astype(jnp.bfloat16)
        masked = jnp.concatenate(
            [jnp.where(lane_group == k, back_rev, jnp.zeros_like(back_rev)) for k in range(groups_here)],
            axis=0,
        )
        gram = lax.dot_general(
            masked, x, (((1,), (1,)), ((), ())), preferred_element_type=jnp.float32
        )
        sums = []
        for k in range(groups_here):
            skew = pltpu.roll(gram[k * rows:(k + 1) * rows], 0, 1, stride=1, stride_axis=0)
            sums.append(jnp.sum(skew, axis=0, keepdims=True))
        f_ref[pl.ds(pl.multiple_of(j * groups_here, groups_here), groups_here), :] = jnp.concatenate(sums, 0)
        return carry

    lax.fori_loop(0, sub, body, 0)


def gram_diag(back, top, bottom, *, group_size):
    rows, chans = back.shape
    block = min(BLOCK_LANES, chans)
    groups_block = block // group_size
    group_count = chans // group_size
    kernel = functools.partial(_gram_kernel, group_size=group_size, sub=block // LANES)
    return pl.pallas_call(
        kernel,
        grid=(chans // block,),
        in_specs=[
            pl.BlockSpec((rows, block), lambda b: (0, b)),
            pl.BlockSpec((rows, block), lambda b: (0, b)),
            pl.BlockSpec((rows, block), lambda b: (0, b)),
        ],
        out_specs=pl.BlockSpec((groups_block, 2 * rows), lambda b: (b, 0)),
        out_shape=jax.ShapeDtypeStruct((group_count, 2 * rows), jnp.float32),
        compiler_params=pltpu.CompilerParams(dimension_semantics=("parallel",)),
    )(back, top, bottom)


def gather_seq(value):
    count = lax.axis_size("seq")
    tiled = jnp.broadcast_to(value[None], (count,) + value.shape)
    return lax.all_to_all(tiled, "seq", split_axis=0, concat_axis=0, tiled=True)


def entering_states(gathered, decays, block_len, group_size, forward):
    count = gathered.shape[0]
    here = lax.axis_index("seq")
    rates = jnp.repeat(decays.T, group_size, axis=1)
    source = jnp.arange(count)
    if forward:
        gap = here - 1 - source
    else:
        gap = source - here - 1
    valid = gap >= 0
    steps = jnp.maximum(gap, 0).astype(jnp.float32)
    coef = jnp.exp(-rates[None] * (float(block_len) * steps)[:, None, None])
    coef = jnp.where(valid[:, None, None], coef, 0.0)
    return jnp.sum(coef * gathered, axis=0)


def on_device(
    query_mr,
    key_mr,
    value_mr,
    query_li,
    key_li,
    cotangent,
    mr_filter,
    norm_gain,
    li_decay,
    li_residue,
):
    row_count, chan_count = query_mr.shape
    group_count, tap_count = mr_filter.shape
    group_size = chan_count // group_count
    assert row_count == tap_count
    grad_scale = float(row_count * lax.axis_size("seq")) ** (-0.5)

    taps_mr = mr_filter.astype(jnp.bfloat16).astype(jnp.float32)
    zero_col = jnp.zeros((group_count, 1), jnp.float32)
    fwd_rows = jnp.concatenate(
        [zero_col, jnp.flip(taps_mr, 1), jnp.zeros((group_count, tap_count - 1), jnp.float32)], 1
    )
    bwd_rows = jnp.concatenate([taps_mr, jnp.zeros_like(taps_mr)], 1)

    mixed_mr = (key_mr.astype(jnp.float32) * value_mr.astype(jnp.float32)).astype(jnp.bfloat16)
    rim_rows = from_behind(mixed_mr, "seq", 1)
    conv_mr = band_conv(fwd_rows, rim_rows, mixed_mr, group_size=group_size, split=False, tri=None)
    out_mr = (query_mr.astype(jnp.float32) * conv_mr).astype(jnp.bfloat16)
    out_full = out_mr.astype(jnp.float32)
    squares = lax.psum(jnp.sum(out_full * out_full, axis=1), "chan")
    inv_rms = lax.rsqrt(squares / D + 1e-06)[:, None]
    normed = out_full * inv_rms * norm_gain
    mixed_li = key_li.astype(jnp.float32) * normed
    cotan_full = cotangent.astype(jnp.float32)
    back_li = cotan_full * query_li.astype(jnp.float32)

    offsets = jnp.arange(row_count, dtype=jnp.float32)
    weights_res = li_residue * jnp.sqrt(2.0 * li_decay)
    taps_li = jnp.einsum(
        "gr,grd->gd", weights_res, jnp.exp(-li_decay[:, :, None] * offsets), precision=HIGHEST
    )
    li_fwd_rows = jnp.concatenate([taps_li[:, :1], jnp.flip(taps_li[:, 1:], 1)], 1)
    fwd_states = jnp.exp(-li_decay[:, :, None] * (row_count - 1.0 - offsets)).astype(jnp.bfloat16)
    bwd_states = jnp.exp(-li_decay[:, :, None] * offsets).astype(jnp.bfloat16)

    back_li_bf = back_li.astype(jnp.bfloat16)
    mixed_li_bf = mixed_li.astype(jnp.bfloat16)
    modes = li_decay.shape[1]
    grad_st = modal_states(bwd_states, back_li_bf, group_size=group_size)
    conv_st = modal_states(fwd_states, mixed_li_bf, group_size=group_size)
    count = lax.axis_size("seq")
    later = (jnp.arange(count) > lax.axis_index("seq"))[:, None, None]
    outgoing = jnp.where(later, conv_st[None], grad_st[None])
    both_st = lax.all_to_all(outgoing, "seq", split_axis=0, concat_axis=0, tiled=True)
    both_st = both_st.astype(jnp.float32)
    grad_loc = band_conv(taps_li, back_li_bf, group_size=group_size, split=False, tri="upper")
    conv_loc = band_conv(li_fwd_rows, mixed_li_bf, group_size=group_size, split=False, tri="lower")
    both_st, grad_loc, conv_loc = lax.optimization_barrier((both_st, grad_loc, conv_loc))
    grad_ent = entering_states(both_st, li_decay, row_count, group_size, False)
    conv_ent = entering_states(both_st, li_decay, row_count, group_size, True)
    grad_mixed_li = modal_out(
        li_decay, weights_res, grad_ent, grad_loc, group_size=group_size, forward=False
    )
    out_li, grad_query_li = modal_out(
        li_decay, weights_res, conv_ent, conv_loc, (query_li, cotangent),
        group_size=group_size, forward=True,
    )

    grad_key_li = (grad_mixed_li * normed).astype(jnp.bfloat16)
    grad_normed = grad_mixed_li * key_li.astype(jnp.float32)
    gain_part = jnp.sum(grad_normed * out_full * inv_rms, axis=0)
    weighted = grad_normed * norm_gain
    cross_dots = lax.psum(jnp.sum(weighted * out_full, axis=1), "chan")[:, None]
    grad_out_mr = inv_rms * weighted - out_full * inv_rms**3 * cross_dots / D
    grad_query_mr = (grad_out_mr * conv_mr).astype(jnp.bfloat16)
    back_mr = (grad_out_mr * query_mr.astype(jnp.float32)).astype(jnp.bfloat16)
    after_rim = from_behind(back_mr, "seq", -1)
    grad_key_mr, grad_value_mr = band_conv(
        bwd_rows, back_mr, after_rim, scale_pair=(value_mr, key_mr),
        group_size=group_size, split=False, tri=None,
    )
    diag_sums = gram_diag(back_mr, rim_rows, mixed_mr, group_size=group_size)
    filter_part = jnp.flip(diag_sums[:, tap_count:], 1)
    packed = jnp.concatenate([gain_part, filter_part.reshape(-1)])
    packed, after_rim = lax.optimization_barrier((packed, after_rim))
    param_sums = jnp.sum(gather_seq(packed), axis=0) * grad_scale
    grad_gain = param_sums[:chan_count]
    grad_filter = param_sums[chan_count:].reshape(group_count, tap_count)
    return (
        out_li,
        grad_query_mr,
        grad_key_mr,
        grad_value_mr,
        grad_query_li,
        grad_key_li,
        grad_gain,
        grad_filter,
    )


def solution(mesh):
    in_specs = (
        P("seq", "chan"),
        P("seq", "chan"),
        P("seq", "chan"),
        P("seq", "chan"),
        P("seq", "chan"),
        P("seq", "chan"),
        P("chan", None),
        P("chan"),
        P("chan", None),
        P("chan", None),
    )
    out_specs = (
        P("seq", "chan"),
        P("seq", "chan"),
        P("seq", "chan"),
        P("seq", "chan"),
        P("seq", "chan"),
        P("seq", "chan"),
        P("chan"),
        P("chan", None),
    )
    return jax.shard_map(
        on_device, mesh=mesh, in_specs=in_specs, out_specs=out_specs, check_vma=False
    )
```

```python
import functools

import jax
import jax.numpy as jnp
from jax import lax
from jax.experimental import pallas as pl
from jax.experimental.pallas import tpu as pltpu
from jax.sharding import PartitionSpec as P

D = 8192
G = 512
LANES = 128
BLOCK_LANES = 1024
HIGHEST = lax.Precision.HIGHEST


def from_behind(value, axis, steps):
    count = lax.axis_size(axis)
    initial, last = (max(0, -steps), min(count, count - steps))
    return lax.ppermute(value, axis, [(source, source + steps) for source in range(initial, last)])


def _split(value):
    high = value.astype(jnp.bfloat16)
    return high, (value - high.astype(jnp.float32)).astype(jnp.bfloat16)


def _band_kernel(*refs, group_size, split, tri, two_inputs, modal, sub, scaled, keep):
    refs = list(refs)
    h_ref = refs.pop(0)
    top_ref = refs.pop(0)
    bot_ref = refs.pop(0) if two_inputs else None
    if modal is not None:
        dec_ref, wt_ref, ent_ref = refs.pop(0), refs.pop(0), refs.pop(0)
    if scaled:
        first_ref, second_ref = refs.pop(0), refs.pop(0)
    if keep:
        first_ref = refs.pop(0)
    out_ref = refs.pop(0)
    if scaled or keep:
        other_ref = refs.pop(0)
    rows = out_ref.shape[0]
    width = h_ref.shape[1]
    groups_here = LANES // group_size
    lane_group = lax.broadcasted_iota(jnp.int32, (rows, LANES), 1) // group_size
    row_id = lax.broadcasted_iota(jnp.int32, (rows, width), 0)
    col_id = lax.broadcasted_iota(jnp.int32, (rows, width), 1)
    if modal is not None:
        modes = dec_ref.shape[1]
        offsets = lax.broadcasted_iota(jnp.int32, (rows, modes), 0).astype(jnp.float32)
        dist = offsets + 1.0 if modal == "forward" else float(rows) - offsets

    def body(j, carry):
        lanes = pl.ds(pl.multiple_of(j * LANES, LANES), LANES)
        if two_inputs:
            x = jnp.concatenate([top_ref[:, lanes], bot_ref[:, lanes]], axis=0)
        else:
            x = top_ref[:, lanes]
        bands = []
        for k in range(groups_here):
            band_row = h_ref[pl.ds(j * groups_here + k, 1), :]
            band = pltpu.roll(jnp.broadcast_to(band_row, (rows, width)), 0, 1, stride=1, stride_axis=0)
            if tri == "lower":
                band = jnp.where(col_id <= row_id, band, 0.0)
            elif tri == "upper":
                band = jnp.where(col_id >= row_id, band, 0.0)
            bands.append(band)
        stacked = jnp.concatenate(bands, axis=0)
        if split:
            high, low = _split(stacked)
            y = jnp.dot(high, x, preferred_element_type=jnp.float32)
            y = y + jnp.dot(low, x, preferred_element_type=jnp.float32)
        else:
            y = jnp.dot(stacked.astype(jnp.bfloat16), x, preferred_element_type=jnp.float32)
        if modal is not None:
            ent_high, ent_low = _split(ent_ref[:, lanes])
            out_w = []
            for k in range(groups_here):
                rate = dec_ref[pl.ds(j * groups_here + k, 1), :]
                weight = wt_ref[pl.ds(j * groups_here + k, 1), :]
                out_w.append(weight * jnp.exp(-rate * dist))
            a_high, a_low = _split(jnp.concatenate(out_w, axis=0))
            y = y + jnp.dot(a_high, ent_high, preferred_element_type=jnp.float32)
            y = y + jnp.dot(a_low, ent_high, preferred_element_type=jnp.float32)
            y = y + jnp.dot(a_high, ent_low, preferred_element_type=jnp.float32)
        acc = y[:rows]
        for k in range(1, groups_here):
            acc = jnp.where(lane_group == k, y[k * rows:(k + 1) * rows], acc)
        if scaled:
            out_ref[:, lanes] = (acc * first_ref[:, lanes].astype(jnp.float32)).astype(out_ref.dtype)
            other_ref[:, lanes] = (acc * second_ref[:, lanes].astype(jnp.float32)).astype(other_ref.dtype)
        elif keep:
            out_ref[:, lanes] = acc
            other_ref[:, lanes] = (acc * first_ref[:, lanes].astype(jnp.float32)).astype(other_ref.dtype)
        else:
            out_ref[:, lanes] = acc
        return carry

    lax.fori_loop(0, sub, body, 0)


def band_conv(
    band_rows, top, bottom=None, modal_args=None, scale_pair=None, gate=None,
    *, group_size, split, tri, modal=None
):
    rows, chans = top.shape
    block = min(BLOCK_LANES, chans)
    groups_block = block // group_size
    width = band_rows.shape[1]
    two_inputs = bottom is not None
    in_specs = [
        pl.BlockSpec((groups_block, width), lambda b: (b, 0)),
        pl.BlockSpec((rows, block), lambda b: (0, b)),
    ]
    args = [band_rows, top]
    if two_inputs:
        in_specs.append(pl.BlockSpec((rows, block), lambda b: (0, b)))
        args.append(bottom)
    if modal is not None:
        decays, weights, entering = modal_args
        modes = decays.shape[1]
        in_specs += [
            pl.BlockSpec((groups_block, modes), lambda b: (b, 0)),
            pl.BlockSpec((groups_block, modes), lambda b: (b, 0)),
            pl.BlockSpec((modes, block), lambda b: (0, b)),
        ]
        args += [decays, weights, entering]
    scaled = scale_pair is not None
    out_specs = pl.BlockSpec((rows, block), lambda b: (0, b))
    out_shape = jax.ShapeDtypeStruct((rows, chans), jnp.float32)
    if scaled:
        in_specs += [pl.BlockSpec((rows, block), lambda b: (0, b))] * 2
        args += list(scale_pair)
        out_specs = [out_specs, out_specs]
        out_shape = [jax.ShapeDtypeStruct((rows, chans), jnp.bfloat16)] * 2
    keep = gate is not None
    if keep:
        in_specs.append(pl.BlockSpec((rows, block), lambda b: (0, b)))
        args.append(gate)
        out_specs = [out_specs, out_specs]
        out_shape = [out_shape, jax.ShapeDtypeStruct((rows, chans), jnp.bfloat16)]
    kernel = functools.partial(
        _band_kernel,
        group_size=group_size,
        split=split,
        tri=tri,
        two_inputs=two_inputs,
        modal=modal,
        sub=block // LANES,
        scaled=scaled,
        keep=keep,
    )
    return pl.pallas_call(
        kernel,
        grid=(chans // block,),
        in_specs=in_specs,
        out_specs=out_specs,
        out_shape=out_shape,
        compiler_params=pltpu.CompilerParams(dimension_semantics=("parallel",)),
    )(*args)


def _state_kernel(e_ref, x_ref, s_ref, *, group_size, sub):
    modes = s_ref.shape[0]
    groups_here = LANES // group_size
    state_group = lax.broadcasted_iota(jnp.int32, (modes, LANES), 1) // group_size

    def body(j, carry):
        lanes = pl.ds(pl.multiple_of(j * LANES, LANES), LANES)
        x = x_ref[:, lanes]
        weights = e_ref[pl.ds(j * groups_here, groups_here)]
        stacked = weights.reshape(groups_here * modes, weights.shape[2]).astype(jnp.bfloat16)
        y = jnp.dot(stacked, x, preferred_element_type=jnp.float32)
        acc = y[:modes]
        for k in range(1, groups_here):
            acc = jnp.where(state_group == k, y[k * modes:(k + 1) * modes], acc)
        s_ref[:, lanes] = acc.astype(s_ref.dtype)
        return carry

    lax.fori_loop(0, sub, body, 0)


def modal_states(state_rows, x, *, group_size):
    rows, chans = x.shape
    block = min(BLOCK_LANES, chans)
    groups_block = block // group_size
    modes = state_rows.shape[1]
    kernel = functools.partial(_state_kernel, group_size=group_size, sub=block // LANES)
    return pl.pallas_call(
        kernel,
        grid=(chans // block,),
        in_specs=[
            pl.BlockSpec((groups_block, modes, rows), lambda b: (b, 0, 0)),
            pl.BlockSpec((rows, block), lambda b: (0, b)),
        ],
        out_specs=pl.BlockSpec((modes, block), lambda b: (0, b)),
        out_shape=jax.ShapeDtypeStruct((modes, chans), jnp.bfloat16),
        compiler_params=pltpu.CompilerParams(dimension_semantics=("parallel",)),
    )(state_rows, x)


def _modal_kernel(*refs, group_size, forward, sub, scaled):
    if scaled:
        dec_ref, wt_ref, ent_ref, loc_ref, first_ref, second_ref, out_ref, other_ref = refs
    else:
        dec_ref, wt_ref, ent_ref, loc_ref, out_ref = refs
    rows = out_ref.shape[0]
    modes = ent_ref.shape[0]
    groups_here = LANES // group_size
    width = groups_here * modes
    offsets = lax.broadcasted_iota(jnp.int32, (rows, width), 0).astype(jnp.float32)
    dist = offsets + 1.0 if forward else float(rows) - offsets
    row_group = lax.broadcasted_iota(jnp.int32, (width, LANES), 0) // modes
    lane_group = lax.broadcasted_iota(jnp.int32, (width, LANES), 1) // group_size

    def body(j, carry):
        lanes = pl.ds(pl.multiple_of(j * LANES, LANES), LANES)
        row = pl.program_id(0) * sub + j
        rate = dec_ref[pl.ds(row, 1), :]
        weight = wt_ref[pl.ds(row, 1), :]
        out_w = (weight * jnp.exp(-rate * dist)).astype(jnp.bfloat16)
        entering = ent_ref[:, lanes]
        tiled = jnp.concatenate([entering] * groups_here, axis=0)
        diag = jnp.where(row_group == lane_group, tiled, 0.0).astype(jnp.bfloat16)
        y = jnp.dot(out_w, diag, preferred_element_type=jnp.float32)
        total = loc_ref[:, lanes] + y
        if scaled:
            out_ref[:, lanes] = (total * first_ref[:, lanes].astype(jnp.float32)).astype(out_ref.dtype)
            other_ref[:, lanes] = (total * second_ref[:, lanes].astype(jnp.float32)).astype(other_ref.dtype)
        else:
            out_ref[:, lanes] = total
        return carry

    lax.fori_loop(0, sub, body, 0)


def modal_out(decays, weights, entering, local, scale_pair=None, *, group_size, forward):
    rows, chans = local.shape
    block = min(BLOCK_LANES, chans)
    groups_block = block // group_size
    modes = decays.shape[1]
    per_row = (LANES // group_size) * modes
    flat_decays = decays.reshape(-1, per_row)
    flat_weights = weights.reshape(-1, per_row)
    sub = block // LANES
    scaled = scale_pair is not None
    kernel = functools.partial(
        _modal_kernel, group_size=group_size, forward=forward, sub=sub, scaled=scaled
    )
    in_specs = [
        pl.BlockSpec(flat_decays.shape, lambda b: (0, 0)),
        pl.BlockSpec(flat_weights.shape, lambda b: (0, 0)),
        pl.BlockSpec((modes, block), lambda b: (0, b)),
        pl.BlockSpec((rows, block), lambda b: (0, b)),
    ]
    args = [flat_decays, flat_weights, entering, local]
    out_specs = pl.BlockSpec((rows, block), lambda b: (0, b))
    out_shape = jax.ShapeDtypeStruct((rows, chans), jnp.float32)
    if scaled:
        in_specs += [pl.BlockSpec((rows, block), lambda b: (0, b))] * 2
        args += list(scale_pair)
        out_specs = [out_specs, out_specs]
        out_shape = [jax.ShapeDtypeStruct((rows, chans), jnp.bfloat16)] * 2
    return pl.pallas_call(
        kernel,
        grid=(chans // block,),
        in_specs=in_specs,
        out_specs=out_specs,
        out_shape=out_shape,
        compiler_params=pltpu.CompilerParams(dimension_semantics=("parallel",)),
    )(*args)


def _gram_kernel(back_ref, top_ref, bot_ref, f_ref, *, group_size, sub):
    rows = back_ref.shape[0]
    groups_here = LANES // group_size
    r_id = lax.broadcasted_iota(jnp.int32, (rows, rows), 0)
    c_id = lax.broadcasted_iota(jnp.int32, (rows, rows), 1)
    exchange = jnp.where(r_id + c_id == rows - 1, 1.0, 0.0).astype(jnp.bfloat16)
    lane_group = lax.broadcasted_iota(jnp.int32, (rows, LANES), 1) // group_size

    def body(j, carry):
        lanes = pl.ds(pl.multiple_of(j * LANES, LANES), LANES)
        back = back_ref[:, lanes]
        x = jnp.concatenate([top_ref[:, lanes], bot_ref[:, lanes]], axis=0)
        back_rev = jnp.dot(exchange, back, preferred_element_type=jnp.float32).astype(jnp.bfloat16)
        masked = jnp.concatenate(
            [jnp.where(lane_group == k, back_rev, jnp.zeros_like(back_rev)) for k in range(groups_here)],
            axis=0,
        )
        gram = lax.dot_general(
            masked, x, (((1,), (1,)), ((), ())), preferred_element_type=jnp.float32
        )
        sums = []
        for k in range(groups_here):
            skew = pltpu.roll(gram[k * rows:(k + 1) * rows], 0, 1, stride=1, stride_axis=0)
            sums.append(jnp.sum(skew, axis=0, keepdims=True))
        f_ref[pl.ds(pl.multiple_of(j * groups_here, groups_here), groups_here), :] = jnp.concatenate(sums, 0)
        return carry

    lax.fori_loop(0, sub, body, 0)


def gram_diag(back, top, bottom, *, group_size):
    rows, chans = back.shape
    block = min(BLOCK_LANES, chans)
    groups_block = block // group_size
    group_count = chans // group_size
    kernel = functools.partial(_gram_kernel, group_size=group_size, sub=block // LANES)
    return pl.pallas_call(
        kernel,
        grid=(chans // block,),
        in_specs=[
            pl.BlockSpec((rows, block), lambda b: (0, b)),
            pl.BlockSpec((rows, block), lambda b: (0, b)),
            pl.BlockSpec((rows, block), lambda b: (0, b)),
        ],
        out_specs=pl.BlockSpec((groups_block, 2 * rows), lambda b: (b, 0)),
        out_shape=jax.ShapeDtypeStruct((group_count, 2 * rows), jnp.float32),
        compiler_params=pltpu.CompilerParams(dimension_semantics=("parallel",)),
    )(back, top, bottom)


def gather_seq(value):
    count = lax.axis_size("seq")
    tiled = jnp.broadcast_to(value[None], (count,) + value.shape)
    return lax.all_to_all(tiled, "seq", split_axis=0, concat_axis=0, tiled=True)


def entering_states(gathered, decays, block_len, group_size, forward):
    count = gathered.shape[0]
    here = lax.axis_index("seq")
    rates = jnp.repeat(decays.T, group_size, axis=1)
    source = jnp.arange(count)
    if forward:
        gap = here - 1 - source
    else:
        gap = source - here - 1
    valid = gap >= 0
    steps = jnp.maximum(gap, 0).astype(jnp.float32)
    coef = jnp.exp(-rates[None] * (float(block_len) * steps)[:, None, None])
    coef = jnp.where(valid[:, None, None], coef, 0.0)
    return jnp.sum(coef * gathered, axis=0)


def on_device(
    query_mr,
    key_mr,
    value_mr,
    query_li,
    key_li,
    cotangent,
    mr_filter,
    norm_gain,
    li_decay,
    li_residue,
):
    row_count, chan_count = query_mr.shape
    group_count, tap_count = mr_filter.shape
    group_size = chan_count // group_count
    assert row_count == tap_count
    grad_scale = float(row_count * lax.axis_size("seq")) ** (-0.5)

    taps_mr = mr_filter.astype(jnp.bfloat16).astype(jnp.float32)
    zero_col = jnp.zeros((group_count, 1), jnp.float32)
    fwd_rows = jnp.concatenate(
        [zero_col, jnp.flip(taps_mr, 1), jnp.zeros((group_count, tap_count - 1), jnp.float32)], 1
    )
    bwd_rows = jnp.concatenate([taps_mr, jnp.zeros_like(taps_mr)], 1)

    mixed_mr = (key_mr.astype(jnp.float32) * value_mr.astype(jnp.float32)).astype(jnp.bfloat16)
    rim_rows = from_behind(mixed_mr, "seq", 1)
    conv_mr, out_mr = band_conv(
        fwd_rows, rim_rows, mixed_mr, gate=query_mr, group_size=group_size, split=False, tri=None
    )
    out_full = out_mr.astype(jnp.float32)
    squares = lax.psum(jnp.sum(out_full * out_full, axis=1), "chan")
    inv_rms = lax.rsqrt(squares / D + 1e-06)[:, None]
    normed = out_full * inv_rms * norm_gain
    mixed_li = key_li.astype(jnp.float32) * normed
    cotan_full = cotangent.astype(jnp.float32)
    back_li = cotan_full * query_li.astype(jnp.float32)

    offsets = jnp.arange(row_count, dtype=jnp.float32)
    weights_res = li_residue * jnp.sqrt(2.0 * li_decay)
    taps_li = jnp.einsum(
        "gr,grd->gd", weights_res, jnp.exp(-li_decay[:, :, None] * offsets), precision=HIGHEST
    )
    li_fwd_rows = jnp.concatenate([taps_li[:, :1], jnp.flip(taps_li[:, 1:], 1)], 1)
    fwd_states = jnp.exp(-li_decay[:, :, None] * (row_count - 1.0 - offsets)).astype(jnp.bfloat16)
    bwd_states = jnp.exp(-li_decay[:, :, None] * offsets).astype(jnp.bfloat16)

    back_li_bf = back_li.astype(jnp.bfloat16)
    mixed_li_bf = mixed_li.astype(jnp.bfloat16)
    modes = li_decay.shape[1]
    grad_st = modal_states(bwd_states, back_li_bf, group_size=group_size)
    conv_st = modal_states(fwd_states, mixed_li_bf, group_size=group_size)
    count = lax.axis_size("seq")
    later = (jnp.arange(count) > lax.axis_index("seq"))[:, None, None]
    outgoing = jnp.where(later, conv_st[None], grad_st[None])
    both_st = lax.all_to_all(outgoing, "seq", split_axis=0, concat_axis=0, tiled=True)
    both_st = both_st.astype(jnp.float32)
    grad_loc = band_conv(taps_li, back_li_bf, group_size=group_size, split=False, tri="upper")
    conv_loc = band_conv(li_fwd_rows, mixed_li_bf, group_size=group_size, split=False, tri="lower")
    both_st, grad_loc, conv_loc = lax.optimization_barrier((both_st, grad_loc, conv_loc))
    grad_ent = entering_states(both_st, li_decay, row_count, group_size, False)
    conv_ent = entering_states(both_st, li_decay, row_count, group_size, True)
    grad_mixed_li = modal_out(
        li_decay, weights_res, grad_ent, grad_loc, group_size=group_size, forward=False
    )
    out_li, grad_query_li = modal_out(
        li_decay, weights_res, conv_ent, conv_loc, (query_li, cotangent),
        group_size=group_size, forward=True,
    )

    grad_key_li = (grad_mixed_li * normed).astype(jnp.bfloat16)
    grad_normed = grad_mixed_li * key_li.astype(jnp.float32)
    gain_part = jnp.sum(grad_normed * out_full * inv_rms, axis=0)
    weighted = grad_normed * norm_gain
    cross_dots = lax.psum(jnp.sum(weighted * out_full, axis=1), "chan")[:, None]
    grad_out_mr = inv_rms * weighted - out_full * inv_rms**3 * cross_dots / D
    grad_query_mr = (grad_out_mr * conv_mr).astype(jnp.bfloat16)
    back_mr = (grad_out_mr * query_mr.astype(jnp.float32)).astype(jnp.bfloat16)
    after_rim = from_behind(back_mr, "seq", -1)
    grad_key_mr, grad_value_mr = band_conv(
        bwd_rows, back_mr, after_rim, scale_pair=(value_mr, key_mr),
        group_size=group_size, split=False, tri=None,
    )
    diag_sums = gram_diag(back_mr, rim_rows, mixed_mr, group_size=group_size)
    filter_part = jnp.flip(diag_sums[:, tap_count:], 1)
    packed = jnp.concatenate([gain_part, filter_part.reshape(-1)])
    packed, after_rim = lax.optimization_barrier((packed, after_rim))
    param_sums = jnp.sum(gather_seq(packed), axis=0) * grad_scale
    grad_gain = param_sums[:chan_count]
    grad_filter = param_sums[chan_count:].reshape(group_count, tap_count)
    return (
        out_li,
        grad_query_mr,
        grad_key_mr,
        grad_value_mr,
        grad_query_li,
        grad_key_li,
        grad_gain,
        grad_filter,
    )


def solution(mesh):
    in_specs = (
        P("seq", "chan"),
        P("seq", "chan"),
        P("seq", "chan"),
        P("seq", "chan"),
        P("seq", "chan"),
        P("seq", "chan"),
        P("chan", None),
        P("chan"),
        P("chan", None),
        P("chan", None),
    )
    out_specs = (
        P("seq", "chan"),
        P("seq", "chan"),
        P("seq", "chan"),
        P("seq", "chan"),
        P("seq", "chan"),
        P("seq", "chan"),
        P("chan"),
        P("chan", None),
    )
    return jax.shard_map(
        on_device, mesh=mesh, in_specs=in_specs, out_specs=out_specs, check_vma=False
    )
```

```python
import functools

import jax
import jax.numpy as jnp
from jax import lax
from jax.experimental import pallas as pl
from jax.experimental.pallas import tpu as pltpu
from jax.sharding import PartitionSpec as P

D = 8192
G = 512
LANES = 128
BLOCK_LANES = 2048
HIGHEST = lax.Precision.HIGHEST


def from_behind(value, axis, steps):
    count = lax.axis_size(axis)
    initial, last = (max(0, -steps), min(count, count - steps))
    return lax.ppermute(value, axis, [(source, source + steps) for source in range(initial, last)])


def _split(value):
    high = value.astype(jnp.bfloat16)
    return high, (value - high.astype(jnp.float32)).astype(jnp.bfloat16)


def _band_kernel(*refs, group_size, split, tri, two_inputs, modal, sub, scaled):
    refs = list(refs)
    h_ref = refs.pop(0)
    top_ref = refs.pop(0)
    bot_ref = refs.pop(0) if two_inputs else None
    if modal is not None:
        dec_ref, wt_ref, ent_ref = refs.pop(0), refs.pop(0), refs.pop(0)
    if scaled:
        first_ref, second_ref = refs.pop(0), refs.pop(0)
    out_ref = refs.pop(0)
    if scaled:
        other_ref = refs.pop(0)
    rows = out_ref.shape[0]
    width = h_ref.shape[1]
    groups_here = LANES // group_size
    lane_group = lax.broadcasted_iota(jnp.int32, (rows, LANES), 1) // group_size
    row_id = lax.broadcasted_iota(jnp.int32, (rows, width), 0)
    col_id = lax.broadcasted_iota(jnp.int32, (rows, width), 1)
    if modal is not None:
        modes = dec_ref.shape[1]
        offsets = lax.broadcasted_iota(jnp.int32, (rows, modes), 0).astype(jnp.float32)
        dist = offsets + 1.0 if modal == "forward" else float(rows) - offsets

    def body(j, carry):
        lanes = pl.ds(pl.multiple_of(j * LANES, LANES), LANES)
        if two_inputs:
            x = jnp.concatenate([top_ref[:, lanes], bot_ref[:, lanes]], axis=0)
        else:
            x = top_ref[:, lanes]
        bands = []
        for k in range(groups_here):
            band_row = h_ref[pl.ds(j * groups_here + k, 1), :]
            band = pltpu.roll(jnp.broadcast_to(band_row, (rows, width)), 0, 1, stride=1, stride_axis=0)
            if tri == "lower":
                band = jnp.where(col_id <= row_id, band, 0.0)
            elif tri == "upper":
                band = jnp.where(col_id >= row_id, band, 0.0)
            bands.append(band)
        stacked = jnp.concatenate(bands, axis=0)
        if split:
            high, low = _split(stacked)
            y = jnp.dot(high, x, preferred_element_type=jnp.float32)
            y = y + jnp.dot(low, x, preferred_element_type=jnp.float32)
        else:
            y = jnp.dot(stacked.astype(jnp.bfloat16), x, preferred_element_type=jnp.float32)
        if modal is not None:
            ent_high, ent_low = _split(ent_ref[:, lanes])
            out_w = []
            for k in range(groups_here):
                rate = dec_ref[pl.ds(j * groups_here + k, 1), :]
                weight = wt_ref[pl.ds(j * groups_here + k, 1), :]
                out_w.append(weight * jnp.exp(-rate * dist))
            a_high, a_low = _split(jnp.concatenate(out_w, axis=0))
            y = y + jnp.dot(a_high, ent_high, preferred_element_type=jnp.float32)
            y = y + jnp.dot(a_low, ent_high, preferred_element_type=jnp.float32)
            y = y + jnp.dot(a_high, ent_low, preferred_element_type=jnp.float32)
        acc = y[:rows]
        for k in range(1, groups_here):
            acc = jnp.where(lane_group == k, y[k * rows:(k + 1) * rows], acc)
        if scaled:
            out_ref[:, lanes] = (acc * first_ref[:, lanes].astype(jnp.float32)).astype(out_ref.dtype)
            other_ref[:, lanes] = (acc * second_ref[:, lanes].astype(jnp.float32)).astype(other_ref.dtype)
        else:
            out_ref[:, lanes] = acc
        return carry

    lax.fori_loop(0, sub, body, 0)


def band_conv(
    band_rows, top, bottom=None, modal_args=None, scale_pair=None, *, group_size, split, tri, modal=None
):
    rows, chans = top.shape
    block = min(BLOCK_LANES, chans)
    groups_block = block // group_size
    width = band_rows.shape[1]
    two_inputs = bottom is not None
    in_specs = [
        pl.BlockSpec((groups_block, width), lambda b: (b, 0)),
        pl.BlockSpec((rows, block), lambda b: (0, b)),
    ]
    args = [band_rows, top]
    if two_inputs:
        in_specs.append(pl.BlockSpec((rows, block), lambda b: (0, b)))
        args.append(bottom)
    if modal is not None:
        decays, weights, entering = modal_args
        modes = decays.shape[1]
        in_specs += [
            pl.BlockSpec((groups_block, modes), lambda b: (b, 0)),
            pl.BlockSpec((groups_block, modes), lambda b: (b, 0)),
            pl.BlockSpec((modes, block), lambda b: (0, b)),
        ]
        args += [decays, weights, entering]
    scaled = scale_pair is not None
    out_specs = pl.BlockSpec((rows, block), lambda b: (0, b))
    out_shape = jax.ShapeDtypeStruct((rows, chans), jnp.float32)
    if scaled:
        in_specs += [pl.BlockSpec((rows, block), lambda b: (0, b))] * 2
        args += list(scale_pair)
        out_specs = [out_specs, out_specs]
        out_shape = [jax.ShapeDtypeStruct((rows, chans), jnp.bfloat16)] * 2
    kernel = functools.partial(
        _band_kernel,
        group_size=group_size,
        split=split,
        tri=tri,
        two_inputs=two_inputs,
        modal=modal,
        sub=block // LANES,
        scaled=scaled,
    )
    return pl.pallas_call(
        kernel,
        grid=(chans // block,),
        in_specs=in_specs,
        out_specs=out_specs,
        out_shape=out_shape,
        compiler_params=pltpu.CompilerParams(dimension_semantics=("parallel",)),
    )(*args)


def _state_kernel(e_ref, x_ref, s_ref, *, group_size, sub):
    modes = s_ref.shape[0]
    groups_here = LANES // group_size
    state_group = lax.broadcasted_iota(jnp.int32, (modes, LANES), 1) // group_size

    def body(j, carry):
        lanes = pl.ds(pl.multiple_of(j * LANES, LANES), LANES)
        x = x_ref[:, lanes]
        weights = e_ref[pl.ds(j * groups_here, groups_here)]
        stacked = weights.reshape(groups_here * modes, weights.shape[2]).astype(jnp.bfloat16)
        y = jnp.dot(stacked, x, preferred_element_type=jnp.float32)
        acc = y[:modes]
        for k in range(1, groups_here):
            acc = jnp.where(state_group == k, y[k * modes:(k + 1) * modes], acc)
        s_ref[:, lanes] = acc.astype(s_ref.dtype)
        return carry

    lax.fori_loop(0, sub, body, 0)


def modal_states(state_rows, x, *, group_size):
    rows, chans = x.shape
    block = min(BLOCK_LANES, chans)
    groups_block = block // group_size
    modes = state_rows.shape[1]
    kernel = functools.partial(_state_kernel, group_size=group_size, sub=block // LANES)
    return pl.pallas_call(
        kernel,
        grid=(chans // block,),
        in_specs=[
            pl.BlockSpec((groups_block, modes, rows), lambda b: (b, 0, 0)),
            pl.BlockSpec((rows, block), lambda b: (0, b)),
        ],
        out_specs=pl.BlockSpec((modes, block), lambda b: (0, b)),
        out_shape=jax.ShapeDtypeStruct((modes, chans), jnp.bfloat16),
        compiler_params=pltpu.CompilerParams(dimension_semantics=("parallel",)),
    )(state_rows, x)


def _modal_kernel(*refs, group_size, forward, sub, scaled):
    if scaled:
        dec_ref, wt_ref, ent_ref, loc_ref, first_ref, second_ref, out_ref, other_ref = refs
    else:
        dec_ref, wt_ref, ent_ref, loc_ref, out_ref = refs
    rows = out_ref.shape[0]
    modes = ent_ref.shape[0]
    groups_here = LANES // group_size
    width = groups_here * modes
    offsets = lax.broadcasted_iota(jnp.int32, (rows, width), 0).astype(jnp.float32)
    dist = offsets + 1.0 if forward else float(rows) - offsets
    row_group = lax.broadcasted_iota(jnp.int32, (width, LANES), 0) // modes
    lane_group = lax.broadcasted_iota(jnp.int32, (width, LANES), 1) // group_size

    def body(j, carry):
        lanes = pl.ds(pl.multiple_of(j * LANES, LANES), LANES)
        row = pl.program_id(0) * sub + j
        rate = dec_ref[pl.ds(row, 1), :]
        weight = wt_ref[pl.ds(row, 1), :]
        out_w = (weight * jnp.exp(-rate * dist)).astype(jnp.bfloat16)
        entering = ent_ref[:, lanes]
        tiled = jnp.concatenate([entering] * groups_here, axis=0)
        diag = jnp.where(row_group == lane_group, tiled, 0.0).astype(jnp.bfloat16)
        y = jnp.dot(out_w, diag, preferred_element_type=jnp.float32)
        total = loc_ref[:, lanes] + y
        if scaled:
            out_ref[:, lanes] = (total * first_ref[:, lanes].astype(jnp.float32)).astype(out_ref.dtype)
            other_ref[:, lanes] = (total * second_ref[:, lanes].astype(jnp.float32)).astype(other_ref.dtype)
        else:
            out_ref[:, lanes] = total
        return carry

    lax.fori_loop(0, sub, body, 0)


def modal_out(decays, weights, entering, local, scale_pair=None, *, group_size, forward):
    rows, chans = local.shape
    block = min(BLOCK_LANES, chans)
    groups_block = block // group_size
    modes = decays.shape[1]
    per_row = (LANES // group_size) * modes
    flat_decays = decays.reshape(-1, per_row)
    flat_weights = weights.reshape(-1, per_row)
    sub = block // LANES
    scaled = scale_pair is not None
    kernel = functools.partial(
        _modal_kernel, group_size=group_size, forward=forward, sub=sub, scaled=scaled
    )
    in_specs = [
        pl.BlockSpec(flat_decays.shape, lambda b: (0, 0)),
        pl.BlockSpec(flat_weights.shape, lambda b: (0, 0)),
        pl.BlockSpec((modes, block), lambda b: (0, b)),
        pl.BlockSpec((rows, block), lambda b: (0, b)),
    ]
    args = [flat_decays, flat_weights, entering, local]
    out_specs = pl.BlockSpec((rows, block), lambda b: (0, b))
    out_shape = jax.ShapeDtypeStruct((rows, chans), jnp.float32)
    if scaled:
        in_specs += [pl.BlockSpec((rows, block), lambda b: (0, b))] * 2
        args += list(scale_pair)
        out_specs = [out_specs, out_specs]
        out_shape = [jax.ShapeDtypeStruct((rows, chans), jnp.bfloat16)] * 2
    return pl.pallas_call(
        kernel,
        grid=(chans // block,),
        in_specs=in_specs,
        out_specs=out_specs,
        out_shape=out_shape,
        compiler_params=pltpu.CompilerParams(dimension_semantics=("parallel",)),
    )(*args)


def _gram_kernel(back_ref, top_ref, bot_ref, f_ref, *, group_size, sub):
    rows = back_ref.shape[0]
    groups_here = LANES // group_size
    r_id = lax.broadcasted_iota(jnp.int32, (rows, rows), 0)
    c_id = lax.broadcasted_iota(jnp.int32, (rows, rows), 1)
    exchange = jnp.where(r_id + c_id == rows - 1, 1.0, 0.0).astype(jnp.bfloat16)
    lane_group = lax.broadcasted_iota(jnp.int32, (rows, LANES), 1) // group_size

    def body(j, carry):
        lanes = pl.ds(pl.multiple_of(j * LANES, LANES), LANES)
        back = back_ref[:, lanes]
        x = jnp.concatenate([top_ref[:, lanes], bot_ref[:, lanes]], axis=0)
        back_rev = jnp.dot(exchange, back, preferred_element_type=jnp.float32).astype(jnp.bfloat16)
        masked = jnp.concatenate(
            [jnp.where(lane_group == k, back_rev, jnp.zeros_like(back_rev)) for k in range(groups_here)],
            axis=0,
        )
        gram = lax.dot_general(
            masked, x, (((1,), (1,)), ((), ())), preferred_element_type=jnp.float32
        )
        sums = []
        for k in range(groups_here):
            skew = pltpu.roll(gram[k * rows:(k + 1) * rows], 0, 1, stride=1, stride_axis=0)
            sums.append(jnp.sum(skew, axis=0, keepdims=True))
        f_ref[pl.ds(pl.multiple_of(j * groups_here, groups_here), groups_here), :] = jnp.concatenate(sums, 0)
        return carry

    lax.fori_loop(0, sub, body, 0)


def gram_diag(back, top, bottom, *, group_size):
    rows, chans = back.shape
    block = min(BLOCK_LANES, chans)
    groups_block = block // group_size
    group_count = chans // group_size
    kernel = functools.partial(_gram_kernel, group_size=group_size, sub=block // LANES)
    return pl.pallas_call(
        kernel,
        grid=(chans // block,),
        in_specs=[
            pl.BlockSpec((rows, block), lambda b: (0, b)),
            pl.BlockSpec((rows, block), lambda b: (0, b)),
            pl.BlockSpec((rows, block), lambda b: (0, b)),
        ],
        out_specs=pl.BlockSpec((groups_block, 2 * rows), lambda b: (b, 0)),
        out_shape=jax.ShapeDtypeStruct((group_count, 2 * rows), jnp.float32),
        compiler_params=pltpu.CompilerParams(dimension_semantics=("parallel",)),
    )(back, top, bottom)


def gather_seq(value):
    count = lax.axis_size("seq")
    tiled = jnp.broadcast_to(value[None], (count,) + value.shape)
    return lax.all_to_all(tiled, "seq", split_axis=0, concat_axis=0, tiled=True)


def entering_states(gathered, decays, block_len, group_size, forward):
    count = gathered.shape[0]
    here = lax.axis_index("seq")
    rates = jnp.repeat(decays.T, group_size, axis=1)
    source = jnp.arange(count)
    if forward:
        gap = here - 1 - source
    else:
        gap = source - here - 1
    valid = gap >= 0
    steps = jnp.maximum(gap, 0).astype(jnp.float32)
    coef = jnp.exp(-rates[None] * (float(block_len) * steps)[:, None, None])
    coef = jnp.where(valid[:, None, None], coef, 0.0)
    return jnp.sum(coef * gathered, axis=0)


def on_device(
    query_mr,
    key_mr,
    value_mr,
    query_li,
    key_li,
    cotangent,
    mr_filter,
    norm_gain,
    li_decay,
    li_residue,
):
    row_count, chan_count = query_mr.shape
    group_count, tap_count = mr_filter.shape
    group_size = chan_count // group_count
    assert row_count == tap_count
    grad_scale = float(row_count * lax.axis_size("seq")) ** (-0.5)

    taps_mr = mr_filter.astype(jnp.bfloat16).astype(jnp.float32)
    zero_col = jnp.zeros((group_count, 1), jnp.float32)
    fwd_rows = jnp.concatenate(
        [zero_col, jnp.flip(taps_mr, 1), jnp.zeros((group_count, tap_count - 1), jnp.float32)], 1
    )
    bwd_rows = jnp.concatenate([taps_mr, jnp.zeros_like(taps_mr)], 1)

    mixed_mr = (key_mr.astype(jnp.float32) * value_mr.astype(jnp.float32)).astype(jnp.bfloat16)
    rim_rows = from_behind(mixed_mr, "seq", 1)
    conv_mr = band_conv(fwd_rows, rim_rows, mixed_mr, group_size=group_size, split=False, tri=None)
    out_mr = (query_mr.astype(jnp.float32) * conv_mr).astype(jnp.bfloat16)
    out_full = out_mr.astype(jnp.float32)
    squares = lax.psum(jnp.sum(out_full * out_full, axis=1), "chan")
    inv_rms = lax.rsqrt(squares / D + 1e-06)[:, None]
    normed = out_full * inv_rms * norm_gain
    mixed_li = key_li.astype(jnp.float32) * normed
    cotan_full = cotangent.astype(jnp.float32)
    back_li = cotan_full * query_li.astype(jnp.float32)

    offsets = jnp.arange(row_count, dtype=jnp.float32)
    weights_res = li_residue * jnp.sqrt(2.0 * li_decay)
    taps_li = jnp.einsum(
        "gr,grd->gd", weights_res, jnp.exp(-li_decay[:, :, None] * offsets), precision=HIGHEST
    )
    li_fwd_rows = jnp.concatenate([taps_li[:, :1], jnp.flip(taps_li[:, 1:], 1)], 1)
    fwd_states = jnp.exp(-li_decay[:, :, None] * (row_count - 1.0 - offsets)).astype(jnp.bfloat16)
    bwd_states = jnp.exp(-li_decay[:, :, None] * offsets).astype(jnp.bfloat16)

    back_li_bf = back_li.astype(jnp.bfloat16)
    mixed_li_bf = mixed_li.astype(jnp.bfloat16)
    modes = li_decay.shape[1]
    grad_st = modal_states(bwd_states, back_li_bf, group_size=group_size)
    conv_st = modal_states(fwd_states, mixed_li_bf, group_size=group_size)
    count = lax.axis_size("seq")
    later = (jnp.arange(count) > lax.axis_index("seq"))[:, None, None]
    outgoing = jnp.where(later, conv_st[None], grad_st[None])
    both_st = lax.all_to_all(outgoing, "seq", split_axis=0, concat_axis=0, tiled=True)
    both_st = both_st.astype(jnp.float32)
    grad_loc = band_conv(taps_li, back_li_bf, group_size=group_size, split=False, tri="upper")
    conv_loc = band_conv(li_fwd_rows, mixed_li_bf, group_size=group_size, split=False, tri="lower")
    both_st, grad_loc, conv_loc = lax.optimization_barrier((both_st, grad_loc, conv_loc))
    grad_ent = entering_states(both_st, li_decay, row_count, group_size, False)
    conv_ent = entering_states(both_st, li_decay, row_count, group_size, True)
    grad_mixed_li = modal_out(
        li_decay, weights_res, grad_ent, grad_loc, group_size=group_size, forward=False
    )
    out_li, grad_query_li = modal_out(
        li_decay, weights_res, conv_ent, conv_loc, (query_li, cotangent),
        group_size=group_size, forward=True,
    )

    grad_key_li = (grad_mixed_li * normed).astype(jnp.bfloat16)
    grad_normed = grad_mixed_li * key_li.astype(jnp.float32)
    gain_part = jnp.sum(grad_normed * out_full * inv_rms, axis=0)
    weighted = grad_normed * norm_gain
    cross_dots = lax.psum(jnp.sum(weighted * out_full, axis=1), "chan")[:, None]
    grad_out_mr = inv_rms * weighted - out_full * inv_rms**3 * cross_dots / D
    grad_query_mr = (grad_out_mr * conv_mr).astype(jnp.bfloat16)
    back_mr = (grad_out_mr * query_mr.astype(jnp.float32)).astype(jnp.bfloat16)
    after_rim = from_behind(back_mr, "seq", -1)
    grad_key_mr, grad_value_mr = band_conv(
        bwd_rows, back_mr, after_rim, scale_pair=(value_mr, key_mr),
        group_size=group_size, split=False, tri=None,
    )
    diag_sums = gram_diag(back_mr, rim_rows, mixed_mr, group_size=group_size)
    filter_part = jnp.flip(diag_sums[:, tap_count:], 1)
    packed = jnp.concatenate([gain_part, filter_part.reshape(-1)])
    packed, after_rim = lax.optimization_barrier((packed, after_rim))
    param_sums = jnp.sum(gather_seq(packed), axis=0) * grad_scale
    grad_gain = param_sums[:chan_count]
    grad_filter = param_sums[chan_count:].reshape(group_count, tap_count)
    return (
        out_li,
        grad_query_mr,
        grad_key_mr,
        grad_value_mr,
        grad_query_li,
        grad_key_li,
        grad_gain,
        grad_filter,
    )


def solution(mesh):
    in_specs = (
        P("seq", "chan"),
        P("seq", "chan"),
        P("seq", "chan"),
        P("seq", "chan"),
        P("seq", "chan"),
        P("seq", "chan"),
        P("chan", None),
        P("chan"),
        P("chan", None),
        P("chan", None),
    )
    out_specs = (
        P("seq", "chan"),
        P("seq", "chan"),
        P("seq", "chan"),
        P("seq", "chan"),
        P("seq", "chan"),
        P("seq", "chan"),
        P("chan"),
        P("chan", None),
    )
    return jax.shard_map(
        on_device, mesh=mesh, in_specs=in_specs, out_specs=out_specs, check_vma=False
    )
```

```python
import functools

import jax
import jax.numpy as jnp
from jax import lax
from jax.experimental import pallas as pl
from jax.experimental.pallas import tpu as pltpu
from jax.sharding import PartitionSpec as P

D = 8192
G = 512
LANES = 128
BLOCK_LANES = 1024
HIGHEST = lax.Precision.HIGHEST


def from_behind(value, axis, steps):
    count = lax.axis_size(axis)
    initial, last = (max(0, -steps), min(count, count - steps))
    return lax.ppermute(value, axis, [(source, source + steps) for source in range(initial, last)])


def _split(value):
    high = value.astype(jnp.bfloat16)
    return high, (value - high.astype(jnp.float32)).astype(jnp.bfloat16)


def _band_kernel(*refs, group_size, split, tri, two_inputs, modal, sub, scaled):
    refs = list(refs)
    h_ref = refs.pop(0)
    top_ref = refs.pop(0)
    bot_ref = refs.pop(0) if two_inputs else None
    if modal is not None:
        dec_ref, wt_ref, ent_ref = refs.pop(0), refs.pop(0), refs.pop(0)
    if scaled:
        first_ref, second_ref = refs.pop(0), refs.pop(0)
    out_ref = refs.pop(0)
    if scaled:
        other_ref = refs.pop(0)
    rows = out_ref.shape[0]
    width = h_ref.shape[1]
    groups_here = LANES // group_size
    lane_group = lax.broadcasted_iota(jnp.int32, (rows, LANES), 1) // group_size
    row_id = lax.broadcasted_iota(jnp.int32, (rows, width), 0)
    col_id = lax.broadcasted_iota(jnp.int32, (rows, width), 1)
    if modal is not None:
        modes = dec_ref.shape[1]
        offsets = lax.broadcasted_iota(jnp.int32, (rows, modes), 0).astype(jnp.float32)
        dist = offsets + 1.0 if modal == "forward" else float(rows) - offsets

    def body(j, carry):
        lanes = pl.ds(pl.multiple_of(j * LANES, LANES), LANES)
        if two_inputs:
            x = jnp.concatenate([top_ref[:, lanes], bot_ref[:, lanes]], axis=0)
        else:
            x = top_ref[:, lanes]
        bands = []
        for k in range(groups_here):
            band_row = h_ref[pl.ds(j * groups_here + k, 1), :]
            band = pltpu.roll(jnp.broadcast_to(band_row, (rows, width)), 0, 1, stride=1, stride_axis=0)
            if tri == "lower":
                band = jnp.where(col_id <= row_id, band, 0.0)
            elif tri == "upper":
                band = jnp.where(col_id >= row_id, band, 0.0)
            bands.append(band)
        stacked = jnp.concatenate(bands, axis=0)
        if split:
            high, low = _split(stacked)
            y = jnp.dot(high, x, preferred_element_type=jnp.float32)
            y = y + jnp.dot(low, x, preferred_element_type=jnp.float32)
        else:
            y = jnp.dot(stacked.astype(jnp.bfloat16), x, preferred_element_type=jnp.float32)
        if modal is not None:
            ent_high, ent_low = _split(ent_ref[:, lanes])
            out_w = []
            for k in range(groups_here):
                rate = dec_ref[pl.ds(j * groups_here + k, 1), :]
                weight = wt_ref[pl.ds(j * groups_here + k, 1), :]
                out_w.append(weight * jnp.exp(-rate * dist))
            a_high, a_low = _split(jnp.concatenate(out_w, axis=0))
            y = y + jnp.dot(a_high, ent_high, preferred_element_type=jnp.float32)
            y = y + jnp.dot(a_low, ent_high, preferred_element_type=jnp.float32)
            y = y + jnp.dot(a_high, ent_low, preferred_element_type=jnp.float32)
        acc = y[:rows]
        for k in range(1, groups_here):
            acc = jnp.where(lane_group == k, y[k * rows:(k + 1) * rows], acc)
        if scaled:
            out_ref[:, lanes] = (acc * first_ref[:, lanes].astype(jnp.float32)).astype(out_ref.dtype)
            other_ref[:, lanes] = (acc * second_ref[:, lanes].astype(jnp.float32)).astype(other_ref.dtype)
        else:
            out_ref[:, lanes] = acc
        return carry

    lax.fori_loop(0, sub, body, 0)


def band_conv(
    band_rows, top, bottom=None, modal_args=None, scale_pair=None, *, group_size, split, tri, modal=None
):
    rows, chans = top.shape
    block = min(BLOCK_LANES, chans)
    groups_block = block // group_size
    width = band_rows.shape[1]
    two_inputs = bottom is not None
    in_specs = [
        pl.BlockSpec((groups_block, width), lambda b: (b, 0)),
        pl.BlockSpec((rows, block), lambda b: (0, b)),
    ]
    args = [band_rows, top]
    if two_inputs:
        in_specs.append(pl.BlockSpec((rows, block), lambda b: (0, b)))
        args.append(bottom)
    if modal is not None:
        decays, weights, entering = modal_args
        modes = decays.shape[1]
        in_specs += [
            pl.BlockSpec((groups_block, modes), lambda b: (b, 0)),
            pl.BlockSpec((groups_block, modes), lambda b: (b, 0)),
            pl.BlockSpec((modes, block), lambda b: (0, b)),
        ]
        args += [decays, weights, entering]
    scaled = scale_pair is not None
    out_specs = pl.BlockSpec((rows, block), lambda b: (0, b))
    out_shape = jax.ShapeDtypeStruct((rows, chans), jnp.float32)
    if scaled:
        in_specs += [pl.BlockSpec((rows, block), lambda b: (0, b))] * 2
        args += list(scale_pair)
        out_specs = [out_specs, out_specs]
        out_shape = [jax.ShapeDtypeStruct((rows, chans), jnp.bfloat16)] * 2
    kernel = functools.partial(
        _band_kernel,
        group_size=group_size,
        split=split,
        tri=tri,
        two_inputs=two_inputs,
        modal=modal,
        sub=block // LANES,
        scaled=scaled,
    )
    return pl.pallas_call(
        kernel,
        grid=(chans // block,),
        in_specs=in_specs,
        out_specs=out_specs,
        out_shape=out_shape,
        compiler_params=pltpu.CompilerParams(dimension_semantics=("parallel",)),
    )(*args)


def _state_kernel(e_ref, x_ref, s_ref, *, group_size, sub):
    modes = s_ref.shape[0]
    groups_here = LANES // group_size
    state_group = lax.broadcasted_iota(jnp.int32, (modes, LANES), 1) // group_size

    def body(j, carry):
        lanes = pl.ds(pl.multiple_of(j * LANES, LANES), LANES)
        x = x_ref[:, lanes]
        weights = e_ref[pl.ds(j * groups_here, groups_here)]
        stacked = weights.reshape(groups_here * modes, weights.shape[2]).astype(jnp.bfloat16)
        y = jnp.dot(stacked, x, preferred_element_type=jnp.float32)
        acc = y[:modes]
        for k in range(1, groups_here):
            acc = jnp.where(state_group == k, y[k * modes:(k + 1) * modes], acc)
        s_ref[:, lanes] = acc.astype(s_ref.dtype)
        return carry

    lax.fori_loop(0, sub, body, 0)


def modal_states(state_rows, x, *, group_size):
    rows, chans = x.shape
    block = min(BLOCK_LANES, chans)
    groups_block = block // group_size
    modes = state_rows.shape[1]
    kernel = functools.partial(_state_kernel, group_size=group_size, sub=block // LANES)
    return pl.pallas_call(
        kernel,
        grid=(chans // block,),
        in_specs=[
            pl.BlockSpec((groups_block, modes, rows), lambda b: (b, 0, 0)),
            pl.BlockSpec((rows, block), lambda b: (0, b)),
        ],
        out_specs=pl.BlockSpec((modes, block), lambda b: (0, b)),
        out_shape=jax.ShapeDtypeStruct((modes, chans), jnp.bfloat16),
        compiler_params=pltpu.CompilerParams(dimension_semantics=("parallel",)),
    )(state_rows, x)


def _modal_kernel(*refs, group_size, forward, sub, scaled):
    if scaled:
        dec_ref, wt_ref, ent_ref, loc_ref, first_ref, second_ref, out_ref, other_ref = refs
    else:
        dec_ref, wt_ref, ent_ref, loc_ref, out_ref = refs
    rows = out_ref.shape[0]
    modes = ent_ref.shape[0]
    groups_here = LANES // group_size
    width = groups_here * modes
    offsets = lax.broadcasted_iota(jnp.int32, (rows, width), 0).astype(jnp.float32)
    dist = offsets + 1.0 if forward else float(rows) - offsets
    row_group = lax.broadcasted_iota(jnp.int32, (width, LANES), 0) // modes
    lane_group = lax.broadcasted_iota(jnp.int32, (width, LANES), 1) // group_size

    def body(j, carry):
        lanes = pl.ds(pl.multiple_of(j * LANES, LANES), LANES)
        row = pl.program_id(0) * sub + j
        rate = dec_ref[pl.ds(row, 1), :]
        weight = wt_ref[pl.ds(row, 1), :]
        out_w = (weight * jnp.exp(-rate * dist)).astype(jnp.bfloat16)
        entering = ent_ref[:, lanes]
        tiled = jnp.concatenate([entering] * groups_here, axis=0)
        diag = jnp.where(row_group == lane_group, tiled, 0.0).astype(jnp.bfloat16)
        y = jnp.dot(out_w, diag, preferred_element_type=jnp.float32)
        total = loc_ref[:, lanes] + y
        if scaled:
            out_ref[:, lanes] = (total * first_ref[:, lanes].astype(jnp.float32)).astype(out_ref.dtype)
            other_ref[:, lanes] = (total * second_ref[:, lanes].astype(jnp.float32)).astype(other_ref.dtype)
        else:
            out_ref[:, lanes] = total
        return carry

    lax.fori_loop(0, sub, body, 0)


def modal_out(decays, weights, entering, local, scale_pair=None, *, group_size, forward):
    rows, chans = local.shape
    block = min(BLOCK_LANES, chans)
    groups_block = block // group_size
    modes = decays.shape[1]
    per_row = (LANES // group_size) * modes
    flat_decays = decays.reshape(-1, per_row)
    flat_weights = weights.reshape(-1, per_row)
    sub = block // LANES
    scaled = scale_pair is not None
    kernel = functools.partial(
        _modal_kernel, group_size=group_size, forward=forward, sub=sub, scaled=scaled
    )
    in_specs = [
        pl.BlockSpec(flat_decays.shape, lambda b: (0, 0)),
        pl.BlockSpec(flat_weights.shape, lambda b: (0, 0)),
        pl.BlockSpec((modes, block), lambda b: (0, b)),
        pl.BlockSpec((rows, block), lambda b: (0, b)),
    ]
    args = [flat_decays, flat_weights, entering, local]
    out_specs = pl.BlockSpec((rows, block), lambda b: (0, b))
    out_shape = jax.ShapeDtypeStruct((rows, chans), jnp.float32)
    if scaled:
        in_specs += [pl.BlockSpec((rows, block), lambda b: (0, b))] * 2
        args += list(scale_pair)
        out_specs = [out_specs, out_specs]
        out_shape = [jax.ShapeDtypeStruct((rows, chans), jnp.bfloat16)] * 2
    return pl.pallas_call(
        kernel,
        grid=(chans // block,),
        in_specs=in_specs,
        out_specs=out_specs,
        out_shape=out_shape,
        compiler_params=pltpu.CompilerParams(dimension_semantics=("parallel",)),
    )(*args)


def _gram_kernel(back_ref, top_ref, bot_ref, f_ref, *, group_size, sub):
    rows = back_ref.shape[0]
    groups_here = LANES // group_size
    r_id = lax.broadcasted_iota(jnp.int32, (rows, rows), 0)
    c_id = lax.broadcasted_iota(jnp.int32, (rows, rows), 1)
    exchange = jnp.where(r_id + c_id == rows - 1, 1.0, 0.0).astype(jnp.bfloat16)
    lane_group = lax.broadcasted_iota(jnp.int32, (rows, LANES), 1) // group_size

    def body(j, carry):
        lanes = pl.ds(pl.multiple_of(j * LANES, LANES), LANES)
        back = back_ref[:, lanes]
        x = jnp.concatenate([top_ref[:, lanes], bot_ref[:, lanes]], axis=0)
        back_rev = jnp.dot(exchange, back, preferred_element_type=jnp.float32).astype(jnp.bfloat16)
        masked = jnp.concatenate(
            [jnp.where(lane_group == k, back_rev, jnp.zeros_like(back_rev)) for k in range(groups_here)],
            axis=0,
        )
        gram = lax.dot_general(
            masked, x, (((1,), (1,)), ((), ())), preferred_element_type=jnp.float32
        )
        sums = []
        for k in range(groups_here):
            skew = pltpu.roll(gram[k * rows:(k + 1) * rows], 0, 1, stride=1, stride_axis=0)
            sums.append(jnp.sum(skew, axis=0, keepdims=True))
        f_ref[pl.ds(pl.multiple_of(j * groups_here, groups_here), groups_here), :] = jnp.concatenate(sums, 0)
        return carry

    lax.fori_loop(0, sub, body, 0)


def gram_diag(back, top, bottom, *, group_size):
    rows, chans = back.shape
    block = min(BLOCK_LANES, chans)
    groups_block = block // group_size
    group_count = chans // group_size
    kernel = functools.partial(_gram_kernel, group_size=group_size, sub=block // LANES)
    return pl.pallas_call(
        kernel,
        grid=(chans // block,),
        in_specs=[
            pl.BlockSpec((rows, block), lambda b: (0, b)),
            pl.BlockSpec((rows, block), lambda b: (0, b)),
            pl.BlockSpec((rows, block), lambda b: (0, b)),
        ],
        out_specs=pl.BlockSpec((groups_block, 2 * rows), lambda b: (b, 0)),
        out_shape=jax.ShapeDtypeStruct((group_count, 2 * rows), jnp.float32),
        compiler_params=pltpu.CompilerParams(dimension_semantics=("parallel",)),
    )(back, top, bottom)


def gather_seq(value):
    count = lax.axis_size("seq")
    tiled = jnp.broadcast_to(value[None], (count,) + value.shape)
    return lax.all_to_all(tiled, "seq", split_axis=0, concat_axis=0, tiled=True)


def entering_both(gathered, decays, block_len, group_size):
    count = gathered.shape[0]
    here = lax.axis_index("seq")
    rates = jnp.repeat(decays.T, group_size, axis=1)
    source = jnp.arange(count)
    steps = jnp.maximum(jnp.abs(here - source) - 1, 0).astype(jnp.float32)
    coef = jnp.exp(-rates[None] * (float(block_len) * steps)[:, None, None])
    weighted_states = coef * gathered
    earlier = (source < here)[:, None, None]
    later = (source > here)[:, None, None]
    forward = jnp.sum(jnp.where(earlier, weighted_states, 0.0), axis=0)
    backward = jnp.sum(jnp.where(later, weighted_states, 0.0), axis=0)
    return forward, backward


def on_device(
    query_mr,
    key_mr,
    value_mr,
    query_li,
    key_li,
    cotangent,
    mr_filter,
    norm_gain,
    li_decay,
    li_residue,
):
    row_count, chan_count = query_mr.shape
    group_count, tap_count = mr_filter.shape
    group_size = chan_count // group_count
    assert row_count == tap_count
    grad_scale = float(row_count * lax.axis_size("seq")) ** (-0.5)

    taps_mr = mr_filter.astype(jnp.bfloat16).astype(jnp.float32)
    zero_col = jnp.zeros((group_count, 1), jnp.float32)
    fwd_rows = jnp.concatenate(
        [zero_col, jnp.flip(taps_mr, 1), jnp.zeros((group_count, tap_count - 1), jnp.float32)], 1
    )
    bwd_rows = jnp.concatenate([taps_mr, jnp.zeros_like(taps_mr)], 1)

    mixed_mr = (key_mr.astype(jnp.float32) * value_mr.astype(jnp.float32)).astype(jnp.bfloat16)
    rim_rows = from_behind(mixed_mr, "seq", 1)
    conv_mr = band_conv(fwd_rows, rim_rows, mixed_mr, group_size=group_size, split=False, tri=None)
    out_mr = (query_mr.astype(jnp.float32) * conv_mr).astype(jnp.bfloat16)
    out_full = out_mr.astype(jnp.float32)
    squares = lax.psum(jnp.sum(out_full * out_full, axis=1), "chan")
    inv_rms = lax.rsqrt(squares / D + 1e-06)[:, None]
    normed = out_full * inv_rms * norm_gain
    mixed_li = key_li.astype(jnp.float32) * normed
    cotan_full = cotangent.astype(jnp.float32)
    back_li = cotan_full * query_li.astype(jnp.float32)

    offsets = jnp.arange(row_count, dtype=jnp.float32)
    weights_res = li_residue * jnp.sqrt(2.0 * li_decay)
    taps_li = jnp.einsum(
        "gr,grd->gd", weights_res, jnp.exp(-li_decay[:, :, None] * offsets), precision=HIGHEST
    )
    li_fwd_rows = jnp.concatenate([taps_li[:, :1], jnp.flip(taps_li[:, 1:], 1)], 1)
    fwd_states = jnp.exp(-li_decay[:, :, None] * (row_count - 1.0 - offsets)).astype(jnp.bfloat16)
    bwd_states = jnp.exp(-li_decay[:, :, None] * offsets).astype(jnp.bfloat16)

    back_li_bf = back_li.astype(jnp.bfloat16)
    mixed_li_bf = mixed_li.astype(jnp.bfloat16)
    modes = li_decay.shape[1]
    grad_st = modal_states(bwd_states, back_li_bf, group_size=group_size)
    conv_st = modal_states(fwd_states, mixed_li_bf, group_size=group_size)
    count = lax.axis_size("seq")
    later = (jnp.arange(count) > lax.axis_index("seq"))[:, None, None]
    outgoing = jnp.where(later, conv_st[None], grad_st[None])
    both_st = lax.all_to_all(outgoing, "seq", split_axis=0, concat_axis=0, tiled=True)
    both_st = both_st.astype(jnp.float32)
    grad_loc = band_conv(taps_li, back_li_bf, group_size=group_size, split=False, tri="upper")
    conv_loc = band_conv(li_fwd_rows, mixed_li_bf, group_size=group_size, split=False, tri="lower")
    both_st, grad_loc, conv_loc = lax.optimization_barrier((both_st, grad_loc, conv_loc))
    conv_ent, grad_ent = entering_both(both_st, li_decay, row_count, group_size)
    grad_mixed_li = modal_out(
        li_decay, weights_res, grad_ent, grad_loc, group_size=group_size, forward=False
    )
    out_li, grad_query_li = modal_out(
        li_decay, weights_res, conv_ent, conv_loc, (query_li, cotangent),
        group_size=group_size, forward=True,
    )

    grad_key_li = (grad_mixed_li * normed).astype(jnp.bfloat16)
    grad_normed = grad_mixed_li * key_li.astype(jnp.float32)
    gain_part = jnp.sum(grad_normed * out_full * inv_rms, axis=0)
    weighted = grad_normed * norm_gain
    cross_dots = lax.psum(jnp.sum(weighted * out_full, axis=1), "chan")[:, None]
    grad_out_mr = inv_rms * weighted - out_full * inv_rms**3 * cross_dots / D
    grad_query_mr = (grad_out_mr * conv_mr).astype(jnp.bfloat16)
    back_mr = (grad_out_mr * query_mr.astype(jnp.float32)).astype(jnp.bfloat16)
    after_rim = from_behind(back_mr, "seq", -1)
    grad_key_mr, grad_value_mr = band_conv(
        bwd_rows, back_mr, after_rim, scale_pair=(value_mr, key_mr),
        group_size=group_size, split=False, tri=None,
    )
    diag_sums = gram_diag(back_mr, rim_rows, mixed_mr, group_size=group_size)
    filter_part = jnp.flip(diag_sums[:, tap_count:], 1)
    packed = jnp.concatenate([gain_part, filter_part.reshape(-1)])
    packed, after_rim = lax.optimization_barrier((packed, after_rim))
    param_sums = jnp.sum(gather_seq(packed), axis=0) * grad_scale
    grad_gain = param_sums[:chan_count]
    grad_filter = param_sums[chan_count:].reshape(group_count, tap_count)
    return (
        out_li,
        grad_query_mr,
        grad_key_mr,
        grad_value_mr,
        grad_query_li,
        grad_key_li,
        grad_gain,
        grad_filter,
    )


def solution(mesh):
    in_specs = (
        P("seq", "chan"),
        P("seq", "chan"),
        P("seq", "chan"),
        P("seq", "chan"),
        P("seq", "chan"),
        P("seq", "chan"),
        P("chan", None),
        P("chan"),
        P("chan", None),
        P("chan", None),
    )
    out_specs = (
        P("seq", "chan"),
        P("seq", "chan"),
        P("seq", "chan"),
        P("seq", "chan"),
        P("seq", "chan"),
        P("seq", "chan"),
        P("chan"),
        P("chan", None),
    )
    return jax.shard_map(
        on_device, mesh=mesh, in_specs=in_specs, out_specs=out_specs, check_vma=False
    )
```
